32 devices in a mesh: batch: 4 (over z), seq: 8 (over y, x, core).
Axes of the slice: x: 2, y: 2, z: 4, core: 2. Of those that a mesh axis runs over, the one named last changes fastest.
Arguments:
- block_input: bfloat16 [16384, 768], P(('batch', 'seq')), may hold values from -6 to 6
- history: bfloat16 [8, 16384, 768], P(None, ('batch', 'seq')), may hold values from -6 to 6
- cotangent: bfloat16 [16384, 768], P(('batch', 'seq')), may hold values from -6 to 6
- qkv_weight: bfloat16 [768, 2304], P('batch', 'seq'), may hold values from -0.21875 to 0.21875
- proj_weight: bfloat16 [768, 768], P('batch', 'seq'), may hold values from -1.25 to 1.25
- up_weight: bfloat16 [768, 3072], P('batch', 'seq'), may hold values from -0.21875 to 0.21875
- down_weight: bfloat16 [3072, 768], P('batch', 'seq'), may hold values from -0.109375 to 0.109375
- norm1_gain: float32 [768], replicated, may hold values from 0.5 to 1.5
- norm1_bias: float32 [768], replicated, may hold values from -1.2 to 1.2
- norm2_gain: float32 [768], replicated, may hold values from 0.5 to 1.5
- norm2_bias: float32 [768], replicated, may hold values from -1.2 to 1.2
- dwa_weights: float32 [9], replicated, may hold values from 0.3 to 1
- pair_order: int32 [4, 24], P('batch'), may hold values from 0 to 23, each once within a row
- long_group: int32 [4, 2], P('batch'), may hold values from 0 to 2
Outputs:
- block_output: bfloat16 [16384, 768], P(('batch', 'seq'))
- input_grad: bfloat16 [16384, 768], P(('batch', 'seq'))
- history_grad: bfloat16 [8, 16384, 768], P(None, ('batch', 'seq'))
- row_lse: float32 [4, 24, 2048], P('batch', 'seq')
- qkv_grad: float32 [768, 2304], P('batch', 'seq')
- proj_grad: float32 [768, 768], P('batch', 'seq')
- up_grad: float32 [768, 3072], P('batch', 'seq')
- down_grad: float32 [3072, 768], P('batch', 'seq')
- norm1_gain_grad: float32 [768], replicated
- norm1_bias_grad: float32 [768], replicated
- norm2_gain_grad: float32 [768], replicated
- norm2_bias_grad: float32 [768], replicated
- dwa_grad: float32 [9], replicated
The draws below stay inside these ranges and needn't reach their ends.
Inputs may be any that keep to these rules, and one draw needn't show every extreme that they name: `pair_order`: each row lists each of its group's 24 pairs once. `long_group`: an entry v: that slot holds 2^v sequences of 2048 // 2^v tokens.
All inputs are finite; a program needn't handle non-finite values.
Results may differ from the reference program's by a relative error of at most 0.017.
Values may be sent and summed in bfloat16 or wider, within the bound.
No kernel may reach another device: no remote copies, remote signals or barrier semaphores. Data moves between devices by JAX's collectives and lax.ppermute only.
A program may use at most 192 MiB of HBM per device.

```python
import jax
import jax.numpy as jnp
from jax import lax

D = 768
HEADS = 12
HD = 64
FF = 3072
SLOT = 2048
HIST = 8
GROUP_ROWS = 4096
TOKENS = 16384
SPAN = 256
SLOTS = 2
PAIRS = 24
N_BATCH = 4
N_SEQ = 8


def touch_ends(values, own_key, smallest, high):
    longest = values.shape.index(max(values.shape))
    spots = []
    for shift in (0, 1):
        where = [jax.random.randint(jax.random.fold_in(own_key, axis), (), 0, length) for axis, length in enumerate(values.shape)]
        where[longest] = (where[longest] + shift) % values.shape[longest]
        spots.append(tuple(where))
    return values.at[spots[0]].set(smallest).at[spots[1]].set(high)


def levels(stream_key, shape, split, smallest, top_value):
    level, own = 1.0, jax.random.fold_in(stream_key, 6)
    for axis_at, blocks in split:
        heights = jnp.exp(jax.random.uniform(jax.random.fold_in(own, axis_at), (blocks,), jnp.float32, smallest / len(split), top_value / len(split)))
        level = level * jnp.repeat(heights, shape[axis_at] // blocks).reshape([-1 if axis == axis_at else 1 for axis in range(len(shape))])
    return level


def normal_values(stream_key, dims, spread, reach, shards=(), kind=jnp.bfloat16):
    result = spread * jax.random.normal(stream_key, dims, jnp.float32)
    if shards:
        result = result * levels(stream_key, dims, shards, -0.22, 0.18)
    return jnp.clip(result, -reach, reach).astype(kind)


def setup_inputs(seed: int = 0) -> dict:
    arg_keys = jax.random.split(jax.random.key(seed), 15)
    return {
        "block_input": normal_values(arg_keys[0], (TOKENS, D), 1.0, 6.0, ((0, 32),)),
        "history": normal_values(arg_keys[1], (HIST, TOKENS, D), 1.0, 6.0, ((1, 32),)),
        "cotangent": normal_values(arg_keys[2], (TOKENS, D), 1.0, 6.0, ((0, 32),)),
        "qkv_weight": normal_values(arg_keys[3], (D, 3 * D), D ** -0.5, 0.21875, ((0, 4), (1, 8))),
        "proj_weight": normal_values(arg_keys[4], (D, D), (D // 32) ** -0.5, 1.25, ((0, 4), (1, 8))),
        "up_weight": normal_values(arg_keys[5], (D, FF), D ** -0.5, 0.21875, ((0, 4), (1, 8))),
        "down_weight": normal_values(arg_keys[6], (FF, D), FF ** -0.5, 0.109375, ((0, 4), (1, 8))),
        "norm1_gain": jnp.clip(1.0 + 0.1 * jax.random.normal(arg_keys[7], (D,), jnp.float32), 0.5, 1.5),
        "norm1_bias": normal_values(arg_keys[8], (D,), 0.2, 1.2, (), jnp.float32),
        "norm2_gain": jnp.clip(1.0 + 0.1 * jax.random.normal(arg_keys[9], (D,), jnp.float32), 0.5, 1.5),
        "norm2_bias": normal_values(arg_keys[10], (D,), 0.2, 1.2, (), jnp.float32),
        "dwa_weights": jnp.clip(jax.random.uniform(arg_keys[11], (HIST + 1,), jnp.float32, 0.3, 1.0), 0.3, 1.0),
        "pair_order": jax.vmap(lambda own: jax.random.permutation(own, PAIRS))(jax.random.split(arg_keys[12], N_BATCH)).reshape((N_BATCH, PAIRS)).astype(jnp.int32),
        "long_group": touch_ends(jax.random.randint(arg_keys[13], (N_BATCH, SLOTS), 0, 3), jax.random.fold_in(arg_keys[13], 1), 0, 2).astype(jnp.int32),
    }


@jax.custom_vjp
def low(v):
    return lax.optimization_barrier(v.astype(jnp.bfloat16)).astype(jnp.float32)

@jax.custom_vjp
def low_back(v):
    return v

def low_keep(v):
    return (low(v), None)

def low_pass(kept, grad):
    return (grad,)

def back_keep(v):
    return (v, None)

def back_low(kept, grad):
    return (low(grad),)
low.defvjp(low_keep, low_pass)
low_back.defvjp(back_keep, back_low)
NORM_EPS = 1e-05
MASKED = -1e+30
PRECISE = lax.Precision.HIGHEST

def norm_rows(values, gain, shift):
    row_mean = lax.optimization_barrier(jnp.mean(values, axis=-1, keepdims=True))
    centred = values - row_mean
    variance = lax.optimization_barrier(jnp.mean(centred * centred, axis=-1, keepdims=True))
    return centred * lax.rsqrt(variance + NORM_EPS) * gain + shift

def rotate(values, cosine, sine_tab):
    half_size = values.shape[-1] // 2
    front = values[..., :half_size]
    behind = values[..., half_size:]
    cos_part = cosine[..., None, :]
    sin_part = sine_tab[..., None, :]
    return jnp.concatenate([front * cos_part - behind * sin_part, behind * cos_part + front * sin_part], axis=-1)

def to_slots(values):
    lead = values.shape[:-2]
    split_rows = values.reshape(lead + (N_SEQ, SLOTS, SPAN, D))
    return jnp.swapaxes(split_rows, -4, -3).reshape(lead + (GROUP_ROWS, D))

def from_slots(values):
    lead = values.shape[:-2]
    split_rows = values.reshape(lead + (SLOTS, N_SEQ, SPAN, D))
    return jnp.swapaxes(split_rows, -4, -3).reshape(lead + (GROUP_ROWS, D))

def slot_attention(queries, keys_in, values_in, segment):
    block_rows = min(512, SLOT)
    block_count = SLOT // block_rows
    score_scale = HD ** (-0.5)
    position = jnp.arange(SLOT, dtype=jnp.int32)

    def block_fn(start_row):
        query_block = lax.dynamic_slice_in_dim(queries, start_row, block_rows, 0)
        raw_scores = low_back(jnp.einsum('qhd,khd->hqk', query_block, keys_in, precision=PRECISE))
        query_place = start_row + jnp.arange(block_rows, dtype=jnp.int32)
        allowed = (position[None, :] <= query_place[:, None]) & (segment[None, :] == jnp.take(segment, query_place)[:, None])
        scores = jnp.where(allowed[None], raw_scores * score_scale, MASKED)
        row_top = lax.optimization_barrier(jnp.max(scores, axis=-1, keepdims=True))
        weights_exp = jnp.exp(scores - row_top)
        row_total = lax.optimization_barrier(jnp.sum(weights_exp, axis=-1, keepdims=True))
        probability = low(weights_exp / row_total)
        attn_block = jnp.einsum('hqk,khd->qhd', probability, values_in, precision=PRECISE)
        return (attn_block, row_top[..., 0] + jnp.log(row_total[..., 0]))
    starts = jnp.arange(block_count, dtype=jnp.int32) * block_rows
    attn_blocks, totals = lax.map(jax.checkpoint(block_fn), starts)
    attended = attn_blocks.reshape(SLOT, HEADS, HD)
    log_total = jnp.transpose(totals, (1, 0, 2)).reshape(HEADS, SLOT)
    return (attended, log_total)

def group_forward(inputs32, hist32, w_qkv, w_proj, w_up, w_down, gain1, bias1, gain2, bias2, dwa, cosine, sine_tab, segment):
    normed1 = low(norm_rows(inputs32, gain1, bias1))
    qkv_out = low_back(jnp.dot(normed1, w_qkv, precision=PRECISE))
    queries = qkv_out[:, :D].reshape(SLOTS, SLOT, HEADS, HD)
    keys_in = qkv_out[:, D:2 * D].reshape(SLOTS, SLOT, HEADS, HD)
    values_in = qkv_out[:, 2 * D:].reshape(SLOTS, SLOT, HEADS, HD)
    queries = low(low_back(rotate(queries, cosine, sine_tab)))
    keys_in = low(low_back(rotate(keys_in, cosine, sine_tab)))
    values_in = low(low_back(values_in))

    def per_slot(operands):
        return slot_attention(operands[0], operands[1], operands[2], operands[3])
    attended, log_total = lax.map(per_slot, (queries, keys_in, values_in, segment))
    attended = low(low_back(attended.reshape(GROUP_ROWS, D)))
    projected = low_back(jnp.dot(attended, w_proj, precision=PRECISE))
    middle = inputs32 + projected
    normed2 = low(norm_rows(middle, gain2, bias2))
    hidden_up = low_back(jnp.dot(normed2, w_up, precision=PRECISE))
    activated = low(jax.nn.gelu(hidden_up, approximate=True))
    down_out = low_back(jnp.dot(activated, w_down, precision=PRECISE))
    block_out = middle + down_out
    dwa_out = dwa[HIST] * block_out
    for layer_idx in range(HIST):
        dwa_out = dwa_out + dwa[layer_idx] * hist32[layer_idx]
    return (dwa_out, log_total.reshape(PAIRS, SLOT))

def reference(block_input, history, cotangent, qkv_weight, proj_weight, up_weight, down_weight, norm1_gain, norm1_bias, norm2_gain, norm2_bias, dwa_weights, pair_order, long_group):
    params = (qkv_weight.astype(jnp.float32), proj_weight.astype(jnp.float32), up_weight.astype(jnp.float32), down_weight.astype(jnp.float32), norm1_gain, norm1_bias, norm2_gain, norm2_bias, dwa_weights)
    zero_sums = tuple((jnp.zeros_like(param) for param in params))
    group_in = block_input.reshape(N_BATCH, GROUP_ROWS, D)
    group_hist = jnp.transpose(history.reshape(HIST, N_BATCH, GROUP_ROWS, D), (1, 0, 2, 3))
    group_cot = cotangent.reshape(N_BATCH, GROUP_ROWS, D)

    def group_step(sums_carry, inputs):
        rows_in, hist_in, cot_in, order_row, slot_flags = inputs
        seg_len = (SLOT // jnp.left_shift(jnp.ones_like(slot_flags), slot_flags)).astype(jnp.int32)
        position = jnp.arange(SLOT, dtype=jnp.int32)
        segment = (position[None, :] // seg_len[:, None]).astype(jnp.int32)
        doc_place = (position[None, :] % seg_len[:, None]).astype(jnp.float32)
        frequency = jnp.power(10000.0, jnp.arange(HD // 2, dtype=jnp.float32) * (-2.0 / HD))
        angles = doc_place[..., None] * frequency
        cosine = jnp.cos(angles)
        sine_tab = jnp.sin(angles)
        inputs32 = to_slots(rows_in.astype(jnp.float32))
        hist32 = to_slots(hist_in.astype(jnp.float32))
        cot32 = to_slots(cot_in.astype(jnp.float32))

        def forward(inputs_f, hist_f, w_qkv, w_proj, w_up, w_down, gain1, bias1, gain2, bias2, dwa):
            return group_forward(inputs_f, hist_f, w_qkv, w_proj, w_up, w_down, gain1, bias1, gain2, bias2, dwa, cosine, sine_tab, segment)
        dwa_out, pullback, log_total = jax.vjp(forward, inputs32, hist32, *params, has_aux=True)
        grads = pullback(cot32)
        new_sums = tuple((old_sum + new_grad for old_sum, new_grad in zip(sums_carry, grads[2:])))
        chosen = jnp.take(log_total, order_row, axis=0)
        outputs = (from_slots(dwa_out).astype(jnp.bfloat16), from_slots(grads[0]).astype(jnp.bfloat16), from_slots(grads[1]).astype(jnp.bfloat16), chosen)
        return (new_sums, outputs)
    sums_final, stacked = lax.scan(group_step, zero_sums, (group_in, group_hist, group_cot, pair_order, long_group))
    block_output = stacked[0].reshape(TOKENS, D)
    input_grad = stacked[1].reshape(TOKENS, D)
    history_grad = jnp.transpose(stacked[2], (1, 0, 2, 3)).reshape(HIST, TOKENS, D)
    row_lse = stacked[3]
    return (block_output, input_grad, history_grad, row_lse, sums_final[0], sums_final[1], sums_final[2], sums_final[3], sums_final[4], sums_final[5], sums_final[6], sums_final[7], sums_final[8])
```

```python
import jax
import jax.numpy as jnp
from jax import lax
from jax.sharding import PartitionSpec as P
from jax.experimental import pallas as pl
from jax.experimental.pallas import tpu as pltpu
import functools

D = 768
HEADS = 12
HD = 64
SLOT = 2048
HIST = 8


NORM_EPS = 1e-05
MASKED = -1e30
NT_DIMS = (((1,), (1,)), ((), ()))


def fwd_kernel(seg_ref, q_ref, k_ref, v_ref, o_ref, lse_ref, *, bq, bk, scale):
    pair = pl.program_id(0)
    qi = pl.program_id(1)
    seg_len = seg_ref[pair]
    q_start = qi * bq
    seg_start = (q_start // seg_len) * seg_len
    query = q_ref[0, 0]

    def step(j, carry, masked):
        m_old, l_old, acc = carry
        k_off = pl.multiple_of(j * bk, bk)
        key = k_ref[0, 0, pl.ds(k_off, bk), :]
        value = v_ref[0, 0, pl.ds(k_off, bk), :]
        s = lax.dot_general(query, key, NT_DIMS, preferred_element_type=jnp.float32) * scale
        if masked:
            rows = q_start + lax.broadcasted_iota(jnp.int32, (bq, bk), 0)
            cols = k_off + lax.broadcasted_iota(jnp.int32, (bq, bk), 1)
            s = jnp.where(cols <= rows, s, MASKED)
        m_new = jnp.maximum(m_old, jnp.max(s, axis=-1, keepdims=True))
        alpha = jnp.exp(m_old - m_new)
        weights = jnp.exp(s - m_new)
        l_new = alpha * l_old + jnp.sum(weights, axis=-1, keepdims=True)
        acc = alpha * acc + jnp.dot(
            weights.astype(jnp.bfloat16), value, preferred_element_type=jnp.float32
        )
        return m_new, l_new, acc

    carry = (
        jnp.full((bq, 1), MASKED, jnp.float32),
        jnp.zeros((bq, 1), jnp.float32),
        jnp.zeros((bq, HD), jnp.float32),
    )
    j_diag = q_start // bk
    carry = lax.fori_loop(
        seg_start // bk, j_diag, lambda j, c: step(j, c, False), carry
    )
    for r in range(bq // bk):
        carry = step(j_diag + r, carry, True)
    m_fin, l_fin, acc = carry
    o_ref[0] = (acc / l_fin).astype(o_ref.dtype)
    lse = m_fin + jnp.log(l_fin)
    lse_ref[0] = jnp.transpose(jnp.broadcast_to(lse, (bq, 128)))[0:1, :]


def attn_forward(qkv, seg_pairs, bq=512, bk=256):
    pairs, _, seq_len, head_size = qkv.shape
    scale = head_size ** (-0.5)
    n_q = seq_len // bq
    blocks_done = pairs * (seq_len // bk) * (seq_len // bk + 1) // 2
    cost = pl.CostEstimate(
        flops=4 * blocks_done * bk * bk * head_size,
        transcendentals=blocks_done * bk * bk,
        bytes_accessed=pairs * seq_len * head_size * 2 * 4 + pairs * seq_len * 4,
    )
    grid_spec = pltpu.PrefetchScalarGridSpec(
        num_scalar_prefetch=1,
        grid=(pairs, n_q),
        in_specs=[
            pl.BlockSpec((1, 1, bq, head_size), lambda p, i, seg: (p, 0, i, 0)),
            pl.BlockSpec((1, 1, seq_len, head_size), lambda p, i, seg: (p, 1, 0, 0)),
            pl.BlockSpec((1, 1, seq_len, head_size), lambda p, i, seg: (p, 2, 0, 0)),
        ],
        out_specs=[
            pl.BlockSpec((1, bq, head_size), lambda p, i, seg: (p, i, 0)),
            pl.BlockSpec((1, 1, bq), lambda p, i, seg: (p, 0, i)),
        ],
    )
    return pl.pallas_call(
        functools.partial(fwd_kernel, bq=bq, bk=bk, scale=scale),
        grid_spec=grid_spec,
        out_shape=[
            jax.ShapeDtypeStruct((pairs, seq_len, head_size), jnp.bfloat16),
            jax.ShapeDtypeStruct((pairs, 1, seq_len), jnp.float32),
        ],
        cost_estimate=cost,
        name="attn_fwd",
    )(seg_pairs, qkv, qkv, qkv)


def bwd_kernel(seg_ref, q_ref, k_ref, v_ref, do_ref, lse_ref, dl_ref, out_ref, dq_acc, *, blk, scale):
    pair = pl.program_id(0)
    kj = pl.program_id(1)

    @pl.when(kj == 0)
    def _():
        dq_acc[...] = jnp.zeros_like(dq_acc)

    seg_len = seg_ref[pair]
    k_start = kj * blk
    seg_end = (k_start // seg_len + 1) * seg_len
    key = k_ref[0, 0]
    value = v_ref[0, 0]

    def step(i, carry, masked):
        dk, dv = carry
        q_off = pl.multiple_of(i * blk, blk)
        query = q_ref[0, 0, pl.ds(q_off, blk), :]
        dout = do_ref[0, pl.ds(q_off, blk), :]
        lse = lse_ref[0, :, pl.ds(q_off, blk)]
        delta = dl_ref[0, :, pl.ds(q_off, blk)]
        s_t = lax.dot_general(key, query, NT_DIMS, preferred_element_type=jnp.float32) * scale
        if masked:
            keys_at = k_start + lax.broadcasted_iota(jnp.int32, (blk, blk), 0)
            queries_at = q_off + lax.broadcasted_iota(jnp.int32, (blk, blk), 1)
            s_t = jnp.where(keys_at <= queries_at, s_t, MASKED)
        p_t = jnp.exp(s_t - lse)
        dv = dv + jnp.dot(p_t.astype(jnp.bfloat16), dout, preferred_element_type=jnp.float32)
        dp_t = lax.dot_general(value, dout, NT_DIMS, preferred_element_type=jnp.float32)
        ds_t = p_t * (dp_t - delta) * scale
        dk = dk + jnp.dot(ds_t.astype(jnp.bfloat16), query, preferred_element_type=jnp.float32)
        dq_acc[pl.ds(q_off, blk), :] += jnp.dot(
            ds_t.T.astype(jnp.bfloat16), key, preferred_element_type=jnp.float32
        )
        return dk, dv

    carry = (jnp.zeros((blk, HD), jnp.float32), jnp.zeros((blk, HD), jnp.float32))
    carry = step(kj, carry, True)
    dk, dv = lax.fori_loop(kj + 1, seg_end // blk, lambda i, c: step(i, c, False), carry)
    out_ref[0, 0] = dq_acc[pl.ds(pl.multiple_of(k_start, blk), blk), :].astype(out_ref.dtype)
    out_ref[0, 1] = dk.astype(out_ref.dtype)
    out_ref[0, 2] = dv.astype(out_ref.dtype)


def attn_backward(qkv, dout, lse, delta, seg_pairs, blk=256):
    pairs, _, seq_len, head_size = qkv.shape
    scale = head_size ** (-0.5)
    n_k = seq_len // blk
    blocks_done = pairs * n_k * (n_k + 1) // 2
    cost = pl.CostEstimate(
        flops=10 * blocks_done * blk * blk * head_size,
        transcendentals=blocks_done * blk * blk,
        bytes_accessed=pairs * seq_len * head_size * 2 * 7 + pairs * seq_len * 8,
    )
    grid_spec = pltpu.PrefetchScalarGridSpec(
        num_scalar_prefetch=1,
        grid=(pairs, n_k),
        in_specs=[
            pl.BlockSpec((1, 1, seq_len, head_size), lambda p, j, seg: (p, 0, 0, 0)),
            pl.BlockSpec((1, 1, blk, head_size), lambda p, j, seg: (p, 1, j, 0)),
            pl.BlockSpec((1, 1, blk, head_size), lambda p, j, seg: (p, 2, j, 0)),
            pl.BlockSpec((1, seq_len, head_size), lambda p, j, seg: (p, 0, 0)),
            pl.BlockSpec((1, 1, seq_len), lambda p, j, seg: (p, 0, 0)),
            pl.BlockSpec((1, 1, seq_len), lambda p, j, seg: (p, 0, 0)),
        ],
        out_specs=pl.BlockSpec((1, 3, blk, head_size), lambda p, j, seg: (p, 0, j, 0)),
        scratch_shapes=[pltpu.VMEM((seq_len, head_size), jnp.float32)],
    )
    return pl.pallas_call(
        functools.partial(bwd_kernel, blk=blk, scale=scale),
        grid_spec=grid_spec,
        out_shape=jax.ShapeDtypeStruct((pairs, 3, seq_len, head_size), jnp.bfloat16),
        cost_estimate=cost,
        name="attn_bwd",
    )(seg_pairs, qkv, qkv, qkv, dout, lse, delta)


def norm_rows(values, gain, shift):
    row_mean = jnp.mean(values, axis=-1, keepdims=True)
    centred = values - row_mean
    variance = jnp.mean(centred * centred, axis=-1, keepdims=True)
    inv_std = lax.rsqrt(variance + NORM_EPS)
    normed = centred * inv_std
    return (normed * gain + shift, normed, inv_std)


def norm_back(grad_in, normed, inv_std, gain):
    scaled = grad_in * gain
    centred = (
        scaled
        - jnp.mean(scaled, axis=-1, keepdims=True)
        - normed * jnp.mean(scaled * normed, axis=-1, keepdims=True)
    )
    return (centred * inv_std, jnp.sum(grad_in * normed, axis=0), jnp.sum(grad_in, axis=0))


def rotate(values, cosine, sine_tab):
    half_size = values.shape[-1] // 2
    front = values[..., :half_size]
    behind = values[..., half_size:]
    cos_part = cosine[..., None, :]
    sin_part = sine_tab[..., None, :]
    return jnp.concatenate(
        [front * cos_part - behind * sin_part, behind * cos_part + front * sin_part], axis=-1
    )


def unrotate(values, cosine, sine_tab):
    half_size = values.shape[-1] // 2
    front = values[..., :half_size]
    behind = values[..., half_size:]
    cos_part = cosine[..., None, :]
    sin_part = sine_tab[..., None, :]
    return jnp.concatenate(
        [front * cos_part + behind * sin_part, behind * cos_part - front * sin_part], axis=-1
    )


def to_pairs(stacked, order_row, n_seq, per_dev):
    slot_count, piece_len, part_count, head_count, head_size = stacked.shape
    reordered = jnp.transpose(stacked, (0, 3, 2, 1, 4)).reshape(
        slot_count * head_count, part_count, piece_len * head_size
    )
    return jnp.take(reordered, order_row, axis=0).reshape(
        n_seq, per_dev, part_count, piece_len * head_size
    )


def pairs_whole(incoming, head_size):
    n_seq, per_dev, part_count, flat_len = incoming.shape
    piece_len = flat_len // head_size
    reordered = jnp.transpose(
        incoming.reshape(n_seq, per_dev, part_count, piece_len, head_size), (1, 2, 0, 3, 4)
    )
    return reordered.reshape(per_dev, part_count, n_seq * piece_len, head_size)


def pairs_split(whole_seq, n_seq):
    per_dev, part_count, seq_len, head_size = whole_seq.shape
    return jnp.transpose(
        whole_seq.reshape(per_dev, part_count, n_seq, seq_len // n_seq * head_size), (2, 0, 1, 3)
    )


def tokens_back(incoming, inverse, slot_count, head_size):
    n_seq, per_dev, part_count, flat_len = incoming.shape
    piece_len = flat_len // head_size
    ordered = jnp.take(incoming.reshape(n_seq * per_dev, part_count, flat_len), inverse, axis=0)
    head_count = n_seq * per_dev // slot_count
    return jnp.transpose(
        ordered.reshape(slot_count, head_count, part_count, piece_len, head_size), (0, 3, 2, 1, 4)
    )


def local(
    block_input,
    history,
    cotangent,
    qkv_weight,
    proj_weight,
    up_weight,
    down_weight,
    norm1_gain,
    norm1_bias,
    norm2_gain,
    norm2_bias,
    dwa_weights,
    pair_order,
    long_group,
):
    n_seq = lax.axis_size("seq")
    row_count = block_input.shape[0]
    piece_len = SLOT // n_seq
    slot_count = row_count // piece_len
    pair_count = slot_count * HEADS
    per_dev = pair_count // n_seq
    slot_flags = long_group[0]
    seg_len = SLOT // jnp.left_shift(jnp.ones_like(slot_flags), slot_flags)
    position = jnp.arange(SLOT, dtype=jnp.int32)
    doc_place = (position[None, :] % seg_len[:, None]).astype(jnp.float32)
    frequency = jnp.power(10000.0, jnp.arange(HD // 2, dtype=jnp.float32) * (-2.0 / HD))
    angles = doc_place[..., None] * frequency
    my_index = lax.axis_index("seq")
    my_start = my_index * piece_len
    cosine = lax.dynamic_slice_in_dim(jnp.cos(angles), my_start, piece_len, 1)
    sine_tab = lax.dynamic_slice_in_dim(jnp.sin(angles), my_start, piece_len, 1)
    order_row = pair_order[0]
    inverse = (
        jnp.zeros((pair_count,), jnp.int32)
        .at[order_row]
        .set(jnp.arange(pair_count, dtype=jnp.int32))
    )
    held_pairs = lax.dynamic_slice_in_dim(order_row, my_index * per_dev, per_dev, 0)
    row_parts = (
        lax.all_gather(qkv_weight, "batch", axis=0, tiled=True),
        lax.all_gather(proj_weight, "batch", axis=0, tiled=True),
        lax.all_gather(up_weight, "batch", axis=0, tiled=True),
        lax.all_gather(down_weight, "batch", axis=0, tiled=True),
    )
    w_qkv, w_proj, w_up, w_down = (
        lax.all_gather(row_parts[0], "seq", axis=1, tiled=True),
        lax.all_gather(row_parts[1], "seq", axis=1, tiled=True),
        lax.all_gather(row_parts[2], "seq", axis=1, tiled=True),
        lax.all_gather(row_parts[3], "seq", axis=1, tiled=True),
    )
    inputs32 = block_input.astype(jnp.float32)
    norm1_out, normed1, inv_std1 = norm_rows(inputs32, norm1_gain, norm1_bias)
    norm1_low = norm1_out.astype(jnp.bfloat16)
    qkv_out = jnp.dot(norm1_low, w_qkv, preferred_element_type=jnp.float32)
    queries = rotate(qkv_out[:, :D].reshape(slot_count, piece_len, HEADS, HD), cosine, sine_tab)
    keys_rot = rotate(
        qkv_out[:, D : 2 * D].reshape(slot_count, piece_len, HEADS, HD), cosine, sine_tab
    )
    values_in = qkv_out[:, 2 * D :].reshape(slot_count, piece_len, HEADS, HD)
    stacked = jnp.stack([queries, keys_rot, values_in], axis=2).astype(jnp.bfloat16)
    incoming = lax.all_to_all(
        to_pairs(stacked, order_row, n_seq, per_dev), "seq", split_axis=0, concat_axis=0, tiled=True
    )
    sequences = pairs_whole(incoming, HD)
    seg_pairs = jnp.take(seg_len, held_pairs // HEADS).astype(jnp.int32)
    attn_out, lse_rows = attn_forward(sequences, seg_pairs)
    attended_pairs = attn_out.reshape(per_dev, 1, SLOT, HD)
    log_total = lse_rows.reshape(per_dev, SLOT)
    returned = lax.all_to_all(
        pairs_split(attended_pairs, n_seq), "seq", split_axis=0, concat_axis=0, tiled=True
    )
    attended = tokens_back(returned, inverse, slot_count, HD).reshape(row_count, D)
    middle = inputs32 + jnp.dot(attended, w_proj, preferred_element_type=jnp.float32)
    norm2_out, normed2, inv_std2 = norm_rows(middle, norm2_gain, norm2_bias)
    norm2_low = norm2_out.astype(jnp.bfloat16)
    hidden_up = jnp.dot(norm2_low, w_up, preferred_element_type=jnp.float32)
    gelu_out, gelu_pull = jax.vjp(lambda hidden: jax.nn.gelu(hidden, approximate=True), hidden_up)
    gelu_low = gelu_out.astype(jnp.bfloat16)
    block_out = middle + jnp.dot(gelu_low, w_down, preferred_element_type=jnp.float32)
    dwa_out = dwa_weights[HIST] * block_out
    for layer_idx in range(HIST):
        dwa_out = dwa_out + dwa_weights[layer_idx] * history[layer_idx].astype(jnp.float32)
    block_output = dwa_out.astype(jnp.bfloat16)
    grad_out = cotangent.astype(jnp.float32)
    history_grad = (dwa_weights[:HIST, None, None] * grad_out[None]).astype(jnp.bfloat16)
    dwa_terms = [
        jnp.sum(history[layer_idx].astype(jnp.float32) * grad_out) for layer_idx in range(HIST)
    ]
    dwa_terms.append(jnp.sum(block_out * grad_out))
    dwa_local = jnp.stack(dwa_terms)
    again_parts = (
        lax.all_gather(qkv_weight, "batch", axis=0, tiled=True),
        lax.all_gather(proj_weight, "batch", axis=0, tiled=True),
        lax.all_gather(up_weight, "batch", axis=0, tiled=True),
        lax.all_gather(down_weight, "batch", axis=0, tiled=True),
    )
    w_qkv, w_proj, w_up, w_down = (
        lax.all_gather(again_parts[0], "seq", axis=1, tiled=True),
        lax.all_gather(again_parts[1], "seq", axis=1, tiled=True),
        lax.all_gather(again_parts[2], "seq", axis=1, tiled=True),
        lax.all_gather(again_parts[3], "seq", axis=1, tiled=True),
    )
    dy_full = dwa_weights[HIST] * grad_out
    dmlp_low = dy_full.astype(jnp.bfloat16)
    down_local = jnp.einsum("nf,nd->fd", gelu_low, dmlp_low, preferred_element_type=jnp.float32)
    dgelu = jnp.einsum("nd,fd->nf", dmlp_low, w_down, preferred_element_type=jnp.float32)
    dup_low = gelu_pull(dgelu)[0].astype(jnp.bfloat16)
    up_local = jnp.einsum("nd,nf->df", norm2_low, dup_low, preferred_element_type=jnp.float32)
    dnorm2 = jnp.einsum("nf,df->nd", dup_low, w_up, preferred_element_type=jnp.float32)
    dmid_norm, gain2_local, bias2_local = norm_back(dnorm2, normed2, inv_std2, norm2_gain)
    dmiddle = dy_full + dmid_norm
    dmiddle_low = dmiddle.astype(jnp.bfloat16)
    proj_local = jnp.einsum("nd,ne->de", attended, dmiddle_low, preferred_element_type=jnp.float32)
    dattended = jnp.einsum(
        "ne,de->nd", dmiddle_low, w_proj, preferred_element_type=jnp.float32
    ).astype(jnp.bfloat16)
    dattn_tokens = dattended.reshape(slot_count, piece_len, 1, HEADS, HD)
    dattn_in = lax.all_to_all(
        to_pairs(dattn_tokens, order_row, n_seq, per_dev),
        "seq",
        split_axis=0,
        concat_axis=0,
        tiled=True,
    )
    dout_pairs = pairs_whole(dattn_in, HD)[:, 0]
    delta = jnp.sum(
        dout_pairs.astype(jnp.float32) * attn_out.astype(jnp.float32), axis=-1
    ).reshape(per_dev, 1, SLOT)
    dpairs = attn_backward(sequences, dout_pairs, lse_rows, delta, seg_pairs)
    dreturned = lax.all_to_all(
        pairs_split(dpairs, n_seq), "seq", split_axis=0, concat_axis=0, tiled=True
    )
    dtokens = tokens_back(dreturned, inverse, slot_count, HD)
    dq_rows = unrotate(dtokens[:, :, 0].astype(jnp.float32), cosine, sine_tab).reshape(row_count, D)
    dk_rows = unrotate(dtokens[:, :, 1].astype(jnp.float32), cosine, sine_tab).reshape(row_count, D)
    dv_rows = dtokens[:, :, 2].astype(jnp.float32).reshape(row_count, D)
    dqkv_low = jnp.concatenate([dq_rows, dk_rows, dv_rows], axis=-1).astype(jnp.bfloat16)
    qkv_local = jnp.einsum("nd,nf->df", norm1_low, dqkv_low, preferred_element_type=jnp.float32)
    dnorm1 = jnp.einsum("nf,df->nd", dqkv_low, w_qkv, preferred_element_type=jnp.float32)
    dinput_norm, gain1_local, bias1_local = norm_back(dnorm1, normed1, inv_std1, norm1_gain)
    input_grad = (dmiddle + dinput_norm).astype(jnp.bfloat16)
    col_sums = (
        lax.psum_scatter(
            qkv_local.astype(jnp.bfloat16), "seq", scatter_dimension=1, tiled=True
        ).astype(jnp.float32),
        lax.psum_scatter(
            proj_local.astype(jnp.bfloat16), "seq", scatter_dimension=1, tiled=True
        ).astype(jnp.float32),
        lax.psum_scatter(
            up_local.astype(jnp.bfloat16), "seq", scatter_dimension=1, tiled=True
        ).astype(jnp.float32),
        lax.psum_scatter(
            down_local.astype(jnp.bfloat16), "seq", scatter_dimension=1, tiled=True
        ).astype(jnp.float32),
    )
    qkv_grad, proj_grad, up_grad, down_grad = (
        lax.psum_scatter(
            col_sums[0].astype(jnp.bfloat16), "batch", scatter_dimension=0, tiled=True
        ).astype(jnp.float32),
        lax.psum_scatter(
            col_sums[1].astype(jnp.bfloat16), "batch", scatter_dimension=0, tiled=True
        ).astype(jnp.float32),
        lax.psum_scatter(
            col_sums[2].astype(jnp.bfloat16), "batch", scatter_dimension=0, tiled=True
        ).astype(jnp.float32),
        lax.psum_scatter(
            col_sums[3].astype(jnp.bfloat16), "batch", scatter_dimension=0, tiled=True
        ).astype(jnp.float32),
    )
    gain1_grad, bias1_grad, gain2_grad, bias2_grad, dwa_grad = lax.psum(
        (gain1_local, bias1_local, gain2_local, bias2_local, dwa_local), ("batch", "seq")
    )
    row_lse = log_total.reshape(1, per_dev, SLOT)
    return (
        block_output,
        input_grad,
        history_grad,
        row_lse,
        qkv_grad,
        proj_grad,
        up_grad,
        down_grad,
        gain1_grad,
        bias1_grad,
        gain2_grad,
        bias2_grad,
        dwa_grad,
    )


def solution(mesh):
    placed = (
        P(("batch", "seq"), None),
        P(None, ("batch", "seq"), None),
        P(("batch", "seq"), None),
        P("batch", "seq"),
        P("batch", "seq"),
        P("batch", "seq"),
        P("batch", "seq"),
        P(),
        P(),
        P(),
        P(),
        P(),
        P("batch", None),
        P("batch", None),
    )
    return jax.shard_map(
        local,
        mesh=mesh,
        in_specs=placed,
        out_specs=(
            P(("batch", "seq"), None),
            P(("batch", "seq"), None),
            P(None, ("batch", "seq"), None),
            P("batch", "seq", None),
            P("batch", "seq"),
            P("batch", "seq"),
            P("batch", "seq"),
            P("batch", "seq"),
            P(),
            P(),
            P(),
            P(),
            P(),
        ),
        check_vma=False,
    )
```

```python
import jax
import jax.numpy as jnp
from jax import lax
from jax.sharding import PartitionSpec as P
from jax.experimental import pallas as pl
from jax.experimental.pallas import tpu as pltpu
import functools

D = 768
HEADS = 12
HD = 64
SLOT = 2048
HIST = 8


NORM_EPS = 1e-05
MASKED = -1e30
NT_DIMS = (((1,), (1,)), ((), ()))


def fwd_kernel(seg_ref, q_ref, k_ref, v_ref, o_ref, lse_ref, *, bq, bk, scale):
    pair = pl.program_id(0)
    qi = pl.program_id(1)
    seg_len = seg_ref[pair]
    q_start = qi * bq
    seg_start = (q_start // seg_len) * seg_len
    query = q_ref[0, 0]

    def step(j, carry, masked):
        m_old, l_old, acc = carry
        k_off = pl.multiple_of(j * bk, bk)
        key = k_ref[0, 0, pl.ds(k_off, bk), :]
        value = v_ref[0, 0, pl.ds(k_off, bk), :]
        s = lax.dot_general(query, key, NT_DIMS, preferred_element_type=jnp.float32) * scale
        if masked:
            rows = q_start + lax.broadcasted_iota(jnp.int32, (bq, bk), 0)
            cols = k_off + lax.broadcasted_iota(jnp.int32, (bq, bk), 1)
            s = jnp.where(cols <= rows, s, MASKED)
        m_new = jnp.maximum(m_old, jnp.max(s, axis=-1, keepdims=True))
        alpha = jnp.exp(m_old - m_new)
        weights = jnp.exp(s - m_new)
        l_new = alpha * l_old + jnp.sum(weights, axis=-1, keepdims=True)
        acc = alpha * acc + jnp.dot(
            weights.astype(jnp.bfloat16), value, preferred_element_type=jnp.float32
        )
        return m_new, l_new, acc

    carry = (
        jnp.full((bq, 1), MASKED, jnp.float32),
        jnp.zeros((bq, 1), jnp.float32),
        jnp.zeros((bq, HD), jnp.float32),
    )
    j_diag = q_start // bk
    carry = lax.fori_loop(
        seg_start // bk, j_diag, lambda j, c: step(j, c, False), carry
    )
    for r in range(bq // bk):
        carry = step(j_diag + r, carry, True)
    m_fin, l_fin, acc = carry
    o_ref[0] = (acc / l_fin).astype(o_ref.dtype)
    lse = m_fin + jnp.log(l_fin)
    lse_ref[0] = jnp.transpose(jnp.broadcast_to(lse, (bq, 128)))[0:1, :]


def attn_forward(qkv, seg_pairs, bq=512, bk=256):
    pairs, _, seq_len, head_size = qkv.shape
    scale = head_size ** (-0.5)
    n_q = seq_len // bq
    blocks_done = pairs * (seq_len // bk) * (seq_len // bk + 1) // 2
    cost = pl.CostEstimate(
        flops=4 * blocks_done * bk * bk * head_size,
        transcendentals=blocks_done * bk * bk,
        bytes_accessed=pairs * seq_len * head_size * 2 * 4 + pairs * seq_len * 4,
    )
    grid_spec = pltpu.PrefetchScalarGridSpec(
        num_scalar_prefetch=1,
        grid=(pairs, n_q),
        in_specs=[
            pl.BlockSpec((1, 1, bq, head_size), lambda p, i, seg: (p, 0, i, 0)),
            pl.BlockSpec((1, 1, seq_len, head_size), lambda p, i, seg: (p, 1, 0, 0)),
            pl.BlockSpec((1, 1, seq_len, head_size), lambda p, i, seg: (p, 2, 0, 0)),
        ],
        out_specs=[
            pl.BlockSpec((1, bq, head_size), lambda p, i, seg: (p, i, 0)),
            pl.BlockSpec((1, 1, bq), lambda p, i, seg: (p, 0, i)),
        ],
    )
    return pl.pallas_call(
        functools.partial(fwd_kernel, bq=bq, bk=bk, scale=scale),
        grid_spec=grid_spec,
        out_shape=[
            jax.ShapeDtypeStruct((pairs, seq_len, head_size), jnp.bfloat16),
            jax.ShapeDtypeStruct((pairs, 1, seq_len), jnp.float32),
        ],
        cost_estimate=cost,
        name="attn_fwd",
    )(seg_pairs, qkv, qkv, qkv)


def bwd_kernel(seg_ref, q_ref, k_ref, v_ref, do_ref, lse_ref, dl_ref, out_ref, dq_acc, *, blk, scale):
    pair = pl.program_id(0)
    kj = pl.program_id(1)

    @pl.when(kj == 0)
    def _():
        dq_acc[...] = jnp.zeros_like(dq_acc)

    seg_len = seg_ref[pair]
    k_start = kj * blk
    seg_end = (k_start // seg_len + 1) * seg_len
    key = k_ref[0, 0]
    value = v_ref[0, 0]

    def step(i, carry, masked):
        dk, dv = carry
        q_off = pl.multiple_of(i * blk, blk)
        query = q_ref[0, 0, pl.ds(q_off, blk), :]
        dout = do_ref[0, pl.ds(q_off, blk), :]
        lse = lse_ref[0, :, pl.ds(q_off, blk)]
        delta = dl_ref[0, :, pl.ds(q_off, blk)]
        s_t = lax.dot_general(key, query, NT_DIMS, preferred_element_type=jnp.float32) * scale
        if masked:
            keys_at = k_start + lax.broadcasted_iota(jnp.int32, (blk, blk), 0)
            queries_at = q_off + lax.broadcasted_iota(jnp.int32, (blk, blk), 1)
            s_t = jnp.where(keys_at <= queries_at, s_t, MASKED)
        p_t = jnp.exp(s_t - lse)
        dv = dv + jnp.dot(p_t.astype(jnp.bfloat16), dout, preferred_element_type=jnp.float32)
        dp_t = lax.dot_general(value, dout, NT_DIMS, preferred_element_type=jnp.float32)
        ds_t = p_t * (dp_t - delta) * scale
        dk = dk + jnp.dot(ds_t.astype(jnp.bfloat16), query, preferred_element_type=jnp.float32)
        dq_acc[pl.ds(q_off, blk), :] += jnp.dot(
            ds_t.T.astype(jnp.bfloat16), key, preferred_element_type=jnp.float32
        )
        return dk, dv

    carry = (jnp.zeros((blk, HD), jnp.float32), jnp.zeros((blk, HD), jnp.float32))
    carry = step(kj, carry, True)
    dk, dv = lax.fori_loop(kj + 1, seg_end // blk, lambda i, c: step(i, c, False), carry)
    out_ref[0, 0] = dq_acc[pl.ds(pl.multiple_of(k_start, blk), blk), :].astype(out_ref.dtype)
    out_ref[0, 1] = dk.astype(out_ref.dtype)
    out_ref[0, 2] = dv.astype(out_ref.dtype)


def attn_backward(qkv, dout, lse, delta, seg_pairs, blk=256):
    pairs, _, seq_len, head_size = qkv.shape
    scale = head_size ** (-0.5)
    n_k = seq_len // blk
    blocks_done = pairs * n_k * (n_k + 1) // 2
    cost = pl.CostEstimate(
        flops=10 * blocks_done * blk * blk * head_size,
        transcendentals=blocks_done * blk * blk,
        bytes_accessed=pairs * seq_len * head_size * 2 * 7 + pairs * seq_len * 8,
    )
    grid_spec = pltpu.PrefetchScalarGridSpec(
        num_scalar_prefetch=1,
        grid=(pairs, n_k),
        in_specs=[
            pl.BlockSpec((1, 1, seq_len, head_size), lambda p, j, seg: (p, 0, 0, 0)),
            pl.BlockSpec((1, 1, blk, head_size), lambda p, j, seg: (p, 1, j, 0)),
            pl.BlockSpec((1, 1, blk, head_size), lambda p, j, seg: (p, 2, j, 0)),
            pl.BlockSpec((1, seq_len, head_size), lambda p, j, seg: (p, 0, 0)),
            pl.BlockSpec((1, 1, seq_len), lambda p, j, seg: (p, 0, 0)),
            pl.BlockSpec((1, 1, seq_len), lambda p, j, seg: (p, 0, 0)),
        ],
        out_specs=pl.BlockSpec((1, 3, blk, head_size), lambda p, j, seg: (p, 0, j, 0)),
        scratch_shapes=[pltpu.VMEM((seq_len, head_size), jnp.float32)],
    )
    return pl.pallas_call(
        functools.partial(bwd_kernel, blk=blk, scale=scale),
        grid_spec=grid_spec,
        out_shape=jax.ShapeDtypeStruct((pairs, 3, seq_len, head_size), jnp.bfloat16),
        cost_estimate=cost,
        name="attn_bwd",
    )(seg_pairs, qkv, qkv, qkv, dout, lse, delta)


def norm_rows(values, gain, shift):
    row_mean = jnp.mean(values, axis=-1, keepdims=True)
    centred = values - row_mean
    variance = jnp.mean(centred * centred, axis=-1, keepdims=True)
    inv_std = lax.rsqrt(variance + NORM_EPS)
    normed = centred * inv_std
    return (normed * gain + shift, normed, inv_std)


def norm_back(grad_in, normed, inv_std, gain):
    scaled = grad_in * gain
    centred = (
        scaled
        - jnp.mean(scaled, axis=-1, keepdims=True)
        - normed * jnp.mean(scaled * normed, axis=-1, keepdims=True)
    )
    return (centred * inv_std, jnp.sum(grad_in * normed, axis=0), jnp.sum(grad_in, axis=0))


def rotate(values, cosine, sine_tab):
    half_size = values.shape[-1] // 2
    front = values[..., :half_size]
    behind = values[..., half_size:]
    cos_part = cosine[..., None, :]
    sin_part = sine_tab[..., None, :]
    return jnp.concatenate(
        [front * cos_part - behind * sin_part, behind * cos_part + front * sin_part], axis=-1
    )


def unrotate(values, cosine, sine_tab):
    half_size = values.shape[-1] // 2
    front = values[..., :half_size]
    behind = values[..., half_size:]
    cos_part = cosine[..., None, :]
    sin_part = sine_tab[..., None, :]
    return jnp.concatenate(
        [front * cos_part + behind * sin_part, behind * cos_part - front * sin_part], axis=-1
    )


def to_pairs(stacked, order_row, n_seq, per_dev):
    slot_count, piece_len, part_count, head_count, head_size = stacked.shape
    reordered = jnp.transpose(stacked, (0, 3, 2, 1, 4)).reshape(
        slot_count * head_count, part_count, piece_len * head_size
    )
    return jnp.take(reordered, order_row, axis=0).reshape(
        n_seq, per_dev, part_count, piece_len * head_size
    )


def pairs_whole(incoming, head_size):
    n_seq, per_dev, part_count, flat_len = incoming.shape
    piece_len = flat_len // head_size
    reordered = jnp.transpose(
        incoming.reshape(n_seq, per_dev, part_count, piece_len, head_size), (1, 2, 0, 3, 4)
    )
    return reordered.reshape(per_dev, part_count, n_seq * piece_len, head_size)


def pairs_split(whole_seq, n_seq):
    per_dev, part_count, seq_len, head_size = whole_seq.shape
    return jnp.transpose(
        whole_seq.reshape(per_dev, part_count, n_seq, seq_len // n_seq * head_size), (2, 0, 1, 3)
    )


def tokens_back(incoming, inverse, slot_count, head_size):
    n_seq, per_dev, part_count, flat_len = incoming.shape
    piece_len = flat_len // head_size
    ordered = jnp.take(incoming.reshape(n_seq * per_dev, part_count, flat_len), inverse, axis=0)
    head_count = n_seq * per_dev // slot_count
    return jnp.transpose(
        ordered.reshape(slot_count, head_count, part_count, piece_len, head_size), (0, 3, 2, 1, 4)
    )


def local(
    block_input,
    history,
    cotangent,
    qkv_weight,
    proj_weight,
    up_weight,
    down_weight,
    norm1_gain,
    norm1_bias,
    norm2_gain,
    norm2_bias,
    dwa_weights,
    pair_order,
    long_group,
):
    n_seq = lax.axis_size("seq")
    row_count = block_input.shape[0]
    piece_len = SLOT // n_seq
    slot_count = row_count // piece_len
    pair_count = slot_count * HEADS
    per_dev = pair_count // n_seq
    slot_flags = long_group[0]
    seg_len = SLOT // jnp.left_shift(jnp.ones_like(slot_flags), slot_flags)
    position = jnp.arange(SLOT, dtype=jnp.int32)
    doc_place = (position[None, :] % seg_len[:, None]).astype(jnp.float32)
    frequency = jnp.power(10000.0, jnp.arange(HD // 2, dtype=jnp.float32) * (-2.0 / HD))
    angles = doc_place[..., None] * frequency
    my_index = lax.axis_index("seq")
    my_start = my_index * piece_len
    cosine = lax.dynamic_slice_in_dim(jnp.cos(angles), my_start, piece_len, 1)
    sine_tab = lax.dynamic_slice_in_dim(jnp.sin(angles), my_start, piece_len, 1)
    order_row = pair_order[0]
    inverse = (
        jnp.zeros((pair_count,), jnp.int32)
        .at[order_row]
        .set(jnp.arange(pair_count, dtype=jnp.int32))
    )
    held_pairs = lax.dynamic_slice_in_dim(order_row, my_index * per_dev, per_dev, 0)
    n_batch = lax.axis_size("batch")
    both = ("batch", "seq")
    g_qkv = lax.all_gather(qkv_weight, both, axis=0, tiled=False)
    rest = jnp.concatenate(
        [proj_weight.reshape(-1), up_weight.reshape(-1), down_weight.reshape(-1)]
    )
    g_rest = lax.all_gather(rest, both, axis=0, tiled=False)

    def regroup(flat, rows, cols):
        return jnp.transpose(flat.reshape(n_batch, n_seq, rows, cols), (0, 2, 1, 3)).reshape(
            n_batch * rows, n_seq * cols
        )

    w_qkv = regroup(g_qkv, *qkv_weight.shape)
    sizes = [proj_weight.size, up_weight.size, down_weight.size]
    w_proj = regroup(g_rest[:, : sizes[0]], *proj_weight.shape)
    w_up = regroup(g_rest[:, sizes[0] : sizes[0] + sizes[1]], *up_weight.shape)
    w_down = regroup(g_rest[:, sizes[0] + sizes[1] :], *down_weight.shape)
    inputs32 = block_input.astype(jnp.float32)
    norm1_out, normed1, inv_std1 = norm_rows(inputs32, norm1_gain, norm1_bias)
    norm1_low = norm1_out.astype(jnp.bfloat16)
    qkv_out = jnp.dot(norm1_low, w_qkv, preferred_element_type=jnp.float32)
    queries = rotate(qkv_out[:, :D].reshape(slot_count, piece_len, HEADS, HD), cosine, sine_tab)
    keys_rot = rotate(
        qkv_out[:, D : 2 * D].reshape(slot_count, piece_len, HEADS, HD), cosine, sine_tab
    )
    values_in = qkv_out[:, 2 * D :].reshape(slot_count, piece_len, HEADS, HD)
    stacked = jnp.stack([queries, keys_rot, values_in], axis=2).astype(jnp.bfloat16)
    incoming = lax.all_to_all(
        to_pairs(stacked, order_row, n_seq, per_dev), "seq", split_axis=0, concat_axis=0, tiled=True
    )
    sequences = pairs_whole(incoming, HD)
    seg_pairs = jnp.take(seg_len, held_pairs // HEADS).astype(jnp.int32)
    attn_out, lse_rows = attn_forward(sequences, seg_pairs)
    attended_pairs = attn_out.reshape(per_dev, 1, SLOT, HD)
    log_total = lse_rows.reshape(per_dev, SLOT)
    returned = lax.all_to_all(
        pairs_split(attended_pairs, n_seq), "seq", split_axis=0, concat_axis=0, tiled=True
    )
    attended = tokens_back(returned, inverse, slot_count, HD).reshape(row_count, D)
    middle = inputs32 + jnp.dot(attended, w_proj, preferred_element_type=jnp.float32)
    norm2_out, normed2, inv_std2 = norm_rows(middle, norm2_gain, norm2_bias)
    norm2_low = norm2_out.astype(jnp.bfloat16)
    hidden_up = jnp.dot(norm2_low, w_up, preferred_element_type=jnp.float32)
    gelu_out, gelu_pull = jax.vjp(lambda hidden: jax.nn.gelu(hidden, approximate=True), hidden_up)
    gelu_low = gelu_out.astype(jnp.bfloat16)
    block_out = middle + jnp.dot(gelu_low, w_down, preferred_element_type=jnp.float32)
    dwa_out = dwa_weights[HIST] * block_out
    for layer_idx in range(HIST):
        dwa_out = dwa_out + dwa_weights[layer_idx] * history[layer_idx].astype(jnp.float32)
    block_output = dwa_out.astype(jnp.bfloat16)
    grad_out = cotangent.astype(jnp.float32)
    history_grad = (dwa_weights[:HIST, None, None] * grad_out[None]).astype(jnp.bfloat16)
    dwa_terms = [
        jnp.sum(history[layer_idx].astype(jnp.float32) * grad_out) for layer_idx in range(HIST)
    ]
    dwa_terms.append(jnp.sum(block_out * grad_out))
    dwa_local = jnp.stack(dwa_terms)
    dy_full = dwa_weights[HIST] * grad_out
    dmlp_low = dy_full.astype(jnp.bfloat16)
    down_local = jnp.einsum("nf,nd->fd", gelu_low, dmlp_low, preferred_element_type=jnp.float32)
    dgelu = jnp.einsum("nd,fd->nf", dmlp_low, w_down, preferred_element_type=jnp.float32)
    dup_low = gelu_pull(dgelu)[0].astype(jnp.bfloat16)
    up_local = jnp.einsum("nd,nf->df", norm2_low, dup_low, preferred_element_type=jnp.float32)
    dnorm2 = jnp.einsum("nf,df->nd", dup_low, w_up, preferred_element_type=jnp.float32)
    dmid_norm, gain2_local, bias2_local = norm_back(dnorm2, normed2, inv_std2, norm2_gain)
    dmiddle = dy_full + dmid_norm
    early_sums = jnp.sum(
        lax.all_gather(jnp.concatenate([gain2_local, bias2_local, dwa_local]), both, axis=0),
        axis=0,
    )
    gain2_grad, bias2_grad, dwa_grad = early_sums[:D], early_sums[D : 2 * D], early_sums[2 * D :]
    dmiddle_low = dmiddle.astype(jnp.bfloat16)
    proj_local = jnp.einsum("nd,ne->de", attended, dmiddle_low, preferred_element_type=jnp.float32)
    dattended = jnp.einsum(
        "ne,de->nd", dmiddle_low, w_proj, preferred_element_type=jnp.float32
    ).astype(jnp.bfloat16)
    dattn_tokens = dattended.reshape(slot_count, piece_len, 1, HEADS, HD)
    dattn_in = lax.all_to_all(
        to_pairs(dattn_tokens, order_row, n_seq, per_dev),
        "seq",
        split_axis=0,
        concat_axis=0,
        tiled=True,
    )
    dout_pairs = pairs_whole(dattn_in, HD)[:, 0]
    delta = jnp.sum(
        dout_pairs.astype(jnp.float32) * attn_out.astype(jnp.float32), axis=-1
    ).reshape(per_dev, 1, SLOT)
    dpairs = attn_backward(sequences, dout_pairs, lse_rows, delta, seg_pairs)
    dreturned = lax.all_to_all(
        pairs_split(dpairs, n_seq), "seq", split_axis=0, concat_axis=0, tiled=True
    )
    dtokens = tokens_back(dreturned, inverse, slot_count, HD)
    dq_rows = unrotate(dtokens[:, :, 0].astype(jnp.float32), cosine, sine_tab).reshape(row_count, D)
    dk_rows = unrotate(dtokens[:, :, 1].astype(jnp.float32), cosine, sine_tab).reshape(row_count, D)
    dv_rows = dtokens[:, :, 2].astype(jnp.float32).reshape(row_count, D)
    dqkv_low = jnp.concatenate([dq_rows, dk_rows, dv_rows], axis=-1).astype(jnp.bfloat16)
    qkv_local = jnp.einsum("nd,nf->df", norm1_low, dqkv_low, preferred_element_type=jnp.float32)
    dnorm1 = jnp.einsum("nf,df->nd", dqkv_low, w_qkv, preferred_element_type=jnp.float32)
    dinput_norm, gain1_local, bias1_local = norm_back(dnorm1, normed1, inv_std1, norm1_gain)
    input_grad = (dmiddle + dinput_norm).astype(jnp.bfloat16)
    def scatter_grad(partial):
        by_cols = lax.psum_scatter(
            partial.astype(jnp.bfloat16), "seq", scatter_dimension=1, tiled=True
        )
        return lax.psum_scatter(by_cols, "batch", scatter_dimension=0, tiled=True).astype(
            jnp.float32
        )

    down_grad = scatter_grad(down_local)
    up_grad = scatter_grad(up_local)
    proj_grad = scatter_grad(proj_local)
    qkv_grad = scatter_grad(qkv_local)
    late_sums = lax.psum(
        lax.psum(jnp.concatenate([gain1_local, bias1_local]), "seq"), "batch"
    )
    gain1_grad, bias1_grad = late_sums[:D], late_sums[D:]
    row_lse = log_total.reshape(1, per_dev, SLOT)
    return (
        block_output,
        input_grad,
        history_grad,
        row_lse,
        qkv_grad,
        proj_grad,
        up_grad,
        down_grad,
        gain1_grad,
        bias1_grad,
        gain2_grad,
        bias2_grad,
        dwa_grad,
    )


def solution(mesh):
    placed = (
        P(("batch", "seq"), None),
        P(None, ("batch", "seq"), None),
        P(("batch", "seq"), None),
        P("batch", "seq"),
        P("batch", "seq"),
        P("batch", "seq"),
        P("batch", "seq"),
        P(),
        P(),
        P(),
        P(),
        P(),
        P("batch", None),
        P("batch", None),
    )
    return jax.shard_map(
        local,
        mesh=mesh,
        in_specs=placed,
        out_specs=(
            P(("batch", "seq"), None),
            P(("batch", "seq"), None),
            P(None, ("batch", "seq"), None),
            P("batch", "seq", None),
            P("batch", "seq"),
            P("batch", "seq"),
            P("batch", "seq"),
            P("batch", "seq"),
            P(),
            P(),
            P(),
            P(),
            P(),
        ),
        check_vma=False,
    )
```

```python
import jax
import jax.numpy as jnp
from jax import lax
from jax.sharding import PartitionSpec as P
from jax.experimental import pallas as pl
from jax.experimental.pallas import tpu as pltpu
import functools

D = 768
HEADS = 12
HD = 64
SLOT = 2048
HIST = 8


NORM_EPS = 1e-05
MASKED = -1e30
NT_DIMS = (((1,), (1,)), ((), ()))


def fwd_kernel(seg_ref, q_ref, k_ref, v_ref, o_ref, lse_ref, *, bq, bk, scale):
    pair = pl.program_id(0)
    qi = pl.program_id(1)
    seg_len = seg_ref[pair]
    q_start = qi * bq
    seg_start = (q_start // seg_len) * seg_len
    query = (q_ref[0, 0].astype(jnp.float32) * scale).astype(jnp.bfloat16)

    def step(j, carry, masked):
        m_old, l_old, acc = carry
        k_off = pl.multiple_of(j * bk, bk)
        key = k_ref[0, 0, pl.ds(k_off, bk), :]
        value = v_ref[0, 0, pl.ds(k_off, bk), :]
        s = lax.dot_general(query, key, NT_DIMS, preferred_element_type=jnp.float32)
        if masked:
            rows = q_start + lax.broadcasted_iota(jnp.int32, (bq, bk), 0)
            cols = k_off + lax.broadcasted_iota(jnp.int32, (bq, bk), 1)
            s = jnp.where(cols <= rows, s, MASKED)
        m_new = jnp.maximum(m_old, jnp.max(s, axis=-1, keepdims=True))
        alpha = jnp.exp(m_old - m_new)
        weights = jnp.exp(s - m_new)
        l_new = alpha * l_old + jnp.sum(weights, axis=-1, keepdims=True)
        acc = alpha * acc + jnp.dot(
            weights.astype(jnp.bfloat16), value, preferred_element_type=jnp.float32
        )
        return m_new, l_new, acc

    carry = (
        jnp.full((bq, 1), MASKED, jnp.float32),
        jnp.zeros((bq, 1), jnp.float32),
        jnp.zeros((bq, HD), jnp.float32),
    )
    j_diag = q_start // bk
    carry = lax.fori_loop(
        seg_start // bk, j_diag, lambda j, c: step(j, c, False), carry
    )
    for r in range(bq // bk):
        carry = step(j_diag + r, carry, True)
    m_fin, l_fin, acc = carry
    o_ref[0] = (acc / l_fin).astype(o_ref.dtype)
    lse = m_fin + jnp.log(l_fin)
    lse_ref[0] = jnp.transpose(jnp.broadcast_to(lse, (bq, 128)))[0:1, :]


def attn_forward(qkv, seg_pairs, bq=512, bk=512):
    pairs, _, seq_len, head_size = qkv.shape
    scale = head_size ** (-0.5)
    n_q = seq_len // bq
    blocks_done = pairs * (seq_len // bk) * (seq_len // bk + 1) // 2
    cost = pl.CostEstimate(
        flops=4 * blocks_done * bk * bk * head_size,
        transcendentals=blocks_done * bk * bk,
        bytes_accessed=pairs * seq_len * head_size * 2 * 4 + pairs * seq_len * 4,
    )
    grid_spec = pltpu.PrefetchScalarGridSpec(
        num_scalar_prefetch=1,
        grid=(pairs, n_q),
        in_specs=[
            pl.BlockSpec((1, 1, bq, head_size), lambda p, i, seg: (p, 0, i, 0)),
            pl.BlockSpec((1, 1, seq_len, head_size), lambda p, i, seg: (p, 1, 0, 0)),
            pl.BlockSpec((1, 1, seq_len, head_size), lambda p, i, seg: (p, 2, 0, 0)),
        ],
        out_specs=[
            pl.BlockSpec((1, bq, head_size), lambda p, i, seg: (p, i, 0)),
            pl.BlockSpec((1, 1, bq), lambda p, i, seg: (p, 0, i)),
        ],
    )
    return pl.pallas_call(
        functools.partial(fwd_kernel, bq=bq, bk=bk, scale=scale),
        grid_spec=grid_spec,
        out_shape=[
            jax.ShapeDtypeStruct((pairs, seq_len, head_size), jnp.bfloat16),
            jax.ShapeDtypeStruct((pairs, 1, seq_len), jnp.float32),
        ],
        cost_estimate=cost,
        name="attn_fwd",
    )(seg_pairs, qkv, qkv, qkv)


def bwd_kernel(seg_ref, q_ref, k_ref, v_ref, do_ref, lse_ref, dl_ref, out_ref, dq_acc, *, bk, bq, scale):
    pair = pl.program_id(0)
    kj = pl.program_id(1)

    @pl.when(kj == 0)
    def _():
        dq_acc[...] = jnp.zeros_like(dq_acc)

    seg_len = seg_ref[pair]
    k_start = kj * bk
    seg_end = (k_start // seg_len + 1) * seg_len
    key = k_ref[0, 0]
    value = (v_ref[0, 0].astype(jnp.float32) * scale).astype(jnp.bfloat16)

    def step(i, carry, masked):
        dk, dv = carry
        q_off = pl.multiple_of(i * bq, bq)
        query = q_ref[0, 0, pl.ds(q_off, bq), :]
        query_s = (query.astype(jnp.float32) * scale).astype(jnp.bfloat16)
        dout = do_ref[0, pl.ds(q_off, bq), :]
        lse = lse_ref[0, :, pl.ds(q_off, bq)]
        delta = dl_ref[0, :, pl.ds(q_off, bq)] * scale
        s_t = lax.dot_general(key, query_s, NT_DIMS, preferred_element_type=jnp.float32)
        if masked:
            keys_at = k_start + lax.broadcasted_iota(jnp.int32, (bk, bq), 0)
            queries_at = q_off + lax.broadcasted_iota(jnp.int32, (bk, bq), 1)
            s_t = jnp.where(keys_at <= queries_at, s_t, MASKED)
        p_t = jnp.exp(s_t - lse)
        dv = dv + jnp.dot(p_t.astype(jnp.bfloat16), dout, preferred_element_type=jnp.float32)
        dp_t = lax.dot_general(value, dout, NT_DIMS, preferred_element_type=jnp.float32)
        ds_t = p_t * (dp_t - delta)
        dk = dk + jnp.dot(ds_t.astype(jnp.bfloat16), query, preferred_element_type=jnp.float32)
        dq_acc[pl.ds(q_off, bq), :] += jnp.dot(
            ds_t.T.astype(jnp.bfloat16), key, preferred_element_type=jnp.float32
        )
        return dk, dv

    carry = (jnp.zeros((bk, HD), jnp.float32), jnp.zeros((bk, HD), jnp.float32))
    for r in range(bk // bq):
        carry = step(k_start // bq + r, carry, True)
    dk, dv = lax.fori_loop(
        (k_start + bk) // bq, seg_end // bq, lambda i, c: step(i, c, False), carry
    )
    out_ref[0, 0] = dq_acc[pl.ds(pl.multiple_of(k_start, bk), bk), :].astype(out_ref.dtype)
    out_ref[0, 1] = dk.astype(out_ref.dtype)
    out_ref[0, 2] = dv.astype(out_ref.dtype)


def attn_backward(qkv, dout, lse, delta, seg_pairs, bk=512, bq=512):
    pairs, _, seq_len, head_size = qkv.shape
    scale = head_size ** (-0.5)
    n_k = seq_len // bk
    blocks_done = pairs * (seq_len // bq) * (seq_len // bq + 1) // 2
    cost = pl.CostEstimate(
        flops=10 * blocks_done * bq * bq * head_size,
        transcendentals=blocks_done * bq * bq,
        bytes_accessed=pairs * seq_len * head_size * 2 * 7 + pairs * seq_len * 8,
    )
    grid_spec = pltpu.PrefetchScalarGridSpec(
        num_scalar_prefetch=1,
        grid=(pairs, n_k),
        in_specs=[
            pl.BlockSpec((1, 1, seq_len, head_size), lambda p, j, seg: (p, 0, 0, 0)),
            pl.BlockSpec((1, 1, bk, head_size), lambda p, j, seg: (p, 1, j, 0)),
            pl.BlockSpec((1, 1, bk, head_size), lambda p, j, seg: (p, 2, j, 0)),
            pl.BlockSpec((1, seq_len, head_size), lambda p, j, seg: (p, 0, 0)),
            pl.BlockSpec((1, 1, seq_len), lambda p, j, seg: (p, 0, 0)),
            pl.BlockSpec((1, 1, seq_len), lambda p, j, seg: (p, 0, 0)),
        ],
        out_specs=pl.BlockSpec((1, 3, bk, head_size), lambda p, j, seg: (p, 0, j, 0)),
        scratch_shapes=[pltpu.VMEM((seq_len, head_size), jnp.float32)],
    )
    return pl.pallas_call(
        functools.partial(bwd_kernel, bk=bk, bq=bq, scale=scale),
        grid_spec=grid_spec,
        out_shape=jax.ShapeDtypeStruct((pairs, 3, seq_len, head_size), jnp.bfloat16),
        cost_estimate=cost,
        name="attn_bwd",
    )(seg_pairs, qkv, qkv, qkv, dout, lse, delta)


def norm_rows(values, gain, shift):
    row_mean = jnp.mean(values, axis=-1, keepdims=True)
    centred = values - row_mean
    variance = jnp.mean(centred * centred, axis=-1, keepdims=True)
    inv_std = lax.rsqrt(variance + NORM_EPS)
    normed = centred * inv_std
    return (normed * gain + shift, normed, inv_std)


def norm_back(grad_in, normed, inv_std, gain):
    scaled = grad_in * gain
    centred = (
        scaled
        - jnp.mean(scaled, axis=-1, keepdims=True)
        - normed * jnp.mean(scaled * normed, axis=-1, keepdims=True)
    )
    return (centred * inv_std, jnp.sum(grad_in * normed, axis=0), jnp.sum(grad_in, axis=0))


def rotate(values, cosine, sine_tab):
    half_size = values.shape[-1] // 2
    front = values[..., :half_size]
    behind = values[..., half_size:]
    cos_part = cosine[..., None, :]
    sin_part = sine_tab[..., None, :]
    return jnp.concatenate(
        [front * cos_part - behind * sin_part, behind * cos_part + front * sin_part], axis=-1
    )


def unrotate(values, cosine, sine_tab):
    half_size = values.shape[-1] // 2
    front = values[..., :half_size]
    behind = values[..., half_size:]
    cos_part = cosine[..., None, :]
    sin_part = sine_tab[..., None, :]
    return jnp.concatenate(
        [front * cos_part + behind * sin_part, behind * cos_part - front * sin_part], axis=-1
    )


def to_pairs(stacked, order_row, n_seq, per_dev):
    slot_count, piece_len, part_count, head_count, head_size = stacked.shape
    reordered = jnp.transpose(stacked, (0, 3, 2, 1, 4)).reshape(
        slot_count * head_count, part_count, piece_len * head_size
    )
    return jnp.take(reordered, order_row, axis=0).reshape(
        n_seq, per_dev, part_count, piece_len * head_size
    )


def pairs_whole(incoming, head_size):
    n_seq, per_dev, part_count, flat_len = incoming.shape
    piece_len = flat_len // head_size
    reordered = jnp.transpose(
        incoming.reshape(n_seq, per_dev, part_count, piece_len, head_size), (1, 2, 0, 3, 4)
    )
    return reordered.reshape(per_dev, part_count, n_seq * piece_len, head_size)


def pairs_split(whole_seq, n_seq):
    per_dev, part_count, seq_len, head_size = whole_seq.shape
    return jnp.transpose(
        whole_seq.reshape(per_dev, part_count, n_seq, seq_len // n_seq * head_size), (2, 0, 1, 3)
    )


def tokens_back(incoming, inverse, slot_count, head_size):
    n_seq, per_dev, part_count, flat_len = incoming.shape
    piece_len = flat_len // head_size
    ordered = jnp.take(incoming.reshape(n_seq * per_dev, part_count, flat_len), inverse, axis=0)
    head_count = n_seq * per_dev // slot_count
    return jnp.transpose(
        ordered.reshape(slot_count, head_count, part_count, piece_len, head_size), (0, 3, 2, 1, 4)
    )


def local(
    block_input,
    history,
    cotangent,
    qkv_weight,
    proj_weight,
    up_weight,
    down_weight,
    norm1_gain,
    norm1_bias,
    norm2_gain,
    norm2_bias,
    dwa_weights,
    pair_order,
    long_group,
):
    n_seq = lax.axis_size("seq")
    row_count = block_input.shape[0]
    piece_len = SLOT // n_seq
    slot_count = row_count // piece_len
    pair_count = slot_count * HEADS
    per_dev = pair_count // n_seq
    slot_flags = long_group[0]
    seg_len = SLOT // jnp.left_shift(jnp.ones_like(slot_flags), slot_flags)
    position = jnp.arange(SLOT, dtype=jnp.int32)
    doc_place = (position[None, :] % seg_len[:, None]).astype(jnp.float32)
    frequency = jnp.power(10000.0, jnp.arange(HD // 2, dtype=jnp.float32) * (-2.0 / HD))
    angles = doc_place[..., None] * frequency
    my_index = lax.axis_index("seq")
    my_start = my_index * piece_len
    cosine = lax.dynamic_slice_in_dim(jnp.cos(angles), my_start, piece_len, 1)
    sine_tab = lax.dynamic_slice_in_dim(jnp.sin(angles), my_start, piece_len, 1)
    order_row = pair_order[0]
    inverse = (
        jnp.zeros((pair_count,), jnp.int32)
        .at[order_row]
        .set(jnp.arange(pair_count, dtype=jnp.int32))
    )
    held_pairs = lax.dynamic_slice_in_dim(order_row, my_index * per_dev, per_dev, 0)
    shards = (qkv_weight, proj_weight, up_weight, down_weight)
    gathered = lax.all_gather(
        jnp.concatenate([w.reshape(-1) for w in shards]), "batch", axis=0
    )
    row_parts = []
    offset = 0
    for w in shards:
        row_parts.append(gathered[:, offset : offset + w.size].reshape(-1, w.shape[1]))
        offset += w.size
    w_qkv, w_proj, w_up, w_down = (
        lax.all_gather(row_parts[0], "seq", axis=1, tiled=True),
        lax.all_gather(row_parts[1], "seq", axis=1, tiled=True),
        lax.all_gather(row_parts[2], "seq", axis=1, tiled=True),
        lax.all_gather(row_parts[3], "seq", axis=1, tiled=True),
    )
    inputs32 = block_input.astype(jnp.float32)
    norm1_out, normed1, inv_std1 = norm_rows(inputs32, norm1_gain, norm1_bias)
    norm1_low = norm1_out.astype(jnp.bfloat16)
    qkv_out = jnp.dot(norm1_low, w_qkv, preferred_element_type=jnp.float32)
    queries = rotate(qkv_out[:, :D].reshape(slot_count, piece_len, HEADS, HD), cosine, sine_tab)
    keys_rot = rotate(
        qkv_out[:, D : 2 * D].reshape(slot_count, piece_len, HEADS, HD), cosine, sine_tab
    )
    values_in = qkv_out[:, 2 * D :].reshape(slot_count, piece_len, HEADS, HD)
    stacked = jnp.stack([queries, keys_rot, values_in], axis=2).astype(jnp.bfloat16)
    incoming = lax.all_to_all(
        to_pairs(stacked, order_row, n_seq, per_dev), "seq", split_axis=0, concat_axis=0, tiled=True
    )
    sequences = pairs_whole(incoming, HD)
    seg_pairs = jnp.take(seg_len, held_pairs // HEADS).astype(jnp.int32)
    attn_out, lse_rows = attn_forward(sequences, seg_pairs)
    attended_pairs = attn_out.reshape(per_dev, 1, SLOT, HD)
    log_total = lse_rows.reshape(per_dev, SLOT)
    returned = lax.all_to_all(
        pairs_split(attended_pairs, n_seq), "seq", split_axis=0, concat_axis=0, tiled=True
    )
    attended = tokens_back(returned, inverse, slot_count, HD).reshape(row_count, D)
    middle = inputs32 + jnp.dot(attended, w_proj, preferred_element_type=jnp.float32)
    norm2_out, normed2, inv_std2 = norm_rows(middle, norm2_gain, norm2_bias)
    norm2_low = norm2_out.astype(jnp.bfloat16)
    hidden_up = jnp.dot(norm2_low, w_up, preferred_element_type=jnp.float32)
    gelu_out, gelu_pull = jax.vjp(lambda hidden: jax.nn.gelu(hidden, approximate=True), hidden_up)
    gelu_low = gelu_out.astype(jnp.bfloat16)
    block_out = middle + jnp.dot(gelu_low, w_down, preferred_element_type=jnp.float32)
    dwa_out = dwa_weights[HIST] * block_out
    for layer_idx in range(HIST):
        dwa_out = dwa_out + dwa_weights[layer_idx] * history[layer_idx].astype(jnp.float32)
    block_output = dwa_out.astype(jnp.bfloat16)
    grad_out = cotangent.astype(jnp.float32)
    history_grad = (dwa_weights[:HIST, None, None] * grad_out[None]).astype(jnp.bfloat16)
    dwa_terms = [
        jnp.sum(history[layer_idx].astype(jnp.float32) * grad_out) for layer_idx in range(HIST)
    ]
    dwa_terms.append(jnp.sum(block_out * grad_out))
    dwa_local = jnp.stack(dwa_terms)
    dy_full = dwa_weights[HIST] * grad_out
    dmlp_low = dy_full.astype(jnp.bfloat16)
    down_local = jnp.einsum("nf,nd->fd", gelu_low, dmlp_low, preferred_element_type=jnp.float32)
    dgelu = jnp.einsum("nd,fd->nf", dmlp_low, w_down, preferred_element_type=jnp.float32)
    dup_low = gelu_pull(dgelu)[0].astype(jnp.bfloat16)
    up_local = jnp.einsum("nd,nf->df", norm2_low, dup_low, preferred_element_type=jnp.float32)
    dnorm2 = jnp.einsum("nf,df->nd", dup_low, w_up, preferred_element_type=jnp.float32)
    dmid_norm, gain2_local, bias2_local = norm_back(dnorm2, normed2, inv_std2, norm2_gain)
    dmiddle = dy_full + dmid_norm
    dmiddle_low = dmiddle.astype(jnp.bfloat16)
    proj_local = jnp.einsum("nd,ne->de", attended, dmiddle_low, preferred_element_type=jnp.float32)
    dattended = jnp.einsum(
        "ne,de->nd", dmiddle_low, w_proj, preferred_element_type=jnp.float32
    ).astype(jnp.bfloat16)
    dattn_tokens = dattended.reshape(slot_count, piece_len, 1, HEADS, HD)
    dattn_in = lax.all_to_all(
        to_pairs(dattn_tokens, order_row, n_seq, per_dev),
        "seq",
        split_axis=0,
        concat_axis=0,
        tiled=True,
    )
    dout_pairs = pairs_whole(dattn_in, HD)[:, 0]
    delta = jnp.sum(
        dout_pairs.astype(jnp.float32) * attn_out.astype(jnp.float32), axis=-1
    ).reshape(per_dev, 1, SLOT)
    dpairs = attn_backward(sequences, dout_pairs, lse_rows, delta, seg_pairs)
    dreturned = lax.all_to_all(
        pairs_split(dpairs, n_seq), "seq", split_axis=0, concat_axis=0, tiled=True
    )
    dtokens = tokens_back(dreturned, inverse, slot_count, HD)
    dq_rows = unrotate(dtokens[:, :, 0].astype(jnp.float32), cosine, sine_tab).reshape(row_count, D)
    dk_rows = unrotate(dtokens[:, :, 1].astype(jnp.float32), cosine, sine_tab).reshape(row_count, D)
    dv_rows = dtokens[:, :, 2].astype(jnp.float32).reshape(row_count, D)
    dqkv_low = jnp.concatenate([dq_rows, dk_rows, dv_rows], axis=-1).astype(jnp.bfloat16)
    qkv_local = jnp.einsum("nd,nf->df", norm1_low, dqkv_low, preferred_element_type=jnp.float32)
    dnorm1 = jnp.einsum("nf,df->nd", dqkv_low, w_qkv, preferred_element_type=jnp.float32)
    dinput_norm, gain1_local, bias1_local = norm_back(dnorm1, normed1, inv_std1, norm1_gain)
    input_grad = (dmiddle + dinput_norm).astype(jnp.bfloat16)
    col_sums = (
        lax.psum_scatter(
            qkv_local.astype(jnp.bfloat16), "seq", scatter_dimension=1, tiled=True
        ).astype(jnp.float32),
        lax.psum_scatter(
            proj_local.astype(jnp.bfloat16), "seq", scatter_dimension=1, tiled=True
        ).astype(jnp.float32),
        lax.psum_scatter(
            up_local.astype(jnp.bfloat16), "seq", scatter_dimension=1, tiled=True
        ).astype(jnp.float32),
        lax.psum_scatter(
            down_local.astype(jnp.bfloat16), "seq", scatter_dimension=1, tiled=True
        ).astype(jnp.float32),
    )
    qkv_grad, proj_grad, up_grad, down_grad = (
        lax.psum_scatter(
            col_sums[0].astype(jnp.bfloat16), "batch", scatter_dimension=0, tiled=True
        ).astype(jnp.float32),
        lax.psum_scatter(
            col_sums[1].astype(jnp.bfloat16), "batch", scatter_dimension=0, tiled=True
        ).astype(jnp.float32),
        lax.psum_scatter(
            col_sums[2].astype(jnp.bfloat16), "batch", scatter_dimension=0, tiled=True
        ).astype(jnp.float32),
        lax.psum_scatter(
            col_sums[3].astype(jnp.bfloat16), "batch", scatter_dimension=0, tiled=True
        ).astype(jnp.float32),
    )
    small_sums = lax.psum(
        lax.psum(
            jnp.concatenate([gain1_local, bias1_local, gain2_local, bias2_local, dwa_local]),
            "seq",
        ),
        "batch",
    )
    gain1_grad, bias1_grad, gain2_grad, bias2_grad = (
        small_sums[k * D : (k + 1) * D] for k in range(4)
    )
    dwa_grad = small_sums[4 * D :]
    row_lse = log_total.reshape(1, per_dev, SLOT)
    return (
        block_output,
        input_grad,
        history_grad,
        row_lse,
        qkv_grad,
        proj_grad,
        up_grad,
        down_grad,
        gain1_grad,
        bias1_grad,
        gain2_grad,
        bias2_grad,
        dwa_grad,
    )


def solution(mesh):
    placed = (
        P(("batch", "seq"), None),
        P(None, ("batch", "seq"), None),
        P(("batch", "seq"), None),
        P("batch", "seq"),
        P("batch", "seq"),
        P("batch", "seq"),
        P("batch", "seq"),
        P(),
        P(),
        P(),
        P(),
        P(),
        P("batch", None),
        P("batch", None),
    )
    return jax.shard_map(
        local,
        mesh=mesh,
        in_specs=placed,
        out_specs=(
            P(("batch", "seq"), None),
            P(("batch", "seq"), None),
            P(None, ("batch", "seq"), None),
            P("batch", "seq", None),
            P("batch", "seq"),
            P("batch", "seq"),
            P("batch", "seq"),
            P("batch", "seq"),
            P(),
            P(),
            P(),
            P(),
            P(),
        ),
        check_vma=False,
    )
```

```python
import jax
import jax.numpy as jnp
from jax import lax
from jax.sharding import PartitionSpec as P
from jax.experimental import pallas as pl
from jax.experimental.pallas import tpu as pltpu
import functools

D = 768
HEADS = 12
HD = 64
SLOT = 2048
HIST = 8


NORM_EPS = 1e-05
MASKED = -1e30
NT_DIMS = (((1,), (1,)), ((), ()))


def fwd_kernel(seg_ref, q_ref, k_ref, v_ref, o_ref, lse_ref, *, bq, bk, scale):
    pair = pl.program_id(0)
    qi = pl.program_id(1)
    seg_len = seg_ref[pair]
    q_start = qi * bq
    seg_start = (q_start // seg_len) * seg_len
    query = (q_ref[0, 0].astype(jnp.float32).T * scale).astype(jnp.bfloat16)

    def step(j, carry, masked):
        m_old, l_old, acc = carry
        k_off = pl.multiple_of(j * bk, bk)
        key_t = k_ref[0, 0, :, pl.ds(k_off, bk)]
        value_t = v_ref[0, 0, :, pl.ds(k_off, bk)]
        s = jnp.dot(query, key_t, preferred_element_type=jnp.float32)
        if masked:
            rows = q_start + lax.broadcasted_iota(jnp.int32, (bq, bk), 0)
            cols = k_off + lax.broadcasted_iota(jnp.int32, (bq, bk), 1)
            s = jnp.where(cols <= rows, s, MASKED)
        m_new = jnp.maximum(m_old, jnp.max(s, axis=-1, keepdims=True))
        alpha = jnp.exp(m_old - m_new)
        weights = jnp.exp(s - m_new)
        l_new = alpha * l_old + jnp.sum(weights, axis=-1, keepdims=True)
        acc = alpha * acc + lax.dot_general(
            weights.astype(jnp.bfloat16), value_t, NT_DIMS, preferred_element_type=jnp.float32
        )
        return m_new, l_new, acc

    carry = (
        jnp.full((bq, 1), MASKED, jnp.float32),
        jnp.zeros((bq, 1), jnp.float32),
        jnp.zeros((bq, HD), jnp.float32),
    )
    j_diag = q_start // bk
    carry = lax.fori_loop(seg_start // bk, j_diag, lambda j, c: step(j, c, False), carry)
    for r in range(bq // bk):
        carry = step(j_diag + r, carry, True)
    m_fin, l_fin, acc = carry
    o_ref[0] = (acc / l_fin).T.astype(o_ref.dtype)
    lse = m_fin + jnp.log(l_fin)
    lse_ref[0] = jnp.transpose(jnp.broadcast_to(lse, (bq, 128)))[0:1, :]


def attn_forward(qkv_t, seg_pairs, bq=512, bk=512):
    pairs, _, head_size, seq_len = qkv_t.shape
    scale = head_size ** (-0.5)
    n_q = seq_len // bq
    blocks_done = pairs * (seq_len // bk) * (seq_len // bk + 1) // 2
    cost = pl.CostEstimate(
        flops=4 * blocks_done * bk * bk * head_size,
        transcendentals=blocks_done * bk * bk,
        bytes_accessed=pairs * seq_len * head_size * 2 * 4 + pairs * seq_len * 4,
    )
    grid_spec = pltpu.PrefetchScalarGridSpec(
        num_scalar_prefetch=1,
        grid=(pairs, n_q),
        in_specs=[
            pl.BlockSpec((1, 1, head_size, bq), lambda p, i, seg: (p, 0, 0, i)),
            pl.BlockSpec((1, 1, head_size, seq_len), lambda p, i, seg: (p, 1, 0, 0)),
            pl.BlockSpec((1, 1, head_size, seq_len), lambda p, i, seg: (p, 2, 0, 0)),
        ],
        out_specs=[
            pl.BlockSpec((1, head_size, bq), lambda p, i, seg: (p, 0, i)),
            pl.BlockSpec((1, 1, bq), lambda p, i, seg: (p, 0, i)),
        ],
    )
    return pl.pallas_call(
        functools.partial(fwd_kernel, bq=bq, bk=bk, scale=scale),
        grid_spec=grid_spec,
        out_shape=[
            jax.ShapeDtypeStruct((pairs, head_size, seq_len), jnp.bfloat16),
            jax.ShapeDtypeStruct((pairs, 1, seq_len), jnp.float32),
        ],
        cost_estimate=cost,
        name="attn_fwd",
    )(seg_pairs, qkv_t, qkv_t, qkv_t)


def bwd_kernel(seg_ref, q_ref, k_ref, v_ref, do_ref, o_ref, lse_ref, out_ref, dq_acc, *, bk, bq, scale):
    pair = pl.program_id(0)
    kj = pl.program_id(1)

    @pl.when(kj == 0)
    def _():
        dq_acc[...] = jnp.zeros_like(dq_acc)

    seg_len = seg_ref[pair]
    k_start = kj * bk
    seg_end = (k_start // seg_len + 1) * seg_len
    key_t = k_ref[0, 0]
    key = key_t.astype(jnp.float32).T.astype(jnp.bfloat16)
    value_s = (v_ref[0, 0].astype(jnp.float32).T * scale).astype(jnp.bfloat16)

    def step(i, carry, masked):
        dk_t, dv_t = carry
        q_off = pl.multiple_of(i * bq, bq)
        query_t = q_ref[0, 0, :, pl.ds(q_off, bq)]
        query_ts = (query_t.astype(jnp.float32) * scale).astype(jnp.bfloat16)
        dout_t = do_ref[0, :, pl.ds(q_off, bq)]
        out_t = o_ref[0, :, pl.ds(q_off, bq)]
        lse = lse_ref[0, :, pl.ds(q_off, bq)]
        delta = jnp.sum(
            dout_t.astype(jnp.float32) * out_t.astype(jnp.float32), axis=0, keepdims=True
        ) * scale
        s_t = jnp.dot(key, query_ts, preferred_element_type=jnp.float32)
        if masked:
            keys_at = k_start + lax.broadcasted_iota(jnp.int32, (bk, bq), 0)
            queries_at = q_off + lax.broadcasted_iota(jnp.int32, (bk, bq), 1)
            s_t = jnp.where(keys_at <= queries_at, s_t, MASKED)
        p_t = jnp.exp(s_t - lse)
        dv_t = dv_t + lax.dot_general(
            dout_t, p_t.astype(jnp.bfloat16), NT_DIMS, preferred_element_type=jnp.float32
        )
        dp_t = jnp.dot(value_s, dout_t, preferred_element_type=jnp.float32)
        ds_t = (p_t * (dp_t - delta)).astype(jnp.bfloat16)
        dk_t = dk_t + lax.dot_general(query_t, ds_t, NT_DIMS, preferred_element_type=jnp.float32)
        dq_acc[:, pl.ds(q_off, bq)] += jnp.dot(key_t, ds_t, preferred_element_type=jnp.float32)
        return dk_t, dv_t

    carry = (jnp.zeros((HD, bk), jnp.float32), jnp.zeros((HD, bk), jnp.float32))
    for r in range(bk // bq):
        carry = step(k_start // bq + r, carry, True)
    dk_t, dv_t = lax.fori_loop(
        (k_start + bk) // bq, seg_end // bq, lambda i, c: step(i, c, False), carry
    )
    out_ref[0, 0] = dq_acc[:, pl.ds(pl.multiple_of(k_start, bk), bk)].astype(out_ref.dtype)
    out_ref[0, 1] = dk_t.astype(out_ref.dtype)
    out_ref[0, 2] = dv_t.astype(out_ref.dtype)


def attn_backward(qkv_t, dout_t, out_t, lse, seg_pairs, bk=512, bq=512):
    pairs, _, head_size, seq_len = qkv_t.shape
    scale = head_size ** (-0.5)
    n_k = seq_len // bk
    blocks_done = pairs * (seq_len // bq) * (seq_len // bq + 1) // 2
    cost = pl.CostEstimate(
        flops=10 * blocks_done * bq * bq * head_size,
        transcendentals=blocks_done * bq * bq,
        bytes_accessed=pairs * seq_len * head_size * 2 * 8 + pairs * seq_len * 4,
    )
    grid_spec = pltpu.PrefetchScalarGridSpec(
        num_scalar_prefetch=1,
        grid=(pairs, n_k),
        in_specs=[
            pl.BlockSpec((1, 1, head_size, seq_len), lambda p, j, seg: (p, 0, 0, 0)),
            pl.BlockSpec((1, 1, head_size, bk), lambda p, j, seg: (p, 1, 0, j)),
            pl.BlockSpec((1, 1, head_size, bk), lambda p, j, seg: (p, 2, 0, j)),
            pl.BlockSpec((1, head_size, seq_len), lambda p, j, seg: (p, 0, 0)),
            pl.BlockSpec((1, head_size, seq_len), lambda p, j, seg: (p, 0, 0)),
            pl.BlockSpec((1, 1, seq_len), lambda p, j, seg: (p, 0, 0)),
        ],
        out_specs=pl.BlockSpec((1, 3, head_size, bk), lambda p, j, seg: (p, 0, 0, j)),
        scratch_shapes=[pltpu.VMEM((head_size, seq_len), jnp.float32)],
    )
    return pl.pallas_call(
        functools.partial(bwd_kernel, bk=bk, bq=bq, scale=scale),
        grid_spec=grid_spec,
        out_shape=jax.ShapeDtypeStruct((pairs, 3, head_size, seq_len), jnp.bfloat16),
        cost_estimate=cost,
        name="attn_bwd",
    )(seg_pairs, qkv_t, qkv_t, qkv_t, dout_t, out_t, lse)


def norm_rows(values, gain, shift):
    row_mean = jnp.mean(values, axis=-1, keepdims=True)
    centred = values - row_mean
    variance = jnp.mean(centred * centred, axis=-1, keepdims=True)
    inv_std = lax.rsqrt(variance + NORM_EPS)
    normed = centred * inv_std
    return (normed * gain + shift, normed, inv_std)


def norm_back(grad_in, normed, inv_std, gain):
    scaled = grad_in * gain
    centred = (
        scaled
        - jnp.mean(scaled, axis=-1, keepdims=True)
        - normed * jnp.mean(scaled * normed, axis=-1, keepdims=True)
    )
    return (centred * inv_std, jnp.sum(grad_in * normed, axis=0), jnp.sum(grad_in, axis=0))


def rotate(values, cosine, sine_tab):
    half_size = values.shape[-1] // 2
    front = values[..., :half_size]
    behind = values[..., half_size:]
    cos_part = cosine[..., None, :]
    sin_part = sine_tab[..., None, :]
    return jnp.concatenate(
        [front * cos_part - behind * sin_part, behind * cos_part + front * sin_part], axis=-1
    )


def unrotate(values, cosine, sine_tab):
    half_size = values.shape[-1] // 2
    front = values[..., :half_size]
    behind = values[..., half_size:]
    cos_part = cosine[..., None, :]
    sin_part = sine_tab[..., None, :]
    return jnp.concatenate(
        [front * cos_part + behind * sin_part, behind * cos_part - front * sin_part], axis=-1
    )


def local(
    block_input,
    history,
    cotangent,
    qkv_weight,
    proj_weight,
    up_weight,
    down_weight,
    norm1_gain,
    norm1_bias,
    norm2_gain,
    norm2_bias,
    dwa_weights,
    pair_order,
    long_group,
):
    n_seq = lax.axis_size("seq")
    row_count = block_input.shape[0]
    piece_len = SLOT // n_seq
    slot_count = row_count // piece_len
    pair_count = slot_count * HEADS
    per_dev = pair_count // n_seq
    slot_flags = long_group[0]
    seg_len = SLOT // jnp.left_shift(jnp.ones_like(slot_flags), slot_flags)
    position = jnp.arange(SLOT, dtype=jnp.int32)
    doc_place = (position[None, :] % seg_len[:, None]).astype(jnp.float32)
    frequency = jnp.power(10000.0, jnp.arange(HD // 2, dtype=jnp.float32) * (-2.0 / HD))
    angles = doc_place[..., None] * frequency
    my_index = lax.axis_index("seq")
    my_start = my_index * piece_len
    cosine = lax.dynamic_slice_in_dim(jnp.cos(angles), my_start, piece_len, 1)
    sine_tab = lax.dynamic_slice_in_dim(jnp.sin(angles), my_start, piece_len, 1)
    head_groups = HEADS // per_dev
    order_row = pair_order[0]
    held_pairs = lax.dynamic_slice_in_dim(order_row, my_index * per_dev, per_dev, 0)
    my_pairs = my_index * per_dev + jnp.arange(per_dev, dtype=jnp.int32)
    seg_pairs = jnp.take(seg_len, my_pairs // HEADS).astype(jnp.int32)
    row_parts = (
        lax.all_gather(qkv_weight, "batch", axis=0, tiled=True),
        lax.all_gather(proj_weight, "batch", axis=0, tiled=True),
        lax.all_gather(up_weight, "batch", axis=0, tiled=True),
        lax.all_gather(down_weight, "batch", axis=0, tiled=True),
    )
    w_qkv, w_proj, w_up, w_down = (
        lax.all_gather(row_parts[0], "seq", axis=1, tiled=True),
        lax.all_gather(row_parts[1], "seq", axis=1, tiled=True),
        lax.all_gather(row_parts[2], "seq", axis=1, tiled=True),
        lax.all_gather(row_parts[3], "seq", axis=1, tiled=True),
    )
    inputs32 = block_input.astype(jnp.float32)
    norm1_out, normed1, inv_std1 = norm_rows(inputs32, norm1_gain, norm1_bias)
    norm1_low = norm1_out.astype(jnp.bfloat16)
    qkv_out = jnp.dot(norm1_low, w_qkv, preferred_element_type=jnp.float32)
    queries = rotate(qkv_out[:, :D].reshape(slot_count, piece_len, HEADS, HD), cosine, sine_tab)
    keys_rot = rotate(
        qkv_out[:, D : 2 * D].reshape(slot_count, piece_len, HEADS, HD), cosine, sine_tab
    )
    values_in = qkv_out[:, 2 * D :].reshape(slot_count, piece_len, HEADS, HD)
    stacked = jnp.stack([queries, keys_rot, values_in], axis=2).astype(jnp.bfloat16)
    send = jnp.transpose(
        stacked.reshape(slot_count, piece_len, 3, head_groups, per_dev, HD), (0, 3, 4, 2, 5, 1)
    ).reshape(n_seq, per_dev, 3, HD, piece_len)
    incoming = lax.all_to_all(send, "seq", split_axis=0, concat_axis=0, tiled=True)
    qkv_t = jnp.transpose(incoming, (1, 2, 3, 0, 4)).reshape(per_dev, 3, HD, SLOT)
    attn_t, lse_rows = attn_forward(qkv_t, seg_pairs)
    back = jnp.transpose(attn_t.reshape(per_dev, HD, n_seq, piece_len), (2, 0, 1, 3))
    returned = lax.all_to_all(back, "seq", split_axis=0, concat_axis=0, tiled=True)
    attended = jnp.transpose(
        returned.reshape(slot_count, head_groups, per_dev, HD, piece_len), (0, 4, 1, 2, 3)
    ).reshape(row_count, D)
    middle = inputs32 + jnp.dot(attended, w_proj, preferred_element_type=jnp.float32)
    norm2_out, normed2, inv_std2 = norm_rows(middle, norm2_gain, norm2_bias)
    norm2_low = norm2_out.astype(jnp.bfloat16)
    hidden_up = jnp.dot(norm2_low, w_up, preferred_element_type=jnp.float32)
    gelu_out, gelu_pull = jax.vjp(lambda hidden: jax.nn.gelu(hidden, approximate=True), hidden_up)
    gelu_low = gelu_out.astype(jnp.bfloat16)
    block_out = middle + jnp.dot(gelu_low, w_down, preferred_element_type=jnp.float32)
    dwa_out = dwa_weights[HIST] * block_out
    for layer_idx in range(HIST):
        dwa_out = dwa_out + dwa_weights[layer_idx] * history[layer_idx].astype(jnp.float32)
    block_output = dwa_out.astype(jnp.bfloat16)
    grad_out = cotangent.astype(jnp.float32)
    history_grad = (dwa_weights[:HIST, None, None] * grad_out[None]).astype(jnp.bfloat16)
    dwa_terms = [
        jnp.sum(history[layer_idx].astype(jnp.float32) * grad_out) for layer_idx in range(HIST)
    ]
    dwa_terms.append(jnp.sum(block_out * grad_out))
    dwa_local = jnp.stack(dwa_terms)
    dy_full = dwa_weights[HIST] * grad_out
    dmlp_low = dy_full.astype(jnp.bfloat16)
    down_local = jnp.einsum("nf,nd->fd", gelu_low, dmlp_low, preferred_element_type=jnp.float32)
    dgelu = jnp.einsum("nd,fd->nf", dmlp_low, w_down, preferred_element_type=jnp.float32)
    dup_low = gelu_pull(dgelu)[0].astype(jnp.bfloat16)
    up_local = jnp.einsum("nd,nf->df", norm2_low, dup_low, preferred_element_type=jnp.float32)
    dnorm2 = jnp.einsum("nf,df->nd", dup_low, w_up, preferred_element_type=jnp.float32)
    dmid_norm, gain2_local, bias2_local = norm_back(dnorm2, normed2, inv_std2, norm2_gain)
    dmiddle = dy_full + dmid_norm
    dmiddle_low = dmiddle.astype(jnp.bfloat16)
    proj_local = jnp.einsum("nd,ne->de", attended, dmiddle_low, preferred_element_type=jnp.float32)
    dattended = jnp.einsum(
        "ne,de->nd", dmiddle_low, w_proj, preferred_element_type=jnp.float32
    ).astype(jnp.bfloat16)
    dsend = jnp.transpose(
        dattended.reshape(slot_count, piece_len, head_groups, per_dev, HD), (0, 2, 3, 4, 1)
    ).reshape(n_seq, per_dev, HD, piece_len)
    dattn_in = lax.all_to_all(dsend, "seq", split_axis=0, concat_axis=0, tiled=True)
    dout_t = jnp.transpose(dattn_in, (1, 2, 0, 3)).reshape(per_dev, HD, SLOT)
    dpairs = attn_backward(qkv_t, dout_t, attn_t, lse_rows, seg_pairs)
    dback = jnp.transpose(
        dpairs.reshape(per_dev, 3, HD, n_seq, piece_len), (3, 0, 1, 2, 4)
    )
    dreturned = lax.all_to_all(dback, "seq", split_axis=0, concat_axis=0, tiled=True)
    dtokens = jnp.transpose(
        dreturned.reshape(slot_count, head_groups, per_dev, 3, HD, piece_len), (0, 5, 3, 1, 2, 4)
    ).reshape(slot_count, piece_len, 3, HEADS, HD)
    dq_rows = unrotate(dtokens[:, :, 0].astype(jnp.float32), cosine, sine_tab).reshape(row_count, D)
    dk_rows = unrotate(dtokens[:, :, 1].astype(jnp.float32), cosine, sine_tab).reshape(row_count, D)
    dv_rows = dtokens[:, :, 2].astype(jnp.float32).reshape(row_count, D)
    dqkv_low = jnp.concatenate([dq_rows, dk_rows, dv_rows], axis=-1).astype(jnp.bfloat16)
    qkv_local = jnp.einsum("nd,nf->df", norm1_low, dqkv_low, preferred_element_type=jnp.float32)
    dnorm1 = jnp.einsum("nf,df->nd", dqkv_low, w_qkv, preferred_element_type=jnp.float32)
    dinput_norm, gain1_local, bias1_local = norm_back(dnorm1, normed1, inv_std1, norm1_gain)
    input_grad = (dmiddle + dinput_norm).astype(jnp.bfloat16)
    col_sums = (
        lax.psum_scatter(
            qkv_local.astype(jnp.bfloat16), "seq", scatter_dimension=1, tiled=True
        ).astype(jnp.float32),
        lax.psum_scatter(
            proj_local.astype(jnp.bfloat16), "seq", scatter_dimension=1, tiled=True
        ).astype(jnp.float32),
        lax.psum_scatter(
            up_local.astype(jnp.bfloat16), "seq", scatter_dimension=1, tiled=True
        ).astype(jnp.float32),
        lax.psum_scatter(
            down_local.astype(jnp.bfloat16), "seq", scatter_dimension=1, tiled=True
        ).astype(jnp.float32),
    )
    qkv_grad, proj_grad, up_grad, down_grad = (
        lax.psum_scatter(
            col_sums[0].astype(jnp.bfloat16), "batch", scatter_dimension=0, tiled=True
        ).astype(jnp.float32),
        lax.psum_scatter(
            col_sums[1].astype(jnp.bfloat16), "batch", scatter_dimension=0, tiled=True
        ).astype(jnp.float32),
        lax.psum_scatter(
            col_sums[2].astype(jnp.bfloat16), "batch", scatter_dimension=0, tiled=True
        ).astype(jnp.float32),
        lax.psum_scatter(
            col_sums[3].astype(jnp.bfloat16), "batch", scatter_dimension=0, tiled=True
        ).astype(jnp.float32),
    )
    small_sums = lax.psum(
        lax.psum(
            jnp.concatenate([gain1_local, bias1_local, gain2_local, bias2_local, dwa_local]),
            "seq",
        ),
        "batch",
    )
    gain1_grad, bias1_grad, gain2_grad, bias2_grad = (
        small_sums[k * D : (k + 1) * D] for k in range(4)
    )
    dwa_grad = small_sums[4 * D :]
    lse_all = lax.all_gather(lse_rows.reshape(per_dev, SLOT), "seq", axis=0, tiled=True)
    row_lse = jnp.take(lse_all, held_pairs, axis=0).reshape(1, per_dev, SLOT)
    return (
        block_output,
        input_grad,
        history_grad,
        row_lse,
        qkv_grad,
        proj_grad,
        up_grad,
        down_grad,
        gain1_grad,
        bias1_grad,
        gain2_grad,
        bias2_grad,
        dwa_grad,
    )


def solution(mesh):
    placed = (
        P(("batch", "seq"), None),
        P(None, ("batch", "seq"), None),
        P(("batch", "seq"), None),
        P("batch", "seq"),
        P("batch", "seq"),
        P("batch", "seq"),
        P("batch", "seq"),
        P(),
        P(),
        P(),
        P(),
        P(),
        P("batch", None),
        P("batch", None),
    )
    return jax.shard_map(
        local,
        mesh=mesh,
        in_specs=placed,
        out_specs=(
            P(("batch", "seq"), None),
            P(("batch", "seq"), None),
            P(None, ("batch", "seq"), None),
            P("batch", "seq", None),
            P("batch", "seq"),
            P("batch", "seq"),
            P("batch", "seq"),
            P("batch", "seq"),
            P(),
            P(),
            P(),
            P(),
            P(),
        ),
        check_vma=False,
    )
```

```python
import jax
import jax.numpy as jnp
from jax import lax
from jax.sharding import PartitionSpec as P
from jax.experimental import pallas as pl
from jax.experimental.pallas import tpu as pltpu
import functools

D = 768
HEADS = 12
HD = 64
SLOT = 2048
HIST = 8


NORM_EPS = 1e-05
MASKED = -1e30
NT_DIMS = (((1,), (1,)), ((), ()))


def fwd_kernel(seg_ref, q_ref, k_ref, v_ref, o_ref, lse_ref, *, bq, bk, scale):
    pair = pl.program_id(0)
    qi = pl.program_id(1)
    seg_len = seg_ref[pair]
    q_start = qi * bq
    seg_start = (q_start // seg_len) * seg_len
    query = (q_ref[0, 0].astype(jnp.float32).T * scale).astype(jnp.bfloat16)

    def step(j, carry, masked):
        m_old, l_old, acc = carry
        k_off = pl.multiple_of(j * bk, bk)
        key_t = k_ref[0, 0, :, pl.ds(k_off, bk)]
        value_t = v_ref[0, 0, :, pl.ds(k_off, bk)]
        s = jnp.dot(query, key_t, preferred_element_type=jnp.float32)
        if masked:
            rows = q_start + lax.broadcasted_iota(jnp.int32, (bq, bk), 0)
            cols = k_off + lax.broadcasted_iota(jnp.int32, (bq, bk), 1)
            s = jnp.where(cols <= rows, s, MASKED)
        m_new = jnp.maximum(m_old, jnp.max(s, axis=-1, keepdims=True))
        alpha = jnp.exp(m_old - m_new)
        weights = jnp.exp(s - m_new)
        l_new = alpha * l_old + jnp.sum(weights, axis=-1, keepdims=True)
        acc = alpha * acc + lax.dot_general(
            weights.astype(jnp.bfloat16), value_t, NT_DIMS, preferred_element_type=jnp.float32
        )
        return m_new, l_new, acc

    carry = (
        jnp.full((bq, 1), MASKED, jnp.float32),
        jnp.zeros((bq, 1), jnp.float32),
        jnp.zeros((bq, HD), jnp.float32),
    )
    j_diag = q_start // bk
    carry = lax.fori_loop(seg_start // bk, j_diag, lambda j, c: step(j, c, False), carry)
    for r in range(bq // bk):
        carry = step(j_diag + r, carry, True)
    m_fin, l_fin, acc = carry
    o_ref[0] = (acc / l_fin).T.astype(o_ref.dtype)
    lse = m_fin + jnp.log(l_fin)
    lse_ref[0] = jnp.transpose(jnp.broadcast_to(lse, (bq, 128)))[0:1, :]


def attn_forward(qkv_t, seg_pairs, bq=512, bk=512):
    pairs, _, head_size, seq_len = qkv_t.shape
    scale = head_size ** (-0.5)
    n_q = seq_len // bq
    blocks_done = pairs * (seq_len // bk) * (seq_len // bk + 1) // 2
    cost = pl.CostEstimate(
        flops=4 * blocks_done * bk * bk * head_size,
        transcendentals=blocks_done * bk * bk,
        bytes_accessed=pairs * seq_len * head_size * 2 * 4 + pairs * seq_len * 4,
    )
    grid_spec = pltpu.PrefetchScalarGridSpec(
        num_scalar_prefetch=1,
        grid=(pairs, n_q),
        in_specs=[
            pl.BlockSpec((1, 1, head_size, bq), lambda p, i, seg: (p, 0, 0, i)),
            pl.BlockSpec((1, 1, head_size, seq_len), lambda p, i, seg: (p, 1, 0, 0)),
            pl.BlockSpec((1, 1, head_size, seq_len), lambda p, i, seg: (p, 2, 0, 0)),
        ],
        out_specs=[
            pl.BlockSpec((1, head_size, bq), lambda p, i, seg: (p, 0, i)),
            pl.BlockSpec((1, 1, bq), lambda p, i, seg: (p, 0, i)),
        ],
    )
    return pl.pallas_call(
        functools.partial(fwd_kernel, bq=bq, bk=bk, scale=scale),
        grid_spec=grid_spec,
        out_shape=[
            jax.ShapeDtypeStruct((pairs, head_size, seq_len), jnp.bfloat16),
            jax.ShapeDtypeStruct((pairs, 1, seq_len), jnp.float32),
        ],
        cost_estimate=cost,
        name="attn_fwd",
    )(seg_pairs, qkv_t, qkv_t, qkv_t)


def bwd_kernel(seg_ref, q_ref, k_ref, v_ref, do_ref, o_ref, lse_ref, out_ref, dq_acc, *, bk, bq, scale):
    pair = pl.program_id(0)
    kj = pl.program_id(1)

    @pl.when(kj == 0)
    def _():
        dq_acc[...] = jnp.zeros_like(dq_acc)

    seg_len = seg_ref[pair]
    k_start = kj * bk
    seg_end = (k_start // seg_len + 1) * seg_len
    key_t = k_ref[0, 0]
    key = key_t.astype(jnp.float32).T.astype(jnp.bfloat16)
    value_s = (v_ref[0, 0].astype(jnp.float32).T * scale).astype(jnp.bfloat16)

    def step(i, carry, masked):
        dk_t, dv_t = carry
        q_off = pl.multiple_of(i * bq, bq)
        query_t = q_ref[0, 0, :, pl.ds(q_off, bq)]
        query_ts = (query_t.astype(jnp.float32) * scale).astype(jnp.bfloat16)
        dout_t = do_ref[0, :, pl.ds(q_off, bq)]
        out_t = o_ref[0, :, pl.ds(q_off, bq)]
        lse = lse_ref[0, :, pl.ds(q_off, bq)]
        delta = jnp.sum(
            dout_t.astype(jnp.float32) * out_t.astype(jnp.float32), axis=0, keepdims=True
        ) * scale
        s_t = jnp.dot(key, query_ts, preferred_element_type=jnp.float32)
        if masked:
            keys_at = k_start + lax.broadcasted_iota(jnp.int32, (bk, bq), 0)
            queries_at = q_off + lax.broadcasted_iota(jnp.int32, (bk, bq), 1)
            s_t = jnp.where(keys_at <= queries_at, s_t, MASKED)
        p_t = jnp.exp(s_t - lse)
        dv_t = dv_t + lax.dot_general(
            dout_t, p_t.astype(jnp.bfloat16), NT_DIMS, preferred_element_type=jnp.float32
        )
        dp_t = jnp.dot(value_s, dout_t, preferred_element_type=jnp.float32)
        ds_t = (p_t * (dp_t - delta)).astype(jnp.bfloat16)
        dk_t = dk_t + lax.dot_general(query_t, ds_t, NT_DIMS, preferred_element_type=jnp.float32)
        dq_acc[:, pl.ds(q_off, bq)] += jnp.dot(key_t, ds_t, preferred_element_type=jnp.float32)
        return dk_t, dv_t

    carry = (jnp.zeros((HD, bk), jnp.float32), jnp.zeros((HD, bk), jnp.float32))
    for r in range(bk // bq):
        carry = step(k_start // bq + r, carry, True)
    dk_t, dv_t = lax.fori_loop(
        (k_start + bk) // bq, seg_end // bq, lambda i, c: step(i, c, False), carry
    )
    out_ref[0, 0] = dq_acc[:, pl.ds(pl.multiple_of(k_start, bk), bk)].astype(out_ref.dtype)
    out_ref[0, 1] = dk_t.astype(out_ref.dtype)
    out_ref[0, 2] = dv_t.astype(out_ref.dtype)


def attn_backward(qkv_t, dout_t, out_t, lse, seg_pairs, bk=512, bq=512):
    pairs, _, head_size, seq_len = qkv_t.shape
    scale = head_size ** (-0.5)
    n_k = seq_len // bk
    blocks_done = pairs * (seq_len // bq) * (seq_len // bq + 1) // 2
    cost = pl.CostEstimate(
        flops=10 * blocks_done * bq * bq * head_size,
        transcendentals=blocks_done * bq * bq,
        bytes_accessed=pairs * seq_len * head_size * 2 * 8 + pairs * seq_len * 4,
    )
    grid_spec = pltpu.PrefetchScalarGridSpec(
        num_scalar_prefetch=1,
        grid=(pairs, n_k),
        in_specs=[
            pl.BlockSpec((1, 1, head_size, seq_len), lambda p, j, seg: (p, 0, 0, 0)),
            pl.BlockSpec((1, 1, head_size, bk), lambda p, j, seg: (p, 1, 0, j)),
            pl.BlockSpec((1, 1, head_size, bk), lambda p, j, seg: (p, 2, 0, j)),
            pl.BlockSpec((1, head_size, seq_len), lambda p, j, seg: (p, 0, 0)),
            pl.BlockSpec((1, head_size, seq_len), lambda p, j, seg: (p, 0, 0)),
            pl.BlockSpec((1, 1, seq_len), lambda p, j, seg: (p, 0, 0)),
        ],
        out_specs=pl.BlockSpec((1, 3, head_size, bk), lambda p, j, seg: (p, 0, 0, j)),
        scratch_shapes=[pltpu.VMEM((head_size, seq_len), jnp.float32)],
    )
    return pl.pallas_call(
        functools.partial(bwd_kernel, bk=bk, bq=bq, scale=scale),
        grid_spec=grid_spec,
        out_shape=jax.ShapeDtypeStruct((pairs, 3, head_size, seq_len), jnp.bfloat16),
        cost_estimate=cost,
        name="attn_bwd",
    )(seg_pairs, qkv_t, qkv_t, qkv_t, dout_t, out_t, lse)


def norm_rows(values, gain, shift):
    row_mean = jnp.mean(values, axis=-1, keepdims=True)
    centred = values - row_mean
    variance = jnp.mean(centred * centred, axis=-1, keepdims=True)
    inv_std = lax.rsqrt(variance + NORM_EPS)
    normed = centred * inv_std
    return (normed * gain + shift, normed, inv_std)


def norm_back(grad_in, normed, inv_std, gain):
    scaled = grad_in * gain
    centred = (
        scaled
        - jnp.mean(scaled, axis=-1, keepdims=True)
        - normed * jnp.mean(scaled * normed, axis=-1, keepdims=True)
    )
    return (centred * inv_std, jnp.sum(grad_in * normed, axis=0), jnp.sum(grad_in, axis=0))


def rotate(values, cosine, sine_tab):
    half_size = values.shape[-1] // 2
    front = values[..., :half_size]
    behind = values[..., half_size:]
    cos_part = cosine[..., None, :]
    sin_part = sine_tab[..., None, :]
    return jnp.concatenate(
        [front * cos_part - behind * sin_part, behind * cos_part + front * sin_part], axis=-1
    )


def unrotate(values, cosine, sine_tab):
    half_size = values.shape[-1] // 2
    front = values[..., :half_size]
    behind = values[..., half_size:]
    cos_part = cosine[..., None, :]
    sin_part = sine_tab[..., None, :]
    return jnp.concatenate(
        [front * cos_part + behind * sin_part, behind * cos_part - front * sin_part], axis=-1
    )


def local(
    block_input,
    history,
    cotangent,
    qkv_weight,
    proj_weight,
    up_weight,
    down_weight,
    norm1_gain,
    norm1_bias,
    norm2_gain,
    norm2_bias,
    dwa_weights,
    pair_order,
    long_group,
):
    n_seq = lax.axis_size("seq")
    row_count = block_input.shape[0]
    piece_len = SLOT // n_seq
    slot_count = row_count // piece_len
    pair_count = slot_count * HEADS
    per_dev = pair_count // n_seq
    slot_flags = long_group[0]
    seg_len = SLOT // jnp.left_shift(jnp.ones_like(slot_flags), slot_flags)
    position = jnp.arange(SLOT, dtype=jnp.int32)
    doc_place = (position[None, :] % seg_len[:, None]).astype(jnp.float32)
    frequency = jnp.power(10000.0, jnp.arange(HD // 2, dtype=jnp.float32) * (-2.0 / HD))
    angles = doc_place[..., None] * frequency
    my_index = lax.axis_index("seq")
    my_start = my_index * piece_len
    cosine = lax.dynamic_slice_in_dim(jnp.cos(angles), my_start, piece_len, 1)
    sine_tab = lax.dynamic_slice_in_dim(jnp.sin(angles), my_start, piece_len, 1)
    head_groups = HEADS // per_dev
    order_row = pair_order[0]
    held_pairs = lax.dynamic_slice_in_dim(order_row, my_index * per_dev, per_dev, 0)
    my_pairs = my_index * per_dev + jnp.arange(per_dev, dtype=jnp.int32)
    seg_pairs = jnp.take(seg_len, my_pairs // HEADS).astype(jnp.int32)
    w_qkv = lax.all_gather(
        lax.all_gather(qkv_weight, "batch", axis=0, tiled=True), "seq", axis=1, tiled=True
    )
    later = (proj_weight, up_weight, down_weight)
    inputs32 = block_input.astype(jnp.float32)
    norm1_out, normed1, inv_std1 = norm_rows(inputs32, norm1_gain, norm1_bias)
    norm1_low = norm1_out.astype(jnp.bfloat16)
    qkv_out = jnp.dot(norm1_low, w_qkv, preferred_element_type=jnp.float32)
    queries = rotate(qkv_out[:, :D].reshape(slot_count, piece_len, HEADS, HD), cosine, sine_tab)
    keys_rot = rotate(
        qkv_out[:, D : 2 * D].reshape(slot_count, piece_len, HEADS, HD), cosine, sine_tab
    )
    values_in = qkv_out[:, 2 * D :].reshape(slot_count, piece_len, HEADS, HD)
    stacked = jnp.stack([queries, keys_rot, values_in], axis=2).astype(jnp.bfloat16)
    send = jnp.transpose(
        stacked.reshape(slot_count, piece_len, 3, head_groups, per_dev, HD), (0, 3, 4, 2, 5, 1)
    ).reshape(n_seq, per_dev, 3, HD, piece_len)
    incoming = lax.all_to_all(send, "seq", split_axis=0, concat_axis=0, tiled=True)
    later_rows = lax.all_gather(jnp.concatenate([w.reshape(-1) for w in later]), "batch", axis=0)
    offset = 0
    later_full = []
    for w in later:
        rows = later_rows[:, offset : offset + w.size].reshape(-1, w.shape[1])
        later_full.append(lax.all_gather(rows, "seq", axis=1, tiled=True))
        offset += w.size
    w_proj, w_up, w_down = later_full
    qkv_t = jnp.transpose(incoming, (1, 2, 3, 0, 4)).reshape(per_dev, 3, HD, SLOT)
    attn_t, lse_rows = attn_forward(qkv_t, seg_pairs)
    back = jnp.transpose(attn_t.reshape(per_dev, HD, n_seq, piece_len), (2, 0, 1, 3))
    returned = lax.all_to_all(back, "seq", split_axis=0, concat_axis=0, tiled=True)
    lse_all = lax.all_gather(lse_rows.reshape(per_dev, SLOT), "seq", axis=0, tiled=True)
    lse_all, returned = lax.optimization_barrier((lse_all, returned))
    attended = jnp.transpose(
        returned.reshape(slot_count, head_groups, per_dev, HD, piece_len), (0, 4, 1, 2, 3)
    ).reshape(row_count, D)
    middle = inputs32 + jnp.dot(attended, w_proj, preferred_element_type=jnp.float32)
    norm2_out, normed2, inv_std2 = norm_rows(middle, norm2_gain, norm2_bias)
    norm2_low = norm2_out.astype(jnp.bfloat16)
    hidden_up = jnp.dot(norm2_low, w_up, preferred_element_type=jnp.float32)
    gelu_out, gelu_pull = jax.vjp(lambda hidden: jax.nn.gelu(hidden, approximate=True), hidden_up)
    gelu_low = gelu_out.astype(jnp.bfloat16)
    block_out = middle + jnp.dot(gelu_low, w_down, preferred_element_type=jnp.float32)
    dwa_out = dwa_weights[HIST] * block_out
    for layer_idx in range(HIST):
        dwa_out = dwa_out + dwa_weights[layer_idx] * history[layer_idx].astype(jnp.float32)
    block_output = dwa_out.astype(jnp.bfloat16)
    grad_out = cotangent.astype(jnp.float32)
    history_grad = (dwa_weights[:HIST, None, None] * grad_out[None]).astype(jnp.bfloat16)
    dwa_terms = [
        jnp.sum(history[layer_idx].astype(jnp.float32) * grad_out) for layer_idx in range(HIST)
    ]
    dwa_terms.append(jnp.sum(block_out * grad_out))
    dwa_local = jnp.stack(dwa_terms)
    dy_full = dwa_weights[HIST] * grad_out
    dmlp_low = dy_full.astype(jnp.bfloat16)
    down_local = jnp.einsum("nf,nd->fd", gelu_low, dmlp_low, preferred_element_type=jnp.float32)
    dgelu = jnp.einsum("nd,fd->nf", dmlp_low, w_down, preferred_element_type=jnp.float32)
    dup_low = gelu_pull(dgelu)[0].astype(jnp.bfloat16)
    up_local = jnp.einsum("nd,nf->df", norm2_low, dup_low, preferred_element_type=jnp.float32)
    dnorm2 = jnp.einsum("nf,df->nd", dup_low, w_up, preferred_element_type=jnp.float32)
    dmid_norm, gain2_local, bias2_local = norm_back(dnorm2, normed2, inv_std2, norm2_gain)
    dmiddle = dy_full + dmid_norm
    dmiddle_low = dmiddle.astype(jnp.bfloat16)
    proj_local = jnp.einsum("nd,ne->de", attended, dmiddle_low, preferred_element_type=jnp.float32)
    dattended = jnp.einsum(
        "ne,de->nd", dmiddle_low, w_proj, preferred_element_type=jnp.float32
    ).astype(jnp.bfloat16)
    dsend = jnp.transpose(
        dattended.reshape(slot_count, piece_len, head_groups, per_dev, HD), (0, 2, 3, 4, 1)
    ).reshape(n_seq, per_dev, HD, piece_len)
    dattn_in = lax.all_to_all(dsend, "seq", split_axis=0, concat_axis=0, tiled=True)
    dout_t = jnp.transpose(dattn_in, (1, 2, 0, 3)).reshape(per_dev, HD, SLOT)
    dpairs = attn_backward(qkv_t, dout_t, attn_t, lse_rows, seg_pairs)
    dback = jnp.transpose(
        dpairs.reshape(per_dev, 3, HD, n_seq, piece_len), (3, 0, 1, 2, 4)
    )
    dreturned = lax.all_to_all(dback, "seq", split_axis=0, concat_axis=0, tiled=True)
    dtokens = jnp.transpose(
        dreturned.reshape(slot_count, head_groups, per_dev, 3, HD, piece_len), (0, 5, 3, 1, 2, 4)
    ).reshape(slot_count, piece_len, 3, HEADS, HD)
    dq_rows = unrotate(dtokens[:, :, 0].astype(jnp.float32), cosine, sine_tab).reshape(row_count, D)
    dk_rows = unrotate(dtokens[:, :, 1].astype(jnp.float32), cosine, sine_tab).reshape(row_count, D)
    dv_rows = dtokens[:, :, 2].astype(jnp.float32).reshape(row_count, D)
    dqkv_low = jnp.concatenate([dq_rows, dk_rows, dv_rows], axis=-1).astype(jnp.bfloat16)
    qkv_local = jnp.einsum("nd,nf->df", norm1_low, dqkv_low, preferred_element_type=jnp.float32)
    dnorm1 = jnp.einsum("nf,df->nd", dqkv_low, w_qkv, preferred_element_type=jnp.float32)
    dinput_norm, gain1_local, bias1_local = norm_back(dnorm1, normed1, inv_std1, norm1_gain)
    input_grad = (dmiddle + dinput_norm).astype(jnp.bfloat16)
    col_sums = (
        lax.psum_scatter(
            qkv_local.astype(jnp.bfloat16), "seq", scatter_dimension=1, tiled=True
        ).astype(jnp.float32),
        lax.psum_scatter(
            proj_local.astype(jnp.bfloat16), "seq", scatter_dimension=1, tiled=True
        ).astype(jnp.float32),
        lax.psum_scatter(
            up_local.astype(jnp.bfloat16), "seq", scatter_dimension=1, tiled=True
        ).astype(jnp.float32),
        lax.psum_scatter(
            down_local.astype(jnp.bfloat16), "seq", scatter_dimension=1, tiled=True
        ).astype(jnp.float32),
    )
    qkv_grad, proj_grad, up_grad, down_grad = (
        lax.psum_scatter(
            col_sums[0].astype(jnp.bfloat16), "batch", scatter_dimension=0, tiled=True
        ).astype(jnp.float32),
        lax.psum_scatter(
            col_sums[1].astype(jnp.bfloat16), "batch", scatter_dimension=0, tiled=True
        ).astype(jnp.float32),
        lax.psum_scatter(
            col_sums[2].astype(jnp.bfloat16), "batch", scatter_dimension=0, tiled=True
        ).astype(jnp.float32),
        lax.psum_scatter(
            col_sums[3].astype(jnp.bfloat16), "batch", scatter_dimension=0, tiled=True
        ).astype(jnp.float32),
    )
    small_sums = lax.psum(
        lax.psum(
            jnp.concatenate([gain1_local, bias1_local, gain2_local, bias2_local, dwa_local]),
            "seq",
        ),
        "batch",
    )
    gain1_grad, bias1_grad, gain2_grad, bias2_grad = (
        small_sums[k * D : (k + 1) * D] for k in range(4)
    )
    dwa_grad = small_sums[4 * D :]
    row_lse = jnp.take(lse_all, held_pairs, axis=0).reshape(1, per_dev, SLOT)
    return (
        block_output,
        input_grad,
        history_grad,
        row_lse,
        qkv_grad,
        proj_grad,
        up_grad,
        down_grad,
        gain1_grad,
        bias1_grad,
        gain2_grad,
        bias2_grad,
        dwa_grad,
    )


def solution(mesh):
    placed = (
        P(("batch", "seq"), None),
        P(None, ("batch", "seq"), None),
        P(("batch", "seq"), None),
        P("batch", "seq"),
        P("batch", "seq"),
        P("batch", "seq"),
        P("batch", "seq"),
        P(),
        P(),
        P(),
        P(),
        P(),
        P("batch", None),
        P("batch", None),
    )

    return jax.shard_map(
        local,
        mesh=mesh,
        in_specs=placed,
        out_specs=(
            P(("batch", "seq"), None),
            P(("batch", "seq"), None),
            P(None, ("batch", "seq"), None),
            P("batch", "seq", None),
            P("batch", "seq"),
            P("batch", "seq"),
            P("batch", "seq"),
            P("batch", "seq"),
            P(),
            P(),
            P(),
            P(),
            P(),
        ),
        check_vma=False,
    )
```

```python
import jax
import jax.numpy as jnp
from jax import lax
from jax.sharding import PartitionSpec as P
from jax.experimental import pallas as pl
from jax.experimental.pallas import tpu as pltpu
import functools

D = 768
HEADS = 12
HD = 64
SLOT = 2048
HIST = 8


NORM_EPS = 1e-05
MASKED = -1e30
NT_DIMS = (((1,), (1,)), ((), ()))


def fwd_kernel(seg_ref, q_ref, k_ref, v_ref, o_ref, lse_ref, *, bq, bk, scale):
    pair = pl.program_id(0)
    qi = pl.program_id(1)
    seg_len = seg_ref[pair]
    q_start = qi * bq
    seg_start = (q_start // seg_len) * seg_len
    query = (q_ref[0, 0].astype(jnp.float32).T * scale).astype(jnp.bfloat16)

    def step(j, carry, masked):
        m_old, l_old, acc = carry
        k_off = pl.multiple_of(j * bk, bk)
        key_t = k_ref[0, 0, :, pl.ds(k_off, bk)]
        value_t = v_ref[0, 0, :, pl.ds(k_off, bk)]
        s = jnp.dot(query, key_t, preferred_element_type=jnp.float32)
        if masked:
            rows = q_start + lax.broadcasted_iota(jnp.int32, (bq, bk), 0)
            cols = k_off + lax.broadcasted_iota(jnp.int32, (bq, bk), 1)
            s = jnp.where(cols <= rows, s, MASKED)
        m_new = jnp.maximum(m_old, jnp.max(s, axis=-1, keepdims=True))
        alpha = jnp.exp(m_old - m_new)
        weights = jnp.exp(s - m_new)
        l_new = alpha * l_old + jnp.sum(weights, axis=-1, keepdims=True)
        acc = alpha * acc + lax.dot_general(
            weights.astype(jnp.bfloat16), value_t, NT_DIMS, preferred_element_type=jnp.float32
        )
        return m_new, l_new, acc

    carry = (
        jnp.full((bq, 1), MASKED, jnp.float32),
        jnp.zeros((bq, 1), jnp.float32),
        jnp.zeros((bq, HD), jnp.float32),
    )
    j_diag = q_start // bk
    carry = lax.fori_loop(seg_start // bk, j_diag, lambda j, c: step(j, c, False), carry)
    for r in range(bq // bk):
        carry = step(j_diag + r, carry, True)
    m_fin, l_fin, acc = carry
    o_ref[0] = (acc / l_fin).T.astype(o_ref.dtype)
    lse = m_fin + jnp.log(l_fin)
    lse_ref[0] = jnp.transpose(jnp.broadcast_to(lse, (bq, 128)))[0:1, :]


def attn_forward(qkv_t, seg_pairs, bq=512, bk=512):
    pairs, _, head_size, seq_len = qkv_t.shape
    scale = head_size ** (-0.5)
    n_q = seq_len // bq
    blocks_done = pairs * (seq_len // bk) * (seq_len // bk + 1) // 2
    cost = pl.CostEstimate(
        flops=4 * blocks_done * bk * bk * head_size,
        transcendentals=blocks_done * bk * bk,
        bytes_accessed=pairs * seq_len * head_size * 2 * 4 + pairs * seq_len * 4,
    )
    grid_spec = pltpu.PrefetchScalarGridSpec(
        num_scalar_prefetch=1,
        grid=(pairs, n_q),
        in_specs=[
            pl.BlockSpec((1, 1, head_size, bq), lambda p, i, seg: (p, 0, 0, i)),
            pl.BlockSpec((1, 1, head_size, seq_len), lambda p, i, seg: (p, 1, 0, 0)),
            pl.BlockSpec((1, 1, head_size, seq_len), lambda p, i, seg: (p, 2, 0, 0)),
        ],
        out_specs=[
            pl.BlockSpec((1, head_size, bq), lambda p, i, seg: (p, 0, i)),
            pl.BlockSpec((1, 1, bq), lambda p, i, seg: (p, 0, i)),
        ],
    )
    return pl.pallas_call(
        functools.partial(fwd_kernel, bq=bq, bk=bk, scale=scale),
        grid_spec=grid_spec,
        out_shape=[
            jax.ShapeDtypeStruct((pairs, head_size, seq_len), jnp.bfloat16),
            jax.ShapeDtypeStruct((pairs, 1, seq_len), jnp.float32),
        ],
        cost_estimate=cost,
        name="attn_fwd",
    )(seg_pairs, qkv_t, qkv_t, qkv_t)


def bwd_kernel(seg_ref, q_ref, k_ref, v_ref, do_ref, o_ref, lse_ref, out_ref, dq_acc, *, bk, bq, scale):
    pair = pl.program_id(0)
    kj = pl.program_id(1)

    @pl.when(kj == 0)
    def _():
        dq_acc[...] = jnp.zeros_like(dq_acc)

    seg_len = seg_ref[pair]
    k_start = kj * bk
    seg_end = (k_start // seg_len + 1) * seg_len
    key_t = k_ref[0, 0]
    key = key_t.astype(jnp.float32).T.astype(jnp.bfloat16)
    value_s = (v_ref[0, 0].astype(jnp.float32).T * scale).astype(jnp.bfloat16)

    def step(i, carry, masked):
        dk_t, dv_t = carry
        q_off = pl.multiple_of(i * bq, bq)
        query_t = q_ref[0, 0, :, pl.ds(q_off, bq)]
        query_ts = (query_t.astype(jnp.float32) * scale).astype(jnp.bfloat16)
        dout_t = do_ref[0, :, pl.ds(q_off, bq)]
        out_t = o_ref[0, :, pl.ds(q_off, bq)]
        lse = lse_ref[0, :, pl.ds(q_off, bq)]
        delta = jnp.sum(
            dout_t.astype(jnp.float32) * out_t.astype(jnp.float32), axis=0, keepdims=True
        ) * scale
        s_t = jnp.dot(key, query_ts, preferred_element_type=jnp.float32)
        if masked:
            keys_at = k_start + lax.broadcasted_iota(jnp.int32, (bk, bq), 0)
            queries_at = q_off + lax.broadcasted_iota(jnp.int32, (bk, bq), 1)
            s_t = jnp.where(keys_at <= queries_at, s_t, MASKED)
        p_t = jnp.exp(s_t - lse)
        dv_t = dv_t + lax.dot_general(
            dout_t, p_t.astype(jnp.bfloat16), NT_DIMS, preferred_element_type=jnp.float32
        )
        dp_t = jnp.dot(value_s, dout_t, preferred_element_type=jnp.float32)
        ds_t = (p_t * (dp_t - delta)).astype(jnp.bfloat16)
        dk_t = dk_t + lax.dot_general(query_t, ds_t, NT_DIMS, preferred_element_type=jnp.float32)
        dq_acc[:, pl.ds(q_off, bq)] += jnp.dot(key_t, ds_t, preferred_element_type=jnp.float32)
        return dk_t, dv_t

    carry = (jnp.zeros((HD, bk), jnp.float32), jnp.zeros((HD, bk), jnp.float32))
    for r in range(bk // bq):
        carry = step(k_start // bq + r, carry, True)
    dk_t, dv_t = lax.fori_loop(
        (k_start + bk) // bq, seg_end // bq, lambda i, c: step(i, c, False), carry
    )
    out_ref[0, 0] = dq_acc[:, pl.ds(pl.multiple_of(k_start, bk), bk)].astype(out_ref.dtype)
    out_ref[0, 1] = dk_t.astype(out_ref.dtype)
    out_ref[0, 2] = dv_t.astype(out_ref.dtype)


def attn_backward(qkv_t, dout_t, out_t, lse, seg_pairs, bk=512, bq=512):
    pairs, _, head_size, seq_len = qkv_t.shape
    scale = head_size ** (-0.5)
    n_k = seq_len // bk
    blocks_done = pairs * (seq_len // bq) * (seq_len // bq + 1) // 2
    cost = pl.CostEstimate(
        flops=10 * blocks_done * bq * bq * head_size,
        transcendentals=blocks_done * bq * bq,
        bytes_accessed=pairs * seq_len * head_size * 2 * 8 + pairs * seq_len * 4,
    )
    grid_spec = pltpu.PrefetchScalarGridSpec(
        num_scalar_prefetch=1,
        grid=(pairs, n_k),
        in_specs=[
            pl.BlockSpec((1, 1, head_size, seq_len), lambda p, j, seg: (p, 0, 0, 0)),
            pl.BlockSpec((1, 1, head_size, bk), lambda p, j, seg: (p, 1, 0, j)),
            pl.BlockSpec((1, 1, head_size, bk), lambda p, j, seg: (p, 2, 0, j)),
            pl.BlockSpec((1, head_size, seq_len), lambda p, j, seg: (p, 0, 0)),
            pl.BlockSpec((1, head_size, seq_len), lambda p, j, seg: (p, 0, 0)),
            pl.BlockSpec((1, 1, seq_len), lambda p, j, seg: (p, 0, 0)),
        ],
        out_specs=pl.BlockSpec((1, 3, head_size, bk), lambda p, j, seg: (p, 0, 0, j)),
        scratch_shapes=[pltpu.VMEM((head_size, seq_len), jnp.float32)],
    )
    return pl.pallas_call(
        functools.partial(bwd_kernel, bk=bk, bq=bq, scale=scale),
        grid_spec=grid_spec,
        out_shape=jax.ShapeDtypeStruct((pairs, 3, head_size, seq_len), jnp.bfloat16),
        cost_estimate=cost,
        name="attn_bwd",
    )(seg_pairs, qkv_t, qkv_t, qkv_t, dout_t, out_t, lse)


def norm_rows(values, gain, shift):
    row_mean = jnp.mean(values, axis=-1, keepdims=True)
    centred = values - row_mean
    variance = jnp.mean(centred * centred, axis=-1, keepdims=True)
    inv_std = lax.rsqrt(variance + NORM_EPS)
    normed = centred * inv_std
    return (normed * gain + shift, normed, inv_std)


def norm_back(grad_in, normed, inv_std, gain):
    scaled = grad_in * gain
    centred = (
        scaled
        - jnp.mean(scaled, axis=-1, keepdims=True)
        - normed * jnp.mean(scaled * normed, axis=-1, keepdims=True)
    )
    return (centred * inv_std, jnp.sum(grad_in * normed, axis=0), jnp.sum(grad_in, axis=0))


def rotate(values, cosine, sine_tab):
    half_size = values.shape[-1] // 2
    front = values[..., :half_size]
    behind = values[..., half_size:]
    cos_part = cosine[..., None, :]
    sin_part = sine_tab[..., None, :]
    return jnp.concatenate(
        [front * cos_part - behind * sin_part, behind * cos_part + front * sin_part], axis=-1
    )


def unrotate(values, cosine, sine_tab):
    half_size = values.shape[-1] // 2
    front = values[..., :half_size]
    behind = values[..., half_size:]
    cos_part = cosine[..., None, :]
    sin_part = sine_tab[..., None, :]
    return jnp.concatenate(
        [front * cos_part + behind * sin_part, behind * cos_part - front * sin_part], axis=-1
    )


def local(
    block_input,
    history,
    cotangent,
    qkv_weight,
    proj_weight,
    up_weight,
    down_weight,
    norm1_gain,
    norm1_bias,
    norm2_gain,
    norm2_bias,
    dwa_weights,
    pair_order,
    long_group,
):
    n_seq = lax.axis_size("seq")
    row_count = block_input.shape[0]
    piece_len = SLOT // n_seq
    slot_count = row_count // piece_len
    pair_count = slot_count * HEADS
    per_dev = pair_count // n_seq
    slot_flags = long_group[0]
    seg_len = SLOT // jnp.left_shift(jnp.ones_like(slot_flags), slot_flags)
    position = jnp.arange(SLOT, dtype=jnp.int32)
    doc_place = (position[None, :] % seg_len[:, None]).astype(jnp.float32)
    frequency = jnp.power(10000.0, jnp.arange(HD // 2, dtype=jnp.float32) * (-2.0 / HD))
    angles = doc_place[..., None] * frequency
    my_index = lax.axis_index("seq")
    my_start = my_index * piece_len
    cosine = lax.dynamic_slice_in_dim(jnp.cos(angles), my_start, piece_len, 1)
    sine_tab = lax.dynamic_slice_in_dim(jnp.sin(angles), my_start, piece_len, 1)
    head_groups = HEADS // per_dev
    order_row = pair_order[0]
    held_pairs = lax.dynamic_slice_in_dim(order_row, my_index * per_dev, per_dev, 0)
    my_pairs = my_index * per_dev + jnp.arange(per_dev, dtype=jnp.int32)
    seg_pairs = jnp.take(seg_len, my_pairs // HEADS).astype(jnp.int32)
    row_parts = (
        lax.all_gather(qkv_weight, "batch", axis=0, tiled=True),
        lax.all_gather(proj_weight, "batch", axis=0, tiled=True),
        lax.all_gather(up_weight, "batch", axis=0, tiled=True),
        lax.all_gather(down_weight, "batch", axis=0, tiled=True),
    )
    w_qkv, w_proj, w_up, w_down = (
        lax.all_gather(row_parts[0], "seq", axis=1, tiled=True),
        lax.all_gather(row_parts[1], "seq", axis=1, tiled=True),
        lax.all_gather(row_parts[2], "seq", axis=1, tiled=True),
        lax.all_gather(row_parts[3], "seq", axis=1, tiled=True),
    )
    inputs32 = block_input.astype(jnp.float32)
    norm1_out, normed1, inv_std1 = norm_rows(inputs32, norm1_gain, norm1_bias)
    norm1_low = norm1_out.astype(jnp.bfloat16)
    qkv_out = jnp.dot(norm1_low, w_qkv, preferred_element_type=jnp.float32)
    queries = rotate(qkv_out[:, :D].reshape(slot_count, piece_len, HEADS, HD), cosine, sine_tab)
    keys_rot = rotate(
        qkv_out[:, D : 2 * D].reshape(slot_count, piece_len, HEADS, HD), cosine, sine_tab
    )
    values_in = qkv_out[:, 2 * D :].reshape(slot_count, piece_len, HEADS, HD)
    stacked = jnp.stack([queries, keys_rot, values_in], axis=2).astype(jnp.bfloat16)
    send = jnp.transpose(
        stacked.reshape(slot_count, piece_len, 3, head_groups, per_dev, HD), (0, 3, 4, 2, 5, 1)
    ).reshape(n_seq, per_dev, 3, HD, piece_len)
    incoming = lax.all_to_all(send, "seq", split_axis=0, concat_axis=0, tiled=True)
    qkv_t = jnp.transpose(incoming, (1, 2, 3, 0, 4)).reshape(per_dev, 3, HD, SLOT)
    attn_t, lse_rows = attn_forward(qkv_t, seg_pairs)
    back = jnp.transpose(attn_t.reshape(per_dev, HD, n_seq, piece_len), (2, 0, 1, 3))
    returned = lax.all_to_all(back, "seq", split_axis=0, concat_axis=0, tiled=True)
    lse_all = lax.all_gather(lse_rows.reshape(per_dev, SLOT), "seq", axis=0, tiled=True)
    lse_all, returned = lax.optimization_barrier((lse_all, returned))
    attended = jnp.transpose(
        returned.reshape(slot_count, head_groups, per_dev, HD, piece_len), (0, 4, 1, 2, 3)
    ).reshape(row_count, D)
    middle = inputs32 + jnp.dot(attended, w_proj, preferred_element_type=jnp.float32)
    norm2_out, normed2, inv_std2 = norm_rows(middle, norm2_gain, norm2_bias)
    norm2_low = norm2_out.astype(jnp.bfloat16)
    hidden_up = jnp.dot(norm2_low, w_up, preferred_element_type=jnp.float32)
    gelu_out, gelu_pull = jax.vjp(lambda hidden: jax.nn.gelu(hidden, approximate=True), hidden_up)
    gelu_low = gelu_out.astype(jnp.bfloat16)
    block_out = middle + jnp.dot(gelu_low, w_down, preferred_element_type=jnp.float32)
    dwa_out = dwa_weights[HIST] * block_out
    for layer_idx in range(HIST):
        dwa_out = dwa_out + dwa_weights[layer_idx] * history[layer_idx].astype(jnp.float32)
    block_output = dwa_out.astype(jnp.bfloat16)
    grad_out = cotangent.astype(jnp.float32)
    history_grad = (dwa_weights[:HIST, None, None] * grad_out[None]).astype(jnp.bfloat16)
    dwa_terms = [
        jnp.sum(history[layer_idx].astype(jnp.float32) * grad_out) for layer_idx in range(HIST)
    ]
    dwa_terms.append(jnp.sum(block_out * grad_out))
    dwa_local = jnp.stack(dwa_terms)
    dy_full = dwa_weights[HIST] * grad_out
    dmlp_low = dy_full.astype(jnp.bfloat16)
    down_local = jnp.einsum("nf,nd->fd", gelu_low, dmlp_low, preferred_element_type=jnp.float32)
    dgelu = jnp.einsum("nd,fd->nf", dmlp_low, w_down, preferred_element_type=jnp.float32)
    dup_low = gelu_pull(dgelu)[0].astype(jnp.bfloat16)
    up_local = jnp.einsum("nd,nf->df", norm2_low, dup_low, preferred_element_type=jnp.float32)
    dnorm2 = jnp.einsum("nf,df->nd", dup_low, w_up, preferred_element_type=jnp.float32)
    dmid_norm, gain2_local, bias2_local = norm_back(dnorm2, normed2, inv_std2, norm2_gain)
    dmiddle = dy_full + dmid_norm
    dmiddle_low = dmiddle.astype(jnp.bfloat16)
    proj_local = jnp.einsum("nd,ne->de", attended, dmiddle_low, preferred_element_type=jnp.float32)
    dattended = jnp.einsum(
        "ne,de->nd", dmiddle_low, w_proj, preferred_element_type=jnp.float32
    ).astype(jnp.bfloat16)
    dsend = jnp.transpose(
        dattended.reshape(slot_count, piece_len, head_groups, per_dev, HD), (0, 2, 3, 4, 1)
    ).reshape(n_seq, per_dev, HD, piece_len)
    dattn_in = lax.all_to_all(dsend, "seq", split_axis=0, concat_axis=0, tiled=True)
    dout_t = jnp.transpose(dattn_in, (1, 2, 0, 3)).reshape(per_dev, HD, SLOT)
    dpairs = attn_backward(qkv_t, dout_t, attn_t, lse_rows, seg_pairs)
    dback = jnp.transpose(
        dpairs.reshape(per_dev, 3, HD, n_seq, piece_len), (3, 0, 1, 2, 4)
    )
    dreturned = lax.all_to_all(dback, "seq", split_axis=0, concat_axis=0, tiled=True)
    dtokens = jnp.transpose(
        dreturned.reshape(slot_count, head_groups, per_dev, 3, HD, piece_len), (0, 5, 3, 1, 2, 4)
    ).reshape(slot_count, piece_len, 3, HEADS, HD)
    dq_rows = unrotate(dtokens[:, :, 0].astype(jnp.float32), cosine, sine_tab).reshape(row_count, D)
    dk_rows = unrotate(dtokens[:, :, 1].astype(jnp.float32), cosine, sine_tab).reshape(row_count, D)
    dv_rows = dtokens[:, :, 2].astype(jnp.float32).reshape(row_count, D)
    dqkv_low = jnp.concatenate([dq_rows, dk_rows, dv_rows], axis=-1).astype(jnp.bfloat16)
    qkv_local = jnp.einsum("nd,nf->df", norm1_low, dqkv_low, preferred_element_type=jnp.float32)
    dnorm1 = jnp.einsum("nf,df->nd", dqkv_low, w_qkv, preferred_element_type=jnp.float32)
    dinput_norm, gain1_local, bias1_local = norm_back(dnorm1, normed1, inv_std1, norm1_gain)
    input_grad = (dmiddle + dinput_norm).astype(jnp.bfloat16)
    def scatter_grad(partial):
        by_rows = lax.psum_scatter(
            partial.astype(jnp.bfloat16), "batch", scatter_dimension=0, tiled=True
        )
        return lax.psum_scatter(by_rows, "seq", scatter_dimension=1, tiled=True).astype(
            jnp.float32
        )

    qkv_grad, proj_grad, up_grad, down_grad = (
        scatter_grad(qkv_local),
        scatter_grad(proj_local),
        scatter_grad(up_local),
        scatter_grad(down_local),
    )
    small_sums = lax.psum(
        lax.psum(
            jnp.concatenate([gain1_local, bias1_local, gain2_local, bias2_local, dwa_local]),
            "seq",
        ),
        "batch",
    )
    gain1_grad, bias1_grad, gain2_grad, bias2_grad = (
        small_sums[k * D : (k + 1) * D] for k in range(4)
    )
    dwa_grad = small_sums[4 * D :]
    row_lse = jnp.take(lse_all, held_pairs, axis=0).reshape(1, per_dev, SLOT)
    return (
        block_output,
        input_grad,
        history_grad,
        row_lse,
        qkv_grad,
        proj_grad,
        up_grad,
        down_grad,
        gain1_grad,
        bias1_grad,
        gain2_grad,
        bias2_grad,
        dwa_grad,
    )


def solution(mesh):
    placed = (
        P(("batch", "seq"), None),
        P(None, ("batch", "seq"), None),
        P(("batch", "seq"), None),
        P("batch", "seq"),
        P("batch", "seq"),
        P("batch", "seq"),
        P("batch", "seq"),
        P(),
        P(),
        P(),
        P(),
        P(),
        P("batch", None),
        P("batch", None),
    )
    return jax.shard_map(
        local,
        mesh=mesh,
        in_specs=placed,
        out_specs=(
            P(("batch", "seq"), None),
            P(("batch", "seq"), None),
            P(None, ("batch", "seq"), None),
            P("batch", "seq", None),
            P("batch", "seq"),
            P("batch", "seq"),
            P("batch", "seq"),
            P("batch", "seq"),
            P(),
            P(),
            P(),
            P(),
            P(),
        ),
        check_vma=False,
    )
```

```python
import jax
import jax.numpy as jnp
from jax import lax
from jax.sharding import PartitionSpec as P
from jax.experimental import pallas as pl
from jax.experimental.pallas import tpu as pltpu
import functools

D = 768
HEADS = 12
HD = 64
SLOT = 2048
HIST = 8


NORM_EPS = 1e-05
MASKED = -1e30
NT_DIMS = (((1,), (1,)), ((), ()))


def fwd_kernel(seg_ref, q_ref, k_ref, v_ref, o_ref, lse_ref, *, bq, bk, scale):
    pair = pl.program_id(0)
    qi = pl.program_id(1)
    seg_len = seg_ref[pair]
    q_start = qi * bq
    seg_start = (q_start // seg_len) * seg_len
    query = (q_ref[0, 0].astype(jnp.float32).T * scale).astype(jnp.bfloat16)

    def step(j, carry, masked):
        m_old, l_old, acc = carry
        k_off = pl.multiple_of(j * bk, bk)
        key_t = k_ref[0, 0, :, pl.ds(k_off, bk)]
        value_t = v_ref[0, 0, :, pl.ds(k_off, bk)]
        s = jnp.dot(query, key_t, preferred_element_type=jnp.float32)
        if masked:
            rows = q_start + lax.broadcasted_iota(jnp.int32, (bq, bk), 0)
            cols = k_off + lax.broadcasted_iota(jnp.int32, (bq, bk), 1)
            s = jnp.where(cols <= rows, s, MASKED)
        m_new = jnp.maximum(m_old, jnp.max(s, axis=-1, keepdims=True))
        alpha = jnp.exp(m_old - m_new)
        weights = jnp.exp(s - m_new)
        l_new = alpha * l_old + jnp.sum(weights, axis=-1, keepdims=True)
        acc = alpha * acc + lax.dot_general(
            weights.astype(jnp.bfloat16), value_t, NT_DIMS, preferred_element_type=jnp.float32
        )
        return m_new, l_new, acc

    carry = (
        jnp.full((bq, 1), MASKED, jnp.float32),
        jnp.zeros((bq, 1), jnp.float32),
        jnp.zeros((bq, HD), jnp.float32),
    )
    j_diag = q_start // bk
    carry = lax.fori_loop(seg_start // bk, j_diag, lambda j, c: step(j, c, False), carry)
    for r in range(bq // bk):
        carry = step(j_diag + r, carry, True)
    m_fin, l_fin, acc = carry
    o_ref[0] = (acc / l_fin).T.astype(o_ref.dtype)
    lse = m_fin + jnp.log(l_fin)
    lse_ref[0] = jnp.transpose(jnp.broadcast_to(lse, (bq, 128)))[0:1, :]


def attn_forward(qkv_t, seg_pairs, bq=512, bk=512):
    pairs, _, head_size, seq_len = qkv_t.shape
    scale = head_size ** (-0.5)
    n_q = seq_len // bq
    blocks_done = pairs * (seq_len // bk) * (seq_len // bk + 1) // 2
    cost = pl.CostEstimate(
        flops=4 * blocks_done * bk * bk * head_size,
        transcendentals=blocks_done * bk * bk,
        bytes_accessed=pairs * seq_len * head_size * 2 * 4 + pairs * seq_len * 4,
    )
    grid_spec = pltpu.PrefetchScalarGridSpec(
        num_scalar_prefetch=1,
        grid=(pairs, n_q),
        in_specs=[
            pl.BlockSpec((1, 1, head_size, bq), lambda p, i, seg: (p, 0, 0, i)),
            pl.BlockSpec((1, 1, head_size, seq_len), lambda p, i, seg: (p, 1, 0, 0)),
            pl.BlockSpec((1, 1, head_size, seq_len), lambda p, i, seg: (p, 2, 0, 0)),
        ],
        out_specs=[
            pl.BlockSpec((1, head_size, bq), lambda p, i, seg: (p, 0, i)),
            pl.BlockSpec((1, 1, bq), lambda p, i, seg: (p, 0, i)),
        ],
    )
    return pl.pallas_call(
        functools.partial(fwd_kernel, bq=bq, bk=bk, scale=scale),
        grid_spec=grid_spec,
        out_shape=[
            jax.ShapeDtypeStruct((pairs, head_size, seq_len), jnp.bfloat16),
            jax.ShapeDtypeStruct((pairs, 1, seq_len), jnp.float32),
        ],
        cost_estimate=cost,
        name="attn_fwd",
    )(seg_pairs, qkv_t, qkv_t, qkv_t)


def bwd_kernel(seg_ref, q_ref, k_ref, v_ref, do_ref, o_ref, lse_ref, out_ref, dq_acc, *, bk, bq, scale):
    pair = pl.program_id(0)
    kj = pl.program_id(1)

    @pl.when(kj == 0)
    def _():
        dq_acc[...] = jnp.zeros_like(dq_acc)

    seg_len = seg_ref[pair]
    k_start = kj * bk
    seg_end = (k_start // seg_len + 1) * seg_len
    key_t = k_ref[0, 0]
    key = key_t.astype(jnp.float32).T.astype(jnp.bfloat16)
    value_s = (v_ref[0, 0].astype(jnp.float32).T * scale).astype(jnp.bfloat16)

    def step(i, carry, masked):
        dk_t, dv_t = carry
        q_off = pl.multiple_of(i * bq, bq)
        query_t = q_ref[0, 0, :, pl.ds(q_off, bq)]
        query_ts = (query_t.astype(jnp.float32) * scale).astype(jnp.bfloat16)
        dout_t = do_ref[0, :, pl.ds(q_off, bq)]
        out_t = o_ref[0, :, pl.ds(q_off, bq)]
        lse = lse_ref[0, :, pl.ds(q_off, bq)]
        delta = jnp.sum(
            dout_t.astype(jnp.float32) * out_t.astype(jnp.float32), axis=0, keepdims=True
        ) * scale
        s_t = jnp.dot(key, query_ts, preferred_element_type=jnp.float32)
        if masked:
            keys_at = k_start + lax.broadcasted_iota(jnp.int32, (bk, bq), 0)
            queries_at = q_off + lax.broadcasted_iota(jnp.int32, (bk, bq), 1)
            s_t = jnp.where(keys_at <= queries_at, s_t, MASKED)
        p_t = jnp.exp(s_t - lse)
        dv_t = dv_t + lax.dot_general(
            dout_t, p_t.astype(jnp.bfloat16), NT_DIMS, preferred_element_type=jnp.float32
        )
        dp_t = jnp.dot(value_s, dout_t, preferred_element_type=jnp.float32)
        ds_t = (p_t * (dp_t - delta)).astype(jnp.bfloat16)
        dk_t = dk_t + lax.dot_general(query_t, ds_t, NT_DIMS, preferred_element_type=jnp.float32)
        dq_acc[:, pl.ds(q_off, bq)] += jnp.dot(key_t, ds_t, preferred_element_type=jnp.float32)
        return dk_t, dv_t

    carry = (jnp.zeros((HD, bk), jnp.float32), jnp.zeros((HD, bk), jnp.float32))
    for r in range(bk // bq):
        carry = step(k_start // bq + r, carry, True)
    dk_t, dv_t = lax.fori_loop(
        (k_start + bk) // bq, seg_end // bq, lambda i, c: step(i, c, False), carry
    )
    out_ref[0, 0] = dq_acc[:, pl.ds(pl.multiple_of(k_start, bk), bk)].astype(out_ref.dtype)
    out_ref[0, 1] = dk_t.astype(out_ref.dtype)
    out_ref[0, 2] = dv_t.astype(out_ref.dtype)


def attn_backward(qkv_t, dout_t, out_t, lse, seg_pairs, bk=512, bq=512):
    pairs, _, head_size, seq_len = qkv_t.shape
    scale = head_size ** (-0.5)
    n_k = seq_len // bk
    blocks_done = pairs * (seq_len // bq) * (seq_len // bq + 1) // 2
    cost = pl.CostEstimate(
        flops=10 * blocks_done * bq * bq * head_size,
        transcendentals=blocks_done * bq * bq,
        bytes_accessed=pairs * seq_len * head_size * 2 * 8 + pairs * seq_len * 4,
    )
    grid_spec = pltpu.PrefetchScalarGridSpec(
        num_scalar_prefetch=1,
        grid=(pairs, n_k),
        in_specs=[
            pl.BlockSpec((1, 1, head_size, seq_len), lambda p, j, seg: (p, 0, 0, 0)),
            pl.BlockSpec((1, 1, head_size, bk), lambda p, j, seg: (p, 1, 0, j)),
            pl.BlockSpec((1, 1, head_size, bk), lambda p, j, seg: (p, 2, 0, j)),
            pl.BlockSpec((1, head_size, seq_len), lambda p, j, seg: (p, 0, 0)),
            pl.BlockSpec((1, head_size, seq_len), lambda p, j, seg: (p, 0, 0)),
            pl.BlockSpec((1, 1, seq_len), lambda p, j, seg: (p, 0, 0)),
        ],
        out_specs=pl.BlockSpec((1, 3, head_size, bk), lambda p, j, seg: (p, 0, 0, j)),
        scratch_shapes=[pltpu.VMEM((head_size, seq_len), jnp.float32)],
    )
    return pl.pallas_call(
        functools.partial(bwd_kernel, bk=bk, bq=bq, scale=scale),
        grid_spec=grid_spec,
        out_shape=jax.ShapeDtypeStruct((pairs, 3, head_size, seq_len), jnp.bfloat16),
        cost_estimate=cost,
        name="attn_bwd",
    )(seg_pairs, qkv_t, qkv_t, qkv_t, dout_t, out_t, lse)


def norm_rows(values, gain, shift):
    row_mean = jnp.mean(values, axis=-1, keepdims=True)
    centred = values - row_mean
    variance = jnp.mean(centred * centred, axis=-1, keepdims=True)
    inv_std = lax.rsqrt(variance + NORM_EPS)
    normed = centred * inv_std
    return (normed * gain + shift, normed, inv_std)


def norm_back(grad_in, normed, inv_std, gain):
    scaled = grad_in * gain
    centred = (
        scaled
        - jnp.mean(scaled, axis=-1, keepdims=True)
        - normed * jnp.mean(scaled * normed, axis=-1, keepdims=True)
    )
    return (centred * inv_std, jnp.sum(grad_in * normed, axis=0), jnp.sum(grad_in, axis=0))


def rotate(values, cosine, sine_tab):
    half_size = values.shape[-1] // 2
    front = values[..., :half_size]
    behind = values[..., half_size:]
    cos_part = cosine[..., None, :]
    sin_part = sine_tab[..., None, :]
    return jnp.concatenate(
        [front * cos_part - behind * sin_part, behind * cos_part + front * sin_part], axis=-1
    )


def unrotate(values, cosine, sine_tab):
    half_size = values.shape[-1] // 2
    front = values[..., :half_size]
    behind = values[..., half_size:]
    cos_part = cosine[..., None, :]
    sin_part = sine_tab[..., None, :]
    return jnp.concatenate(
        [front * cos_part + behind * sin_part, behind * cos_part - front * sin_part], axis=-1
    )


def local(
    block_input,
    history,
    cotangent,
    qkv_weight,
    proj_weight,
    up_weight,
    down_weight,
    norm1_gain,
    norm1_bias,
    norm2_gain,
    norm2_bias,
    dwa_weights,
    pair_order,
    long_group,
):
    n_seq = lax.axis_size("seq")
    row_count = block_input.shape[0]
    piece_len = SLOT // n_seq
    slot_count = row_count // piece_len
    pair_count = slot_count * HEADS
    per_dev = pair_count // n_seq
    slot_flags = long_group[0]
    seg_len = SLOT // jnp.left_shift(jnp.ones_like(slot_flags), slot_flags)
    position = jnp.arange(SLOT, dtype=jnp.int32)
    doc_place = (position[None, :] % seg_len[:, None]).astype(jnp.float32)
    frequency = jnp.power(10000.0, jnp.arange(HD // 2, dtype=jnp.float32) * (-2.0 / HD))
    angles = doc_place[..., None] * frequency
    my_index = lax.axis_index("seq")
    my_start = my_index * piece_len
    cosine = lax.dynamic_slice_in_dim(jnp.cos(angles), my_start, piece_len, 1)
    sine_tab = lax.dynamic_slice_in_dim(jnp.sin(angles), my_start, piece_len, 1)
    head_groups = HEADS // per_dev
    order_row = pair_order[0]
    held_pairs = lax.dynamic_slice_in_dim(order_row, my_index * per_dev, per_dev, 0)
    my_pairs = my_index * per_dev + jnp.arange(per_dev, dtype=jnp.int32)
    seg_pairs = jnp.take(seg_len, my_pairs // HEADS).astype(jnp.int32)
    w_qkv = lax.all_gather(
        lax.all_gather(qkv_weight, "batch", axis=0, tiled=True), "seq", axis=1, tiled=True
    )
    inputs32 = block_input.astype(jnp.float32)
    norm1_out, normed1, inv_std1 = norm_rows(inputs32, norm1_gain, norm1_bias)
    norm1_low = norm1_out.astype(jnp.bfloat16)
    qkv_out = jnp.dot(norm1_low, w_qkv, preferred_element_type=jnp.float32)
    queries = rotate(qkv_out[:, :D].reshape(slot_count, piece_len, HEADS, HD), cosine, sine_tab)
    keys_rot = rotate(
        qkv_out[:, D : 2 * D].reshape(slot_count, piece_len, HEADS, HD), cosine, sine_tab
    )
    values_in = qkv_out[:, 2 * D :].reshape(slot_count, piece_len, HEADS, HD)
    stacked = jnp.stack([queries, keys_rot, values_in], axis=2).astype(jnp.bfloat16)
    send = jnp.transpose(
        stacked.reshape(slot_count, piece_len, 3, head_groups, per_dev, HD), (0, 3, 4, 2, 5, 1)
    ).reshape(n_seq, per_dev, 3, HD, piece_len)
    incoming = lax.all_to_all(send, "seq", split_axis=0, concat_axis=0, tiled=True)
    later_rows = [
        lax.all_gather(w, "batch", axis=0, tiled=True)
        for w in (proj_weight, up_weight, down_weight)
    ]
    w_proj, w_up, w_down = (
        lax.all_gather(rows, "seq", axis=1, tiled=True) for rows in later_rows
    )
    qkv_t = jnp.transpose(incoming, (1, 2, 3, 0, 4)).reshape(per_dev, 3, HD, SLOT)
    attn_t, lse_rows = attn_forward(qkv_t, seg_pairs)
    back = jnp.transpose(attn_t.reshape(per_dev, HD, n_seq, piece_len), (2, 0, 1, 3))
    returned = lax.all_to_all(back, "seq", split_axis=0, concat_axis=0, tiled=True)
    lse_all = lax.all_gather(lse_rows.reshape(per_dev, SLOT), "seq", axis=0, tiled=True)
    lse_all, returned = lax.optimization_barrier((lse_all, returned))
    attended = jnp.transpose(
        returned.reshape(slot_count, head_groups, per_dev, HD, piece_len), (0, 4, 1, 2, 3)
    ).reshape(row_count, D)
    middle = inputs32 + jnp.dot(attended, w_proj, preferred_element_type=jnp.float32)
    norm2_out, normed2, inv_std2 = norm_rows(middle, norm2_gain, norm2_bias)
    norm2_low = norm2_out.astype(jnp.bfloat16)
    hidden_up = jnp.dot(norm2_low, w_up, preferred_element_type=jnp.float32)
    gelu_out, gelu_pull = jax.vjp(lambda hidden: jax.nn.gelu(hidden, approximate=True), hidden_up)
    gelu_low = gelu_out.astype(jnp.bfloat16)
    block_out = middle + jnp.dot(gelu_low, w_down, preferred_element_type=jnp.float32)
    dwa_out = dwa_weights[HIST] * block_out
    for layer_idx in range(HIST):
        dwa_out = dwa_out + dwa_weights[layer_idx] * history[layer_idx].astype(jnp.float32)
    block_output = dwa_out.astype(jnp.bfloat16)
    grad_out = cotangent.astype(jnp.float32)
    history_grad = (dwa_weights[:HIST, None, None] * grad_out[None]).astype(jnp.bfloat16)
    dwa_terms = [
        jnp.sum(history[layer_idx].astype(jnp.float32) * grad_out) for layer_idx in range(HIST)
    ]
    dwa_terms.append(jnp.sum(block_out * grad_out))
    dwa_local = jnp.stack(dwa_terms)
    dy_full = dwa_weights[HIST] * grad_out
    dmlp_low = dy_full.astype(jnp.bfloat16)
    down_local = jnp.einsum("nf,nd->fd", gelu_low, dmlp_low, preferred_element_type=jnp.float32)
    dgelu = jnp.einsum("nd,fd->nf", dmlp_low, w_down, preferred_element_type=jnp.float32)
    dup_low = gelu_pull(dgelu)[0].astype(jnp.bfloat16)
    up_local = jnp.einsum("nd,nf->df", norm2_low, dup_low, preferred_element_type=jnp.float32)
    dnorm2 = jnp.einsum("nf,df->nd", dup_low, w_up, preferred_element_type=jnp.float32)
    dmid_norm, gain2_local, bias2_local = norm_back(dnorm2, normed2, inv_std2, norm2_gain)
    dmiddle = dy_full + dmid_norm
    dmiddle_low = dmiddle.astype(jnp.bfloat16)
    proj_local = jnp.einsum("nd,ne->de", attended, dmiddle_low, preferred_element_type=jnp.float32)
    dattended = jnp.einsum(
        "ne,de->nd", dmiddle_low, w_proj, preferred_element_type=jnp.float32
    ).astype(jnp.bfloat16)
    dsend = jnp.transpose(
        dattended.reshape(slot_count, piece_len, head_groups, per_dev, HD), (0, 2, 3, 4, 1)
    ).reshape(n_seq, per_dev, HD, piece_len)
    dattn_in = lax.all_to_all(dsend, "seq", split_axis=0, concat_axis=0, tiled=True)
    dout_t = jnp.transpose(dattn_in, (1, 2, 0, 3)).reshape(per_dev, HD, SLOT)
    dpairs = attn_backward(qkv_t, dout_t, attn_t, lse_rows, seg_pairs)
    dback = jnp.transpose(
        dpairs.reshape(per_dev, 3, HD, n_seq, piece_len), (3, 0, 1, 2, 4)
    )
    dreturned = lax.all_to_all(dback, "seq", split_axis=0, concat_axis=0, tiled=True)
    dtokens = jnp.transpose(
        dreturned.reshape(slot_count, head_groups, per_dev, 3, HD, piece_len), (0, 5, 3, 1, 2, 4)
    ).reshape(slot_count, piece_len, 3, HEADS, HD)
    dq_rows = unrotate(dtokens[:, :, 0].astype(jnp.float32), cosine, sine_tab).reshape(row_count, D)
    dk_rows = unrotate(dtokens[:, :, 1].astype(jnp.float32), cosine, sine_tab).reshape(row_count, D)
    dv_rows = dtokens[:, :, 2].astype(jnp.float32).reshape(row_count, D)
    dqkv_low = jnp.concatenate([dq_rows, dk_rows, dv_rows], axis=-1).astype(jnp.bfloat16)
    qkv_local = jnp.einsum("nd,nf->df", norm1_low, dqkv_low, preferred_element_type=jnp.float32)
    dnorm1 = jnp.einsum("nf,df->nd", dqkv_low, w_qkv, preferred_element_type=jnp.float32)
    dinput_norm, gain1_local, bias1_local = norm_back(dnorm1, normed1, inv_std1, norm1_gain)
    input_grad = (dmiddle + dinput_norm).astype(jnp.bfloat16)
    col_sums = (
        lax.psum_scatter(
            qkv_local.astype(jnp.bfloat16), "seq", scatter_dimension=1, tiled=True
        ).astype(jnp.float32),
        lax.psum_scatter(
            proj_local.astype(jnp.bfloat16), "seq", scatter_dimension=1, tiled=True
        ).astype(jnp.float32),
        lax.psum_scatter(
            up_local.astype(jnp.bfloat16), "seq", scatter_dimension=1, tiled=True
        ).astype(jnp.float32),
        lax.psum_scatter(
            down_local.astype(jnp.bfloat16), "seq", scatter_dimension=1, tiled=True
        ).astype(jnp.float32),
    )
    qkv_grad, proj_grad, up_grad, down_grad = (
        lax.psum_scatter(
            col_sums[0].astype(jnp.bfloat16), "batch", scatter_dimension=0, tiled=True
        ).astype(jnp.float32),
        lax.psum_scatter(
            col_sums[1].astype(jnp.bfloat16), "batch", scatter_dimension=0, tiled=True
        ).astype(jnp.float32),
        lax.psum_scatter(
            col_sums[2].astype(jnp.bfloat16), "batch", scatter_dimension=0, tiled=True
        ).astype(jnp.float32),
        lax.psum_scatter(
            col_sums[3].astype(jnp.bfloat16), "batch", scatter_dimension=0, tiled=True
        ).astype(jnp.float32),
    )
    small_sums = lax.psum(
        lax.psum(
            jnp.concatenate([gain1_local, bias1_local, gain2_local, bias2_local, dwa_local]),
            "seq",
        ),
        "batch",
    )
    gain1_grad, bias1_grad, gain2_grad, bias2_grad = (
        small_sums[k * D : (k + 1) * D] for k in range(4)
    )
    dwa_grad = small_sums[4 * D :]
    row_lse = jnp.take(lse_all, held_pairs, axis=0).reshape(1, per_dev, SLOT)
    return (
        block_output,
        input_grad,
        history_grad,
        row_lse,
        qkv_grad,
        proj_grad,
        up_grad,
        down_grad,
        gain1_grad,
        bias1_grad,
        gain2_grad,
        bias2_grad,
        dwa_grad,
    )


def solution(mesh):
    placed = (
        P(("batch", "seq"), None),
        P(None, ("batch", "seq"), None),
        P(("batch", "seq"), None),
        P("batch", "seq"),
        P("batch", "seq"),
        P("batch", "seq"),
        P("batch", "seq"),
        P(),
        P(),
        P(),
        P(),
        P(),
        P("batch", None),
        P("batch", None),
    )

    return jax.shard_map(
        local,
        mesh=mesh,
        in_specs=placed,
        out_specs=(
            P(("batch", "seq"), None),
            P(("batch", "seq"), None),
            P(None, ("batch", "seq"), None),
            P("batch", "seq", None),
            P("batch", "seq"),
            P("batch", "seq"),
            P("batch", "seq"),
            P("batch", "seq"),
            P(),
            P(),
            P(),
            P(),
            P(),
        ),
        check_vma=False,
    )
```

```python
import jax
import jax.numpy as jnp
from jax import lax
from jax.sharding import PartitionSpec as P
from jax.experimental import pallas as pl
from jax.experimental.pallas import tpu as pltpu
import functools

D = 768
HEADS = 12
HD = 64
SLOT = 2048
HIST = 8


NORM_EPS = 1e-05
MASKED = -1e30
NT_DIMS = (((1,), (1,)), ((), ()))


def fwd_kernel(seg_ref, q_ref, k_ref, v_ref, o_ref, lse_ref, *, bq, bk, scale):
    pair = pl.program_id(0)
    qi = pl.program_id(1)
    seg_len = seg_ref[pair]
    q_start = qi * bq
    seg_start = (q_start // seg_len) * seg_len
    query = (q_ref[0, 0].astype(jnp.float32).T * scale).astype(jnp.bfloat16)

    def step(j, carry, masked):
        m_old, l_old, acc = carry
        k_off = pl.multiple_of(j * bk, bk)
        key_t = k_ref[0, 0, :, pl.ds(k_off, bk)]
        value_t = v_ref[0, 0, :, pl.ds(k_off, bk)]
        s = jnp.dot(query, key_t, preferred_element_type=jnp.float32)
        if masked:
            rows = q_start + lax.broadcasted_iota(jnp.int32, (bq, bk), 0)
            cols = k_off + lax.broadcasted_iota(jnp.int32, (bq, bk), 1)
            s = jnp.where(cols <= rows, s, MASKED)
        m_new = jnp.maximum(m_old, jnp.max(s, axis=-1, keepdims=True))
        alpha = jnp.exp(m_old - m_new)
        weights = jnp.exp(s - m_new)
        l_new = alpha * l_old + jnp.sum(weights, axis=-1, keepdims=True)
        acc = alpha * acc + lax.dot_general(
            weights.astype(jnp.bfloat16), value_t, NT_DIMS, preferred_element_type=jnp.float32
        )
        return m_new, l_new, acc

    carry = (
        jnp.full((bq, 1), MASKED, jnp.float32),
        jnp.zeros((bq, 1), jnp.float32),
        jnp.zeros((bq, HD), jnp.float32),
    )
    j_diag = q_start // bk
    carry = lax.fori_loop(seg_start // bk, j_diag, lambda j, c: step(j, c, False), carry)
    for r in range(bq // bk):
        carry = step(j_diag + r, carry, True)
    m_fin, l_fin, acc = carry
    o_ref[0] = (acc / l_fin).T.astype(o_ref.dtype)
    lse = m_fin + jnp.log(l_fin)
    lse_ref[0] = jnp.transpose(jnp.broadcast_to(lse, (bq, 128)))[0:1, :]


def attn_forward(qkv_t, seg_pairs, bq=512, bk=512):
    pairs, _, head_size, seq_len = qkv_t.shape
    scale = head_size ** (-0.5)
    n_q = seq_len // bq
    blocks_done = pairs * (seq_len // bk) * (seq_len // bk + 1) // 2
    cost = pl.CostEstimate(
        flops=4 * blocks_done * bk * bk * head_size,
        transcendentals=blocks_done * bk * bk,
        bytes_accessed=pairs * seq_len * head_size * 2 * 4 + pairs * seq_len * 4,
    )
    grid_spec = pltpu.PrefetchScalarGridSpec(
        num_scalar_prefetch=1,
        grid=(pairs, n_q),
        in_specs=[
            pl.BlockSpec((1, 1, head_size, bq), lambda p, i, seg: (p, 0, 0, i)),
            pl.BlockSpec((1, 1, head_size, seq_len), lambda p, i, seg: (p, 1, 0, 0)),
            pl.BlockSpec((1, 1, head_size, seq_len), lambda p, i, seg: (p, 2, 0, 0)),
        ],
        out_specs=[
            pl.BlockSpec((1, head_size, bq), lambda p, i, seg: (p, 0, i)),
            pl.BlockSpec((1, 1, bq), lambda p, i, seg: (p, 0, i)),
        ],
    )
    return pl.pallas_call(
        functools.partial(fwd_kernel, bq=bq, bk=bk, scale=scale),
        grid_spec=grid_spec,
        out_shape=[
            jax.ShapeDtypeStruct((pairs, head_size, seq_len), jnp.bfloat16),
            jax.ShapeDtypeStruct((pairs, 1, seq_len), jnp.float32),
        ],
        cost_estimate=cost,
        name="attn_fwd",
    )(seg_pairs, qkv_t, qkv_t, qkv_t)


def bwd_kernel(seg_ref, q_ref, k_ref, v_ref, do_ref, o_ref, lse_ref, out_ref, dq_acc, *, bk, bq, scale):
    pair = pl.program_id(0)
    kj = pl.program_id(1)

    @pl.when(kj == 0)
    def _():
        dq_acc[...] = jnp.zeros_like(dq_acc)

    seg_len = seg_ref[pair]
    k_start = kj * bk
    seg_end = (k_start // seg_len + 1) * seg_len
    key_t = k_ref[0, 0]
    key = key_t.astype(jnp.float32).T.astype(jnp.bfloat16)
    value_s = (v_ref[0, 0].astype(jnp.float32).T * scale).astype(jnp.bfloat16)

    def step(i, carry, masked):
        dk_t, dv_t = carry
        q_off = pl.multiple_of(i * bq, bq)
        query_t = q_ref[0, 0, :, pl.ds(q_off, bq)]
        query_ts = (query_t.astype(jnp.float32) * scale).astype(jnp.bfloat16)
        dout_t = do_ref[0, :, pl.ds(q_off, bq)]
        out_t = o_ref[0, :, pl.ds(q_off, bq)]
        lse = lse_ref[0, :, pl.ds(q_off, bq)]
        delta = jnp.sum(
            dout_t.astype(jnp.float32) * out_t.astype(jnp.float32), axis=0, keepdims=True
        ) * scale
        s_t = jnp.dot(key, query_ts, preferred_element_type=jnp.float32)
        if masked:
            keys_at = k_start + lax.broadcasted_iota(jnp.int32, (bk, bq), 0)
            queries_at = q_off + lax.broadcasted_iota(jnp.int32, (bk, bq), 1)
            s_t = jnp.where(keys_at <= queries_at, s_t, MASKED)
        p_t = jnp.exp(s_t - lse)
        dv_t = dv_t + lax.dot_general(
            dout_t, p_t.astype(jnp.bfloat16), NT_DIMS, preferred_element_type=jnp.float32
        )
        dp_t = jnp.dot(value_s, dout_t, preferred_element_type=jnp.float32)
        ds_t = (p_t * (dp_t - delta)).astype(jnp.bfloat16)
        dk_t = dk_t + lax.dot_general(query_t, ds_t, NT_DIMS, preferred_element_type=jnp.float32)
        dq_acc[:, pl.ds(q_off, bq)] += jnp.dot(key_t, ds_t, preferred_element_type=jnp.float32)
        return dk_t, dv_t

    carry = (jnp.zeros((HD, bk), jnp.float32), jnp.zeros((HD, bk), jnp.float32))
    for r in range(bk // bq):
        carry = step(k_start // bq + r, carry, True)
    dk_t, dv_t = lax.fori_loop(
        (k_start + bk) // bq, seg_end // bq, lambda i, c: step(i, c, False), carry
    )
    out_ref[0, 0] = dq_acc[:, pl.ds(pl.multiple_of(k_start, bk), bk)].astype(out_ref.dtype)
    out_ref[0, 1] = dk_t.astype(out_ref.dtype)
    out_ref[0, 2] = dv_t.astype(out_ref.dtype)


def attn_backward(qkv_t, dout_t, out_t, lse, seg_pairs, bk=512, bq=512):
    pairs, _, head_size, seq_len = qkv_t.shape
    scale = head_size ** (-0.5)
    n_k = seq_len // bk
    blocks_done = pairs * (seq_len // bq) * (seq_len // bq + 1) // 2
    cost = pl.CostEstimate(
        flops=10 * blocks_done * bq * bq * head_size,
        transcendentals=blocks_done * bq * bq,
        bytes_accessed=pairs * seq_len * head_size * 2 * 8 + pairs * seq_len * 4,
    )
    grid_spec = pltpu.PrefetchScalarGridSpec(
        num_scalar_prefetch=1,
        grid=(pairs, n_k),
        in_specs=[
            pl.BlockSpec((1, 1, head_size, seq_len), lambda p, j, seg: (p, 0, 0, 0)),
            pl.BlockSpec((1, 1, head_size, bk), lambda p, j, seg: (p, 1, 0, j)),
            pl.BlockSpec((1, 1, head_size, bk), lambda p, j, seg: (p, 2, 0, j)),
            pl.BlockSpec((1, head_size, seq_len), lambda p, j, seg: (p, 0, 0)),
            pl.BlockSpec((1, head_size, seq_len), lambda p, j, seg: (p, 0, 0)),
            pl.BlockSpec((1, 1, seq_len), lambda p, j, seg: (p, 0, 0)),
        ],
        out_specs=pl.BlockSpec((1, 3, head_size, bk), lambda p, j, seg: (p, 0, 0, j)),
        scratch_shapes=[pltpu.VMEM((head_size, seq_len), jnp.float32)],
    )
    return pl.pallas_call(
        functools.partial(bwd_kernel, bk=bk, bq=bq, scale=scale),
        grid_spec=grid_spec,
        out_shape=jax.ShapeDtypeStruct((pairs, 3, head_size, seq_len), jnp.bfloat16),
        cost_estimate=cost,
        name="attn_bwd",
    )(seg_pairs, qkv_t, qkv_t, qkv_t, dout_t, out_t, lse)


def norm_rows(values, gain, shift):
    row_mean = jnp.mean(values, axis=-1, keepdims=True)
    centred = values - row_mean
    variance = jnp.mean(centred * centred, axis=-1, keepdims=True)
    inv_std = lax.rsqrt(variance + NORM_EPS)
    normed = centred * inv_std
    return (normed * gain + shift, normed, inv_std)


def norm_back(grad_in, normed, inv_std, gain):
    scaled = grad_in * gain
    centred = (
        scaled
        - jnp.mean(scaled, axis=-1, keepdims=True)
        - normed * jnp.mean(scaled * normed, axis=-1, keepdims=True)
    )
    return (centred * inv_std, jnp.sum(grad_in * normed, axis=0), jnp.sum(grad_in, axis=0))


def rotate(values, cosine, sine_tab):
    half_size = values.shape[-1] // 2
    front = values[..., :half_size]
    behind = values[..., half_size:]
    cos_part = cosine[..., None, :]
    sin_part = sine_tab[..., None, :]
    return jnp.concatenate(
        [front * cos_part - behind * sin_part, behind * cos_part + front * sin_part], axis=-1
    )


def unrotate(values, cosine, sine_tab):
    half_size = values.shape[-1] // 2
    front = values[..., :half_size]
    behind = values[..., half_size:]
    cos_part = cosine[..., None, :]
    sin_part = sine_tab[..., None, :]
    return jnp.concatenate(
        [front * cos_part + behind * sin_part, behind * cos_part - front * sin_part], axis=-1
    )


def local(
    block_input,
    history,
    cotangent,
    qkv_weight,
    proj_weight,
    up_weight,
    down_weight,
    norm1_gain,
    norm1_bias,
    norm2_gain,
    norm2_bias,
    dwa_weights,
    pair_order,
    long_group,
):
    n_seq = lax.axis_size("seq")
    row_count = block_input.shape[0]
    piece_len = SLOT // n_seq
    slot_count = row_count // piece_len
    pair_count = slot_count * HEADS
    per_dev = pair_count // n_seq
    slot_flags = long_group[0]
    seg_len = SLOT // jnp.left_shift(jnp.ones_like(slot_flags), slot_flags)
    position = jnp.arange(SLOT, dtype=jnp.int32)
    doc_place = (position[None, :] % seg_len[:, None]).astype(jnp.float32)
    frequency = jnp.power(10000.0, jnp.arange(HD // 2, dtype=jnp.float32) * (-2.0 / HD))
    angles = doc_place[..., None] * frequency
    my_index = lax.axis_index("seq")
    my_start = my_index * piece_len
    cosine = lax.dynamic_slice_in_dim(jnp.cos(angles), my_start, piece_len, 1)
    sine_tab = lax.dynamic_slice_in_dim(jnp.sin(angles), my_start, piece_len, 1)
    head_groups = HEADS // per_dev
    order_row = pair_order[0]
    held_pairs = lax.dynamic_slice_in_dim(order_row, my_index * per_dev, per_dev, 0)
    my_pairs = my_index * per_dev + jnp.arange(per_dev, dtype=jnp.int32)
    seg_pairs = jnp.take(seg_len, my_pairs // HEADS).astype(jnp.int32)
    w_qkv = lax.all_gather(
        lax.all_gather(qkv_weight, "batch", axis=0, tiled=True), "seq", axis=1, tiled=True
    )
    inputs32 = block_input.astype(jnp.float32)
    norm1_out, normed1, inv_std1 = norm_rows(inputs32, norm1_gain, norm1_bias)
    norm1_low = norm1_out.astype(jnp.bfloat16)
    qkv_out = jnp.dot(norm1_low, w_qkv, preferred_element_type=jnp.float32)
    queries = rotate(qkv_out[:, :D].reshape(slot_count, piece_len, HEADS, HD), cosine, sine_tab)
    keys_rot = rotate(
        qkv_out[:, D : 2 * D].reshape(slot_count, piece_len, HEADS, HD), cosine, sine_tab
    )
    values_in = qkv_out[:, 2 * D :].reshape(slot_count, piece_len, HEADS, HD)
    stacked = jnp.stack([queries, keys_rot, values_in], axis=2).astype(jnp.bfloat16)
    send = jnp.transpose(
        stacked.reshape(slot_count, piece_len, 3, head_groups, per_dev, HD), (0, 3, 4, 2, 5, 1)
    ).reshape(n_seq, per_dev, 3, HD, piece_len)
    incoming = lax.all_to_all(send, "seq", split_axis=0, concat_axis=0, tiled=True)
    later_rows = [
        lax.all_gather(w, "batch", axis=0, tiled=True)
        for w in (proj_weight, up_weight, down_weight)
    ]
    w_proj, w_up, w_down = (
        lax.all_gather(rows, "seq", axis=1, tiled=True) for rows in later_rows
    )
    qkv_t = jnp.transpose(incoming, (1, 2, 3, 0, 4)).reshape(per_dev, 3, HD, SLOT)
    attn_t, lse_rows = attn_forward(qkv_t, seg_pairs)
    back = jnp.transpose(attn_t.reshape(per_dev, HD, n_seq, piece_len), (2, 0, 1, 3))
    returned = lax.all_to_all(back, "seq", split_axis=0, concat_axis=0, tiled=True)
    lse_all = lax.all_gather(lse_rows.reshape(per_dev, SLOT), "seq", axis=0, tiled=True)
    lse_all, returned = lax.optimization_barrier((lse_all, returned))
    attended = jnp.transpose(
        returned.reshape(slot_count, head_groups, per_dev, HD, piece_len), (0, 4, 1, 2, 3)
    ).reshape(row_count, D)
    middle = inputs32 + jnp.dot(attended, w_proj, preferred_element_type=jnp.float32)
    norm2_out, normed2, inv_std2 = norm_rows(middle, norm2_gain, norm2_bias)
    norm2_low = norm2_out.astype(jnp.bfloat16)
    hidden_up = jnp.dot(norm2_low, w_up, preferred_element_type=jnp.float32)
    gelu_out, gelu_pull = jax.vjp(lambda hidden: jax.nn.gelu(hidden, approximate=True), hidden_up)
    gelu_low = gelu_out.astype(jnp.bfloat16)
    block_out = middle + jnp.dot(gelu_low, w_down, preferred_element_type=jnp.float32)
    dwa_out = dwa_weights[HIST] * block_out
    for layer_idx in range(HIST):
        dwa_out = dwa_out + dwa_weights[layer_idx] * history[layer_idx].astype(jnp.float32)
    block_output = dwa_out.astype(jnp.bfloat16)
    grad_out = cotangent.astype(jnp.float32)
    history_grad = (dwa_weights[:HIST, None, None] * grad_out[None]).astype(jnp.bfloat16)
    dwa_terms = [
        jnp.sum(history[layer_idx].astype(jnp.float32) * grad_out) for layer_idx in range(HIST)
    ]
    dwa_terms.append(jnp.sum(block_out * grad_out))
    dwa_local = jnp.stack(dwa_terms)
    dy_full = dwa_weights[HIST] * grad_out
    dmlp_low = dy_full.astype(jnp.bfloat16)
    down_local = jnp.einsum("nf,nd->fd", gelu_low, dmlp_low, preferred_element_type=jnp.float32)
    dgelu = jnp.einsum("nd,fd->nf", dmlp_low, w_down, preferred_element_type=jnp.float32)
    dup_low = gelu_pull(dgelu)[0].astype(jnp.bfloat16)
    up_local = jnp.einsum("nd,nf->df", norm2_low, dup_low, preferred_element_type=jnp.float32)
    dnorm2 = jnp.einsum("nf,df->nd", dup_low, w_up, preferred_element_type=jnp.float32)
    dmid_norm, gain2_local, bias2_local = norm_back(dnorm2, normed2, inv_std2, norm2_gain)
    dmiddle = dy_full + dmid_norm
    dmiddle_low = dmiddle.astype(jnp.bfloat16)
    proj_local = jnp.einsum("nd,ne->de", attended, dmiddle_low, preferred_element_type=jnp.float32)
    dattended = jnp.einsum(
        "ne,de->nd", dmiddle_low, w_proj, preferred_element_type=jnp.float32
    ).astype(jnp.bfloat16)
    dsend = jnp.transpose(
        dattended.reshape(slot_count, piece_len, head_groups, per_dev, HD), (0, 2, 3, 4, 1)
    ).reshape(n_seq, per_dev, HD, piece_len)
    dattn_in = lax.all_to_all(dsend, "seq", split_axis=0, concat_axis=0, tiled=True)
    dout_t = jnp.transpose(dattn_in, (1, 2, 0, 3)).reshape(per_dev, HD, SLOT)
    dpairs = attn_backward(qkv_t, dout_t, attn_t, lse_rows, seg_pairs)
    dback = jnp.transpose(
        dpairs.reshape(per_dev, 3, HD, n_seq, piece_len), (3, 0, 1, 2, 4)
    )
    dreturned = lax.all_to_all(dback, "seq", split_axis=0, concat_axis=0, tiled=True)
    dtokens = jnp.transpose(
        dreturned.reshape(slot_count, head_groups, per_dev, 3, HD, piece_len), (0, 5, 3, 1, 2, 4)
    ).reshape(slot_count, piece_len, 3, HEADS, HD)
    dq_rows = unrotate(dtokens[:, :, 0].astype(jnp.float32), cosine, sine_tab).reshape(row_count, D)
    dk_rows = unrotate(dtokens[:, :, 1].astype(jnp.float32), cosine, sine_tab).reshape(row_count, D)
    dv_rows = dtokens[:, :, 2].astype(jnp.float32).reshape(row_count, D)
    dqkv_low = jnp.concatenate([dq_rows, dk_rows, dv_rows], axis=-1).astype(jnp.bfloat16)
    qkv_local = jnp.einsum("nd,nf->df", norm1_low, dqkv_low, preferred_element_type=jnp.float32)
    dnorm1 = jnp.einsum("nf,df->nd", dqkv_low, w_qkv, preferred_element_type=jnp.float32)
    dinput_norm, gain1_local, bias1_local = norm_back(dnorm1, normed1, inv_std1, norm1_gain)
    input_grad = (dmiddle + dinput_norm).astype(jnp.bfloat16)

    def by_cols_offloaded(partial):
        return lax.psum_scatter(
            partial.astype(jnp.bfloat16), "seq", scatter_dimension=1, tiled=True
        )

    def by_cols_exchanged(partial):
        rows, cols = partial.shape
        blocks = jnp.transpose(
            partial.astype(jnp.bfloat16).reshape(rows, n_seq, cols // n_seq), (1, 0, 2)
        )
        got = lax.all_to_all(blocks, "seq", split_axis=0, concat_axis=0, tiled=True)
        return jnp.sum(got.astype(jnp.float32), axis=0).astype(jnp.bfloat16)

    def by_rows(col_sum):
        return lax.psum_scatter(col_sum, "batch", scatter_dimension=0, tiled=True).astype(
            jnp.float32
        )

    qkv_grad = by_rows(by_cols_offloaded(qkv_local))
    proj_grad = by_rows(by_cols_offloaded(proj_local))
    up_grad = by_rows(by_cols_exchanged(up_local))
    down_grad = by_rows(by_cols_exchanged(down_local))
    small_sums = lax.psum(
        lax.psum(
            jnp.concatenate([gain1_local, bias1_local, gain2_local, bias2_local, dwa_local]),
            "seq",
        ),
        "batch",
    )
    gain1_grad, bias1_grad, gain2_grad, bias2_grad = (
        small_sums[k * D : (k + 1) * D] for k in range(4)
    )
    dwa_grad = small_sums[4 * D :]
    row_lse = jnp.take(lse_all, held_pairs, axis=0).reshape(1, per_dev, SLOT)
    return (
        block_output,
        input_grad,
        history_grad,
        row_lse,
        qkv_grad,
        proj_grad,
        up_grad,
        down_grad,
        gain1_grad,
        bias1_grad,
        gain2_grad,
        bias2_grad,
        dwa_grad,
    )


def solution(mesh):
    placed = (
        P(("batch", "seq"), None),
        P(None, ("batch", "seq"), None),
        P(("batch", "seq"), None),
        P("batch", "seq"),
        P("batch", "seq"),
        P("batch", "seq"),
        P("batch", "seq"),
        P(),
        P(),
        P(),
        P(),
        P(),
        P("batch", None),
        P("batch", None),
    )

    return jax.shard_map(
        local,
        mesh=mesh,
        in_specs=placed,
        out_specs=(
            P(("batch", "seq"), None),
            P(("batch", "seq"), None),
            P(None, ("batch", "seq"), None),
            P("batch", "seq", None),
            P("batch", "seq"),
            P("batch", "seq"),
            P("batch", "seq"),
            P("batch", "seq"),
            P(),
            P(),
            P(),
            P(),
            P(),
        ),
        check_vma=False,
    )
```

```python
import jax
import jax.numpy as jnp
from jax import lax
from jax.sharding import PartitionSpec as P
from jax.experimental import pallas as pl
from jax.experimental.pallas import tpu as pltpu
import functools

D = 768
HEADS = 12
HD = 64
SLOT = 2048
HIST = 8


NORM_EPS = 1e-05
MASKED = -1e30
NT_DIMS = (((1,), (1,)), ((), ()))


def fwd_kernel(seg_ref, q_ref, k_ref, v_ref, o_ref, lse_ref, *, bq, bk, scale):
    pair = pl.program_id(0)
    qi = pl.program_id(1)
    seg_len = seg_ref[pair]
    q_start = qi * bq
    seg_start = (q_start // seg_len) * seg_len
    query = (q_ref[0, 0].astype(jnp.float32).T * scale).astype(jnp.bfloat16)

    def step(j, carry, masked):
        m_old, l_old, acc = carry
        k_off = pl.multiple_of(j * bk, bk)
        key_t = k_ref[0, 0, :, pl.ds(k_off, bk)]
        value_t = v_ref[0, 0, :, pl.ds(k_off, bk)]
        s = jnp.dot(query, key_t, preferred_element_type=jnp.float32)
        if masked:
            rows = q_start + lax.broadcasted_iota(jnp.int32, (bq, bk), 0)
            cols = k_off + lax.broadcasted_iota(jnp.int32, (bq, bk), 1)
            s = jnp.where(cols <= rows, s, MASKED)
        m_new = jnp.maximum(m_old, jnp.max(s, axis=-1, keepdims=True))
        alpha = jnp.exp(m_old - m_new)
        weights = jnp.exp(s - m_new)
        l_new = alpha * l_old + jnp.sum(weights, axis=-1, keepdims=True)
        acc = alpha * acc + lax.dot_general(
            weights.astype(jnp.bfloat16), value_t, NT_DIMS, preferred_element_type=jnp.float32
        )
        return m_new, l_new, acc

    carry = (
        jnp.full((bq, 1), MASKED, jnp.float32),
        jnp.zeros((bq, 1), jnp.float32),
        jnp.zeros((bq, HD), jnp.float32),
    )
    j_diag = q_start // bk
    carry = lax.fori_loop(seg_start // bk, j_diag, lambda j, c: step(j, c, False), carry)
    for r in range(bq // bk):
        carry = step(j_diag + r, carry, True)
    m_fin, l_fin, acc = carry
    o_ref[0] = (acc / l_fin).T.astype(o_ref.dtype)
    lse = m_fin + jnp.log(l_fin)
    lse_ref[0] = jnp.transpose(jnp.broadcast_to(lse, (bq, 128)))[0:1, :]


def attn_forward(qkv_t, seg_pairs, bq=512, bk=512):
    pairs, _, head_size, seq_len = qkv_t.shape
    scale = head_size ** (-0.5)
    n_q = seq_len // bq
    blocks_done = pairs * (seq_len // bk) * (seq_len // bk + 1) // 2
    cost = pl.CostEstimate(
        flops=4 * blocks_done * bk * bk * head_size,
        transcendentals=blocks_done * bk * bk,
        bytes_accessed=pairs * seq_len * head_size * 2 * 4 + pairs * seq_len * 4,
    )
    grid_spec = pltpu.PrefetchScalarGridSpec(
        num_scalar_prefetch=1,
        grid=(pairs, n_q),
        in_specs=[
            pl.BlockSpec((1, 1, head_size, bq), lambda p, i, seg: (p, 0, 0, i)),
            pl.BlockSpec((1, 1, head_size, seq_len), lambda p, i, seg: (p, 1, 0, 0)),
            pl.BlockSpec((1, 1, head_size, seq_len), lambda p, i, seg: (p, 2, 0, 0)),
        ],
        out_specs=[
            pl.BlockSpec((1, head_size, bq), lambda p, i, seg: (p, 0, i)),
            pl.BlockSpec((1, 1, bq), lambda p, i, seg: (p, 0, i)),
        ],
    )
    return pl.pallas_call(
        functools.partial(fwd_kernel, bq=bq, bk=bk, scale=scale),
        grid_spec=grid_spec,
        out_shape=[
            jax.ShapeDtypeStruct((pairs, head_size, seq_len), jnp.bfloat16),
            jax.ShapeDtypeStruct((pairs, 1, seq_len), jnp.float32),
        ],
        cost_estimate=cost,
        name="attn_fwd",
    )(seg_pairs, qkv_t, qkv_t, qkv_t)


def bwd_kernel(seg_ref, q_ref, k_ref, v_ref, do_ref, o_ref, lse_ref, out_ref, dq_acc, *, bk, bq, scale):
    pair = pl.program_id(0)
    kj = pl.program_id(1)

    @pl.when(kj == 0)
    def _():
        dq_acc[...] = jnp.zeros_like(dq_acc)

    seg_len = seg_ref[pair]
    k_start = kj * bk
    seg_end = (k_start // seg_len + 1) * seg_len
    key_t = k_ref[0, 0]
    key = key_t.astype(jnp.float32).T.astype(jnp.bfloat16)
    value_s = (v_ref[0, 0].astype(jnp.float32).T * scale).astype(jnp.bfloat16)

    def step(i, carry, masked):
        dk_t, dv_t = carry
        q_off = pl.multiple_of(i * bq, bq)
        query_t = q_ref[0, 0, :, pl.ds(q_off, bq)]
        query_ts = (query_t.astype(jnp.float32) * scale).astype(jnp.bfloat16)
        dout_t = do_ref[0, :, pl.ds(q_off, bq)]
        out_t = o_ref[0, :, pl.ds(q_off, bq)]
        lse = lse_ref[0, :, pl.ds(q_off, bq)]
        delta = jnp.sum(
            dout_t.astype(jnp.float32) * out_t.astype(jnp.float32), axis=0, keepdims=True
        ) * scale
        s_t = jnp.dot(key, query_ts, preferred_element_type=jnp.float32)
        if masked:
            keys_at = k_start + lax.broadcasted_iota(jnp.int32, (bk, bq), 0)
            queries_at = q_off + lax.broadcasted_iota(jnp.int32, (bk, bq), 1)
            s_t = jnp.where(keys_at <= queries_at, s_t, MASKED)
        p_t = jnp.exp(s_t - lse)
        dv_t = dv_t + lax.dot_general(
            dout_t, p_t.astype(jnp.bfloat16), NT_DIMS, preferred_element_type=jnp.float32
        )
        dp_t = jnp.dot(value_s, dout_t, preferred_element_type=jnp.float32)
        ds_t = (p_t * (dp_t - delta)).astype(jnp.bfloat16)
        dk_t = dk_t + lax.dot_general(query_t, ds_t, NT_DIMS, preferred_element_type=jnp.float32)
        dq_acc[:, pl.ds(q_off, bq)] += jnp.dot(key_t, ds_t, preferred_element_type=jnp.float32)
        return dk_t, dv_t

    carry = (jnp.zeros((HD, bk), jnp.float32), jnp.zeros((HD, bk), jnp.float32))
    for r in range(bk // bq):
        carry = step(k_start // bq + r, carry, True)
    dk_t, dv_t = lax.fori_loop(
        (k_start + bk) // bq, seg_end // bq, lambda i, c: step(i, c, False), carry
    )
    out_ref[0, 0] = dq_acc[:, pl.ds(pl.multiple_of(k_start, bk), bk)].astype(out_ref.dtype)
    out_ref[0, 1] = dk_t.astype(out_ref.dtype)
    out_ref[0, 2] = dv_t.astype(out_ref.dtype)


def attn_backward(qkv_t, dout_t, out_t, lse, seg_pairs, bk=512, bq=512):
    pairs, _, head_size, seq_len = qkv_t.shape
    scale = head_size ** (-0.5)
    n_k = seq_len // bk
    blocks_done = pairs * (seq_len // bq) * (seq_len // bq + 1) // 2
    cost = pl.CostEstimate(
        flops=10 * blocks_done * bq * bq * head_size,
        transcendentals=blocks_done * bq * bq,
        bytes_accessed=pairs * seq_len * head_size * 2 * 8 + pairs * seq_len * 4,
    )
    grid_spec = pltpu.PrefetchScalarGridSpec(
        num_scalar_prefetch=1,
        grid=(pairs, n_k),
        in_specs=[
            pl.BlockSpec((1, 1, head_size, seq_len), lambda p, j, seg: (p, 0, 0, 0)),
            pl.BlockSpec((1, 1, head_size, bk), lambda p, j, seg: (p, 1, 0, j)),
            pl.BlockSpec((1, 1, head_size, bk), lambda p, j, seg: (p, 2, 0, j)),
            pl.BlockSpec((1, head_size, seq_len), lambda p, j, seg: (p, 0, 0)),
            pl.BlockSpec((1, head_size, seq_len), lambda p, j, seg: (p, 0, 0)),
            pl.BlockSpec((1, 1, seq_len), lambda p, j, seg: (p, 0, 0)),
        ],
        out_specs=pl.BlockSpec((1, 3, head_size, bk), lambda p, j, seg: (p, 0, 0, j)),
        scratch_shapes=[pltpu.VMEM((head_size, seq_len), jnp.float32)],
    )
    return pl.pallas_call(
        functools.partial(bwd_kernel, bk=bk, bq=bq, scale=scale),
        grid_spec=grid_spec,
        out_shape=jax.ShapeDtypeStruct((pairs, 3, head_size, seq_len), jnp.bfloat16),
        cost_estimate=cost,
        name="attn_bwd",
    )(seg_pairs, qkv_t, qkv_t, qkv_t, dout_t, out_t, lse)


def norm_rows(values, gain, shift):
    row_mean = jnp.mean(values, axis=-1, keepdims=True)
    centred = values - row_mean
    variance = jnp.mean(centred * centred, axis=-1, keepdims=True)
    inv_std = lax.rsqrt(variance + NORM_EPS)
    normed = centred * inv_std
    return (normed * gain + shift, normed, inv_std)


def norm_back(grad_in, normed, inv_std, gain):
    scaled = grad_in * gain
    centred = (
        scaled
        - jnp.mean(scaled, axis=-1, keepdims=True)
        - normed * jnp.mean(scaled * normed, axis=-1, keepdims=True)
    )
    return (centred * inv_std, jnp.sum(grad_in * normed, axis=0), jnp.sum(grad_in, axis=0))


def rotate(values, cosine, sine_tab):
    half_size = values.shape[-1] // 2
    front = values[..., :half_size]
    behind = values[..., half_size:]
    cos_part = cosine[..., None, :]
    sin_part = sine_tab[..., None, :]
    return jnp.concatenate(
        [front * cos_part - behind * sin_part, behind * cos_part + front * sin_part], axis=-1
    )


def unrotate(values, cosine, sine_tab):
    half_size = values.shape[-1] // 2
    front = values[..., :half_size]
    behind = values[..., half_size:]
    cos_part = cosine[..., None, :]
    sin_part = sine_tab[..., None, :]
    return jnp.concatenate(
        [front * cos_part + behind * sin_part, behind * cos_part - front * sin_part], axis=-1
    )


def local(
    block_input,
    history,
    cotangent,
    qkv_weight,
    proj_weight,
    up_weight,
    down_weight,
    norm1_gain,
    norm1_bias,
    norm2_gain,
    norm2_bias,
    dwa_weights,
    pair_order,
    long_group,
):
    n_seq = lax.axis_size("seq")
    row_count = block_input.shape[0]
    piece_len = SLOT // n_seq
    slot_count = row_count // piece_len
    pair_count = slot_count * HEADS
    per_dev = pair_count // n_seq
    slot_flags = long_group[0]
    seg_len = SLOT // jnp.left_shift(jnp.ones_like(slot_flags), slot_flags)
    position = jnp.arange(SLOT, dtype=jnp.int32)
    doc_place = (position[None, :] % seg_len[:, None]).astype(jnp.float32)
    frequency = jnp.power(10000.0, jnp.arange(HD // 2, dtype=jnp.float32) * (-2.0 / HD))
    angles = doc_place[..., None] * frequency
    my_index = lax.axis_index("seq")
    my_start = my_index * piece_len
    cosine = lax.dynamic_slice_in_dim(jnp.cos(angles), my_start, piece_len, 1)
    sine_tab = lax.dynamic_slice_in_dim(jnp.sin(angles), my_start, piece_len, 1)
    head_groups = HEADS // per_dev
    order_row = pair_order[0]
    held_pairs = lax.dynamic_slice_in_dim(order_row, my_index * per_dev, per_dev, 0)
    my_pairs = my_index * per_dev + jnp.arange(per_dev, dtype=jnp.int32)
    seg_pairs = jnp.take(seg_len, my_pairs // HEADS).astype(jnp.int32)
    w_qkv = lax.all_gather(
        lax.all_gather(qkv_weight, "batch", axis=0, tiled=True), "seq", axis=1, tiled=True
    )
    inputs32 = block_input.astype(jnp.float32)
    norm1_out, normed1, inv_std1 = norm_rows(inputs32, norm1_gain, norm1_bias)
    norm1_low = norm1_out.astype(jnp.bfloat16)
    qkv_out = jnp.dot(norm1_low, w_qkv, preferred_element_type=jnp.float32)
    queries = rotate(qkv_out[:, :D].reshape(slot_count, piece_len, HEADS, HD), cosine, sine_tab)
    keys_rot = rotate(
        qkv_out[:, D : 2 * D].reshape(slot_count, piece_len, HEADS, HD), cosine, sine_tab
    )
    values_in = qkv_out[:, 2 * D :].reshape(slot_count, piece_len, HEADS, HD)
    stacked = jnp.stack([queries, keys_rot, values_in], axis=2).astype(jnp.bfloat16)
    send = jnp.transpose(
        stacked.reshape(slot_count, piece_len, 3, head_groups, per_dev, HD), (0, 3, 4, 2, 5, 1)
    ).reshape(n_seq, per_dev, 3, HD, piece_len)
    incoming = lax.all_to_all(send, "seq", split_axis=0, concat_axis=0, tiled=True)
    later_rows = [
        lax.all_gather(w, "batch", axis=0, tiled=True)
        for w in (proj_weight, up_weight, down_weight)
    ]
    w_proj, w_up, w_down = (
        lax.all_gather(rows, "seq", axis=1, tiled=True) for rows in later_rows
    )
    qkv_t = jnp.transpose(incoming, (1, 2, 3, 0, 4)).reshape(per_dev, 3, HD, SLOT)
    attn_t, lse_rows = attn_forward(qkv_t, seg_pairs)
    back = jnp.transpose(attn_t.reshape(per_dev, HD, n_seq, piece_len), (2, 0, 1, 3))
    returned = lax.all_to_all(back, "seq", split_axis=0, concat_axis=0, tiled=True)
    lse_all = lax.all_gather(lse_rows.reshape(per_dev, SLOT), "seq", axis=0, tiled=True)
    lse_all, returned = lax.optimization_barrier((lse_all, returned))
    attended = jnp.transpose(
        returned.reshape(slot_count, head_groups, per_dev, HD, piece_len), (0, 4, 1, 2, 3)
    ).reshape(row_count, D)
    middle = inputs32 + jnp.dot(attended, w_proj, preferred_element_type=jnp.float32)
    norm2_out, normed2, inv_std2 = norm_rows(middle, norm2_gain, norm2_bias)
    norm2_low = norm2_out.astype(jnp.bfloat16)
    hidden_up = jnp.dot(norm2_low, w_up, preferred_element_type=jnp.float32)
    gelu_out, gelu_pull = jax.vjp(lambda hidden: jax.nn.gelu(hidden, approximate=True), hidden_up)
    gelu_low = gelu_out.astype(jnp.bfloat16)
    block_out = middle + jnp.dot(gelu_low, w_down, preferred_element_type=jnp.float32)
    dwa_out = dwa_weights[HIST] * block_out
    for layer_idx in range(HIST):
        dwa_out = dwa_out + dwa_weights[layer_idx] * history[layer_idx].astype(jnp.float32)
    block_output = dwa_out.astype(jnp.bfloat16)
    grad_out = cotangent.astype(jnp.float32)
    history_grad = (dwa_weights[:HIST, None, None] * grad_out[None]).astype(jnp.bfloat16)
    dwa_terms = [
        jnp.sum(history[layer_idx].astype(jnp.float32) * grad_out) for layer_idx in range(HIST)
    ]
    dwa_terms.append(jnp.sum(block_out * grad_out))
    dwa_local = jnp.stack(dwa_terms)
    dy_full = dwa_weights[HIST] * grad_out
    dmlp_low = dy_full.astype(jnp.bfloat16)
    down_local = jnp.einsum("nf,nd->fd", gelu_low, dmlp_low, preferred_element_type=jnp.float32)
    dgelu = jnp.einsum("nd,fd->nf", dmlp_low, w_down, preferred_element_type=jnp.float32)
    dup_low = gelu_pull(dgelu)[0].astype(jnp.bfloat16)
    up_local = jnp.einsum("nd,nf->df", norm2_low, dup_low, preferred_element_type=jnp.float32)
    dnorm2 = jnp.einsum("nf,df->nd", dup_low, w_up, preferred_element_type=jnp.float32)
    dmid_norm, gain2_local, bias2_local = norm_back(dnorm2, normed2, inv_std2, norm2_gain)
    dmiddle = dy_full + dmid_norm
    dmiddle_low = dmiddle.astype(jnp.bfloat16)
    proj_local = jnp.einsum("nd,ne->de", attended, dmiddle_low, preferred_element_type=jnp.float32)
    dattended = jnp.einsum(
        "ne,de->nd", dmiddle_low, w_proj, preferred_element_type=jnp.float32
    ).astype(jnp.bfloat16)
    dsend = jnp.transpose(
        dattended.reshape(slot_count, piece_len, head_groups, per_dev, HD), (0, 2, 3, 4, 1)
    ).reshape(n_seq, per_dev, HD, piece_len)
    dattn_in = lax.all_to_all(dsend, "seq", split_axis=0, concat_axis=0, tiled=True)
    dout_t = jnp.transpose(dattn_in, (1, 2, 0, 3)).reshape(per_dev, HD, SLOT)
    dpairs = attn_backward(qkv_t, dout_t, attn_t, lse_rows, seg_pairs)
    dback = jnp.transpose(
        dpairs.reshape(per_dev, 3, HD, n_seq, piece_len), (3, 0, 1, 2, 4)
    )
    dreturned = lax.all_to_all(dback, "seq", split_axis=0, concat_axis=0, tiled=True)
    dtokens = jnp.transpose(
        dreturned.reshape(slot_count, head_groups, per_dev, 3, HD, piece_len), (0, 5, 3, 1, 2, 4)
    ).reshape(slot_count, piece_len, 3, HEADS, HD)
    dq_rows = unrotate(dtokens[:, :, 0].astype(jnp.float32), cosine, sine_tab).reshape(row_count, D)
    dk_rows = unrotate(dtokens[:, :, 1].astype(jnp.float32), cosine, sine_tab).reshape(row_count, D)
    dv_rows = dtokens[:, :, 2].astype(jnp.float32).reshape(row_count, D)
    dqkv_low = jnp.concatenate([dq_rows, dk_rows, dv_rows], axis=-1).astype(jnp.bfloat16)
    qkv_local = jnp.einsum("nd,nf->df", norm1_low, dqkv_low, preferred_element_type=jnp.float32)
    dnorm1 = jnp.einsum("nf,df->nd", dqkv_low, w_qkv, preferred_element_type=jnp.float32)
    dinput_norm, gain1_local, bias1_local = norm_back(dnorm1, normed1, inv_std1, norm1_gain)
    input_grad = (dmiddle + dinput_norm).astype(jnp.bfloat16)

    def by_cols_offloaded(partial):
        return lax.psum_scatter(
            partial.astype(jnp.bfloat16), "seq", scatter_dimension=1, tiled=True
        )

    def by_cols_exchanged(partial):
        rows, cols = partial.shape
        blocks = jnp.transpose(
            partial.astype(jnp.bfloat16).reshape(rows, n_seq, cols // n_seq), (1, 0, 2)
        )
        got = lax.all_to_all(blocks, "seq", split_axis=0, concat_axis=0, tiled=True)
        return jnp.sum(got.astype(jnp.float32), axis=0).astype(jnp.bfloat16)

    def by_rows(col_sum):
        return lax.psum_scatter(col_sum, "batch", scatter_dimension=0, tiled=True).astype(
            jnp.float32
        )

    qkv_grad = by_rows(by_cols_offloaded(qkv_local))
    proj_grad = by_rows(by_cols_offloaded(proj_local))
    up_grad = by_rows(by_cols_exchanged(up_local))
    down_grad = by_rows(by_cols_offloaded(down_local))
    small_sums = jnp.concatenate([gain1_local, bias1_local, gain2_local, bias2_local, dwa_local])
    for axis in ("seq", "batch"):
        size = lax.axis_size(axis)
        hop = 1
        while hop < size:
            partner = [(i, i ^ hop) for i in range(size)]
            small_sums = small_sums + lax.ppermute(small_sums, axis, partner)
            hop *= 2
    gain1_grad, bias1_grad, gain2_grad, bias2_grad = (
        small_sums[k * D : (k + 1) * D] for k in range(4)
    )
    dwa_grad = small_sums[4 * D :]
    row_lse = jnp.take(lse_all, held_pairs, axis=0).reshape(1, per_dev, SLOT)
    return (
        block_output,
        input_grad,
        history_grad,
        row_lse,
        qkv_grad,
        proj_grad,
        up_grad,
        down_grad,
        gain1_grad,
        bias1_grad,
        gain2_grad,
        bias2_grad,
        dwa_grad,
    )


def solution(mesh):
    placed = (
        P(("batch", "seq"), None),
        P(None, ("batch", "seq"), None),
        P(("batch", "seq"), None),
        P("batch", "seq"),
        P("batch", "seq"),
        P("batch", "seq"),
        P("batch", "seq"),
        P(),
        P(),
        P(),
        P(),
        P(),
        P("batch", None),
        P("batch", None),
    )

    return jax.shard_map(
        local,
        mesh=mesh,
        in_specs=placed,
        out_specs=(
            P(("batch", "seq"), None),
            P(("batch", "seq"), None),
            P(None, ("batch", "seq"), None),
            P("batch", "seq", None),
            P("batch", "seq"),
            P("batch", "seq"),
            P("batch", "seq"),
            P("batch", "seq"),
            P(),
            P(),
            P(),
            P(),
            P(),
        ),
        check_vma=False,
    )
```

```python
import jax
import jax.numpy as jnp
from jax import lax
from jax.sharding import PartitionSpec as P
from jax.experimental import pallas as pl
from jax.experimental.pallas import tpu as pltpu
import functools

D = 768
HEADS = 12
HD = 64
SLOT = 2048
HIST = 8


NORM_EPS = 1e-05
MASKED = -1e30
NT_DIMS = (((1,), (1,)), ((), ()))


def fwd_kernel(seg_ref, q_ref, k_ref, v_ref, o_ref, lse_ref, *, bq, bk, scale):
    pair = pl.program_id(0)
    qi = pl.program_id(1)
    seg_len = seg_ref[pair]
    q_start = qi * bq
    seg_start = (q_start // seg_len) * seg_len
    query = (q_ref[0, 0].astype(jnp.float32).T * scale).astype(jnp.bfloat16)

    def step(j, carry, masked):
        m_old, l_old, acc = carry
        k_off = pl.multiple_of(j * bk, bk)
        key_t = k_ref[0, 0, :, pl.ds(k_off, bk)]
        value_t = v_ref[0, 0, :, pl.ds(k_off, bk)]
        s = jnp.dot(query, key_t, preferred_element_type=jnp.float32)
        if masked:
            rows = q_start + lax.broadcasted_iota(jnp.int32, (bq, bk), 0)
            cols = k_off + lax.broadcasted_iota(jnp.int32, (bq, bk), 1)
            s = jnp.where(cols <= rows, s, MASKED)
        m_new = jnp.maximum(m_old, jnp.max(s, axis=-1, keepdims=True))
        alpha = jnp.exp(m_old - m_new)
        weights = jnp.exp(s - m_new)
        l_new = alpha * l_old + jnp.sum(weights, axis=-1, keepdims=True)
        acc = alpha * acc + lax.dot_general(
            weights.astype(jnp.bfloat16), value_t, NT_DIMS, preferred_element_type=jnp.float32
        )
        return m_new, l_new, acc

    carry = (
        jnp.full((bq, 1), MASKED, jnp.float32),
        jnp.zeros((bq, 1), jnp.float32),
        jnp.zeros((bq, HD), jnp.float32),
    )
    j_diag = q_start // bk
    carry = lax.fori_loop(seg_start // bk, j_diag, lambda j, c: step(j, c, False), carry)
    for r in range(bq // bk):
        carry = step(j_diag + r, carry, True)
    m_fin, l_fin, acc = carry
    o_ref[0] = (acc / l_fin).T.astype(o_ref.dtype)
    lse = m_fin + jnp.log(l_fin)
    lse_ref[0] = jnp.transpose(jnp.broadcast_to(lse, (bq, 128)))[0:1, :]


def attn_forward(qkv_t, seg_pairs, bq=512, bk=512):
    pairs, _, head_size, seq_len = qkv_t.shape
    scale = head_size ** (-0.5)
    n_q = seq_len // bq
    blocks_done = pairs * (seq_len // bk) * (seq_len // bk + 1) // 2
    cost = pl.CostEstimate(
        flops=4 * blocks_done * bk * bk * head_size,
        transcendentals=blocks_done * bk * bk,
        bytes_accessed=pairs * seq_len * head_size * 2 * 4 + pairs * seq_len * 4,
    )
    grid_spec = pltpu.PrefetchScalarGridSpec(
        num_scalar_prefetch=1,
        grid=(pairs, n_q),
        in_specs=[
            pl.BlockSpec((1, 1, head_size, bq), lambda p, i, seg: (p, 0, 0, i)),
            pl.BlockSpec((1, 1, head_size, seq_len), lambda p, i, seg: (p, 1, 0, 0)),
            pl.BlockSpec((1, 1, head_size, seq_len), lambda p, i, seg: (p, 2, 0, 0)),
        ],
        out_specs=[
            pl.BlockSpec((1, head_size, bq), lambda p, i, seg: (p, 0, i)),
            pl.BlockSpec((1, 1, bq), lambda p, i, seg: (p, 0, i)),
        ],
    )
    return pl.pallas_call(
        functools.partial(fwd_kernel, bq=bq, bk=bk, scale=scale),
        grid_spec=grid_spec,
        out_shape=[
            jax.ShapeDtypeStruct((pairs, head_size, seq_len), jnp.bfloat16),
            jax.ShapeDtypeStruct((pairs, 1, seq_len), jnp.float32),
        ],
        cost_estimate=cost,
        name="attn_fwd",
    )(seg_pairs, qkv_t, qkv_t, qkv_t)


def bwd_kernel(seg_ref, q_ref, k_ref, v_ref, do_ref, o_ref, lse_ref, out_ref, dq_acc, *, bk, bq, scale):
    pair = pl.program_id(0)
    kj = pl.program_id(1)

    @pl.when(kj == 0)
    def _():
        dq_acc[...] = jnp.zeros_like(dq_acc)

    seg_len = seg_ref[pair]
    k_start = kj * bk
    seg_end = (k_start // seg_len + 1) * seg_len
    key_t = k_ref[0, 0]
    key = key_t.astype(jnp.float32).T.astype(jnp.bfloat16)
    value_s = (v_ref[0, 0].astype(jnp.float32).T * scale).astype(jnp.bfloat16)

    def step(i, carry, masked):
        dk_t, dv_t = carry
        q_off = pl.multiple_of(i * bq, bq)
        query_t = q_ref[0, 0, :, pl.ds(q_off, bq)]
        query_ts = (query_t.astype(jnp.float32) * scale).astype(jnp.bfloat16)
        dout_t = do_ref[0, :, pl.ds(q_off, bq)]
        out_t = o_ref[0, :, pl.ds(q_off, bq)]
        lse = lse_ref[0, :, pl.ds(q_off, bq)]
        delta = jnp.sum(
            dout_t.astype(jnp.float32) * out_t.astype(jnp.float32), axis=0, keepdims=True
        ) * scale
        s_t = jnp.dot(key, query_ts, preferred_element_type=jnp.float32)
        if masked:
            keys_at = k_start + lax.broadcasted_iota(jnp.int32, (bk, bq), 0)
            queries_at = q_off + lax.broadcasted_iota(jnp.int32, (bk, bq), 1)
            s_t = jnp.where(keys_at <= queries_at, s_t, MASKED)
        p_t = jnp.exp(s_t - lse)
        dv_t = dv_t + lax.dot_general(
            dout_t, p_t.astype(jnp.bfloat16), NT_DIMS, preferred_element_type=jnp.float32
        )
        dp_t = jnp.dot(value_s, dout_t, preferred_element_type=jnp.float32)
        ds_t = (p_t * (dp_t - delta)).astype(jnp.bfloat16)
        dk_t = dk_t + lax.dot_general(query_t, ds_t, NT_DIMS, preferred_element_type=jnp.float32)
        dq_acc[:, pl.ds(q_off, bq)] += jnp.dot(key_t, ds_t, preferred_element_type=jnp.float32)
        return dk_t, dv_t

    carry = (jnp.zeros((HD, bk), jnp.float32), jnp.zeros((HD, bk), jnp.float32))
    for r in range(bk // bq):
        carry = step(k_start // bq + r, carry, True)
    dk_t, dv_t = lax.fori_loop(
        (k_start + bk) // bq, seg_end // bq, lambda i, c: step(i, c, False), carry
    )
    out_ref[0, 0] = dq_acc[:, pl.ds(pl.multiple_of(k_start, bk), bk)].astype(out_ref.dtype)
    out_ref[0, 1] = dk_t.astype(out_ref.dtype)
    out_ref[0, 2] = dv_t.astype(out_ref.dtype)


def attn_backward(qkv_t, dout_t, out_t, lse, seg_pairs, bk=512, bq=512):
    pairs, _, head_size, seq_len = qkv_t.shape
    scale = head_size ** (-0.5)
    n_k = seq_len // bk
    blocks_done = pairs * (seq_len // bq) * (seq_len // bq + 1) // 2
    cost = pl.CostEstimate(
        flops=10 * blocks_done * bq * bq * head_size,
        transcendentals=blocks_done * bq * bq,
        bytes_accessed=pairs * seq_len * head_size * 2 * 8 + pairs * seq_len * 4,
    )
    grid_spec = pltpu.PrefetchScalarGridSpec(
        num_scalar_prefetch=1,
        grid=(pairs, n_k),
        in_specs=[
            pl.BlockSpec((1, 1, head_size, seq_len), lambda p, j, seg: (p, 0, 0, 0)),
            pl.BlockSpec((1, 1, head_size, bk), lambda p, j, seg: (p, 1, 0, j)),
            pl.BlockSpec((1, 1, head_size, bk), lambda p, j, seg: (p, 2, 0, j)),
            pl.BlockSpec((1, head_size, seq_len), lambda p, j, seg: (p, 0, 0)),
            pl.BlockSpec((1, head_size, seq_len), lambda p, j, seg: (p, 0, 0)),
            pl.BlockSpec((1, 1, seq_len), lambda p, j, seg: (p, 0, 0)),
        ],
        out_specs=pl.BlockSpec((1, 3, head_size, bk), lambda p, j, seg: (p, 0, 0, j)),
        scratch_shapes=[pltpu.VMEM((head_size, seq_len), jnp.float32)],
    )
    return pl.pallas_call(
        functools.partial(bwd_kernel, bk=bk, bq=bq, scale=scale),
        grid_spec=grid_spec,
        out_shape=jax.ShapeDtypeStruct((pairs, 3, head_size, seq_len), jnp.bfloat16),
        cost_estimate=cost,
        name="attn_bwd",
    )(seg_pairs, qkv_t, qkv_t, qkv_t, dout_t, out_t, lse)


def norm_rows(values, gain, shift):
    row_mean = jnp.mean(values, axis=-1, keepdims=True)
    centred = values - row_mean
    variance = jnp.mean(centred * centred, axis=-1, keepdims=True)
    inv_std = lax.rsqrt(variance + NORM_EPS)
    normed = centred * inv_std
    return (normed * gain + shift, normed, inv_std)


def norm_back(grad_in, normed, inv_std, gain):
    scaled = grad_in * gain
    centred = (
        scaled
        - jnp.mean(scaled, axis=-1, keepdims=True)
        - normed * jnp.mean(scaled * normed, axis=-1, keepdims=True)
    )
    return (centred * inv_std, jnp.sum(grad_in * normed, axis=0), jnp.sum(grad_in, axis=0))


def rotate(values, cosine, sine_tab):
    half_size = values.shape[-1] // 2
    front = values[..., :half_size]
    behind = values[..., half_size:]
    cos_part = cosine[..., None, :]
    sin_part = sine_tab[..., None, :]
    return jnp.concatenate(
        [front * cos_part - behind * sin_part, behind * cos_part + front * sin_part], axis=-1
    )


def unrotate(values, cosine, sine_tab):
    half_size = values.shape[-1] // 2
    front = values[..., :half_size]
    behind = values[..., half_size:]
    cos_part = cosine[..., None, :]
    sin_part = sine_tab[..., None, :]
    return jnp.concatenate(
        [front * cos_part + behind * sin_part, behind * cos_part - front * sin_part], axis=-1
    )


def local(
    block_input,
    history,
    cotangent,
    qkv_weight,
    proj_weight,
    up_weight,
    down_weight,
    norm1_gain,
    norm1_bias,
    norm2_gain,
    norm2_bias,
    dwa_weights,
    pair_order,
    long_group,
):
    n_seq = lax.axis_size("seq")
    row_count = block_input.shape[0]
    piece_len = SLOT // n_seq
    slot_count = row_count // piece_len
    pair_count = slot_count * HEADS
    per_dev = pair_count // n_seq
    slot_flags = long_group[0]
    seg_len = SLOT // jnp.left_shift(jnp.ones_like(slot_flags), slot_flags)
    position = jnp.arange(SLOT, dtype=jnp.int32)
    doc_place = (position[None, :] % seg_len[:, None]).astype(jnp.float32)
    frequency = jnp.power(10000.0, jnp.arange(HD // 2, dtype=jnp.float32) * (-2.0 / HD))
    angles = doc_place[..., None] * frequency
    my_index = lax.axis_index("seq")
    my_start = my_index * piece_len
    cosine = lax.dynamic_slice_in_dim(jnp.cos(angles), my_start, piece_len, 1)
    sine_tab = lax.dynamic_slice_in_dim(jnp.sin(angles), my_start, piece_len, 1)
    head_groups = HEADS // per_dev
    order_row = pair_order[0]
    held_pairs = lax.dynamic_slice_in_dim(order_row, my_index * per_dev, per_dev, 0)
    my_pairs = my_index * per_dev + jnp.arange(per_dev, dtype=jnp.int32)
    seg_pairs = jnp.take(seg_len, my_pairs // HEADS).astype(jnp.int32)
    w_qkv = lax.all_gather(
        lax.all_gather(qkv_weight, "batch", axis=0, tiled=True), "seq", axis=1, tiled=True
    )
    inputs32 = block_input.astype(jnp.float32)
    norm1_out, normed1, inv_std1 = norm_rows(inputs32, norm1_gain, norm1_bias)
    norm1_low = norm1_out.astype(jnp.bfloat16)
    qkv_out = jnp.dot(norm1_low, w_qkv, preferred_element_type=jnp.float32)
    queries = rotate(qkv_out[:, :D].reshape(slot_count, piece_len, HEADS, HD), cosine, sine_tab)
    keys_rot = rotate(
        qkv_out[:, D : 2 * D].reshape(slot_count, piece_len, HEADS, HD), cosine, sine_tab
    )
    values_in = qkv_out[:, 2 * D :].reshape(slot_count, piece_len, HEADS, HD)
    stacked = jnp.stack([queries, keys_rot, values_in], axis=2).astype(jnp.bfloat16)
    send = jnp.transpose(
        stacked.reshape(slot_count, piece_len, 3, head_groups, per_dev, HD), (0, 3, 4, 2, 5, 1)
    ).reshape(n_seq, per_dev, 3, HD, piece_len)
    incoming = lax.all_to_all(send, "seq", split_axis=0, concat_axis=0, tiled=True)
    later_rows = [
        lax.all_gather(w, "batch", axis=0, tiled=True)
        for w in (proj_weight, up_weight, down_weight)
    ]
    w_proj, w_up, w_down = (
        lax.all_gather(rows, "seq", axis=1, tiled=True) for rows in later_rows
    )
    qkv_t = jnp.transpose(incoming, (1, 2, 3, 0, 4)).reshape(per_dev, 3, HD, SLOT)
    attn_t, lse_rows = attn_forward(qkv_t, seg_pairs)
    back = jnp.transpose(attn_t.reshape(per_dev, HD, n_seq, piece_len), (2, 0, 1, 3))
    returned = lax.all_to_all(back, "seq", split_axis=0, concat_axis=0, tiled=True)
    lse_all = lax.all_gather(lse_rows.reshape(per_dev, SLOT), "seq", axis=0, tiled=True)
    lse_all, returned = lax.optimization_barrier((lse_all, returned))
    attended = jnp.transpose(
        returned.reshape(slot_count, head_groups, per_dev, HD, piece_len), (0, 4, 1, 2, 3)
    ).reshape(row_count, D)
    middle = inputs32 + jnp.dot(attended, w_proj, preferred_element_type=jnp.float32)
    norm2_out, normed2, inv_std2 = norm_rows(middle, norm2_gain, norm2_bias)
    norm2_low = norm2_out.astype(jnp.bfloat16)
    hidden_up = jnp.dot(norm2_low, w_up, preferred_element_type=jnp.float32)
    gelu_out, gelu_pull = jax.vjp(lambda hidden: jax.nn.gelu(hidden, approximate=True), hidden_up)
    gelu_low = gelu_out.astype(jnp.bfloat16)
    block_out = middle + jnp.dot(gelu_low, w_down, preferred_element_type=jnp.float32)
    dwa_out = dwa_weights[HIST] * block_out
    for layer_idx in range(HIST):
        dwa_out = dwa_out + dwa_weights[layer_idx] * history[layer_idx].astype(jnp.float32)
    block_output = dwa_out.astype(jnp.bfloat16)
    grad_out = cotangent.astype(jnp.float32)
    history_grad = (dwa_weights[:HIST, None, None] * grad_out[None]).astype(jnp.bfloat16)
    dwa_terms = [
        jnp.sum(history[layer_idx].astype(jnp.float32) * grad_out) for layer_idx in range(HIST)
    ]
    dwa_terms.append(jnp.sum(block_out * grad_out))
    dwa_local = jnp.stack(dwa_terms)
    dy_full = dwa_weights[HIST] * grad_out
    dmlp_low = dy_full.astype(jnp.bfloat16)
    down_local = jnp.einsum("nf,nd->fd", gelu_low, dmlp_low, preferred_element_type=jnp.float32)
    dgelu = jnp.einsum("nd,fd->nf", dmlp_low, w_down, preferred_element_type=jnp.float32)
    dup_low = gelu_pull(dgelu)[0].astype(jnp.bfloat16)
    up_local = jnp.einsum("nd,nf->df", norm2_low, dup_low, preferred_element_type=jnp.float32)
    dnorm2 = jnp.einsum("nf,df->nd", dup_low, w_up, preferred_element_type=jnp.float32)
    dmid_norm, gain2_local, bias2_local = norm_back(dnorm2, normed2, inv_std2, norm2_gain)
    dmiddle = dy_full + dmid_norm
    dmiddle_low = dmiddle.astype(jnp.bfloat16)
    proj_local = jnp.einsum("nd,ne->de", attended, dmiddle_low, preferred_element_type=jnp.float32)
    dattended = jnp.einsum(
        "ne,de->nd", dmiddle_low, w_proj, preferred_element_type=jnp.float32
    ).astype(jnp.bfloat16)
    dsend = jnp.transpose(
        dattended.reshape(slot_count, piece_len, head_groups, per_dev, HD), (0, 2, 3, 4, 1)
    ).reshape(n_seq, per_dev, HD, piece_len)
    dattn_in = lax.all_to_all(dsend, "seq", split_axis=0, concat_axis=0, tiled=True)
    dout_t = jnp.transpose(dattn_in, (1, 2, 0, 3)).reshape(per_dev, HD, SLOT)
    dpairs = attn_backward(qkv_t, dout_t, attn_t, lse_rows, seg_pairs)
    dback = jnp.transpose(
        dpairs.reshape(per_dev, 3, HD, n_seq, piece_len), (3, 0, 1, 2, 4)
    )
    dreturned = lax.all_to_all(dback, "seq", split_axis=0, concat_axis=0, tiled=True)
    dtokens = jnp.transpose(
        dreturned.reshape(slot_count, head_groups, per_dev, 3, HD, piece_len), (0, 5, 3, 1, 2, 4)
    ).reshape(slot_count, piece_len, 3, HEADS, HD)
    dq_rows = unrotate(dtokens[:, :, 0].astype(jnp.float32), cosine, sine_tab).reshape(row_count, D)
    dk_rows = unrotate(dtokens[:, :, 1].astype(jnp.float32), cosine, sine_tab).reshape(row_count, D)
    dv_rows = dtokens[:, :, 2].astype(jnp.float32).reshape(row_count, D)
    dqkv_low = jnp.concatenate([dq_rows, dk_rows, dv_rows], axis=-1).astype(jnp.bfloat16)
    qkv_local = jnp.einsum("nd,nf->df", norm1_low, dqkv_low, preferred_element_type=jnp.float32)
    dnorm1 = jnp.einsum("nf,df->nd", dqkv_low, w_qkv, preferred_element_type=jnp.float32)
    dinput_norm, gain1_local, bias1_local = norm_back(dnorm1, normed1, inv_std1, norm1_gain)
    input_grad = (dmiddle + dinput_norm).astype(jnp.bfloat16)

    def by_cols(partial):
        rows, cols = partial.shape
        bits = n_seq.bit_length() - 1
        acc = partial.reshape((rows,) + (2,) * bits + (cols // n_seq,))
        for bit in range(bits):
            mine = (my_index >> bit) & 1
            keep = lax.dynamic_index_in_dim(acc, mine, axis=acc.ndim - 2, keepdims=False)
            send = lax.dynamic_index_in_dim(acc, 1 - mine, axis=acc.ndim - 2, keepdims=False)
            partner = [(i, i ^ (1 << bit)) for i in range(n_seq)]
            got = lax.ppermute(send.astype(jnp.bfloat16), "seq", partner)
            acc = keep + got.astype(jnp.float32)
        return acc.astype(jnp.bfloat16)

    def by_rows(col_sum):
        return lax.psum_scatter(col_sum, "batch", scatter_dimension=0, tiled=True).astype(
            jnp.float32
        )

    qkv_grad = by_rows(by_cols(qkv_local))
    proj_grad = by_rows(by_cols(proj_local))
    up_grad = by_rows(by_cols(up_local))
    down_grad = by_rows(by_cols(down_local))
    small_sums = jnp.concatenate([gain1_local, bias1_local, gain2_local, bias2_local, dwa_local])
    for axis in ("seq", "batch"):
        size = lax.axis_size(axis)
        hop = 1
        while hop < size:
            partner = [(i, i ^ hop) for i in range(size)]
            small_sums = small_sums + lax.ppermute(small_sums, axis, partner)
            hop *= 2
    gain1_grad, bias1_grad, gain2_grad, bias2_grad = (
        small_sums[k * D : (k + 1) * D] for k in range(4)
    )
    dwa_grad = small_sums[4 * D :]
    row_lse = jnp.take(lse_all, held_pairs, axis=0).reshape(1, per_dev, SLOT)
    return (
        block_output,
        input_grad,
        history_grad,
        row_lse,
        qkv_grad,
        proj_grad,
        up_grad,
        down_grad,
        gain1_grad,
        bias1_grad,
        gain2_grad,
        bias2_grad,
        dwa_grad,
    )


def solution(mesh):
    placed = (
        P(("batch", "seq"), None),
        P(None, ("batch", "seq"), None),
        P(("batch", "seq"), None),
        P("batch", "seq"),
        P("batch", "seq"),
        P("batch", "seq"),
        P("batch", "seq"),
        P(),
        P(),
        P(),
        P(),
        P(),
        P("batch", None),
        P("batch", None),
    )

    return jax.shard_map(
        local,
        mesh=mesh,
        in_specs=placed,
        out_specs=(
            P(("batch", "seq"), None),
            P(("batch", "seq"), None),
            P(None, ("batch", "seq"), None),
            P("batch", "seq", None),
            P("batch", "seq"),
            P("batch", "seq"),
            P("batch", "seq"),
            P("batch", "seq"),
            P(),
            P(),
            P(),
            P(),
            P(),
        ),
        check_vma=False,
    )
```

```python
import jax
import jax.numpy as jnp
from jax import lax
from jax.sharding import PartitionSpec as P
from jax.experimental import pallas as pl
from jax.experimental.pallas import tpu as pltpu
import functools

D = 768
HEADS = 12
HD = 64
SLOT = 2048
HIST = 8


NORM_EPS = 1e-05
MASKED = -1e30
NT_DIMS = (((1,), (1,)), ((), ()))


def fwd_kernel(seg_ref, q_ref, k_ref, v_ref, o_ref, lse_ref, *, bq, bk, scale):
    pair = pl.program_id(0)
    qi = pl.program_id(1)
    seg_len = seg_ref[pair]
    q_start = qi * bq
    seg_start = (q_start // seg_len) * seg_len
    query = (q_ref[0, 0].astype(jnp.float32).T * scale).astype(jnp.bfloat16)

    def step(j, carry, masked):
        m_old, l_old, acc = carry
        k_off = pl.multiple_of(j * bk, bk)
        key_t = k_ref[0, 0, :, pl.ds(k_off, bk)]
        value_t = v_ref[0, 0, :, pl.ds(k_off, bk)]
        s = jnp.dot(query, key_t, preferred_element_type=jnp.float32)
        if masked:
            rows = q_start + lax.broadcasted_iota(jnp.int32, (bq, bk), 0)
            cols = k_off + lax.broadcasted_iota(jnp.int32, (bq, bk), 1)
            s = jnp.where(cols <= rows, s, MASKED)
        m_new = jnp.maximum(m_old, jnp.max(s, axis=-1, keepdims=True))
        alpha = jnp.exp(m_old - m_new)
        weights = jnp.exp(s - m_new)
        l_new = alpha * l_old + jnp.sum(weights, axis=-1, keepdims=True)
        acc = alpha * acc + lax.dot_general(
            weights.astype(jnp.bfloat16), value_t, NT_DIMS, preferred_element_type=jnp.float32
        )
        return m_new, l_new, acc

    carry = (
        jnp.full((bq, 1), MASKED, jnp.float32),
        jnp.zeros((bq, 1), jnp.float32),
        jnp.zeros((bq, HD), jnp.float32),
    )
    j_diag = q_start // bk
    carry = lax.fori_loop(seg_start // bk, j_diag, lambda j, c: step(j, c, False), carry)
    for r in range(bq // bk):
        carry = step(j_diag + r, carry, True)
    m_fin, l_fin, acc = carry
    o_ref[0] = (acc / l_fin).T.astype(o_ref.dtype)
    lse = m_fin + jnp.log(l_fin)
    lse_ref[0] = jnp.transpose(jnp.broadcast_to(lse, (bq, 128)))[0:1, :]


def attn_forward(qkv_t, seg_pairs, bq=512, bk=512):
    pairs, _, head_size, seq_len = qkv_t.shape
    scale = head_size ** (-0.5)
    n_q = seq_len // bq
    blocks_done = pairs * (seq_len // bk) * (seq_len // bk + 1) // 2
    cost = pl.CostEstimate(
        flops=4 * blocks_done * bk * bk * head_size,
        transcendentals=blocks_done * bk * bk,
        bytes_accessed=pairs * seq_len * head_size * 2 * 4 + pairs * seq_len * 4,
    )
    grid_spec = pltpu.PrefetchScalarGridSpec(
        num_scalar_prefetch=1,
        grid=(pairs, n_q),
        in_specs=[
            pl.BlockSpec((1, 1, head_size, bq), lambda p, i, seg: (p, 0, 0, i)),
            pl.BlockSpec((1, 1, head_size, seq_len), lambda p, i, seg: (p, 1, 0, 0)),
            pl.BlockSpec((1, 1, head_size, seq_len), lambda p, i, seg: (p, 2, 0, 0)),
        ],
        out_specs=[
            pl.BlockSpec((1, head_size, bq), lambda p, i, seg: (p, 0, i)),
            pl.BlockSpec((1, 1, bq), lambda p, i, seg: (p, 0, i)),
        ],
    )
    return pl.pallas_call(
        functools.partial(fwd_kernel, bq=bq, bk=bk, scale=scale),
        grid_spec=grid_spec,
        out_shape=[
            jax.ShapeDtypeStruct((pairs, head_size, seq_len), jnp.bfloat16),
            jax.ShapeDtypeStruct((pairs, 1, seq_len), jnp.float32),
        ],
        cost_estimate=cost,
        name="attn_fwd",
    )(seg_pairs, qkv_t, qkv_t, qkv_t)


def bwd_kernel(seg_ref, q_ref, k_ref, v_ref, do_ref, o_ref, lse_ref, out_ref, dq_acc, *, bk, bq, scale):
    pair = pl.program_id(0)
    kj = pl.program_id(1)

    @pl.when(kj == 0)
    def _():
        dq_acc[...] = jnp.zeros_like(dq_acc)

    seg_len = seg_ref[pair]
    k_start = kj * bk
    seg_end = (k_start // seg_len + 1) * seg_len
    key_t = k_ref[0, 0]
    key = key_t.astype(jnp.float32).T.astype(jnp.bfloat16)
    value_s = (v_ref[0, 0].astype(jnp.float32).T * scale).astype(jnp.bfloat16)

    def step(i, carry, masked):
        dk_t, dv_t = carry
        q_off = pl.multiple_of(i * bq, bq)
        query_t = q_ref[0, 0, :, pl.ds(q_off, bq)]
        query_ts = (query_t.astype(jnp.float32) * scale).astype(jnp.bfloat16)
        dout_t = do_ref[0, :, pl.ds(q_off, bq)]
        out_t = o_ref[0, :, pl.ds(q_off, bq)]
        lse = lse_ref[0, :, pl.ds(q_off, bq)]
        delta = jnp.sum(
            dout_t.astype(jnp.float32) * out_t.astype(jnp.float32), axis=0, keepdims=True
        ) * scale
        s_t = jnp.dot(key, query_ts, preferred_element_type=jnp.float32)
        if masked:
            keys_at = k_start + lax.broadcasted_iota(jnp.int32, (bk, bq), 0)
            queries_at = q_off + lax.broadcasted_iota(jnp.int32, (bk, bq), 1)
            s_t = jnp.where(keys_at <= queries_at, s_t, MASKED)
        p_t = jnp.exp(s_t - lse)
        dv_t = dv_t + lax.dot_general(
            dout_t, p_t.astype(jnp.bfloat16), NT_DIMS, preferred_element_type=jnp.float32
        )
        dp_t = jnp.dot(value_s, dout_t, preferred_element_type=jnp.float32)
        ds_t = (p_t * (dp_t - delta)).astype(jnp.bfloat16)
        dk_t = dk_t + lax.dot_general(query_t, ds_t, NT_DIMS, preferred_element_type=jnp.float32)
        dq_acc[:, pl.ds(q_off, bq)] += jnp.dot(key_t, ds_t, preferred_element_type=jnp.float32)
        return dk_t, dv_t

    carry = (jnp.zeros((HD, bk), jnp.float32), jnp.zeros((HD, bk), jnp.float32))
    for r in range(bk // bq):
        carry = step(k_start // bq + r, carry, True)
    dk_t, dv_t = lax.fori_loop(
        (k_start + bk) // bq, seg_end // bq, lambda i, c: step(i, c, False), carry
    )
    out_ref[0, 0] = dq_acc[:, pl.ds(pl.multiple_of(k_start, bk), bk)].astype(out_ref.dtype)
    out_ref[0, 1] = dk_t.astype(out_ref.dtype)
    out_ref[0, 2] = dv_t.astype(out_ref.dtype)


def attn_backward(qkv_t, dout_t, out_t, lse, seg_pairs, bk=512, bq=512):
    pairs, _, head_size, seq_len = qkv_t.shape
    scale = head_size ** (-0.5)
    n_k = seq_len // bk
    blocks_done = pairs * (seq_len // bq) * (seq_len // bq + 1) // 2
    cost = pl.CostEstimate(
        flops=10 * blocks_done * bq * bq * head_size,
        transcendentals=blocks_done * bq * bq,
        bytes_accessed=pairs * seq_len * head_size * 2 * 8 + pairs * seq_len * 4,
    )
    grid_spec = pltpu.PrefetchScalarGridSpec(
        num_scalar_prefetch=1,
        grid=(pairs, n_k),
        in_specs=[
            pl.BlockSpec((1, 1, head_size, seq_len), lambda p, j, seg: (p, 0, 0, 0)),
            pl.BlockSpec((1, 1, head_size, bk), lambda p, j, seg: (p, 1, 0, j)),
            pl.BlockSpec((1, 1, head_size, bk), lambda p, j, seg: (p, 2, 0, j)),
            pl.BlockSpec((1, head_size, seq_len), lambda p, j, seg: (p, 0, 0)),
            pl.BlockSpec((1, head_size, seq_len), lambda p, j, seg: (p, 0, 0)),
            pl.BlockSpec((1, 1, seq_len), lambda p, j, seg: (p, 0, 0)),
        ],
        out_specs=pl.BlockSpec((1, 3, head_size, bk), lambda p, j, seg: (p, 0, 0, j)),
        scratch_shapes=[pltpu.VMEM((head_size, seq_len), jnp.float32)],
    )
    return pl.pallas_call(
        functools.partial(bwd_kernel, bk=bk, bq=bq, scale=scale),
        grid_spec=grid_spec,
        out_shape=jax.ShapeDtypeStruct((pairs, 3, head_size, seq_len), jnp.bfloat16),
        cost_estimate=cost,
        name="attn_bwd",
    )(seg_pairs, qkv_t, qkv_t, qkv_t, dout_t, out_t, lse)


def norm_rows(values, gain, shift):
    row_mean = jnp.mean(values, axis=-1, keepdims=True)
    centred = values - row_mean
    variance = jnp.mean(centred * centred, axis=-1, keepdims=True)
    inv_std = lax.rsqrt(variance + NORM_EPS)
    normed = centred * inv_std
    return (normed * gain + shift, normed, inv_std)


def norm_back(grad_in, normed, inv_std, gain):
    scaled = grad_in * gain
    centred = (
        scaled
        - jnp.mean(scaled, axis=-1, keepdims=True)
        - normed * jnp.mean(scaled * normed, axis=-1, keepdims=True)
    )
    return (centred * inv_std, jnp.sum(grad_in * normed, axis=0), jnp.sum(grad_in, axis=0))


def rotate(values, cosine, sine_tab):
    half_size = values.shape[-1] // 2
    front = values[..., :half_size]
    behind = values[..., half_size:]
    cos_part = cosine[..., None, :]
    sin_part = sine_tab[..., None, :]
    return jnp.concatenate(
        [front * cos_part - behind * sin_part, behind * cos_part + front * sin_part], axis=-1
    )


def unrotate(values, cosine, sine_tab):
    half_size = values.shape[-1] // 2
    front = values[..., :half_size]
    behind = values[..., half_size:]
    cos_part = cosine[..., None, :]
    sin_part = sine_tab[..., None, :]
    return jnp.concatenate(
        [front * cos_part + behind * sin_part, behind * cos_part - front * sin_part], axis=-1
    )


def local(
    block_input,
    history,
    cotangent,
    qkv_weight,
    proj_weight,
    up_weight,
    down_weight,
    norm1_gain,
    norm1_bias,
    norm2_gain,
    norm2_bias,
    dwa_weights,
    pair_order,
    long_group,
):
    n_seq = lax.axis_size("seq")
    row_count = block_input.shape[0]
    piece_len = SLOT // n_seq
    slot_count = row_count // piece_len
    pair_count = slot_count * HEADS
    per_dev = pair_count // n_seq
    slot_flags = long_group[0]
    seg_len = SLOT // jnp.left_shift(jnp.ones_like(slot_flags), slot_flags)
    position = jnp.arange(SLOT, dtype=jnp.int32)
    doc_place = (position[None, :] % seg_len[:, None]).astype(jnp.float32)
    frequency = jnp.power(10000.0, jnp.arange(HD // 2, dtype=jnp.float32) * (-2.0 / HD))
    angles = doc_place[..., None] * frequency
    my_index = lax.axis_index("seq")
    my_start = my_index * piece_len
    cosine = lax.dynamic_slice_in_dim(jnp.cos(angles), my_start, piece_len, 1)
    sine_tab = lax.dynamic_slice_in_dim(jnp.sin(angles), my_start, piece_len, 1)
    head_groups = HEADS // per_dev
    order_row = pair_order[0]
    held_pairs = lax.dynamic_slice_in_dim(order_row, my_index * per_dev, per_dev, 0)
    my_pairs = my_index * per_dev + jnp.arange(per_dev, dtype=jnp.int32)
    seg_pairs = jnp.take(seg_len, my_pairs // HEADS).astype(jnp.int32)
    n_batch = lax.axis_size("batch")
    batch_index = lax.axis_index("batch")

    def gather_doubling(local):
        acc = local
        stacked = 0
        for axis, size, me in (("batch", n_batch, batch_index), ("seq", n_seq, my_index)):
            bits = size.bit_length() - 1
            for bit in reversed(range(bits)):
                partner = [(i, i ^ (1 << bit)) for i in range(size)]
                got = lax.ppermute(acc, axis, partner)
                low = ((me >> bit) & 1) == 0
                acc = jnp.where(low, jnp.stack([acc, got]), jnp.stack([got, acc]))
                stacked += 1
        bit_axes = list(range(stacked))[::-1]
        return jnp.transpose(acc, bit_axes + list(range(stacked, acc.ndim))).reshape(
            (n_batch, n_seq) + local.shape
        )

    def assemble(blocks, rows, cols):
        return jnp.transpose(blocks.reshape(n_batch, n_seq, rows, cols), (0, 2, 1, 3)).reshape(
            n_batch * rows, n_seq * cols
        )

    w_qkv = assemble(gather_doubling(qkv_weight), *qkv_weight.shape)
    later = (proj_weight, up_weight, down_weight)
    later_flat, w_qkv = lax.optimization_barrier(
        (jnp.concatenate([w.reshape(-1) for w in later]), w_qkv)
    )
    later_blocks = gather_doubling(later_flat)
    offset = 0
    later_full = []
    for w in later:
        later_full.append(assemble(later_blocks[:, :, offset : offset + w.size], *w.shape))
        offset += w.size
    w_proj, w_up, w_down = later_full
    inputs32 = block_input.astype(jnp.float32)
    norm1_out, normed1, inv_std1 = norm_rows(inputs32, norm1_gain, norm1_bias)
    norm1_low = norm1_out.astype(jnp.bfloat16)
    qkv_out = jnp.dot(norm1_low, w_qkv, preferred_element_type=jnp.float32)
    queries = rotate(qkv_out[:, :D].reshape(slot_count, piece_len, HEADS, HD), cosine, sine_tab)
    keys_rot = rotate(
        qkv_out[:, D : 2 * D].reshape(slot_count, piece_len, HEADS, HD), cosine, sine_tab
    )
    values_in = qkv_out[:, 2 * D :].reshape(slot_count, piece_len, HEADS, HD)
    stacked = jnp.stack([queries, keys_rot, values_in], axis=2).astype(jnp.bfloat16)
    send = jnp.transpose(
        stacked.reshape(slot_count, piece_len, 3, head_groups, per_dev, HD), (0, 3, 4, 2, 5, 1)
    ).reshape(n_seq, per_dev, 3, HD, piece_len)
    incoming = lax.all_to_all(send, "seq", split_axis=0, concat_axis=0, tiled=True)
    qkv_t = jnp.transpose(incoming, (1, 2, 3, 0, 4)).reshape(per_dev, 3, HD, SLOT)
    attn_t, lse_rows = attn_forward(qkv_t, seg_pairs)
    back = jnp.transpose(attn_t.reshape(per_dev, HD, n_seq, piece_len), (2, 0, 1, 3))
    returned = lax.all_to_all(back, "seq", split_axis=0, concat_axis=0, tiled=True)
    lse_all = lax.all_gather(lse_rows.reshape(per_dev, SLOT), "seq", axis=0, tiled=True)
    lse_all, returned = lax.optimization_barrier((lse_all, returned))
    attended = jnp.transpose(
        returned.reshape(slot_count, head_groups, per_dev, HD, piece_len), (0, 4, 1, 2, 3)
    ).reshape(row_count, D)
    middle = inputs32 + jnp.dot(attended, w_proj, preferred_element_type=jnp.float32)
    norm2_out, normed2, inv_std2 = norm_rows(middle, norm2_gain, norm2_bias)
    norm2_low = norm2_out.astype(jnp.bfloat16)
    hidden_up = jnp.dot(norm2_low, w_up, preferred_element_type=jnp.float32)
    gelu_out, gelu_pull = jax.vjp(lambda hidden: jax.nn.gelu(hidden, approximate=True), hidden_up)
    gelu_low = gelu_out.astype(jnp.bfloat16)
    block_out = middle + jnp.dot(gelu_low, w_down, preferred_element_type=jnp.float32)
    dwa_out = dwa_weights[HIST] * block_out
    for layer_idx in range(HIST):
        dwa_out = dwa_out + dwa_weights[layer_idx] * history[layer_idx].astype(jnp.float32)
    block_output = dwa_out.astype(jnp.bfloat16)
    grad_out = cotangent.astype(jnp.float32)
    history_grad = (dwa_weights[:HIST, None, None] * grad_out[None]).astype(jnp.bfloat16)
    dwa_terms = [
        jnp.sum(history[layer_idx].astype(jnp.float32) * grad_out) for layer_idx in range(HIST)
    ]
    dwa_terms.append(jnp.sum(block_out * grad_out))
    dwa_local = jnp.stack(dwa_terms)
    dy_full = dwa_weights[HIST] * grad_out
    dmlp_low = dy_full.astype(jnp.bfloat16)
    down_local = jnp.einsum("nf,nd->fd", gelu_low, dmlp_low, preferred_element_type=jnp.float32)
    dgelu = jnp.einsum("nd,fd->nf", dmlp_low, w_down, preferred_element_type=jnp.float32)
    dup_low = gelu_pull(dgelu)[0].astype(jnp.bfloat16)
    up_local = jnp.einsum("nd,nf->df", norm2_low, dup_low, preferred_element_type=jnp.float32)
    dnorm2 = jnp.einsum("nf,df->nd", dup_low, w_up, preferred_element_type=jnp.float32)
    dmid_norm, gain2_local, bias2_local = norm_back(dnorm2, normed2, inv_std2, norm2_gain)
    dmiddle = dy_full + dmid_norm
    dmiddle_low = dmiddle.astype(jnp.bfloat16)
    proj_local = jnp.einsum("nd,ne->de", attended, dmiddle_low, preferred_element_type=jnp.float32)
    dattended = jnp.einsum(
        "ne,de->nd", dmiddle_low, w_proj, preferred_element_type=jnp.float32
    ).astype(jnp.bfloat16)
    dsend = jnp.transpose(
        dattended.reshape(slot_count, piece_len, head_groups, per_dev, HD), (0, 2, 3, 4, 1)
    ).reshape(n_seq, per_dev, HD, piece_len)
    dattn_in = lax.all_to_all(dsend, "seq", split_axis=0, concat_axis=0, tiled=True)
    dout_t = jnp.transpose(dattn_in, (1, 2, 0, 3)).reshape(per_dev, HD, SLOT)
    dpairs = attn_backward(qkv_t, dout_t, attn_t, lse_rows, seg_pairs)
    dback = jnp.transpose(
        dpairs.reshape(per_dev, 3, HD, n_seq, piece_len), (3, 0, 1, 2, 4)
    )
    dreturned = lax.all_to_all(dback, "seq", split_axis=0, concat_axis=0, tiled=True)
    dtokens = jnp.transpose(
        dreturned.reshape(slot_count, head_groups, per_dev, 3, HD, piece_len), (0, 5, 3, 1, 2, 4)
    ).reshape(slot_count, piece_len, 3, HEADS, HD)
    dq_rows = unrotate(dtokens[:, :, 0].astype(jnp.float32), cosine, sine_tab).reshape(row_count, D)
    dk_rows = unrotate(dtokens[:, :, 1].astype(jnp.float32), cosine, sine_tab).reshape(row_count, D)
    dv_rows = dtokens[:, :, 2].astype(jnp.float32).reshape(row_count, D)
    dqkv_low = jnp.concatenate([dq_rows, dk_rows, dv_rows], axis=-1).astype(jnp.bfloat16)
    qkv_local = jnp.einsum("nd,nf->df", norm1_low, dqkv_low, preferred_element_type=jnp.float32)
    dnorm1 = jnp.einsum("nf,df->nd", dqkv_low, w_qkv, preferred_element_type=jnp.float32)
    dinput_norm, gain1_local, bias1_local = norm_back(dnorm1, normed1, inv_std1, norm1_gain)
    input_grad = (dmiddle + dinput_norm).astype(jnp.bfloat16)

    def by_cols(partial):
        rows, cols = partial.shape
        bits = n_seq.bit_length() - 1
        acc = partial.reshape((rows,) + (2,) * bits + (cols // n_seq,))
        for bit in range(bits):
            mine = (my_index >> bit) & 1
            keep = lax.dynamic_index_in_dim(acc, mine, axis=acc.ndim - 2, keepdims=False)
            send = lax.dynamic_index_in_dim(acc, 1 - mine, axis=acc.ndim - 2, keepdims=False)
            partner = [(i, i ^ (1 << bit)) for i in range(n_seq)]
            got = lax.ppermute(send.astype(jnp.bfloat16), "seq", partner)
            acc = keep + got.astype(jnp.float32)
        return acc.astype(jnp.bfloat16)

    def by_rows(col_sum):
        return lax.psum_scatter(col_sum, "batch", scatter_dimension=0, tiled=True).astype(
            jnp.float32
        )

    qkv_grad = by_rows(by_cols(qkv_local))
    proj_grad = by_rows(by_cols(proj_local))
    up_grad = by_rows(by_cols(up_local))
    down_grad = by_rows(by_cols(down_local))
    small_sums = jnp.concatenate([gain1_local, bias1_local, gain2_local, bias2_local, dwa_local])
    for axis in ("seq", "batch"):
        size = lax.axis_size(axis)
        hop = 1
        while hop < size:
            partner = [(i, i ^ hop) for i in range(size)]
            small_sums = small_sums + lax.ppermute(small_sums, axis, partner)
            hop *= 2
    gain1_grad, bias1_grad, gain2_grad, bias2_grad = (
        small_sums[k * D : (k + 1) * D] for k in range(4)
    )
    dwa_grad = small_sums[4 * D :]
    row_lse = jnp.take(lse_all, held_pairs, axis=0).reshape(1, per_dev, SLOT)
    return (
        block_output,
        input_grad,
        history_grad,
        row_lse,
        qkv_grad,
        proj_grad,
        up_grad,
        down_grad,
        gain1_grad,
        bias1_grad,
        gain2_grad,
        bias2_grad,
        dwa_grad,
    )


def solution(mesh):
    placed = (
        P(("batch", "seq"), None),
        P(None, ("batch", "seq"), None),
        P(("batch", "seq"), None),
        P("batch", "seq"),
        P("batch", "seq"),
        P("batch", "seq"),
        P("batch", "seq"),
        P(),
        P(),
        P(),
        P(),
        P(),
        P("batch", None),
        P("batch", None),
    )

    return jax.shard_map(
        local,
        mesh=mesh,
        in_specs=placed,
        out_specs=(
            P(("batch", "seq"), None),
            P(("batch", "seq"), None),
            P(None, ("batch", "seq"), None),
            P("batch", "seq", None),
            P("batch", "seq"),
            P("batch", "seq"),
            P("batch", "seq"),
            P("batch", "seq"),
            P(),
            P(),
            P(),
            P(),
            P(),
        ),
        check_vma=False,
    )
```

```python
import jax
import jax.numpy as jnp
from jax import lax
from jax.sharding import PartitionSpec as P
from jax.experimental import pallas as pl
from jax.experimental.pallas import tpu as pltpu
import functools

D = 768
HEADS = 12
HD = 64
SLOT = 2048
HIST = 8


NORM_EPS = 1e-05
MASKED = -1e30
NT_DIMS = (((1,), (1,)), ((), ()))


def fwd_kernel(seg_ref, q_ref, k_ref, v_ref, o_ref, lse_ref, *, bq, bk, scale):
    pair = pl.program_id(0)
    qi = pl.program_id(1)
    seg_len = seg_ref[pair]
    q_start = qi * bq
    seg_start = (q_start // seg_len) * seg_len
    query = (q_ref[0, 0].astype(jnp.float32).T * scale).astype(jnp.bfloat16)

    def step(j, carry, masked):
        m_old, l_old, acc = carry
        k_off = pl.multiple_of(j * bk, bk)
        key_t = k_ref[0, 0, :, pl.ds(k_off, bk)]
        value_t = v_ref[0, 0, :, pl.ds(k_off, bk)]
        s = jnp.dot(query, key_t, preferred_element_type=jnp.float32)
        if masked:
            rows = q_start + lax.broadcasted_iota(jnp.int32, (bq, bk), 0)
            cols = k_off + lax.broadcasted_iota(jnp.int32, (bq, bk), 1)
            s = jnp.where(cols <= rows, s, MASKED)
        m_new = jnp.maximum(m_old, jnp.max(s, axis=-1, keepdims=True))
        alpha = jnp.exp(m_old - m_new)
        weights = jnp.exp(s - m_new)
        l_new = alpha * l_old + jnp.sum(weights, axis=-1, keepdims=True)
        acc = alpha * acc + lax.dot_general(
            weights.astype(jnp.bfloat16), value_t, NT_DIMS, preferred_element_type=jnp.float32
        )
        return m_new, l_new, acc

    carry = (
        jnp.full((bq, 1), MASKED, jnp.float32),
        jnp.zeros((bq, 1), jnp.float32),
        jnp.zeros((bq, HD), jnp.float32),
    )
    j_diag = q_start // bk
    carry = lax.fori_loop(seg_start // bk, j_diag, lambda j, c: step(j, c, False), carry)
    for r in range(bq // bk):
        carry = step(j_diag + r, carry, True)
    m_fin, l_fin, acc = carry
    o_ref[0] = (acc / l_fin).T.astype(o_ref.dtype)
    lse = m_fin + jnp.log(l_fin)
    lse_ref[0] = jnp.transpose(jnp.broadcast_to(lse, (bq, 128)))[0:1, :]


def attn_forward(qkv_t, seg_pairs, bq=512, bk=512):
    pairs, _, head_size, seq_len = qkv_t.shape
    scale = head_size ** (-0.5)
    n_q = seq_len // bq
    blocks_done = pairs * (seq_len // bk) * (seq_len // bk + 1) // 2
    cost = pl.CostEstimate(
        flops=4 * blocks_done * bk * bk * head_size,
        transcendentals=blocks_done * bk * bk,
        bytes_accessed=pairs * seq_len * head_size * 2 * 4 + pairs * seq_len * 4,
    )
    grid_spec = pltpu.PrefetchScalarGridSpec(
        num_scalar_prefetch=1,
        grid=(pairs, n_q),
        in_specs=[
            pl.BlockSpec((1, 1, head_size, bq), lambda p, i, seg: (p, 0, 0, i)),
            pl.BlockSpec((1, 1, head_size, seq_len), lambda p, i, seg: (p, 1, 0, 0)),
            pl.BlockSpec((1, 1, head_size, seq_len), lambda p, i, seg: (p, 2, 0, 0)),
        ],
        out_specs=[
            pl.BlockSpec((1, head_size, bq), lambda p, i, seg: (p, 0, i)),
            pl.BlockSpec((1, 1, bq), lambda p, i, seg: (p, 0, i)),
        ],
    )
    return pl.pallas_call(
        functools.partial(fwd_kernel, bq=bq, bk=bk, scale=scale),
        grid_spec=grid_spec,
        out_shape=[
            jax.ShapeDtypeStruct((pairs, head_size, seq_len), jnp.bfloat16),
            jax.ShapeDtypeStruct((pairs, 1, seq_len), jnp.float32),
        ],
        cost_estimate=cost,
        name="attn_fwd",
    )(seg_pairs, qkv_t, qkv_t, qkv_t)


def bwd_kernel(seg_ref, q_ref, k_ref, v_ref, do_ref, o_ref, lse_ref, out_ref, dq_acc, *, bk, bq, scale):
    pair = pl.program_id(0)
    kj = pl.program_id(1)

    @pl.when(kj == 0)
    def _():
        dq_acc[...] = jnp.zeros_like(dq_acc)

    seg_len = seg_ref[pair]
    k_start = kj * bk
    seg_end = (k_start // seg_len + 1) * seg_len
    key_t = k_ref[0, 0]
    key = key_t.astype(jnp.float32).T.astype(jnp.bfloat16)
    value_s = (v_ref[0, 0].astype(jnp.float32).T * scale).astype(jnp.bfloat16)

    def step(i, carry, masked):
        dk_t, dv_t = carry
        q_off = pl.multiple_of(i * bq, bq)
        query_t = q_ref[0, 0, :, pl.ds(q_off, bq)]
        query_ts = (query_t.astype(jnp.float32) * scale).astype(jnp.bfloat16)
        dout_t = do_ref[0, :, pl.ds(q_off, bq)]
        out_t = o_ref[0, :, pl.ds(q_off, bq)]
        lse = lse_ref[0, :, pl.ds(q_off, bq)]
        delta = jnp.sum(
            dout_t.astype(jnp.float32) * out_t.astype(jnp.float32), axis=0, keepdims=True
        ) * scale
        s_t = jnp.dot(key, query_ts, preferred_element_type=jnp.float32)
        if masked:
            keys_at = k_start + lax.broadcasted_iota(jnp.int32, (bk, bq), 0)
            queries_at = q_off + lax.broadcasted_iota(jnp.int32, (bk, bq), 1)
            s_t = jnp.where(keys_at <= queries_at, s_t, MASKED)
        p_t = jnp.exp(s_t - lse)
        dv_t = dv_t + lax.dot_general(
            dout_t, p_t.astype(jnp.bfloat16), NT_DIMS, preferred_element_type=jnp.float32
        )
        dp_t = jnp.dot(value_s, dout_t, preferred_element_type=jnp.float32)
        ds_t = (p_t * (dp_t - delta)).astype(jnp.bfloat16)
        dk_t = dk_t + lax.dot_general(query_t, ds_t, NT_DIMS, preferred_element_type=jnp.float32)
        dq_acc[:, pl.ds(q_off, bq)] += jnp.dot(key_t, ds_t, preferred_element_type=jnp.float32)
        return dk_t, dv_t

    carry = (jnp.zeros((HD, bk), jnp.float32), jnp.zeros((HD, bk), jnp.float32))
    for r in range(bk // bq):
        carry = step(k_start // bq + r, carry, True)
    dk_t, dv_t = lax.fori_loop(
        (k_start + bk) // bq, seg_end // bq, lambda i, c: step(i, c, False), carry
    )
    out_ref[0, 0] = dq_acc[:, pl.ds(pl.multiple_of(k_start, bk), bk)].astype(out_ref.dtype)
    out_ref[0, 1] = dk_t.astype(out_ref.dtype)
    out_ref[0, 2] = dv_t.astype(out_ref.dtype)


def attn_backward(qkv_t, dout_t, out_t, lse, seg_pairs, bk=512, bq=512):
    pairs, _, head_size, seq_len = qkv_t.shape
    scale = head_size ** (-0.5)
    n_k = seq_len // bk
    blocks_done = pairs * (seq_len // bq) * (seq_len // bq + 1) // 2
    cost = pl.CostEstimate(
        flops=10 * blocks_done * bq * bq * head_size,
        transcendentals=blocks_done * bq * bq,
        bytes_accessed=pairs * seq_len * head_size * 2 * 8 + pairs * seq_len * 4,
    )
    grid_spec = pltpu.PrefetchScalarGridSpec(
        num_scalar_prefetch=1,
        grid=(pairs, n_k),
        in_specs=[
            pl.BlockSpec((1, 1, head_size, seq_len), lambda p, j, seg: (p, 0, 0, 0)),
            pl.BlockSpec((1, 1, head_size, bk), lambda p, j, seg: (p, 1, 0, j)),
            pl.BlockSpec((1, 1, head_size, bk), lambda p, j, seg: (p, 2, 0, j)),
            pl.BlockSpec((1, head_size, seq_len), lambda p, j, seg: (p, 0, 0)),
            pl.BlockSpec((1, head_size, seq_len), lambda p, j, seg: (p, 0, 0)),
            pl.BlockSpec((1, 1, seq_len), lambda p, j, seg: (p, 0, 0)),
        ],
        out_specs=pl.BlockSpec((1, 3, head_size, bk), lambda p, j, seg: (p, 0, 0, j)),
        scratch_shapes=[pltpu.VMEM((head_size, seq_len), jnp.float32)],
    )
    return pl.pallas_call(
        functools.partial(bwd_kernel, bk=bk, bq=bq, scale=scale),
        grid_spec=grid_spec,
        out_shape=jax.ShapeDtypeStruct((pairs, 3, head_size, seq_len), jnp.bfloat16),
        cost_estimate=cost,
        name="attn_bwd",
    )(seg_pairs, qkv_t, qkv_t, qkv_t, dout_t, out_t, lse)


def norm_rows(values, gain, shift):
    row_mean = jnp.mean(values, axis=-1, keepdims=True)
    centred = values - row_mean
    variance = jnp.mean(centred * centred, axis=-1, keepdims=True)
    inv_std = lax.rsqrt(variance + NORM_EPS)
    normed = centred * inv_std
    return (normed * gain + shift, normed, inv_std)


def norm_back(grad_in, normed, inv_std, gain):
    scaled = grad_in * gain
    centred = (
        scaled
        - jnp.mean(scaled, axis=-1, keepdims=True)
        - normed * jnp.mean(scaled * normed, axis=-1, keepdims=True)
    )
    return (centred * inv_std, jnp.sum(grad_in * normed, axis=0), jnp.sum(grad_in, axis=0))


def rotate(values, cosine, sine_tab):
    half_size = values.shape[-1] // 2
    front = values[..., :half_size]
    behind = values[..., half_size:]
    cos_part = cosine[..., None, :]
    sin_part = sine_tab[..., None, :]
    return jnp.concatenate(
        [front * cos_part - behind * sin_part, behind * cos_part + front * sin_part], axis=-1
    )


def unrotate(values, cosine, sine_tab):
    half_size = values.shape[-1] // 2
    front = values[..., :half_size]
    behind = values[..., half_size:]
    cos_part = cosine[..., None, :]
    sin_part = sine_tab[..., None, :]
    return jnp.concatenate(
        [front * cos_part + behind * sin_part, behind * cos_part - front * sin_part], axis=-1
    )


def local(
    block_input,
    history,
    cotangent,
    qkv_weight,
    proj_weight,
    up_weight,
    down_weight,
    norm1_gain,
    norm1_bias,
    norm2_gain,
    norm2_bias,
    dwa_weights,
    pair_order,
    long_group,
):
    n_seq = lax.axis_size("seq")
    row_count = block_input.shape[0]
    piece_len = SLOT // n_seq
    slot_count = row_count // piece_len
    pair_count = slot_count * HEADS
    per_dev = pair_count // n_seq
    slot_flags = long_group[0]
    seg_len = SLOT // jnp.left_shift(jnp.ones_like(slot_flags), slot_flags)
    position = jnp.arange(SLOT, dtype=jnp.int32)
    doc_place = (position[None, :] % seg_len[:, None]).astype(jnp.float32)
    frequency = jnp.power(10000.0, jnp.arange(HD // 2, dtype=jnp.float32) * (-2.0 / HD))
    angles = doc_place[..., None] * frequency
    my_index = lax.axis_index("seq")
    my_start = my_index * piece_len
    cosine = lax.dynamic_slice_in_dim(jnp.cos(angles), my_start, piece_len, 1)
    sine_tab = lax.dynamic_slice_in_dim(jnp.sin(angles), my_start, piece_len, 1)
    head_groups = HEADS // per_dev
    order_row = pair_order[0]
    held_pairs = lax.dynamic_slice_in_dim(order_row, my_index * per_dev, per_dev, 0)
    my_pairs = my_index * per_dev + jnp.arange(per_dev, dtype=jnp.int32)
    seg_pairs = jnp.take(seg_len, my_pairs // HEADS).astype(jnp.int32)
    n_batch = lax.axis_size("batch")
    batch_index = lax.axis_index("batch")

    def gather_rows(local):
        acc = local
        bits = n_batch.bit_length() - 1
        for bit in reversed(range(bits)):
            partner = [(i, i ^ (1 << bit)) for i in range(n_batch)]
            got = lax.ppermute(acc, "batch", partner)
            low = ((batch_index >> bit) & 1) == 0
            acc = jnp.where(low, jnp.stack([acc, got]), jnp.stack([got, acc]))
        return jnp.transpose(acc, list(range(bits))[::-1] + list(range(bits, acc.ndim))).reshape(
            (n_batch,) + local.shape
        )

    w_qkv = lax.all_gather(
        gather_rows(qkv_weight).reshape(-1, qkv_weight.shape[1]), "seq", axis=1, tiled=True
    )
    inputs32 = block_input.astype(jnp.float32)
    norm1_out, normed1, inv_std1 = norm_rows(inputs32, norm1_gain, norm1_bias)
    norm1_low = norm1_out.astype(jnp.bfloat16)
    qkv_out = jnp.dot(norm1_low, w_qkv, preferred_element_type=jnp.float32)
    queries = rotate(qkv_out[:, :D].reshape(slot_count, piece_len, HEADS, HD), cosine, sine_tab)
    keys_rot = rotate(
        qkv_out[:, D : 2 * D].reshape(slot_count, piece_len, HEADS, HD), cosine, sine_tab
    )
    values_in = qkv_out[:, 2 * D :].reshape(slot_count, piece_len, HEADS, HD)
    stacked = jnp.stack([queries, keys_rot, values_in], axis=2).astype(jnp.bfloat16)
    send = jnp.transpose(
        stacked.reshape(slot_count, piece_len, 3, head_groups, per_dev, HD), (0, 3, 4, 2, 5, 1)
    ).reshape(n_seq, per_dev, 3, HD, piece_len)
    incoming = lax.all_to_all(send, "seq", split_axis=0, concat_axis=0, tiled=True)
    later = (proj_weight, up_weight, down_weight)
    later_rows = gather_rows(jnp.concatenate([w.reshape(-1) for w in later]))
    offset = 0
    later_full = []
    for w in later:
        rows = later_rows[:, offset : offset + w.size].reshape(-1, w.shape[1])
        later_full.append(lax.all_gather(rows, "seq", axis=1, tiled=True))
        offset += w.size
    w_proj, w_up, w_down = later_full
    qkv_t = jnp.transpose(incoming, (1, 2, 3, 0, 4)).reshape(per_dev, 3, HD, SLOT)
    attn_t, lse_rows = attn_forward(qkv_t, seg_pairs)
    back = jnp.transpose(attn_t.reshape(per_dev, HD, n_seq, piece_len), (2, 0, 1, 3))
    returned = lax.all_to_all(back, "seq", split_axis=0, concat_axis=0, tiled=True)
    lse_all = lax.all_gather(lse_rows.reshape(per_dev, SLOT), "seq", axis=0, tiled=True)
    lse_all, returned = lax.optimization_barrier((lse_all, returned))
    attended = jnp.transpose(
        returned.reshape(slot_count, head_groups, per_dev, HD, piece_len), (0, 4, 1, 2, 3)
    ).reshape(row_count, D)
    middle = inputs32 + jnp.dot(attended, w_proj, preferred_element_type=jnp.float32)
    norm2_out, normed2, inv_std2 = norm_rows(middle, norm2_gain, norm2_bias)
    norm2_low = norm2_out.astype(jnp.bfloat16)
    hidden_up = jnp.dot(norm2_low, w_up, preferred_element_type=jnp.float32)
    gelu_out, gelu_pull = jax.vjp(lambda hidden: jax.nn.gelu(hidden, approximate=True), hidden_up)
    gelu_low = gelu_out.astype(jnp.bfloat16)
    block_out = middle + jnp.dot(gelu_low, w_down, preferred_element_type=jnp.float32)
    dwa_out = dwa_weights[HIST] * block_out
    for layer_idx in range(HIST):
        dwa_out = dwa_out + dwa_weights[layer_idx] * history[layer_idx].astype(jnp.float32)
    block_output = dwa_out.astype(jnp.bfloat16)
    grad_out = cotangent.astype(jnp.float32)
    history_grad = (dwa_weights[:HIST, None, None] * grad_out[None]).astype(jnp.bfloat16)
    dwa_terms = [
        jnp.sum(history[layer_idx].astype(jnp.float32) * grad_out) for layer_idx in range(HIST)
    ]
    dwa_terms.append(jnp.sum(block_out * grad_out))
    dwa_local = jnp.stack(dwa_terms)
    dy_full = dwa_weights[HIST] * grad_out
    dmlp_low = dy_full.astype(jnp.bfloat16)
    down_local = jnp.einsum("nf,nd->fd", gelu_low, dmlp_low, preferred_element_type=jnp.float32)
    dgelu = jnp.einsum("nd,fd->nf", dmlp_low, w_down, preferred_element_type=jnp.float32)
    dup_low = gelu_pull(dgelu)[0].astype(jnp.bfloat16)
    up_local = jnp.einsum("nd,nf->df", norm2_low, dup_low, preferred_element_type=jnp.float32)
    dnorm2 = jnp.einsum("nf,df->nd", dup_low, w_up, preferred_element_type=jnp.float32)
    dmid_norm, gain2_local, bias2_local = norm_back(dnorm2, normed2, inv_std2, norm2_gain)
    dmiddle = dy_full + dmid_norm
    dmiddle_low = dmiddle.astype(jnp.bfloat16)
    proj_local = jnp.einsum("nd,ne->de", attended, dmiddle_low, preferred_element_type=jnp.float32)
    dattended = jnp.einsum(
        "ne,de->nd", dmiddle_low, w_proj, preferred_element_type=jnp.float32
    ).astype(jnp.bfloat16)
    dsend = jnp.transpose(
        dattended.reshape(slot_count, piece_len, head_groups, per_dev, HD), (0, 2, 3, 4, 1)
    ).reshape(n_seq, per_dev, HD, piece_len)
    dattn_in = lax.all_to_all(dsend, "seq", split_axis=0, concat_axis=0, tiled=True)
    dout_t = jnp.transpose(dattn_in, (1, 2, 0, 3)).reshape(per_dev, HD, SLOT)
    dpairs = attn_backward(qkv_t, dout_t, attn_t, lse_rows, seg_pairs)
    dback = jnp.transpose(
        dpairs.reshape(per_dev, 3, HD, n_seq, piece_len), (3, 0, 1, 2, 4)
    )
    dreturned = lax.all_to_all(dback, "seq", split_axis=0, concat_axis=0, tiled=True)
    dtokens = jnp.transpose(
        dreturned.reshape(slot_count, head_groups, per_dev, 3, HD, piece_len), (0, 5, 3, 1, 2, 4)
    ).reshape(slot_count, piece_len, 3, HEADS, HD)
    dq_rows = unrotate(dtokens[:, :, 0].astype(jnp.float32), cosine, sine_tab).reshape(row_count, D)
    dk_rows = unrotate(dtokens[:, :, 1].astype(jnp.float32), cosine, sine_tab).reshape(row_count, D)
    dv_rows = dtokens[:, :, 2].astype(jnp.float32).reshape(row_count, D)
    dqkv_low = jnp.concatenate([dq_rows, dk_rows, dv_rows], axis=-1).astype(jnp.bfloat16)
    qkv_local = jnp.einsum("nd,nf->df", norm1_low, dqkv_low, preferred_element_type=jnp.float32)
    dnorm1 = jnp.einsum("nf,df->nd", dqkv_low, w_qkv, preferred_element_type=jnp.float32)
    dinput_norm, gain1_local, bias1_local = norm_back(dnorm1, normed1, inv_std1, norm1_gain)
    input_grad = (dmiddle + dinput_norm).astype(jnp.bfloat16)

    def by_cols(partial):
        rows, cols = partial.shape
        bits = n_seq.bit_length() - 1
        acc = partial.reshape((rows,) + (2,) * bits + (cols // n_seq,))
        for bit in range(bits):
            mine = (my_index >> bit) & 1
            keep = lax.dynamic_index_in_dim(acc, mine, axis=acc.ndim - 2, keepdims=False)
            send = lax.dynamic_index_in_dim(acc, 1 - mine, axis=acc.ndim - 2, keepdims=False)
            partner = [(i, i ^ (1 << bit)) for i in range(n_seq)]
            got = lax.ppermute(send.astype(jnp.bfloat16), "seq", partner)
            acc = keep + got.astype(jnp.float32)
        return acc.astype(jnp.bfloat16)

    def by_rows(col_sum):
        return lax.psum_scatter(col_sum, "batch", scatter_dimension=0, tiled=True).astype(
            jnp.float32
        )

    qkv_grad = by_rows(by_cols(qkv_local))
    proj_grad = by_rows(by_cols(proj_local))
    up_grad = by_rows(by_cols(up_local))
    down_grad = by_rows(by_cols(down_local))
    small_sums = jnp.concatenate([gain1_local, bias1_local, gain2_local, bias2_local, dwa_local])
    for axis in ("seq", "batch"):
        size = lax.axis_size(axis)
        hop = 1
        while hop < size:
            partner = [(i, i ^ hop) for i in range(size)]
            small_sums = small_sums + lax.ppermute(small_sums, axis, partner)
            hop *= 2
    gain1_grad, bias1_grad, gain2_grad, bias2_grad = (
        small_sums[k * D : (k + 1) * D] for k in range(4)
    )
    dwa_grad = small_sums[4 * D :]
    row_lse = jnp.take(lse_all, held_pairs, axis=0).reshape(1, per_dev, SLOT)
    return (
        block_output,
        input_grad,
        history_grad,
        row_lse,
        qkv_grad,
        proj_grad,
        up_grad,
        down_grad,
        gain1_grad,
        bias1_grad,
        gain2_grad,
        bias2_grad,
        dwa_grad,
    )


def solution(mesh):
    placed = (
        P(("batch", "seq"), None),
        P(None, ("batch", "seq"), None),
        P(("batch", "seq"), None),
        P("batch", "seq"),
        P("batch", "seq"),
        P("batch", "seq"),
        P("batch", "seq"),
        P(),
        P(),
        P(),
        P(),
        P(),
        P("batch", None),
        P("batch", None),
    )

    return jax.shard_map(
        local,
        mesh=mesh,
        in_specs=placed,
        out_specs=(
            P(("batch", "seq"), None),
            P(("batch", "seq"), None),
            P(None, ("batch", "seq"), None),
            P("batch", "seq", None),
            P("batch", "seq"),
            P("batch", "seq"),
            P("batch", "seq"),
            P("batch", "seq"),
            P(),
            P(),
            P(),
            P(),
            P(),
        ),
        check_vma=False,
    )
```

```python
import jax
import jax.numpy as jnp
from jax import lax
from jax.sharding import PartitionSpec as P
from jax.experimental import pallas as pl
from jax.experimental.pallas import tpu as pltpu
import functools

D = 768
HEADS = 12
HD = 64
SLOT = 2048
HIST = 8


NORM_EPS = 1e-05
MASKED = -1e30
NT_DIMS = (((1,), (1,)), ((), ()))


def fwd_kernel(seg_ref, q_ref, k_ref, v_ref, o_ref, lse_ref, *, bq, bk, scale):
    pair = pl.program_id(0)
    qi = pl.program_id(1)
    seg_len = seg_ref[pair]
    q_start = qi * bq
    seg_start = (q_start // seg_len) * seg_len
    query = (q_ref[0, 0].astype(jnp.float32).T * scale).astype(jnp.bfloat16)

    def step(j, carry, masked):
        m_old, l_old, acc = carry
        k_off = pl.multiple_of(j * bk, bk)
        key_t = k_ref[0, 0, :, pl.ds(k_off, bk)]
        value_t = v_ref[0, 0, :, pl.ds(k_off, bk)]
        s = jnp.dot(query, key_t, preferred_element_type=jnp.float32)
        if masked:
            rows = q_start + lax.broadcasted_iota(jnp.int32, (bq, bk), 0)
            cols = k_off + lax.broadcasted_iota(jnp.int32, (bq, bk), 1)
            s = jnp.where(cols <= rows, s, MASKED)
        m_new = jnp.maximum(m_old, jnp.max(s, axis=-1, keepdims=True))
        alpha = jnp.exp(m_old - m_new)
        weights = jnp.exp(s - m_new)
        l_new = alpha * l_old + jnp.sum(weights, axis=-1, keepdims=True)
        acc = alpha * acc + lax.dot_general(
            weights.astype(jnp.bfloat16), value_t, NT_DIMS, preferred_element_type=jnp.float32
        )
        return m_new, l_new, acc

    carry = (
        jnp.full((bq, 1), MASKED, jnp.float32),
        jnp.zeros((bq, 1), jnp.float32),
        jnp.zeros((bq, HD), jnp.float32),
    )
    j_diag = q_start // bk
    carry = lax.fori_loop(seg_start // bk, j_diag, lambda j, c: step(j, c, False), carry)
    for r in range(bq // bk):
        carry = step(j_diag + r, carry, True)
    m_fin, l_fin, acc = carry
    o_ref[0] = (acc / l_fin).T.astype(o_ref.dtype)
    lse = m_fin + jnp.log(l_fin)
    lse_ref[0] = jnp.transpose(jnp.broadcast_to(lse, (bq, 128)))[0:1, :]


def attn_forward(qkv_t, seg_pairs, bq=512, bk=512):
    pairs, _, head_size, seq_len = qkv_t.shape
    scale = head_size ** (-0.5)
    n_q = seq_len // bq
    blocks_done = pairs * (seq_len // bk) * (seq_len // bk + 1) // 2
    cost = pl.CostEstimate(
        flops=4 * blocks_done * bk * bk * head_size,
        transcendentals=blocks_done * bk * bk,
        bytes_accessed=pairs * seq_len * head_size * 2 * 4 + pairs * seq_len * 4,
    )
    grid_spec = pltpu.PrefetchScalarGridSpec(
        num_scalar_prefetch=1,
        grid=(pairs, n_q),
        in_specs=[
            pl.BlockSpec((1, 1, head_size, bq), lambda p, i, seg: (p, 0, 0, i)),
            pl.BlockSpec((1, 1, head_size, seq_len), lambda p, i, seg: (p, 1, 0, 0)),
            pl.BlockSpec((1, 1, head_size, seq_len), lambda p, i, seg: (p, 2, 0, 0)),
        ],
        out_specs=[
            pl.BlockSpec((1, head_size, bq), lambda p, i, seg: (p, 0, i)),
            pl.BlockSpec((1, 1, bq), lambda p, i, seg: (p, 0, i)),
        ],
    )
    return pl.pallas_call(
        functools.partial(fwd_kernel, bq=bq, bk=bk, scale=scale),
        grid_spec=grid_spec,
        out_shape=[
            jax.ShapeDtypeStruct((pairs, head_size, seq_len), jnp.bfloat16),
            jax.ShapeDtypeStruct((pairs, 1, seq_len), jnp.float32),
        ],
        cost_estimate=cost,
        name="attn_fwd",
    )(seg_pairs, qkv_t, qkv_t, qkv_t)


def bwd_kernel(seg_ref, q_ref, k_ref, v_ref, do_ref, o_ref, lse_ref, out_ref, dq_acc, *, bk, bq, scale):
    pair = pl.program_id(0)
    kj = pl.program_id(1)

    @pl.when(kj == 0)
    def _():
        dq_acc[...] = jnp.zeros_like(dq_acc)

    seg_len = seg_ref[pair]
    k_start = kj * bk
    seg_end = (k_start // seg_len + 1) * seg_len
    key_t = k_ref[0, 0]
    key = key_t.astype(jnp.float32).T.astype(jnp.bfloat16)
    value_s = (v_ref[0, 0].astype(jnp.float32).T * scale).astype(jnp.bfloat16)

    def step(i, carry, masked):
        dk_t, dv_t = carry
        q_off = pl.multiple_of(i * bq, bq)
        query_t = q_ref[0, 0, :, pl.ds(q_off, bq)]
        query_ts = (query_t.astype(jnp.float32) * scale).astype(jnp.bfloat16)
        dout_t = do_ref[0, :, pl.ds(q_off, bq)]
        out_t = o_ref[0, :, pl.ds(q_off, bq)]
        lse = lse_ref[0, :, pl.ds(q_off, bq)]
        delta = jnp.sum(
            dout_t.astype(jnp.float32) * out_t.astype(jnp.float32), axis=0, keepdims=True
        ) * scale
        s_t = jnp.dot(key, query_ts, preferred_element_type=jnp.float32)
        if masked:
            keys_at = k_start + lax.broadcasted_iota(jnp.int32, (bk, bq), 0)
            queries_at = q_off + lax.broadcasted_iota(jnp.int32, (bk, bq), 1)
            s_t = jnp.where(keys_at <= queries_at, s_t, MASKED)
        p_t = jnp.exp(s_t - lse)
        dv_t = dv_t + lax.dot_general(
            dout_t, p_t.astype(jnp.bfloat16), NT_DIMS, preferred_element_type=jnp.float32
        )
        dp_t = jnp.dot(value_s, dout_t, preferred_element_type=jnp.float32)
        ds_t = (p_t * (dp_t - delta)).astype(jnp.bfloat16)
        dk_t = dk_t + lax.dot_general(query_t, ds_t, NT_DIMS, preferred_element_type=jnp.float32)
        dq_acc[:, pl.ds(q_off, bq)] += jnp.dot(key_t, ds_t, preferred_element_type=jnp.float32)
        return dk_t, dv_t

    carry = (jnp.zeros((HD, bk), jnp.float32), jnp.zeros((HD, bk), jnp.float32))
    for r in range(bk // bq):
        carry = step(k_start // bq + r, carry, True)
    dk_t, dv_t = lax.fori_loop(
        (k_start + bk) // bq, seg_end // bq, lambda i, c: step(i, c, False), carry
    )
    out_ref[0, 0] = dq_acc[:, pl.ds(pl.multiple_of(k_start, bk), bk)].astype(out_ref.dtype)
    out_ref[0, 1] = dk_t.astype(out_ref.dtype)
    out_ref[0, 2] = dv_t.astype(out_ref.dtype)


def attn_backward(qkv_t, dout_t, out_t, lse, seg_pairs, bk=512, bq=512):
    pairs, _, head_size, seq_len = qkv_t.shape
    scale = head_size ** (-0.5)
    n_k = seq_len // bk
    blocks_done = pairs * (seq_len // bq) * (seq_len // bq + 1) // 2
    cost = pl.CostEstimate(
        flops=10 * blocks_done * bq * bq * head_size,
        transcendentals=blocks_done * bq * bq,
        bytes_accessed=pairs * seq_len * head_size * 2 * 8 + pairs * seq_len * 4,
    )
    grid_spec = pltpu.PrefetchScalarGridSpec(
        num_scalar_prefetch=1,
        grid=(pairs, n_k),
        in_specs=[
            pl.BlockSpec((1, 1, head_size, seq_len), lambda p, j, seg: (p, 0, 0, 0)),
            pl.BlockSpec((1, 1, head_size, bk), lambda p, j, seg: (p, 1, 0, j)),
            pl.BlockSpec((1, 1, head_size, bk), lambda p, j, seg: (p, 2, 0, j)),
            pl.BlockSpec((1, head_size, seq_len), lambda p, j, seg: (p, 0, 0)),
            pl.BlockSpec((1, head_size, seq_len), lambda p, j, seg: (p, 0, 0)),
            pl.BlockSpec((1, 1, seq_len), lambda p, j, seg: (p, 0, 0)),
        ],
        out_specs=pl.BlockSpec((1, 3, head_size, bk), lambda p, j, seg: (p, 0, 0, j)),
        scratch_shapes=[pltpu.VMEM((head_size, seq_len), jnp.float32)],
    )
    return pl.pallas_call(
        functools.partial(bwd_kernel, bk=bk, bq=bq, scale=scale),
        grid_spec=grid_spec,
        out_shape=jax.ShapeDtypeStruct((pairs, 3, head_size, seq_len), jnp.bfloat16),
        cost_estimate=cost,
        name="attn_bwd",
    )(seg_pairs, qkv_t, qkv_t, qkv_t, dout_t, out_t, lse)


def norm_rows(values, gain, shift):
    row_mean = jnp.mean(values, axis=-1, keepdims=True)
    centred = values - row_mean
    variance = jnp.mean(centred * centred, axis=-1, keepdims=True)
    inv_std = lax.rsqrt(variance + NORM_EPS)
    normed = centred * inv_std
    return (normed * gain + shift, normed, inv_std)


def norm_back(grad_in, normed, inv_std, gain):
    scaled = grad_in * gain
    centred = (
        scaled
        - jnp.mean(scaled, axis=-1, keepdims=True)
        - normed * jnp.mean(scaled * normed, axis=-1, keepdims=True)
    )
    return (centred * inv_std, jnp.sum(grad_in * normed, axis=0), jnp.sum(grad_in, axis=0))


def rotate(values, cosine, sine_tab):
    half_size = values.shape[-1] // 2
    front = values[..., :half_size]
    behind = values[..., half_size:]
    cos_part = cosine[..., None, :]
    sin_part = sine_tab[..., None, :]
    return jnp.concatenate(
        [front * cos_part - behind * sin_part, behind * cos_part + front * sin_part], axis=-1
    )


def unrotate(values, cosine, sine_tab):
    half_size = values.shape[-1] // 2
    front = values[..., :half_size]
    behind = values[..., half_size:]
    cos_part = cosine[..., None, :]
    sin_part = sine_tab[..., None, :]
    return jnp.concatenate(
        [front * cos_part + behind * sin_part, behind * cos_part - front * sin_part], axis=-1
    )


def local(
    block_input,
    history,
    cotangent,
    qkv_weight,
    proj_weight,
    up_weight,
    down_weight,
    norm1_gain,
    norm1_bias,
    norm2_gain,
    norm2_bias,
    dwa_weights,
    pair_order,
    long_group,
):
    n_seq = lax.axis_size("seq")
    row_count = block_input.shape[0]
    piece_len = SLOT // n_seq
    slot_count = row_count // piece_len
    pair_count = slot_count * HEADS
    per_dev = pair_count // n_seq
    slot_flags = long_group[0]
    seg_len = SLOT // jnp.left_shift(jnp.ones_like(slot_flags), slot_flags)
    position = jnp.arange(SLOT, dtype=jnp.int32)
    doc_place = (position[None, :] % seg_len[:, None]).astype(jnp.float32)
    frequency = jnp.power(10000.0, jnp.arange(HD // 2, dtype=jnp.float32) * (-2.0 / HD))
    angles = doc_place[..., None] * frequency
    my_index = lax.axis_index("seq")
    my_start = my_index * piece_len
    cosine = lax.dynamic_slice_in_dim(jnp.cos(angles), my_start, piece_len, 1)
    sine_tab = lax.dynamic_slice_in_dim(jnp.sin(angles), my_start, piece_len, 1)
    head_groups = HEADS // per_dev
    order_row = pair_order[0]
    held_pairs = lax.dynamic_slice_in_dim(order_row, my_index * per_dev, per_dev, 0)
    my_pairs = my_index * per_dev + jnp.arange(per_dev, dtype=jnp.int32)
    seg_pairs = jnp.take(seg_len, my_pairs // HEADS).astype(jnp.int32)
    n_batch = lax.axis_size("batch")
    batch_index = lax.axis_index("batch")

    def gather_rows(local):
        acc = local
        bits = n_batch.bit_length() - 1
        for bit in reversed(range(bits)):
            partner = [(i, i ^ (1 << bit)) for i in range(n_batch)]
            got = lax.ppermute(acc, "batch", partner)
            low = ((batch_index >> bit) & 1) == 0
            acc = jnp.where(low, jnp.stack([acc, got]), jnp.stack([got, acc]))
        return jnp.transpose(acc, list(range(bits))[::-1] + list(range(bits, acc.ndim))).reshape(
            (n_batch,) + local.shape
        )

    qkv_rows = gather_rows(qkv_weight).reshape(-1, qkv_weight.shape[1])
    w_qkv = lax.all_gather(qkv_rows, "seq", axis=1, tiled=True)
    inputs32 = block_input.astype(jnp.float32)
    norm1_out, normed1, inv_std1 = norm_rows(inputs32, norm1_gain, norm1_bias)
    norm1_low = norm1_out.astype(jnp.bfloat16)
    qkv_out = jnp.dot(norm1_low, w_qkv, preferred_element_type=jnp.float32)
    queries = rotate(qkv_out[:, :D].reshape(slot_count, piece_len, HEADS, HD), cosine, sine_tab)
    keys_rot = rotate(
        qkv_out[:, D : 2 * D].reshape(slot_count, piece_len, HEADS, HD), cosine, sine_tab
    )
    values_in = qkv_out[:, 2 * D :].reshape(slot_count, piece_len, HEADS, HD)
    stacked = jnp.stack([queries, keys_rot, values_in], axis=2).astype(jnp.bfloat16)
    send = jnp.transpose(
        stacked.reshape(slot_count, piece_len, 3, head_groups, per_dev, HD), (0, 3, 4, 2, 5, 1)
    ).reshape(n_seq, per_dev, 3, HD, piece_len)
    incoming = lax.all_to_all(send, "seq", split_axis=0, concat_axis=0, tiled=True)
    later = (proj_weight, up_weight, down_weight)
    later_flat, _ = lax.optimization_barrier(
        (jnp.concatenate([w.reshape(-1) for w in later]), qkv_rows)
    )
    later_rows = gather_rows(later_flat)
    offset = 0
    later_full = []
    for w in later:
        rows = later_rows[:, offset : offset + w.size].reshape(-1, w.shape[1])
        later_full.append(lax.all_gather(rows, "seq", axis=1, tiled=True))
        offset += w.size
    w_proj, w_up, w_down = later_full
    qkv_t = jnp.transpose(incoming, (1, 2, 3, 0, 4)).reshape(per_dev, 3, HD, SLOT)
    attn_t, lse_rows = attn_forward(qkv_t, seg_pairs)
    back = jnp.transpose(attn_t.reshape(per_dev, HD, n_seq, piece_len), (2, 0, 1, 3))
    returned = lax.all_to_all(back, "seq", split_axis=0, concat_axis=0, tiled=True)
    lse_all = lax.all_gather(lse_rows.reshape(per_dev, SLOT), "seq", axis=0, tiled=True)
    lse_all, returned = lax.optimization_barrier((lse_all, returned))
    attended = jnp.transpose(
        returned.reshape(slot_count, head_groups, per_dev, HD, piece_len), (0, 4, 1, 2, 3)
    ).reshape(row_count, D)
    middle = inputs32 + jnp.dot(attended, w_proj, preferred_element_type=jnp.float32)
    norm2_out, normed2, inv_std2 = norm_rows(middle, norm2_gain, norm2_bias)
    norm2_low = norm2_out.astype(jnp.bfloat16)
    hidden_up = jnp.dot(norm2_low, w_up, preferred_element_type=jnp.float32)
    gelu_out, gelu_pull = jax.vjp(lambda hidden: jax.nn.gelu(hidden, approximate=True), hidden_up)
    gelu_low = gelu_out.astype(jnp.bfloat16)
    block_out = middle + jnp.dot(gelu_low, w_down, preferred_element_type=jnp.float32)
    dwa_out = dwa_weights[HIST] * block_out
    for layer_idx in range(HIST):
        dwa_out = dwa_out + dwa_weights[layer_idx] * history[layer_idx].astype(jnp.float32)
    block_output = dwa_out.astype(jnp.bfloat16)
    grad_out = cotangent.astype(jnp.float32)
    history_grad = (dwa_weights[:HIST, None, None] * grad_out[None]).astype(jnp.bfloat16)
    dwa_terms = [
        jnp.sum(history[layer_idx].astype(jnp.float32) * grad_out) for layer_idx in range(HIST)
    ]
    dwa_terms.append(jnp.sum(block_out * grad_out))
    dwa_local = jnp.stack(dwa_terms)
    dy_full = dwa_weights[HIST] * grad_out
    dmlp_low = dy_full.astype(jnp.bfloat16)
    down_local = jnp.einsum(
        "nf,nbd->bfd", gelu_low, dmlp_low.reshape(row_count, n_seq, -1),
        preferred_element_type=jnp.float32,
    )
    dgelu = jnp.einsum("nd,fd->nf", dmlp_low, w_down, preferred_element_type=jnp.float32)
    dup_low = gelu_pull(dgelu)[0].astype(jnp.bfloat16)
    up_local = jnp.einsum(
        "nd,nbf->bdf", norm2_low, dup_low.reshape(row_count, n_seq, -1),
        preferred_element_type=jnp.float32,
    )
    dnorm2 = jnp.einsum("nf,df->nd", dup_low, w_up, preferred_element_type=jnp.float32)
    dmid_norm, gain2_local, bias2_local = norm_back(dnorm2, normed2, inv_std2, norm2_gain)
    dmiddle = dy_full + dmid_norm
    dmiddle_low = dmiddle.astype(jnp.bfloat16)
    proj_local = jnp.einsum(
        "nd,nbe->bde", attended, dmiddle_low.reshape(row_count, n_seq, -1),
        preferred_element_type=jnp.float32,
    )
    dattended = jnp.einsum(
        "ne,de->nd", dmiddle_low, w_proj, preferred_element_type=jnp.float32
    ).astype(jnp.bfloat16)
    dsend = jnp.transpose(
        dattended.reshape(slot_count, piece_len, head_groups, per_dev, HD), (0, 2, 3, 4, 1)
    ).reshape(n_seq, per_dev, HD, piece_len)
    dattn_in = lax.all_to_all(dsend, "seq", split_axis=0, concat_axis=0, tiled=True)
    dout_t = jnp.transpose(dattn_in, (1, 2, 0, 3)).reshape(per_dev, HD, SLOT)
    dpairs = attn_backward(qkv_t, dout_t, attn_t, lse_rows, seg_pairs)
    dback = jnp.transpose(
        dpairs.reshape(per_dev, 3, HD, n_seq, piece_len), (3, 0, 1, 2, 4)
    )
    dreturned = lax.all_to_all(dback, "seq", split_axis=0, concat_axis=0, tiled=True)
    dtokens = jnp.transpose(
        dreturned.reshape(slot_count, head_groups, per_dev, 3, HD, piece_len), (0, 5, 3, 1, 2, 4)
    ).reshape(slot_count, piece_len, 3, HEADS, HD)
    dq_rows = unrotate(dtokens[:, :, 0].astype(jnp.float32), cosine, sine_tab).reshape(row_count, D)
    dk_rows = unrotate(dtokens[:, :, 1].astype(jnp.float32), cosine, sine_tab).reshape(row_count, D)
    dv_rows = dtokens[:, :, 2].astype(jnp.float32).reshape(row_count, D)
    dqkv_low = jnp.concatenate([dq_rows, dk_rows, dv_rows], axis=-1).astype(jnp.bfloat16)
    qkv_local = jnp.einsum(
        "nd,nbf->bdf", norm1_low, dqkv_low.reshape(row_count, n_seq, -1),
        preferred_element_type=jnp.float32,
    )
    dnorm1 = jnp.einsum("nf,df->nd", dqkv_low, w_qkv, preferred_element_type=jnp.float32)
    dinput_norm, gain1_local, bias1_local = norm_back(dnorm1, normed1, inv_std1, norm1_gain)
    input_grad = (dmiddle + dinput_norm).astype(jnp.bfloat16)

    def by_cols(blocks):
        bits = n_seq.bit_length() - 1
        acc = blocks.reshape((2,) * bits + blocks.shape[1:])
        for bit in range(bits):
            mine = (my_index >> bit) & 1
            keep = lax.dynamic_index_in_dim(acc, mine, axis=bits - 1 - bit, keepdims=False)
            send = lax.dynamic_index_in_dim(acc, 1 - mine, axis=bits - 1 - bit, keepdims=False)
            partner = [(i, i ^ (1 << bit)) for i in range(n_seq)]
            got = lax.ppermute(send.astype(jnp.bfloat16), "seq", partner)
            acc = keep + got.astype(jnp.float32)
        return acc.astype(jnp.bfloat16)

    def by_rows(col_sum):
        return lax.psum_scatter(col_sum, "batch", scatter_dimension=0, tiled=True).astype(
            jnp.float32
        )

    qkv_grad = by_rows(by_cols(qkv_local))
    proj_grad = by_rows(by_cols(proj_local))
    up_grad = by_rows(by_cols(up_local))
    down_grad = by_rows(by_cols(down_local))
    small_sums = jnp.concatenate([gain1_local, bias1_local, gain2_local, bias2_local, dwa_local])
    for axis in ("seq", "batch"):
        size = lax.axis_size(axis)
        hop = 1
        while hop < size:
            partner = [(i, i ^ hop) for i in range(size)]
            small_sums = small_sums + lax.ppermute(small_sums, axis, partner)
            hop *= 2
    gain1_grad, bias1_grad, gain2_grad, bias2_grad = (
        small_sums[k * D : (k + 1) * D] for k in range(4)
    )
    dwa_grad = small_sums[4 * D :]
    row_lse = jnp.take(lse_all, held_pairs, axis=0).reshape(1, per_dev, SLOT)
    return (
        block_output,
        input_grad,
        history_grad,
        row_lse,
        qkv_grad,
        proj_grad,
        up_grad,
        down_grad,
        gain1_grad,
        bias1_grad,
        gain2_grad,
        bias2_grad,
        dwa_grad,
    )


def solution(mesh):
    placed = (
        P(("batch", "seq"), None),
        P(None, ("batch", "seq"), None),
        P(("batch", "seq"), None),
        P("batch", "seq"),
        P("batch", "seq"),
        P("batch", "seq"),
        P("batch", "seq"),
        P(),
        P(),
        P(),
        P(),
        P(),
        P("batch", None),
        P("batch", None),
    )

    return jax.shard_map(
        local,
        mesh=mesh,
        in_specs=placed,
        out_specs=(
            P(("batch", "seq"), None),
            P(("batch", "seq"), None),
            P(None, ("batch", "seq"), None),
            P("batch", "seq", None),
            P("batch", "seq"),
            P("batch", "seq"),
            P("batch", "seq"),
            P("batch", "seq"),
            P(),
            P(),
            P(),
            P(),
            P(),
        ),
        check_vma=False,
    )
```

```python
import jax
import jax.numpy as jnp
from jax import lax
from jax.sharding import PartitionSpec as P
from jax.experimental import pallas as pl
from jax.experimental.pallas import tpu as pltpu
import functools

D = 768
HEADS = 12
HD = 64
SLOT = 2048
HIST = 8


NORM_EPS = 1e-05
MASKED = -1e30
NT_DIMS = (((1,), (1,)), ((), ()))


def fwd_kernel(seg_ref, q_ref, k_ref, v_ref, o_ref, lse_ref, *, bq, bk, scale):
    pair = pl.program_id(0)
    qi = pl.program_id(1)
    seg_len = seg_ref[pair]
    q_start = qi * bq
    seg_start = (q_start // seg_len) * seg_len
    query = (q_ref[0, 0].astype(jnp.float32).T * scale).astype(jnp.bfloat16)

    def step(j, carry, masked):
        m_old, l_old, acc = carry
        k_off = pl.multiple_of(j * bk, bk)
        key_t = k_ref[0, 0, :, pl.ds(k_off, bk)]
        value_t = v_ref[0, 0, :, pl.ds(k_off, bk)]
        s = jnp.dot(query, key_t, preferred_element_type=jnp.float32)
        if masked:
            rows = q_start + lax.broadcasted_iota(jnp.int32, (bq, bk), 0)
            cols = k_off + lax.broadcasted_iota(jnp.int32, (bq, bk), 1)
            s = jnp.where(cols <= rows, s, MASKED)
        m_new = jnp.maximum(m_old, jnp.max(s, axis=-1, keepdims=True))
        alpha = jnp.exp(m_old - m_new)
        weights = jnp.exp(s - m_new)
        l_new = alpha * l_old + jnp.sum(weights, axis=-1, keepdims=True)
        acc = alpha * acc + lax.dot_general(
            weights.astype(jnp.bfloat16), value_t, NT_DIMS, preferred_element_type=jnp.float32
        )
        return m_new, l_new, acc

    carry = (
        jnp.full((bq, 1), MASKED, jnp.float32),
        jnp.zeros((bq, 1), jnp.float32),
        jnp.zeros((bq, HD), jnp.float32),
    )
    j_diag = q_start // bk
    carry = lax.fori_loop(seg_start // bk, j_diag, lambda j, c: step(j, c, False), carry)
    for r in range(bq // bk):
        carry = step(j_diag + r, carry, True)
    m_fin, l_fin, acc = carry
    o_ref[0] = (acc / l_fin).T.astype(o_ref.dtype)
    lse = m_fin + jnp.log(l_fin)
    lse_ref[0] = jnp.transpose(jnp.broadcast_to(lse, (bq, 128)))[0:1, :]


def attn_forward(qkv_t, seg_pairs, bq=512, bk=512):
    pairs, _, head_size, seq_len = qkv_t.shape
    scale = head_size ** (-0.5)
    n_q = seq_len // bq
    blocks_done = pairs * (seq_len // bk) * (seq_len // bk + 1) // 2
    cost = pl.CostEstimate(
        flops=4 * blocks_done * bk * bk * head_size,
        transcendentals=blocks_done * bk * bk,
        bytes_accessed=pairs * seq_len * head_size * 2 * 4 + pairs * seq_len * 4,
    )
    grid_spec = pltpu.PrefetchScalarGridSpec(
        num_scalar_prefetch=1,
        grid=(pairs, n_q),
        in_specs=[
            pl.BlockSpec((1, 1, head_size, bq), lambda p, i, seg: (p, 0, 0, i)),
            pl.BlockSpec((1, 1, head_size, seq_len), lambda p, i, seg: (p, 1, 0, 0)),
            pl.BlockSpec((1, 1, head_size, seq_len), lambda p, i, seg: (p, 2, 0, 0)),
        ],
        out_specs=[
            pl.BlockSpec((1, head_size, bq), lambda p, i, seg: (p, 0, i)),
            pl.BlockSpec((1, 1, bq), lambda p, i, seg: (p, 0, i)),
        ],
    )
    return pl.pallas_call(
        functools.partial(fwd_kernel, bq=bq, bk=bk, scale=scale),
        grid_spec=grid_spec,
        out_shape=[
            jax.ShapeDtypeStruct((pairs, head_size, seq_len), jnp.bfloat16),
            jax.ShapeDtypeStruct((pairs, 1, seq_len), jnp.float32),
        ],
        cost_estimate=cost,
        name="attn_fwd",
    )(seg_pairs, qkv_t, qkv_t, qkv_t)


def bwd_kernel(seg_ref, q_ref, k_ref, v_ref, do_ref, o_ref, lse_ref, out_ref, dq_acc, *, bk, bq, scale):
    pair = pl.program_id(0)
    kj = pl.program_id(1)

    @pl.when(kj == 0)
    def _():
        dq_acc[...] = jnp.zeros_like(dq_acc)

    seg_len = seg_ref[pair]
    k_start = kj * bk
    seg_end = (k_start // seg_len + 1) * seg_len
    key_t = k_ref[0, 0]
    key = key_t.astype(jnp.float32).T.astype(jnp.bfloat16)
    value_s = (v_ref[0, 0].astype(jnp.float32).T * scale).astype(jnp.bfloat16)

    def step(i, carry, masked):
        dk_t, dv_t = carry
        q_off = pl.multiple_of(i * bq, bq)
        query_t = q_ref[0, 0, :, pl.ds(q_off, bq)]
        query_ts = (query_t.astype(jnp.float32) * scale).astype(jnp.bfloat16)
        dout_t = do_ref[0, :, pl.ds(q_off, bq)]
        out_t = o_ref[0, :, pl.ds(q_off, bq)]
        lse = lse_ref[0, :, pl.ds(q_off, bq)]
        delta = jnp.sum(
            dout_t.astype(jnp.float32) * out_t.astype(jnp.float32), axis=0, keepdims=True
        ) * scale
        s_t = jnp.dot(key, query_ts, preferred_element_type=jnp.float32)
        if masked:
            keys_at = k_start + lax.broadcasted_iota(jnp.int32, (bk, bq), 0)
            queries_at = q_off + lax.broadcasted_iota(jnp.int32, (bk, bq), 1)
            s_t = jnp.where(keys_at <= queries_at, s_t, MASKED)
        p_t = jnp.exp(s_t - lse)
        dv_t = dv_t + lax.dot_general(
            dout_t, p_t.astype(jnp.bfloat16), NT_DIMS, preferred_element_type=jnp.float32
        )
        dp_t = jnp.dot(value_s, dout_t, preferred_element_type=jnp.float32)
        ds_t = (p_t * (dp_t - delta)).astype(jnp.bfloat16)
        dk_t = dk_t + lax.dot_general(query_t, ds_t, NT_DIMS, preferred_element_type=jnp.float32)
        dq_acc[:, pl.ds(q_off, bq)] += jnp.dot(key_t, ds_t, preferred_element_type=jnp.float32)
        return dk_t, dv_t

    carry = (jnp.zeros((HD, bk), jnp.float32), jnp.zeros((HD, bk), jnp.float32))
    for r in range(bk // bq):
        carry = step(k_start // bq + r, carry, True)
    dk_t, dv_t = lax.fori_loop(
        (k_start + bk) // bq, seg_end // bq, lambda i, c: step(i, c, False), carry
    )
    out_ref[0, 0] = dq_acc[:, pl.ds(pl.multiple_of(k_start, bk), bk)].astype(out_ref.dtype)
    out_ref[0, 1] = dk_t.astype(out_ref.dtype)
    out_ref[0, 2] = dv_t.astype(out_ref.dtype)


def attn_backward(qkv_t, dout_t, out_t, lse, seg_pairs, bk=512, bq=512):
    pairs, _, head_size, seq_len = qkv_t.shape
    scale = head_size ** (-0.5)
    n_k = seq_len // bk
    blocks_done = pairs * (seq_len // bq) * (seq_len // bq + 1) // 2
    cost = pl.CostEstimate(
        flops=10 * blocks_done * bq * bq * head_size,
        transcendentals=blocks_done * bq * bq,
        bytes_accessed=pairs * seq_len * head_size * 2 * 8 + pairs * seq_len * 4,
    )
    grid_spec = pltpu.PrefetchScalarGridSpec(
        num_scalar_prefetch=1,
        grid=(pairs, n_k),
        in_specs=[
            pl.BlockSpec((1, 1, head_size, seq_len), lambda p, j, seg: (p, 0, 0, 0)),
            pl.BlockSpec((1, 1, head_size, bk), lambda p, j, seg: (p, 1, 0, j)),
            pl.BlockSpec((1, 1, head_size, bk), lambda p, j, seg: (p, 2, 0, j)),
            pl.BlockSpec((1, head_size, seq_len), lambda p, j, seg: (p, 0, 0)),
            pl.BlockSpec((1, head_size, seq_len), lambda p, j, seg: (p, 0, 0)),
            pl.BlockSpec((1, 1, seq_len), lambda p, j, seg: (p, 0, 0)),
        ],
        out_specs=pl.BlockSpec((1, 3, head_size, bk), lambda p, j, seg: (p, 0, 0, j)),
        scratch_shapes=[pltpu.VMEM((head_size, seq_len), jnp.float32)],
    )
    return pl.pallas_call(
        functools.partial(bwd_kernel, bk=bk, bq=bq, scale=scale),
        grid_spec=grid_spec,
        out_shape=jax.ShapeDtypeStruct((pairs, 3, head_size, seq_len), jnp.bfloat16),
        cost_estimate=cost,
        name="attn_bwd",
    )(seg_pairs, qkv_t, qkv_t, qkv_t, dout_t, out_t, lse)


def norm_rows(values, gain, shift):
    row_mean = jnp.mean(values, axis=-1, keepdims=True)
    centred = values - row_mean
    variance = jnp.mean(centred * centred, axis=-1, keepdims=True)
    inv_std = lax.rsqrt(variance + NORM_EPS)
    normed = centred * inv_std
    return (normed * gain + shift, normed, inv_std)


def norm_back(grad_in, normed, inv_std, gain):
    scaled = grad_in * gain
    centred = (
        scaled
        - jnp.mean(scaled, axis=-1, keepdims=True)
        - normed * jnp.mean(scaled * normed, axis=-1, keepdims=True)
    )
    return (centred * inv_std, jnp.sum(grad_in * normed, axis=0), jnp.sum(grad_in, axis=0))


def rotate(values, cosine, sine_tab):
    half_size = values.shape[-1] // 2
    front = values[..., :half_size]
    behind = values[..., half_size:]
    cos_part = cosine[..., None, :]
    sin_part = sine_tab[..., None, :]
    return jnp.concatenate(
        [front * cos_part - behind * sin_part, behind * cos_part + front * sin_part], axis=-1
    )


def unrotate(values, cosine, sine_tab):
    half_size = values.shape[-1] // 2
    front = values[..., :half_size]
    behind = values[..., half_size:]
    cos_part = cosine[..., None, :]
    sin_part = sine_tab[..., None, :]
    return jnp.concatenate(
        [front * cos_part + behind * sin_part, behind * cos_part - front * sin_part], axis=-1
    )


def local(
    block_input,
    history,
    cotangent,
    qkv_weight,
    proj_weight,
    up_weight,
    down_weight,
    norm1_gain,
    norm1_bias,
    norm2_gain,
    norm2_bias,
    dwa_weights,
    pair_order,
    long_group,
):
    n_seq = lax.axis_size("seq")
    row_count = block_input.shape[0]
    piece_len = SLOT // n_seq
    slot_count = row_count // piece_len
    pair_count = slot_count * HEADS
    per_dev = pair_count // n_seq
    slot_flags = long_group[0]
    seg_len = SLOT // jnp.left_shift(jnp.ones_like(slot_flags), slot_flags)
    position = jnp.arange(SLOT, dtype=jnp.int32)
    doc_place = (position[None, :] % seg_len[:, None]).astype(jnp.float32)
    frequency = jnp.power(10000.0, jnp.arange(HD // 2, dtype=jnp.float32) * (-2.0 / HD))
    angles = doc_place[..., None] * frequency
    my_index = lax.axis_index("seq")
    my_start = my_index * piece_len
    cosine = lax.dynamic_slice_in_dim(jnp.cos(angles), my_start, piece_len, 1)
    sine_tab = lax.dynamic_slice_in_dim(jnp.sin(angles), my_start, piece_len, 1)
    head_groups = HEADS // per_dev
    order_row = pair_order[0]
    held_pairs = lax.dynamic_slice_in_dim(order_row, my_index * per_dev, per_dev, 0)
    my_pairs = my_index * per_dev + jnp.arange(per_dev, dtype=jnp.int32)
    seg_pairs = jnp.take(seg_len, my_pairs // HEADS).astype(jnp.int32)
    n_batch = lax.axis_size("batch")
    batch_index = lax.axis_index("batch")

    def gather_rows(local):
        acc = local
        bits = n_batch.bit_length() - 1
        for bit in reversed(range(bits)):
            partner = [(i, i ^ (1 << bit)) for i in range(n_batch)]
            got = lax.ppermute(acc, "batch", partner)
            low = ((batch_index >> bit) & 1) == 0
            acc = jnp.where(low, jnp.stack([acc, got]), jnp.stack([got, acc]))
        return jnp.transpose(acc, list(range(bits))[::-1] + list(range(bits, acc.ndim))).reshape(
            (n_batch,) + local.shape
        )

    qkv_rows = gather_rows(qkv_weight).reshape(-1, qkv_weight.shape[1])
    w_qkv = lax.all_gather(qkv_rows, "seq", axis=1, tiled=True)
    inputs32 = block_input.astype(jnp.float32)
    norm1_out, normed1, inv_std1 = norm_rows(inputs32, norm1_gain, norm1_bias)
    norm1_low = norm1_out.astype(jnp.bfloat16)
    qkv_out = jnp.dot(norm1_low, w_qkv, preferred_element_type=jnp.float32)
    queries = rotate(qkv_out[:, :D].reshape(slot_count, piece_len, HEADS, HD), cosine, sine_tab)
    keys_rot = rotate(
        qkv_out[:, D : 2 * D].reshape(slot_count, piece_len, HEADS, HD), cosine, sine_tab
    )
    values_in = qkv_out[:, 2 * D :].reshape(slot_count, piece_len, HEADS, HD)
    stacked = jnp.stack([queries, keys_rot, values_in], axis=2).astype(jnp.bfloat16)
    send = jnp.transpose(
        stacked.reshape(slot_count, piece_len, 3, head_groups, per_dev, HD), (0, 3, 4, 2, 5, 1)
    ).reshape(n_seq, per_dev, 3, HD, piece_len)
    incoming = lax.all_to_all(send, "seq", split_axis=0, concat_axis=0, tiled=True)
    later = (proj_weight, up_weight, down_weight)
    later_rows = gather_rows(jnp.concatenate([w.reshape(-1) for w in later]))
    offset = 0
    later_full = []
    for w in later:
        rows = later_rows[:, offset : offset + w.size].reshape(-1, w.shape[1])
        later_full.append(lax.all_gather(rows, "seq", axis=1, tiled=True))
        offset += w.size
    w_proj, w_up, w_down = later_full
    qkv_t = jnp.transpose(incoming, (1, 2, 3, 0, 4)).reshape(per_dev, 3, HD, SLOT)
    attn_t, lse_rows = attn_forward(qkv_t, seg_pairs)
    back = jnp.transpose(attn_t.reshape(per_dev, HD, n_seq, piece_len), (2, 0, 1, 3))
    returned = lax.all_to_all(back, "seq", split_axis=0, concat_axis=0, tiled=True)
    lse_all = lax.all_gather(lse_rows.reshape(per_dev, SLOT), "seq", axis=0, tiled=True)
    lse_all, returned = lax.optimization_barrier((lse_all, returned))
    attended = jnp.transpose(
        returned.reshape(slot_count, head_groups, per_dev, HD, piece_len), (0, 4, 1, 2, 3)
    ).reshape(row_count, D)
    middle = inputs32 + jnp.dot(attended, w_proj, preferred_element_type=jnp.float32)
    norm2_out, normed2, inv_std2 = norm_rows(middle, norm2_gain, norm2_bias)
    norm2_low = norm2_out.astype(jnp.bfloat16)
    hidden_up = jnp.dot(norm2_low, w_up, preferred_element_type=jnp.float32)
    gelu_out, gelu_pull = jax.vjp(lambda hidden: jax.nn.gelu(hidden, approximate=True), hidden_up)
    gelu_low = gelu_out.astype(jnp.bfloat16)
    block_out = middle + jnp.dot(gelu_low, w_down, preferred_element_type=jnp.float32)
    dwa_out = dwa_weights[HIST] * block_out
    for layer_idx in range(HIST):
        dwa_out = dwa_out + dwa_weights[layer_idx] * history[layer_idx].astype(jnp.float32)
    block_output = dwa_out.astype(jnp.bfloat16)
    grad_out = cotangent.astype(jnp.float32)
    history_grad = (dwa_weights[:HIST, None, None] * grad_out[None]).astype(jnp.bfloat16)
    dwa_terms = [
        jnp.sum(history[layer_idx].astype(jnp.float32) * grad_out) for layer_idx in range(HIST)
    ]
    dwa_terms.append(jnp.sum(block_out * grad_out))
    dwa_local = jnp.stack(dwa_terms)
    dy_full = dwa_weights[HIST] * grad_out
    dmlp_low = dy_full.astype(jnp.bfloat16)
    down_local = jnp.einsum(
        "nf,nbd->bfd", gelu_low, dmlp_low.reshape(row_count, n_seq, -1),
        preferred_element_type=jnp.float32,
    )
    dgelu = jnp.einsum("nd,fd->nf", dmlp_low, w_down, preferred_element_type=jnp.float32)
    dup_low = gelu_pull(dgelu)[0].astype(jnp.bfloat16)
    up_local = jnp.einsum(
        "nd,nbf->bdf", norm2_low, dup_low.reshape(row_count, n_seq, -1),
        preferred_element_type=jnp.float32,
    )
    dnorm2 = jnp.einsum("nf,df->nd", dup_low, w_up, preferred_element_type=jnp.float32)
    dmid_norm, gain2_local, bias2_local = norm_back(dnorm2, normed2, inv_std2, norm2_gain)
    dmiddle = dy_full + dmid_norm
    dmiddle_low = dmiddle.astype(jnp.bfloat16)
    proj_local = jnp.einsum(
        "nd,nbe->bde", attended, dmiddle_low.reshape(row_count, n_seq, -1),
        preferred_element_type=jnp.float32,
    )
    dattended = jnp.einsum(
        "ne,de->nd", dmiddle_low, w_proj, preferred_element_type=jnp.float32
    ).astype(jnp.bfloat16)
    dsend = jnp.transpose(
        dattended.reshape(slot_count, piece_len, head_groups, per_dev, HD), (0, 2, 3, 4, 1)
    ).reshape(n_seq, per_dev, HD, piece_len)
    dattn_in = lax.all_to_all(dsend, "seq", split_axis=0, concat_axis=0, tiled=True)
    dout_t = jnp.transpose(dattn_in, (1, 2, 0, 3)).reshape(per_dev, HD, SLOT)
    dpairs = attn_backward(qkv_t, dout_t, attn_t, lse_rows, seg_pairs)
    dback = jnp.transpose(
        dpairs.reshape(per_dev, 3, HD, n_seq, piece_len), (3, 0, 1, 2, 4)
    )
    dreturned = lax.all_to_all(dback, "seq", split_axis=0, concat_axis=0, tiled=True)
    dtokens = jnp.transpose(
        dreturned.reshape(slot_count, head_groups, per_dev, 3, HD, piece_len), (0, 5, 3, 1, 2, 4)
    ).reshape(slot_count, piece_len, 3, HEADS, HD)
    dq_rows = unrotate(dtokens[:, :, 0].astype(jnp.float32), cosine, sine_tab).reshape(row_count, D)
    dk_rows = unrotate(dtokens[:, :, 1].astype(jnp.float32), cosine, sine_tab).reshape(row_count, D)
    dv_rows = dtokens[:, :, 2].astype(jnp.float32).reshape(row_count, D)
    dqkv_low = jnp.concatenate([dq_rows, dk_rows, dv_rows], axis=-1).astype(jnp.bfloat16)
    qkv_local = jnp.einsum(
        "nd,nbf->bdf", norm1_low, dqkv_low.reshape(row_count, n_seq, -1),
        preferred_element_type=jnp.float32,
    )
    dnorm1 = jnp.einsum("nf,df->nd", dqkv_low, w_qkv, preferred_element_type=jnp.float32)
    dinput_norm, gain1_local, bias1_local = norm_back(dnorm1, normed1, inv_std1, norm1_gain)
    input_grad = (dmiddle + dinput_norm).astype(jnp.bfloat16)

    def by_cols(blocks):
        bits = n_seq.bit_length() - 1
        acc = blocks.reshape((2,) * bits + blocks.shape[1:])
        for bit in range(bits):
            mine = (my_index >> bit) & 1
            keep = lax.dynamic_index_in_dim(acc, mine, axis=bits - 1 - bit, keepdims=False)
            send = lax.dynamic_index_in_dim(acc, 1 - mine, axis=bits - 1 - bit, keepdims=False)
            partner = [(i, i ^ (1 << bit)) for i in range(n_seq)]
            got = lax.ppermute(send.astype(jnp.bfloat16), "seq", partner)
            acc = keep + got.astype(jnp.float32)
        return acc.astype(jnp.bfloat16)

    def by_rows(col_sum):
        return lax.psum_scatter(col_sum, "batch", scatter_dimension=0, tiled=True).astype(
            jnp.float32
        )

    qkv_grad = by_rows(by_cols(qkv_local))
    proj_grad = by_rows(by_cols(proj_local))
    up_grad = by_rows(by_cols(up_local))
    down_grad = by_rows(by_cols(down_local))
    small_sums = jnp.concatenate([gain1_local, bias1_local, gain2_local, bias2_local, dwa_local])
    for axis in ("seq", "batch"):
        size = lax.axis_size(axis)
        hop = 1
        while hop < size:
            partner = [(i, i ^ hop) for i in range(size)]
            small_sums = small_sums + lax.ppermute(small_sums, axis, partner)
            hop *= 2
    gain1_grad, bias1_grad, gain2_grad, bias2_grad = (
        small_sums[k * D : (k + 1) * D] for k in range(4)
    )
    dwa_grad = small_sums[4 * D :]
    row_lse = jnp.take(lse_all, held_pairs, axis=0).reshape(1, per_dev, SLOT)
    return (
        block_output,
        input_grad,
        history_grad,
        row_lse,
        qkv_grad,
        proj_grad,
        up_grad,
        down_grad,
        gain1_grad,
        bias1_grad,
        gain2_grad,
        bias2_grad,
        dwa_grad,
    )


def solution(mesh):
    placed = (
        P(("batch", "seq"), None),
        P(None, ("batch", "seq"), None),
        P(("batch", "seq"), None),
        P("batch", "seq"),
        P("batch", "seq"),
        P("batch", "seq"),
        P("batch", "seq"),
        P(),
        P(),
        P(),
        P(),
        P(),
        P("batch", None),
        P("batch", None),
    )

    return jax.shard_map(
        local,
        mesh=mesh,
        in_specs=placed,
        out_specs=(
            P(("batch", "seq"), None),
            P(("batch", "seq"), None),
            P(None, ("batch", "seq"), None),
            P("batch", "seq", None),
            P("batch", "seq"),
            P("batch", "seq"),
            P("batch", "seq"),
            P("batch", "seq"),
            P(),
            P(),
            P(),
            P(),
            P(),
        ),
        check_vma=False,
    )
```

```python
import jax
import jax.numpy as jnp
from jax import lax
from jax.sharding import PartitionSpec as P
from jax.experimental import pallas as pl
from jax.experimental.pallas import tpu as pltpu
import functools

D = 768
HEADS = 12
HD = 64
SLOT = 2048
HIST = 8


NORM_EPS = 1e-05
MASKED = -1e30
NT_DIMS = (((1,), (1,)), ((), ()))


def fwd_kernel(seg_ref, q_ref, k_ref, v_ref, o_ref, lse_ref, *, bq, bk, scale):
    pair = pl.program_id(0)
    qi = pl.program_id(1)
    seg_len = seg_ref[pair]
    q_start = qi * bq
    seg_start = (q_start // seg_len) * seg_len
    query = (q_ref[0, 0].astype(jnp.float32).T * scale).astype(jnp.bfloat16)

    def step(j, carry, masked):
        m_old, l_old, acc = carry
        k_off = pl.multiple_of(j * bk, bk)
        key_t = k_ref[0, 0, :, pl.ds(k_off, bk)]
        value_t = v_ref[0, 0, :, pl.ds(k_off, bk)]
        s = jnp.dot(query, key_t, preferred_element_type=jnp.float32)
        if masked:
            rows = q_start + lax.broadcasted_iota(jnp.int32, (bq, bk), 0)
            cols = k_off + lax.broadcasted_iota(jnp.int32, (bq, bk), 1)
            s = jnp.where(cols <= rows, s, MASKED)
        m_new = jnp.maximum(m_old, jnp.max(s, axis=-1, keepdims=True))
        alpha = jnp.exp(m_old - m_new)
        weights = jnp.exp(s - m_new)
        l_new = alpha * l_old + jnp.sum(weights, axis=-1, keepdims=True)
        acc = alpha * acc + lax.dot_general(
            weights.astype(jnp.bfloat16), value_t, NT_DIMS, preferred_element_type=jnp.float32
        )
        return m_new, l_new, acc

    carry = (
        jnp.full((bq, 1), MASKED, jnp.float32),
        jnp.zeros((bq, 1), jnp.float32),
        jnp.zeros((bq, HD), jnp.float32),
    )
    j_diag = q_start // bk
    carry = lax.fori_loop(seg_start // bk, j_diag, lambda j, c: step(j, c, False), carry)
    for r in range(bq // bk):
        carry = step(j_diag + r, carry, True)
    m_fin, l_fin, acc = carry
    o_ref[0] = (acc / l_fin).T.astype(o_ref.dtype)
    lse = m_fin + jnp.log(l_fin)
    lse_ref[0] = jnp.transpose(jnp.broadcast_to(lse, (bq, 128)))[0:1, :]


def attn_forward(qkv_t, seg_pairs, bq=512, bk=512):
    pairs, _, head_size, seq_len = qkv_t.shape
    scale = head_size ** (-0.5)
    n_q = seq_len // bq
    blocks_done = pairs * (seq_len // bk) * (seq_len // bk + 1) // 2
    cost = pl.CostEstimate(
        flops=4 * blocks_done * bk * bk * head_size,
        transcendentals=blocks_done * bk * bk,
        bytes_accessed=pairs * seq_len * head_size * 2 * 4 + pairs * seq_len * 4,
    )
    grid_spec = pltpu.PrefetchScalarGridSpec(
        num_scalar_prefetch=1,
        grid=(pairs, n_q),
        in_specs=[
            pl.BlockSpec((1, 1, head_size, bq), lambda p, i, seg: (p, 0, 0, i)),
            pl.BlockSpec((1, 1, head_size, seq_len), lambda p, i, seg: (p, 1, 0, 0)),
            pl.BlockSpec((1, 1, head_size, seq_len), lambda p, i, seg: (p, 2, 0, 0)),
        ],
        out_specs=[
            pl.BlockSpec((1, head_size, bq), lambda p, i, seg: (p, 0, i)),
            pl.BlockSpec((1, 1, bq), lambda p, i, seg: (p, 0, i)),
        ],
    )
    return pl.pallas_call(
        functools.partial(fwd_kernel, bq=bq, bk=bk, scale=scale),
        grid_spec=grid_spec,
        out_shape=[
            jax.ShapeDtypeStruct((pairs, head_size, seq_len), jnp.bfloat16),
            jax.ShapeDtypeStruct((pairs, 1, seq_len), jnp.float32),
        ],
        cost_estimate=cost,
        name="attn_fwd",
    )(seg_pairs, qkv_t, qkv_t, qkv_t)


def bwd_kernel(seg_ref, q_ref, k_ref, v_ref, do_ref, o_ref, lse_ref, out_ref, dq_acc, *, bk, bq, scale):
    pair = pl.program_id(0)
    kj = pl.program_id(1)

    @pl.when(kj == 0)
    def _():
        dq_acc[...] = jnp.zeros_like(dq_acc)

    seg_len = seg_ref[pair]
    k_start = kj * bk
    seg_end = (k_start // seg_len + 1) * seg_len
    key_t = k_ref[0, 0]
    key = key_t.astype(jnp.float32).T.astype(jnp.bfloat16)
    value_s = (v_ref[0, 0].astype(jnp.float32).T * scale).astype(jnp.bfloat16)

    def step(i, carry, masked):
        dk_t, dv_t = carry
        q_off = pl.multiple_of(i * bq, bq)
        query_t = q_ref[0, 0, :, pl.ds(q_off, bq)]
        query_ts = (query_t.astype(jnp.float32) * scale).astype(jnp.bfloat16)
        dout_t = do_ref[0, :, pl.ds(q_off, bq)]
        out_t = o_ref[0, :, pl.ds(q_off, bq)]
        lse = lse_ref[0, :, pl.ds(q_off, bq)]
        delta = jnp.sum(
            dout_t.astype(jnp.float32) * out_t.astype(jnp.float32), axis=0, keepdims=True
        ) * scale
        s_t = jnp.dot(key, query_ts, preferred_element_type=jnp.float32)
        if masked:
            keys_at = k_start + lax.broadcasted_iota(jnp.int32, (bk, bq), 0)
            queries_at = q_off + lax.broadcasted_iota(jnp.int32, (bk, bq), 1)
            s_t = jnp.where(keys_at <= queries_at, s_t, MASKED)
        p_t = jnp.exp(s_t - lse)
        dv_t = dv_t + lax.dot_general(
            dout_t, p_t.astype(jnp.bfloat16), NT_DIMS, preferred_element_type=jnp.float32
        )
        dp_t = jnp.dot(value_s, dout_t, preferred_element_type=jnp.float32)
        ds_t = (p_t * (dp_t - delta)).astype(jnp.bfloat16)
        dk_t = dk_t + lax.dot_general(query_t, ds_t, NT_DIMS, preferred_element_type=jnp.float32)
        dq_acc[:, pl.ds(q_off, bq)] += jnp.dot(key_t, ds_t, preferred_element_type=jnp.float32)
        return dk_t, dv_t

    carry = (jnp.zeros((HD, bk), jnp.float32), jnp.zeros((HD, bk), jnp.float32))
    for r in range(bk // bq):
        carry = step(k_start // bq + r, carry, True)
    dk_t, dv_t = lax.fori_loop(
        (k_start + bk) // bq, seg_end // bq, lambda i, c: step(i, c, False), carry
    )
    out_ref[0, 0] = dq_acc[:, pl.ds(pl.multiple_of(k_start, bk), bk)].astype(out_ref.dtype)
    out_ref[0, 1] = dk_t.astype(out_ref.dtype)
    out_ref[0, 2] = dv_t.astype(out_ref.dtype)


def attn_backward(qkv_t, dout_t, out_t, lse, seg_pairs, bk=512, bq=512):
    pairs, _, head_size, seq_len = qkv_t.shape
    scale = head_size ** (-0.5)
    n_k = seq_len // bk
    blocks_done = pairs * (seq_len // bq) * (seq_len // bq + 1) // 2
    cost = pl.CostEstimate(
        flops=10 * blocks_done * bq * bq * head_size,
        transcendentals=blocks_done * bq * bq,
        bytes_accessed=pairs * seq_len * head_size * 2 * 8 + pairs * seq_len * 4,
    )
    grid_spec = pltpu.PrefetchScalarGridSpec(
        num_scalar_prefetch=1,
        grid=(pairs, n_k),
        in_specs=[
            pl.BlockSpec((1, 1, head_size, seq_len), lambda p, j, seg: (p, 0, 0, 0)),
            pl.BlockSpec((1, 1, head_size, bk), lambda p, j, seg: (p, 1, 0, j)),
            pl.BlockSpec((1, 1, head_size, bk), lambda p, j, seg: (p, 2, 0, j)),
            pl.BlockSpec((1, head_size, seq_len), lambda p, j, seg: (p, 0, 0)),
            pl.BlockSpec((1, head_size, seq_len), lambda p, j, seg: (p, 0, 0)),
            pl.BlockSpec((1, 1, seq_len), lambda p, j, seg: (p, 0, 0)),
        ],
        out_specs=pl.BlockSpec((1, 3, head_size, bk), lambda p, j, seg: (p, 0, 0, j)),
        scratch_shapes=[pltpu.VMEM((head_size, seq_len), jnp.float32)],
    )
    return pl.pallas_call(
        functools.partial(bwd_kernel, bk=bk, bq=bq, scale=scale),
        grid_spec=grid_spec,
        out_shape=jax.ShapeDtypeStruct((pairs, 3, head_size, seq_len), jnp.bfloat16),
        cost_estimate=cost,
        name="attn_bwd",
    )(seg_pairs, qkv_t, qkv_t, qkv_t, dout_t, out_t, lse)


def norm_rows(values, gain, shift):
    row_mean = jnp.mean(values, axis=-1, keepdims=True)
    centred = values - row_mean
    variance = jnp.mean(centred * centred, axis=-1, keepdims=True)
    inv_std = lax.rsqrt(variance + NORM_EPS)
    normed = centred * inv_std
    return (normed * gain + shift, normed, inv_std)


def norm_back(grad_in, normed, inv_std, gain):
    scaled = grad_in * gain
    centred = (
        scaled
        - jnp.mean(scaled, axis=-1, keepdims=True)
        - normed * jnp.mean(scaled * normed, axis=-1, keepdims=True)
    )
    return (centred * inv_std, jnp.sum(grad_in * normed, axis=0), jnp.sum(grad_in, axis=0))


def rotate(values, cosine, sine_tab):
    half_size = values.shape[-1] // 2
    front = values[..., :half_size]
    behind = values[..., half_size:]
    cos_part = cosine[..., None, :]
    sin_part = sine_tab[..., None, :]
    return jnp.concatenate(
        [front * cos_part - behind * sin_part, behind * cos_part + front * sin_part], axis=-1
    )


def unrotate(values, cosine, sine_tab):
    half_size = values.shape[-1] // 2
    front = values[..., :half_size]
    behind = values[..., half_size:]
    cos_part = cosine[..., None, :]
    sin_part = sine_tab[..., None, :]
    return jnp.concatenate(
        [front * cos_part + behind * sin_part, behind * cos_part - front * sin_part], axis=-1
    )


def local(
    block_input,
    history,
    cotangent,
    qkv_weight,
    proj_weight,
    up_weight,
    down_weight,
    norm1_gain,
    norm1_bias,
    norm2_gain,
    norm2_bias,
    dwa_weights,
    pair_order,
    long_group,
):
    n_seq = lax.axis_size("seq")
    row_count = block_input.shape[0]
    piece_len = SLOT // n_seq
    slot_count = row_count // piece_len
    pair_count = slot_count * HEADS
    per_dev = pair_count // n_seq
    slot_flags = long_group[0]
    seg_len = SLOT // jnp.left_shift(jnp.ones_like(slot_flags), slot_flags)
    position = jnp.arange(SLOT, dtype=jnp.int32)
    doc_place = (position[None, :] % seg_len[:, None]).astype(jnp.float32)
    frequency = jnp.power(10000.0, jnp.arange(HD // 2, dtype=jnp.float32) * (-2.0 / HD))
    angles = doc_place[..., None] * frequency
    my_index = lax.axis_index("seq")
    my_start = my_index * piece_len
    cosine = lax.dynamic_slice_in_dim(jnp.cos(angles), my_start, piece_len, 1)
    sine_tab = lax.dynamic_slice_in_dim(jnp.sin(angles), my_start, piece_len, 1)
    head_groups = HEADS // per_dev
    order_row = pair_order[0]
    held_pairs = lax.dynamic_slice_in_dim(order_row, my_index * per_dev, per_dev, 0)
    my_pairs = my_index * per_dev + jnp.arange(per_dev, dtype=jnp.int32)
    seg_pairs = jnp.take(seg_len, my_pairs // HEADS).astype(jnp.int32)
    n_batch = lax.axis_size("batch")
    batch_index = lax.axis_index("batch")

    def gather_rows(local):
        acc = local
        bits = n_batch.bit_length() - 1
        for bit in reversed(range(bits)):
            partner = [(i, i ^ (1 << bit)) for i in range(n_batch)]
            got = lax.ppermute(acc, "batch", partner)
            low = ((batch_index >> bit) & 1) == 0
            acc = jnp.where(low, jnp.stack([acc, got]), jnp.stack([got, acc]))
        return jnp.transpose(acc, list(range(bits))[::-1] + list(range(bits, acc.ndim))).reshape(
            (n_batch,) + local.shape
        )

    qkv_rows = gather_rows(qkv_weight).reshape(-1, qkv_weight.shape[1])
    w_qkv = lax.all_gather(qkv_rows, "seq", axis=1, tiled=True)
    inputs32 = block_input.astype(jnp.float32)
    norm1_out, normed1, inv_std1 = norm_rows(inputs32, norm1_gain, norm1_bias)
    norm1_low = norm1_out.astype(jnp.bfloat16)
    qkv_out = jnp.dot(norm1_low, w_qkv, preferred_element_type=jnp.float32)
    queries = rotate(qkv_out[:, :D].reshape(slot_count, piece_len, HEADS, HD), cosine, sine_tab)
    keys_rot = rotate(
        qkv_out[:, D : 2 * D].reshape(slot_count, piece_len, HEADS, HD), cosine, sine_tab
    )
    values_in = qkv_out[:, 2 * D :].reshape(slot_count, piece_len, HEADS, HD)
    stacked = jnp.stack([queries, keys_rot, values_in], axis=2).astype(jnp.bfloat16)
    send = jnp.transpose(
        stacked.reshape(slot_count, piece_len, 3, head_groups, per_dev, HD), (0, 3, 4, 2, 5, 1)
    ).reshape(n_seq, per_dev, 3, HD, piece_len)
    incoming = lax.all_to_all(send, "seq", split_axis=0, concat_axis=0, tiled=True)
    later = (proj_weight, up_weight, down_weight)
    later_flat, _ = lax.optimization_barrier(
        (jnp.concatenate([w.reshape(-1) for w in later]), qkv_rows)
    )
    later_rows = gather_rows(later_flat)
    offset = 0
    later_full = []
    for w in later:
        rows = later_rows[:, offset : offset + w.size].reshape(-1, w.shape[1])
        later_full.append(lax.all_gather(rows, "seq", axis=1, tiled=True))
        offset += w.size
    w_proj, w_up, w_down = later_full
    qkv_t = jnp.transpose(incoming, (1, 2, 3, 0, 4)).reshape(per_dev, 3, HD, SLOT)
    attn_t, lse_rows = attn_forward(qkv_t, seg_pairs)
    back = jnp.transpose(attn_t.reshape(per_dev, HD, n_seq, piece_len), (2, 0, 1, 3))
    returned = lax.all_to_all(back, "seq", split_axis=0, concat_axis=0, tiled=True)
    lse_all = lax.all_gather(lse_rows.reshape(per_dev, SLOT), "seq", axis=0, tiled=True)
    lse_all, returned = lax.optimization_barrier((lse_all, returned))
    attended = jnp.transpose(
        returned.reshape(slot_count, head_groups, per_dev, HD, piece_len), (0, 4, 1, 2, 3)
    ).reshape(row_count, D)
    middle = inputs32 + jnp.dot(attended, w_proj, preferred_element_type=jnp.float32)
    norm2_out, normed2, inv_std2 = norm_rows(middle, norm2_gain, norm2_bias)
    norm2_low = norm2_out.astype(jnp.bfloat16)
    hidden_up = jnp.dot(norm2_low, w_up, preferred_element_type=jnp.float32)
    gelu_out, gelu_pull = jax.vjp(lambda hidden: jax.nn.gelu(hidden, approximate=True), hidden_up)
    gelu_low = gelu_out.astype(jnp.bfloat16)
    block_out = middle + jnp.dot(gelu_low, w_down, preferred_element_type=jnp.float32)
    dwa_out = dwa_weights[HIST] * block_out
    for layer_idx in range(HIST):
        dwa_out = dwa_out + dwa_weights[layer_idx] * history[layer_idx].astype(jnp.float32)
    block_output = dwa_out.astype(jnp.bfloat16)
    grad_out = cotangent.astype(jnp.float32)
    history_grad = (dwa_weights[:HIST, None, None] * grad_out[None]).astype(jnp.bfloat16)
    dwa_terms = [
        jnp.sum(history[layer_idx].astype(jnp.float32) * grad_out) for layer_idx in range(HIST)
    ]
    dwa_terms.append(jnp.sum(block_out * grad_out))
    dwa_local = jnp.stack(dwa_terms)
    dy_full = dwa_weights[HIST] * grad_out
    dmlp_low = dy_full.astype(jnp.bfloat16)
    down_local = jnp.einsum(
        "nf,nbd->bfd", gelu_low, dmlp_low.reshape(row_count, n_seq, -1),
        preferred_element_type=jnp.float32,
    )
    dgelu = jnp.einsum("nd,fd->nf", dmlp_low, w_down, preferred_element_type=jnp.float32)
    dup_low = gelu_pull(dgelu)[0].astype(jnp.bfloat16)
    up_local = jnp.einsum(
        "nd,nbf->bdf", norm2_low, dup_low.reshape(row_count, n_seq, -1),
        preferred_element_type=jnp.float32,
    )
    dnorm2 = jnp.einsum("nf,df->nd", dup_low, w_up, preferred_element_type=jnp.float32)
    dmid_norm, gain2_local, bias2_local = norm_back(dnorm2, normed2, inv_std2, norm2_gain)
    dmiddle = dy_full + dmid_norm
    dmiddle_low = dmiddle.astype(jnp.bfloat16)
    proj_local = jnp.einsum(
        "nd,nbe->bde", attended, dmiddle_low.reshape(row_count, n_seq, -1),
        preferred_element_type=jnp.float32,
    )
    dattended = jnp.einsum(
        "ne,de->nd", dmiddle_low, w_proj, preferred_element_type=jnp.float32
    ).astype(jnp.bfloat16)
    dsend = jnp.transpose(
        dattended.reshape(slot_count, piece_len, head_groups, per_dev, HD), (0, 2, 3, 4, 1)
    ).reshape(n_seq, per_dev, HD, piece_len)
    dattn_in = lax.all_to_all(dsend, "seq", split_axis=0, concat_axis=0, tiled=True)
    dout_t = jnp.transpose(dattn_in, (1, 2, 0, 3)).reshape(per_dev, HD, SLOT)
    dpairs = attn_backward(qkv_t, dout_t, attn_t, lse_rows, seg_pairs)
    dback = jnp.transpose(
        dpairs.reshape(per_dev, 3, HD, n_seq, piece_len), (3, 0, 1, 2, 4)
    )
    dreturned = lax.all_to_all(dback, "seq", split_axis=0, concat_axis=0, tiled=True)
    dtokens = jnp.transpose(
        dreturned.reshape(slot_count, head_groups, per_dev, 3, HD, piece_len), (0, 5, 3, 1, 2, 4)
    ).reshape(slot_count, piece_len, 3, HEADS, HD)
    dq_rows = unrotate(dtokens[:, :, 0].astype(jnp.float32), cosine, sine_tab).reshape(row_count, D)
    dk_rows = unrotate(dtokens[:, :, 1].astype(jnp.float32), cosine, sine_tab).reshape(row_count, D)
    dv_rows = dtokens[:, :, 2].astype(jnp.float32).reshape(row_count, D)
    dqkv_low = jnp.concatenate([dq_rows, dk_rows, dv_rows], axis=-1).astype(jnp.bfloat16)
    qkv_local = jnp.einsum(
        "nd,nbf->bdf", norm1_low, dqkv_low.reshape(row_count, n_seq, -1),
        preferred_element_type=jnp.float32,
    )
    dnorm1 = jnp.einsum("nf,df->nd", dqkv_low, w_qkv, preferred_element_type=jnp.float32)
    dinput_norm, gain1_local, bias1_local = norm_back(dnorm1, normed1, inv_std1, norm1_gain)
    input_grad = (dmiddle + dinput_norm).astype(jnp.bfloat16)

    def by_cols(blocks):
        bits = n_seq.bit_length() - 1
        acc = blocks.reshape((2,) * bits + blocks.shape[1:])
        for bit in range(bits):
            mine = (my_index >> bit) & 1
            keep = lax.dynamic_index_in_dim(acc, mine, axis=bits - 1 - bit, keepdims=False)
            send = lax.dynamic_index_in_dim(acc, 1 - mine, axis=bits - 1 - bit, keepdims=False)
            partner = [(i, i ^ (1 << bit)) for i in range(n_seq)]
            got = lax.ppermute(send.astype(jnp.bfloat16), "seq", partner)
            acc = keep + got.astype(jnp.float32)
        return acc.astype(jnp.bfloat16)

    def by_rows(col_sum):
        rows, cols = col_sum.shape
        bits = n_batch.bit_length() - 1
        acc = col_sum.astype(jnp.float32).reshape((2,) * bits + (rows // n_batch, cols))
        for bit in range(bits):
            mine = (batch_index >> bit) & 1
            keep = lax.dynamic_index_in_dim(acc, mine, axis=bits - 1 - bit, keepdims=False)
            send = lax.dynamic_index_in_dim(acc, 1 - mine, axis=bits - 1 - bit, keepdims=False)
            partner = [(i, i ^ (1 << bit)) for i in range(n_batch)]
            got = lax.ppermute(send.astype(jnp.bfloat16), "batch", partner)
            acc = keep + got.astype(jnp.float32)
        return acc

    qkv_grad = by_rows(by_cols(qkv_local))
    proj_grad = by_rows(by_cols(proj_local))
    up_grad = by_rows(by_cols(up_local))
    down_grad = by_rows(by_cols(down_local))
    small_sums = jnp.concatenate([gain1_local, bias1_local, gain2_local, bias2_local, dwa_local])
    for axis in ("seq", "batch"):
        size = lax.axis_size(axis)
        hop = 1
        while hop < size:
            partner = [(i, i ^ hop) for i in range(size)]
            small_sums = small_sums + lax.ppermute(small_sums, axis, partner)
            hop *= 2
    gain1_grad, bias1_grad, gain2_grad, bias2_grad = (
        small_sums[k * D : (k + 1) * D] for k in range(4)
    )
    dwa_grad = small_sums[4 * D :]
    row_lse = jnp.take(lse_all, held_pairs, axis=0).reshape(1, per_dev, SLOT)
    return (
        block_output,
        input_grad,
        history_grad,
        row_lse,
        qkv_grad,
        proj_grad,
        up_grad,
        down_grad,
        gain1_grad,
        bias1_grad,
        gain2_grad,
        bias2_grad,
        dwa_grad,
    )


def solution(mesh):
    placed = (
        P(("batch", "seq"), None),
        P(None, ("batch", "seq"), None),
        P(("batch", "seq"), None),
        P("batch", "seq"),
        P("batch", "seq"),
        P("batch", "seq"),
        P("batch", "seq"),
        P(),
        P(),
        P(),
        P(),
        P(),
        P("batch", None),
        P("batch", None),
    )

    return jax.shard_map(
        local,
        mesh=mesh,
        in_specs=placed,
        out_specs=(
            P(("batch", "seq"), None),
            P(("batch", "seq"), None),
            P(None, ("batch", "seq"), None),
            P("batch", "seq", None),
            P("batch", "seq"),
            P("batch", "seq"),
            P("batch", "seq"),
            P("batch", "seq"),
            P(),
            P(),
            P(),
            P(),
            P(),
        ),
        check_vma=False,
    )
```

```python
import jax
import jax.numpy as jnp
from jax import lax
from jax.sharding import PartitionSpec as P
from jax.experimental import pallas as pl
from jax.experimental.pallas import tpu as pltpu
import functools

D = 768
HEADS = 12
HD = 64
SLOT = 2048
HIST = 8


NORM_EPS = 1e-05
MASKED = -1e30
NT_DIMS = (((1,), (1,)), ((), ()))


def fwd_kernel(seg_ref, q_ref, k_ref, v_ref, o_ref, lse_ref, *, bq, bk, scale, first):
    pair = first + pl.program_id(0)
    qi = pl.program_id(1)
    seg_len = seg_ref[pair]
    q_start = qi * bq
    seg_start = (q_start // seg_len) * seg_len
    query = (q_ref[0, 0].astype(jnp.float32).T * scale).astype(jnp.bfloat16)

    def step(j, carry, masked):
        m_old, l_old, acc = carry
        k_off = pl.multiple_of(j * bk, bk)
        key_t = k_ref[0, 0, :, pl.ds(k_off, bk)]
        value_t = v_ref[0, 0, :, pl.ds(k_off, bk)]
        s = jnp.dot(query, key_t, preferred_element_type=jnp.float32)
        if masked:
            rows = q_start + lax.broadcasted_iota(jnp.int32, (bq, bk), 0)
            cols = k_off + lax.broadcasted_iota(jnp.int32, (bq, bk), 1)
            s = jnp.where(cols <= rows, s, MASKED)
        m_new = jnp.maximum(m_old, jnp.max(s, axis=-1, keepdims=True))
        alpha = jnp.exp(m_old - m_new)
        weights = jnp.exp(s - m_new)
        l_new = alpha * l_old + jnp.sum(weights, axis=-1, keepdims=True)
        acc = alpha * acc + lax.dot_general(
            weights.astype(jnp.bfloat16), value_t, NT_DIMS, preferred_element_type=jnp.float32
        )
        return m_new, l_new, acc

    carry = (
        jnp.full((bq, 1), MASKED, jnp.float32),
        jnp.zeros((bq, 1), jnp.float32),
        jnp.zeros((bq, HD), jnp.float32),
    )
    j_diag = q_start // bk
    carry = lax.fori_loop(seg_start // bk, j_diag, lambda j, c: step(j, c, False), carry)
    for r in range(bq // bk):
        carry = step(j_diag + r, carry, True)
    m_fin, l_fin, acc = carry
    o_ref[0] = (acc / l_fin).T.astype(o_ref.dtype)
    lse = m_fin + jnp.log(l_fin)
    lse_ref[0] = jnp.transpose(jnp.broadcast_to(lse, (bq, 128)))[0:1, :]


def attn_forward(qkv_t, seg_pairs, first, pairs, bq=512, bk=512):
    _, _, head_size, seq_len = qkv_t.shape
    scale = head_size ** (-0.5)
    n_q = seq_len // bq
    blocks_done = pairs * (seq_len // bk) * (seq_len // bk + 1) // 2
    cost = pl.CostEstimate(
        flops=4 * blocks_done * bk * bk * head_size,
        transcendentals=blocks_done * bk * bk,
        bytes_accessed=pairs * seq_len * head_size * 2 * 4 + pairs * seq_len * 4,
    )
    grid_spec = pltpu.PrefetchScalarGridSpec(
        num_scalar_prefetch=1,
        grid=(pairs, n_q),
        in_specs=[
            pl.BlockSpec((1, 1, head_size, bq), lambda p, i, seg: (p + first, 0, 0, i)),
            pl.BlockSpec((1, 1, head_size, seq_len), lambda p, i, seg: (p + first, 1, 0, 0)),
            pl.BlockSpec((1, 1, head_size, seq_len), lambda p, i, seg: (p + first, 2, 0, 0)),
        ],
        out_specs=[
            pl.BlockSpec((1, head_size, bq), lambda p, i, seg: (p, 0, i)),
            pl.BlockSpec((1, 1, bq), lambda p, i, seg: (p, 0, i)),
        ],
    )
    return pl.pallas_call(
        functools.partial(fwd_kernel, bq=bq, bk=bk, scale=scale, first=first),
        grid_spec=grid_spec,
        out_shape=[
            jax.ShapeDtypeStruct((pairs, head_size, seq_len), jnp.bfloat16),
            jax.ShapeDtypeStruct((pairs, 1, seq_len), jnp.float32),
        ],
        cost_estimate=cost,
        name="attn_fwd",
    )(seg_pairs, qkv_t, qkv_t, qkv_t)


def bwd_kernel(seg_ref, q_ref, k_ref, v_ref, do_ref, o_ref, lse_ref, out_ref, dq_acc, *, bk, bq, scale, first):
    pair = first + pl.program_id(0)
    kj = pl.program_id(1)

    @pl.when(kj == 0)
    def _():
        dq_acc[...] = jnp.zeros_like(dq_acc)

    seg_len = seg_ref[pair]
    k_start = kj * bk
    seg_end = (k_start // seg_len + 1) * seg_len
    key_t = k_ref[0, 0]
    key = key_t.astype(jnp.float32).T.astype(jnp.bfloat16)
    value_s = (v_ref[0, 0].astype(jnp.float32).T * scale).astype(jnp.bfloat16)

    def step(i, carry, masked):
        dk_t, dv_t = carry
        q_off = pl.multiple_of(i * bq, bq)
        query_t = q_ref[0, 0, :, pl.ds(q_off, bq)]
        query_ts = (query_t.astype(jnp.float32) * scale).astype(jnp.bfloat16)
        dout_t = do_ref[0, :, pl.ds(q_off, bq)]
        out_t = o_ref[0, :, pl.ds(q_off, bq)]
        lse = lse_ref[0, :, pl.ds(q_off, bq)]
        delta = jnp.sum(
            dout_t.astype(jnp.float32) * out_t.astype(jnp.float32), axis=0, keepdims=True
        ) * scale
        s_t = jnp.dot(key, query_ts, preferred_element_type=jnp.float32)
        if masked:
            keys_at = k_start + lax.broadcasted_iota(jnp.int32, (bk, bq), 0)
            queries_at = q_off + lax.broadcasted_iota(jnp.int32, (bk, bq), 1)
            s_t = jnp.where(keys_at <= queries_at, s_t, MASKED)
        p_t = jnp.exp(s_t - lse)
        dv_t = dv_t + lax.dot_general(
            dout_t, p_t.astype(jnp.bfloat16), NT_DIMS, preferred_element_type=jnp.float32
        )
        dp_t = jnp.dot(value_s, dout_t, preferred_element_type=jnp.float32)
        ds_t = (p_t * (dp_t - delta)).astype(jnp.bfloat16)
        dk_t = dk_t + lax.dot_general(query_t, ds_t, NT_DIMS, preferred_element_type=jnp.float32)
        dq_acc[:, pl.ds(q_off, bq)] += jnp.dot(key_t, ds_t, preferred_element_type=jnp.float32)
        return dk_t, dv_t

    carry = (jnp.zeros((HD, bk), jnp.float32), jnp.zeros((HD, bk), jnp.float32))
    for r in range(bk // bq):
        carry = step(k_start // bq + r, carry, True)
    dk_t, dv_t = lax.fori_loop(
        (k_start + bk) // bq, seg_end // bq, lambda i, c: step(i, c, False), carry
    )
    out_ref[0, 0] = dq_acc[:, pl.ds(pl.multiple_of(k_start, bk), bk)].astype(out_ref.dtype)
    out_ref[0, 1] = dk_t.astype(out_ref.dtype)
    out_ref[0, 2] = dv_t.astype(out_ref.dtype)


def attn_backward(qkv_t, dout_t, out_t, lse, seg_pairs, first, pairs, bk=512, bq=512):
    _, _, head_size, seq_len = qkv_t.shape
    scale = head_size ** (-0.5)
    n_k = seq_len // bk
    blocks_done = pairs * (seq_len // bq) * (seq_len // bq + 1) // 2
    cost = pl.CostEstimate(
        flops=10 * blocks_done * bq * bq * head_size,
        transcendentals=blocks_done * bq * bq,
        bytes_accessed=pairs * seq_len * head_size * 2 * 8 + pairs * seq_len * 4,
    )
    grid_spec = pltpu.PrefetchScalarGridSpec(
        num_scalar_prefetch=1,
        grid=(pairs, n_k),
        in_specs=[
            pl.BlockSpec((1, 1, head_size, seq_len), lambda p, j, seg: (p + first, 0, 0, 0)),
            pl.BlockSpec((1, 1, head_size, bk), lambda p, j, seg: (p + first, 1, 0, j)),
            pl.BlockSpec((1, 1, head_size, bk), lambda p, j, seg: (p + first, 2, 0, j)),
            pl.BlockSpec((1, head_size, seq_len), lambda p, j, seg: (p + first, 0, 0)),
            pl.BlockSpec((1, head_size, seq_len), lambda p, j, seg: (p + first, 0, 0)),
            pl.BlockSpec((1, 1, seq_len), lambda p, j, seg: (p + first, 0, 0)),
        ],
        out_specs=pl.BlockSpec((1, 3, head_size, bk), lambda p, j, seg: (p, 0, 0, j)),
        scratch_shapes=[pltpu.VMEM((head_size, seq_len), jnp.float32)],
    )
    return pl.pallas_call(
        functools.partial(bwd_kernel, bk=bk, bq=bq, scale=scale, first=first),
        grid_spec=grid_spec,
        out_shape=jax.ShapeDtypeStruct((pairs, 3, head_size, seq_len), jnp.bfloat16),
        cost_estimate=cost,
        name="attn_bwd",
    )(seg_pairs, qkv_t, qkv_t, qkv_t, dout_t, out_t, lse)


def norm_rows(values, gain, shift):
    row_mean = jnp.mean(values, axis=-1, keepdims=True)
    centred = values - row_mean
    variance = jnp.mean(centred * centred, axis=-1, keepdims=True)
    inv_std = lax.rsqrt(variance + NORM_EPS)
    normed = centred * inv_std
    return (normed * gain + shift, normed, inv_std)


def norm_back(grad_in, normed, inv_std, gain):
    scaled = grad_in * gain
    centred = (
        scaled
        - jnp.mean(scaled, axis=-1, keepdims=True)
        - normed * jnp.mean(scaled * normed, axis=-1, keepdims=True)
    )
    return (centred * inv_std, jnp.sum(grad_in * normed, axis=0), jnp.sum(grad_in, axis=0))


def rotate(values, cosine, sine_tab):
    half_size = values.shape[-1] // 2
    front = values[..., :half_size]
    behind = values[..., half_size:]
    cos_part = cosine[..., None, :]
    sin_part = sine_tab[..., None, :]
    return jnp.concatenate(
        [front * cos_part - behind * sin_part, behind * cos_part + front * sin_part], axis=-1
    )


def unrotate(values, cosine, sine_tab):
    half_size = values.shape[-1] // 2
    front = values[..., :half_size]
    behind = values[..., half_size:]
    cos_part = cosine[..., None, :]
    sin_part = sine_tab[..., None, :]
    return jnp.concatenate(
        [front * cos_part + behind * sin_part, behind * cos_part - front * sin_part], axis=-1
    )


def local(
    block_input,
    history,
    cotangent,
    qkv_weight,
    proj_weight,
    up_weight,
    down_weight,
    norm1_gain,
    norm1_bias,
    norm2_gain,
    norm2_bias,
    dwa_weights,
    pair_order,
    long_group,
):
    n_seq = lax.axis_size("seq")
    row_count = block_input.shape[0]
    piece_len = SLOT // n_seq
    slot_count = row_count // piece_len
    pair_count = slot_count * HEADS
    per_dev = pair_count // n_seq
    slot_flags = long_group[0]
    seg_len = SLOT // jnp.left_shift(jnp.ones_like(slot_flags), slot_flags)
    position = jnp.arange(SLOT, dtype=jnp.int32)
    doc_place = (position[None, :] % seg_len[:, None]).astype(jnp.float32)
    frequency = jnp.power(10000.0, jnp.arange(HD // 2, dtype=jnp.float32) * (-2.0 / HD))
    angles = doc_place[..., None] * frequency
    my_index = lax.axis_index("seq")
    my_start = my_index * piece_len
    cosine = lax.dynamic_slice_in_dim(jnp.cos(angles), my_start, piece_len, 1)
    sine_tab = lax.dynamic_slice_in_dim(jnp.sin(angles), my_start, piece_len, 1)
    head_groups = HEADS // per_dev
    order_row = pair_order[0]
    held_pairs = lax.dynamic_slice_in_dim(order_row, my_index * per_dev, per_dev, 0)
    my_pairs = my_index * per_dev + jnp.arange(per_dev, dtype=jnp.int32)
    seg_pairs = jnp.take(seg_len, my_pairs // HEADS).astype(jnp.int32)
    n_batch = lax.axis_size("batch")
    batch_index = lax.axis_index("batch")

    def gather_rows(local):
        acc = local
        bits = n_batch.bit_length() - 1
        for bit in reversed(range(bits)):
            partner = [(i, i ^ (1 << bit)) for i in range(n_batch)]
            got = lax.ppermute(acc, "batch", partner)
            low = ((batch_index >> bit) & 1) == 0
            acc = jnp.where(low, jnp.stack([acc, got]), jnp.stack([got, acc]))
        return jnp.transpose(acc, list(range(bits))[::-1] + list(range(bits, acc.ndim))).reshape(
            (n_batch,) + local.shape
        )

    qkv_rows = gather_rows(qkv_weight).reshape(-1, qkv_weight.shape[1])
    w_qkv = lax.all_gather(qkv_rows, "seq", axis=1, tiled=True)
    inputs32 = block_input.astype(jnp.float32)
    norm1_out, normed1, inv_std1 = norm_rows(inputs32, norm1_gain, norm1_bias)
    norm1_low = norm1_out.astype(jnp.bfloat16)
    qkv_out = jnp.dot(norm1_low, w_qkv, preferred_element_type=jnp.float32)
    queries = rotate(qkv_out[:, :D].reshape(slot_count, piece_len, HEADS, HD), cosine, sine_tab)
    keys_rot = rotate(
        qkv_out[:, D : 2 * D].reshape(slot_count, piece_len, HEADS, HD), cosine, sine_tab
    )
    values_in = qkv_out[:, 2 * D :].reshape(slot_count, piece_len, HEADS, HD)
    stacked = jnp.stack([queries, keys_rot, values_in], axis=2).astype(jnp.bfloat16)
    send = jnp.transpose(
        stacked.reshape(slot_count, piece_len, 3, head_groups, per_dev, HD), (0, 3, 4, 2, 5, 1)
    ).reshape(n_seq, per_dev, 3, HD, piece_len)
    incoming = lax.all_to_all(send, "seq", split_axis=0, concat_axis=0, tiled=True)
    later = (proj_weight, up_weight, down_weight)
    later_flat, _ = lax.optimization_barrier(
        (jnp.concatenate([w.reshape(-1) for w in later]), qkv_rows)
    )
    later_rows = gather_rows(later_flat)
    offset = 0
    later_full = []
    for w in later:
        rows = later_rows[:, offset : offset + w.size].reshape(-1, w.shape[1])
        later_full.append(lax.all_gather(rows, "seq", axis=1, tiled=True))
        offset += w.size
    w_proj, w_up, w_down = later_full
    qkv_t = jnp.transpose(incoming, (1, 2, 3, 0, 4)).reshape(per_dev, 3, HD, SLOT)
    fwd_parts = [attn_forward(qkv_t, seg_pairs, c, 1) for c in range(per_dev)]
    attn_t = jnp.concatenate([part[0] for part in fwd_parts], axis=0)
    lse_rows = jnp.concatenate([part[1] for part in fwd_parts], axis=0)
    back = jnp.transpose(attn_t.reshape(per_dev, HD, n_seq, piece_len), (2, 0, 1, 3))
    returned = lax.all_to_all(back, "seq", split_axis=0, concat_axis=0, tiled=True)
    lse_all = lax.all_gather(lse_rows.reshape(per_dev, SLOT), "seq", axis=0, tiled=True)
    lse_all, returned = lax.optimization_barrier((lse_all, returned))
    attended = jnp.transpose(
        returned.reshape(slot_count, head_groups, per_dev, HD, piece_len), (0, 4, 1, 2, 3)
    ).reshape(row_count, D)
    middle = inputs32 + jnp.dot(attended, w_proj, preferred_element_type=jnp.float32)
    norm2_out, normed2, inv_std2 = norm_rows(middle, norm2_gain, norm2_bias)
    norm2_low = norm2_out.astype(jnp.bfloat16)
    hidden_up = jnp.dot(norm2_low, w_up, preferred_element_type=jnp.float32)
    gelu_out, gelu_pull = jax.vjp(lambda hidden: jax.nn.gelu(hidden, approximate=True), hidden_up)
    gelu_low = gelu_out.astype(jnp.bfloat16)
    block_out = middle + jnp.dot(gelu_low, w_down, preferred_element_type=jnp.float32)
    dwa_out = dwa_weights[HIST] * block_out
    for layer_idx in range(HIST):
        dwa_out = dwa_out + dwa_weights[layer_idx] * history[layer_idx].astype(jnp.float32)
    block_output = dwa_out.astype(jnp.bfloat16)
    grad_out = cotangent.astype(jnp.float32)
    history_grad = (dwa_weights[:HIST, None, None] * grad_out[None]).astype(jnp.bfloat16)
    dwa_terms = [
        jnp.sum(history[layer_idx].astype(jnp.float32) * grad_out) for layer_idx in range(HIST)
    ]
    dwa_terms.append(jnp.sum(block_out * grad_out))
    dwa_local = jnp.stack(dwa_terms)
    dy_full = dwa_weights[HIST] * grad_out
    dmlp_low = dy_full.astype(jnp.bfloat16)
    down_local = jnp.einsum(
        "nf,nbd->bfd", gelu_low, dmlp_low.reshape(row_count, n_seq, -1),
        preferred_element_type=jnp.float32,
    )
    dgelu = jnp.einsum("nd,fd->nf", dmlp_low, w_down, preferred_element_type=jnp.float32)
    dup_low = gelu_pull(dgelu)[0].astype(jnp.bfloat16)
    up_local = jnp.einsum(
        "nd,nbf->bdf", norm2_low, dup_low.reshape(row_count, n_seq, -1),
        preferred_element_type=jnp.float32,
    )
    dnorm2 = jnp.einsum("nf,df->nd", dup_low, w_up, preferred_element_type=jnp.float32)
    dmid_norm, gain2_local, bias2_local = norm_back(dnorm2, normed2, inv_std2, norm2_gain)
    dmiddle = dy_full + dmid_norm
    dmiddle_low = dmiddle.astype(jnp.bfloat16)
    proj_local = jnp.einsum(
        "nd,nbe->bde", attended, dmiddle_low.reshape(row_count, n_seq, -1),
        preferred_element_type=jnp.float32,
    )
    dattended = jnp.einsum(
        "ne,de->nd", dmiddle_low, w_proj, preferred_element_type=jnp.float32
    ).astype(jnp.bfloat16)
    dsend = jnp.transpose(
        dattended.reshape(slot_count, piece_len, head_groups, per_dev, HD), (0, 2, 3, 4, 1)
    ).reshape(n_seq, per_dev, HD, piece_len)
    dattn_in = lax.all_to_all(dsend, "seq", split_axis=0, concat_axis=0, tiled=True)
    dout_t = jnp.transpose(dattn_in, (1, 2, 0, 3)).reshape(per_dev, HD, SLOT)
    dpairs = jnp.concatenate(
        [attn_backward(qkv_t, dout_t, attn_t, lse_rows, seg_pairs, c, 1) for c in range(per_dev)],
        axis=0,
    )
    dback = jnp.transpose(
        dpairs.reshape(per_dev, 3, HD, n_seq, piece_len), (3, 0, 1, 2, 4)
    )
    dreturned = lax.all_to_all(dback, "seq", split_axis=0, concat_axis=0, tiled=True)
    dtokens = jnp.transpose(
        dreturned.reshape(slot_count, head_groups, per_dev, 3, HD, piece_len), (0, 5, 3, 1, 2, 4)
    ).reshape(slot_count, piece_len, 3, HEADS, HD)
    dq_rows = unrotate(dtokens[:, :, 0].astype(jnp.float32), cosine, sine_tab).reshape(row_count, D)
    dk_rows = unrotate(dtokens[:, :, 1].astype(jnp.float32), cosine, sine_tab).reshape(row_count, D)
    dv_rows = dtokens[:, :, 2].astype(jnp.float32).reshape(row_count, D)
    dqkv_low = jnp.concatenate([dq_rows, dk_rows, dv_rows], axis=-1).astype(jnp.bfloat16)
    qkv_local = jnp.einsum(
        "nd,nbf->bdf", norm1_low, dqkv_low.reshape(row_count, n_seq, -1),
        preferred_element_type=jnp.float32,
    )
    dnorm1 = jnp.einsum("nf,df->nd", dqkv_low, w_qkv, preferred_element_type=jnp.float32)
    dinput_norm, gain1_local, bias1_local = norm_back(dnorm1, normed1, inv_std1, norm1_gain)
    input_grad = (dmiddle + dinput_norm).astype(jnp.bfloat16)

    def by_cols(blocks):
        bits = n_seq.bit_length() - 1
        acc = blocks.reshape((2,) * bits + blocks.shape[1:])
        for bit in range(bits):
            mine = (my_index >> bit) & 1
            keep = lax.dynamic_index_in_dim(acc, mine, axis=bits - 1 - bit, keepdims=False)
            send = lax.dynamic_index_in_dim(acc, 1 - mine, axis=bits - 1 - bit, keepdims=False)
            partner = [(i, i ^ (1 << bit)) for i in range(n_seq)]
            got = lax.ppermute(send.astype(jnp.bfloat16), "seq", partner)
            acc = keep + got.astype(jnp.float32)
        return acc.astype(jnp.bfloat16)

    def by_rows(col_sum):
        return lax.psum_scatter(col_sum, "batch", scatter_dimension=0, tiled=True).astype(
            jnp.float32
        )

    qkv_grad = by_rows(by_cols(qkv_local))
    proj_grad = by_rows(by_cols(proj_local))
    up_grad = by_rows(by_cols(up_local))
    down_grad = by_rows(by_cols(down_local))
    small_sums = jnp.concatenate([gain1_local, bias1_local, gain2_local, bias2_local, dwa_local])
    for axis in ("seq", "batch"):
        size = lax.axis_size(axis)
        hop = 1
        while hop < size:
            partner = [(i, i ^ hop) for i in range(size)]
            small_sums = small_sums + lax.ppermute(small_sums, axis, partner)
            hop *= 2
    gain1_grad, bias1_grad, gain2_grad, bias2_grad = (
        small_sums[k * D : (k + 1) * D] for k in range(4)
    )
    dwa_grad = small_sums[4 * D :]
    row_lse = jnp.take(lse_all, held_pairs, axis=0).reshape(1, per_dev, SLOT)
    return (
        block_output,
        input_grad,
        history_grad,
        row_lse,
        qkv_grad,
        proj_grad,
        up_grad,
        down_grad,
        gain1_grad,
        bias1_grad,
        gain2_grad,
        bias2_grad,
        dwa_grad,
    )


def solution(mesh):
    placed = (
        P(("batch", "seq"), None),
        P(None, ("batch", "seq"), None),
        P(("batch", "seq"), None),
        P("batch", "seq"),
        P("batch", "seq"),
        P("batch", "seq"),
        P("batch", "seq"),
        P(),
        P(),
        P(),
        P(),
        P(),
        P("batch", None),
        P("batch", None),
    )

    return jax.shard_map(
        local,
        mesh=mesh,
        in_specs=placed,
        out_specs=(
            P(("batch", "seq"), None),
            P(("batch", "seq"), None),
            P(None, ("batch", "seq"), None),
            P("batch", "seq", None),
            P("batch", "seq"),
            P("batch", "seq"),
            P("batch", "seq"),
            P("batch", "seq"),
            P(),
            P(),
            P(),
            P(),
            P(),
        ),
        check_vma=False,
    )
```

```python
import jax
import jax.numpy as jnp
from jax import lax
from jax.sharding import PartitionSpec as P
from jax.experimental import pallas as pl
from jax.experimental.pallas import tpu as pltpu
import functools

D = 768
HEADS = 12
HD = 64
SLOT = 2048
HIST = 8


NORM_EPS = 1e-05
MASKED = -1e30
NT_DIMS = (((1,), (1,)), ((), ()))


def fwd_kernel(seg_ref, q_ref, k_ref, v_ref, o_ref, lse_ref, *, bq, bk, scale):
    pair = pl.program_id(0)
    qi = pl.program_id(1)
    seg_len = seg_ref[pair]
    q_start = qi * bq
    seg_start = (q_start // seg_len) * seg_len
    query = (q_ref[0, 0].astype(jnp.float32).T * scale).astype(jnp.bfloat16)

    def step(j, carry, masked):
        m_old, l_old, acc = carry
        k_off = pl.multiple_of(j * bk, bk)
        key_t = k_ref[0, 0, :, pl.ds(k_off, bk)]
        value_t = v_ref[0, 0, :, pl.ds(k_off, bk)]
        s = jnp.dot(query, key_t, preferred_element_type=jnp.float32)
        if masked:
            rows = q_start + lax.broadcasted_iota(jnp.int32, (bq, bk), 0)
            cols = k_off + lax.broadcasted_iota(jnp.int32, (bq, bk), 1)
            s = jnp.where(cols <= rows, s, MASKED)
        m_new = jnp.maximum(m_old, jnp.max(s, axis=-1, keepdims=True))
        alpha = jnp.exp(m_old - m_new)
        weights = jnp.exp(s - m_new)
        l_new = alpha * l_old + jnp.sum(weights, axis=-1, keepdims=True)
        acc = alpha * acc + lax.dot_general(
            weights.astype(jnp.bfloat16), value_t, NT_DIMS, preferred_element_type=jnp.float32
        )
        return m_new, l_new, acc

    carry = (
        jnp.full((bq, 1), MASKED, jnp.float32),
        jnp.zeros((bq, 1), jnp.float32),
        jnp.zeros((bq, HD), jnp.float32),
    )
    j_diag = q_start // bk
    carry = lax.fori_loop(seg_start // bk, j_diag, lambda j, c: step(j, c, False), carry)
    for r in range(bq // bk):
        carry = step(j_diag + r, carry, True)
    m_fin, l_fin, acc = carry
    o_ref[0] = (acc / l_fin).T.astype(o_ref.dtype)
    lse = m_fin + jnp.log(l_fin)
    lse_ref[0] = jnp.transpose(jnp.broadcast_to(lse, (bq, 128)))[0:1, :]


def attn_forward(qkv_t, seg_pairs, bq=512, bk=512):
    pairs, _, head_size, seq_len = qkv_t.shape
    scale = head_size ** (-0.5)
    n_q = seq_len // bq
    blocks_done = pairs * (seq_len // bk) * (seq_len // bk + 1) // 2
    cost = pl.CostEstimate(
        flops=4 * blocks_done * bk * bk * head_size,
        transcendentals=blocks_done * bk * bk,
        bytes_accessed=pairs * seq_len * head_size * 2 * 4 + pairs * seq_len * 4,
    )
    grid_spec = pltpu.PrefetchScalarGridSpec(
        num_scalar_prefetch=1,
        grid=(pairs, n_q),
        in_specs=[
            pl.BlockSpec((1, 1, head_size, bq), lambda p, i, seg: (p, 0, 0, i)),
            pl.BlockSpec((1, 1, head_size, seq_len), lambda p, i, seg: (p, 1, 0, 0)),
            pl.BlockSpec((1, 1, head_size, seq_len), lambda p, i, seg: (p, 2, 0, 0)),
        ],
        out_specs=[
            pl.BlockSpec((1, head_size, bq), lambda p, i, seg: (p, 0, i)),
            pl.BlockSpec((1, 1, bq), lambda p, i, seg: (p, 0, i)),
        ],
    )
    return pl.pallas_call(
        functools.partial(fwd_kernel, bq=bq, bk=bk, scale=scale),
        grid_spec=grid_spec,
        out_shape=[
            jax.ShapeDtypeStruct((pairs, head_size, seq_len), jnp.bfloat16),
            jax.ShapeDtypeStruct((pairs, 1, seq_len), jnp.float32),
        ],
        cost_estimate=cost,
        name="attn_fwd",
    )(seg_pairs, qkv_t, qkv_t, qkv_t)


def bwd_kernel(seg_ref, q_ref, k_ref, v_ref, do_ref, o_ref, lse_ref, out_ref, dq_acc, *, bk, bq, scale):
    pair = pl.program_id(0)
    kj = pl.program_id(1)

    @pl.when(kj == 0)
    def _():
        dq_acc[...] = jnp.zeros_like(dq_acc)

    seg_len = seg_ref[pair]
    k_start = kj * bk
    seg_end = (k_start // seg_len + 1) * seg_len
    key_t = k_ref[0, 0]
    key = key_t.astype(jnp.float32).T.astype(jnp.bfloat16)
    value_s = (v_ref[0, 0].astype(jnp.float32).T * scale).astype(jnp.bfloat16)

    def step(i, carry, masked):
        dk_t, dv_t = carry
        q_off = pl.multiple_of(i * bq, bq)
        query_t = q_ref[0, 0, :, pl.ds(q_off, bq)]
        query_ts = (query_t.astype(jnp.float32) * scale).astype(jnp.bfloat16)
        dout_t = do_ref[0, :, pl.ds(q_off, bq)]
        out_t = o_ref[0, :, pl.ds(q_off, bq)]
        lse = lse_ref[0, :, pl.ds(q_off, bq)]
        delta = jnp.sum(
            dout_t.astype(jnp.float32) * out_t.astype(jnp.float32), axis=0, keepdims=True
        ) * scale
        s_t = jnp.dot(key, query_ts, preferred_element_type=jnp.float32)
        if masked:
            keys_at = k_start + lax.broadcasted_iota(jnp.int32, (bk, bq), 0)
            queries_at = q_off + lax.broadcasted_iota(jnp.int32, (bk, bq), 1)
            s_t = jnp.where(keys_at <= queries_at, s_t, MASKED)
        p_t = jnp.exp(s_t - lse)
        dv_t = dv_t + lax.dot_general(
            dout_t, p_t.astype(jnp.bfloat16), NT_DIMS, preferred_element_type=jnp.float32
        )
        dp_t = jnp.dot(value_s, dout_t, preferred_element_type=jnp.float32)
        ds_t = (p_t * (dp_t - delta)).astype(jnp.bfloat16)
        dk_t = dk_t + lax.dot_general(query_t, ds_t, NT_DIMS, preferred_element_type=jnp.float32)
        dq_acc[:, pl.ds(q_off, bq)] += jnp.dot(key_t, ds_t, preferred_element_type=jnp.float32)
        return dk_t, dv_t

    carry = (jnp.zeros((HD, bk), jnp.float32), jnp.zeros((HD, bk), jnp.float32))
    for r in range(bk // bq):
        carry = step(k_start // bq + r, carry, True)
    dk_t, dv_t = lax.fori_loop(
        (k_start + bk) // bq, seg_end // bq, lambda i, c: step(i, c, False), carry
    )
    out_ref[0, 0] = dq_acc[:, pl.ds(pl.multiple_of(k_start, bk), bk)].astype(out_ref.dtype)
    out_ref[0, 1] = dk_t.astype(out_ref.dtype)
    out_ref[0, 2] = dv_t.astype(out_ref.dtype)


def attn_backward(qkv_t, dout_t, out_t, lse, seg_pairs, bk=512, bq=512):
    pairs, _, head_size, seq_len = qkv_t.shape
    scale = head_size ** (-0.5)
    n_k = seq_len // bk
    blocks_done = pairs * (seq_len // bq) * (seq_len // bq + 1) // 2
    cost = pl.CostEstimate(
        flops=10 * blocks_done * bq * bq * head_size,
        transcendentals=blocks_done * bq * bq,
        bytes_accessed=pairs * seq_len * head_size * 2 * 8 + pairs * seq_len * 4,
    )
    grid_spec = pltpu.PrefetchScalarGridSpec(
        num_scalar_prefetch=1,
        grid=(pairs, n_k),
        in_specs=[
            pl.BlockSpec((1, 1, head_size, seq_len), lambda p, j, seg: (p, 0, 0, 0)),
            pl.BlockSpec((1, 1, head_size, bk), lambda p, j, seg: (p, 1, 0, j)),
            pl.BlockSpec((1, 1, head_size, bk), lambda p, j, seg: (p, 2, 0, j)),
            pl.BlockSpec((1, head_size, seq_len), lambda p, j, seg: (p, 0, 0)),
            pl.BlockSpec((1, head_size, seq_len), lambda p, j, seg: (p, 0, 0)),
            pl.BlockSpec((1, 1, seq_len), lambda p, j, seg: (p, 0, 0)),
        ],
        out_specs=pl.BlockSpec((1, 3, head_size, bk), lambda p, j, seg: (p, 0, 0, j)),
        scratch_shapes=[pltpu.VMEM((head_size, seq_len), jnp.float32)],
    )
    return pl.pallas_call(
        functools.partial(bwd_kernel, bk=bk, bq=bq, scale=scale),
        grid_spec=grid_spec,
        out_shape=jax.ShapeDtypeStruct((pairs, 3, head_size, seq_len), jnp.bfloat16),
        cost_estimate=cost,
        name="attn_bwd",
    )(seg_pairs, qkv_t, qkv_t, qkv_t, dout_t, out_t, lse)


def norm_rows(values, gain, shift):
    row_mean = jnp.mean(values, axis=-1, keepdims=True)
    centred = values - row_mean
    variance = jnp.mean(centred * centred, axis=-1, keepdims=True)
    inv_std = lax.rsqrt(variance + NORM_EPS)
    normed = centred * inv_std
    return (normed * gain + shift, normed, inv_std)


def norm_back(grad_in, normed, inv_std, gain):
    scaled = grad_in * gain
    centred = (
        scaled
        - jnp.mean(scaled, axis=-1, keepdims=True)
        - normed * jnp.mean(scaled * normed, axis=-1, keepdims=True)
    )
    return (centred * inv_std, jnp.sum(grad_in * normed, axis=0), jnp.sum(grad_in, axis=0))


def rotate(values, cosine, sine_tab):
    half_size = values.shape[-1] // 2
    front = values[..., :half_size]
    behind = values[..., half_size:]
    cos_part = cosine[..., None, :]
    sin_part = sine_tab[..., None, :]
    return jnp.concatenate(
        [front * cos_part - behind * sin_part, behind * cos_part + front * sin_part], axis=-1
    )


def unrotate(values, cosine, sine_tab):
    half_size = values.shape[-1] // 2
    front = values[..., :half_size]
    behind = values[..., half_size:]
    cos_part = cosine[..., None, :]
    sin_part = sine_tab[..., None, :]
    return jnp.concatenate(
        [front * cos_part + behind * sin_part, behind * cos_part - front * sin_part], axis=-1
    )


def local(
    block_input,
    history,
    cotangent,
    qkv_weight,
    proj_weight,
    up_weight,
    down_weight,
    norm1_gain,
    norm1_bias,
    norm2_gain,
    norm2_bias,
    dwa_weights,
    pair_order,
    long_group,
):
    n_seq = lax.axis_size("seq")
    row_count = block_input.shape[0]
    piece_len = SLOT // n_seq
    slot_count = row_count // piece_len
    pair_count = slot_count * HEADS
    per_dev = pair_count // n_seq
    slot_flags = long_group[0]
    seg_len = SLOT // jnp.left_shift(jnp.ones_like(slot_flags), slot_flags)
    position = jnp.arange(SLOT, dtype=jnp.int32)
    doc_place = (position[None, :] % seg_len[:, None]).astype(jnp.float32)
    frequency = jnp.power(10000.0, jnp.arange(HD // 2, dtype=jnp.float32) * (-2.0 / HD))
    angles = doc_place[..., None] * frequency
    my_index = lax.axis_index("seq")
    my_start = my_index * piece_len
    cosine = lax.dynamic_slice_in_dim(jnp.cos(angles), my_start, piece_len, 1)
    sine_tab = lax.dynamic_slice_in_dim(jnp.sin(angles), my_start, piece_len, 1)
    head_groups = HEADS // per_dev
    order_row = pair_order[0]
    held_pairs = lax.dynamic_slice_in_dim(order_row, my_index * per_dev, per_dev, 0)
    my_pairs = my_index * per_dev + jnp.arange(per_dev, dtype=jnp.int32)
    seg_pairs = jnp.take(seg_len, my_pairs // HEADS).astype(jnp.int32)
    n_batch = lax.axis_size("batch")
    batch_index = lax.axis_index("batch")

    def gather_rows(local):
        acc = local
        bits = n_batch.bit_length() - 1
        for bit in reversed(range(bits)):
            partner = [(i, i ^ (1 << bit)) for i in range(n_batch)]
            got = lax.ppermute(acc, "batch", partner)
            low = ((batch_index >> bit) & 1) == 0
            acc = jnp.where(low, jnp.stack([acc, got]), jnp.stack([got, acc]))
        return jnp.transpose(acc, list(range(bits))[::-1] + list(range(bits, acc.ndim))).reshape(
            (n_batch,) + local.shape
        )

    qkv_rows = gather_rows(qkv_weight).reshape(-1, qkv_weight.shape[1])
    w_qkv = lax.all_gather(qkv_rows, "seq", axis=1, tiled=True)
    inputs32 = block_input.astype(jnp.float32)
    norm1_out, normed1, inv_std1 = norm_rows(inputs32, norm1_gain, norm1_bias)
    norm1_low = norm1_out.astype(jnp.bfloat16)
    qkv_out = jnp.dot(norm1_low, w_qkv, preferred_element_type=jnp.float32)
    queries = rotate(qkv_out[:, :D].reshape(slot_count, piece_len, HEADS, HD), cosine, sine_tab)
    keys_rot = rotate(
        qkv_out[:, D : 2 * D].reshape(slot_count, piece_len, HEADS, HD), cosine, sine_tab
    )
    values_in = qkv_out[:, 2 * D :].reshape(slot_count, piece_len, HEADS, HD)
    stacked = jnp.stack([queries, keys_rot, values_in], axis=2).astype(jnp.bfloat16)
    send = jnp.transpose(
        stacked.reshape(slot_count, piece_len, 3, head_groups, per_dev, HD), (0, 3, 4, 2, 5, 1)
    ).reshape(n_seq, per_dev, 3, HD, piece_len)
    incoming = lax.all_to_all(send, "seq", split_axis=0, concat_axis=0, tiled=True)
    later = (proj_weight, up_weight, down_weight)
    later_flat, _ = lax.optimization_barrier(
        (jnp.concatenate([w.reshape(-1) for w in later]), qkv_rows)
    )
    later_rows = gather_rows(later_flat)
    offset = 0
    later_full = []
    for w in later:
        rows = later_rows[:, offset : offset + w.size].reshape(-1, w.shape[1])
        later_full.append(lax.all_gather(rows, "seq", axis=1, tiled=True))
        offset += w.size
    w_proj, w_up, w_down = later_full
    qkv_t = jnp.transpose(incoming, (1, 2, 3, 0, 4)).reshape(per_dev, 3, HD, SLOT)
    attn_t, lse_rows = attn_forward(qkv_t, seg_pairs)
    back = jnp.transpose(attn_t.reshape(per_dev, HD, n_seq, piece_len), (2, 0, 1, 3))
    returned = lax.all_to_all(back, "seq", split_axis=0, concat_axis=0, tiled=True)
    lse_all = lax.all_gather(lse_rows.reshape(per_dev, SLOT), "seq", axis=0, tiled=True)
    lse_all, returned = lax.optimization_barrier((lse_all, returned))
    attended = jnp.transpose(
        returned.reshape(slot_count, head_groups, per_dev, HD, piece_len), (0, 4, 1, 2, 3)
    ).reshape(row_count, D)
    middle = inputs32 + jnp.dot(attended, w_proj, preferred_element_type=jnp.float32)
    norm2_out, normed2, inv_std2 = norm_rows(middle, norm2_gain, norm2_bias)
    norm2_low = norm2_out.astype(jnp.bfloat16)
    hidden_up = jnp.dot(norm2_low, w_up, preferred_element_type=jnp.float32)
    gelu_out, gelu_pull = jax.vjp(lambda hidden: jax.nn.gelu(hidden, approximate=True), hidden_up)
    gelu_low = gelu_out.astype(jnp.bfloat16)
    block_out = middle + jnp.dot(gelu_low, w_down, preferred_element_type=jnp.float32)
    dwa_out = dwa_weights[HIST] * block_out
    for layer_idx in range(HIST):
        dwa_out = dwa_out + dwa_weights[layer_idx] * history[layer_idx].astype(jnp.float32)
    block_output = dwa_out.astype(jnp.bfloat16)
    grad_out = cotangent.astype(jnp.float32)
    history_grad = (dwa_weights[:HIST, None, None] * grad_out[None]).astype(jnp.bfloat16)
    dwa_terms = [
        jnp.sum(history[layer_idx].astype(jnp.float32) * grad_out) for layer_idx in range(HIST)
    ]
    dwa_terms.append(jnp.sum(block_out * grad_out))
    dwa_local = jnp.stack(dwa_terms)
    dy_full = dwa_weights[HIST] * grad_out
    dmlp_low = dy_full.astype(jnp.bfloat16)
    down_local = jnp.einsum(
        "nf,nbd->bfd", gelu_low, dmlp_low.reshape(row_count, n_seq, -1),
        preferred_element_type=jnp.float32,
    )
    dgelu = jnp.einsum("nd,fd->nf", dmlp_low, w_down, preferred_element_type=jnp.float32)
    dup_low = gelu_pull(dgelu)[0].astype(jnp.bfloat16)
    up_local = jnp.einsum(
        "nd,nbf->bdf", norm2_low, dup_low.reshape(row_count, n_seq, -1),
        preferred_element_type=jnp.float32,
    )
    dnorm2 = jnp.einsum("nf,df->nd", dup_low, w_up, preferred_element_type=jnp.float32)
    dmid_norm, gain2_local, bias2_local = norm_back(dnorm2, normed2, inv_std2, norm2_gain)
    dmiddle = dy_full + dmid_norm
    dmiddle_low = dmiddle.astype(jnp.bfloat16)
    proj_local = jnp.einsum(
        "nd,nbe->bde", attended, dmiddle_low.reshape(row_count, n_seq, -1),
        preferred_element_type=jnp.float32,
    )
    dattended = jnp.einsum(
        "ne,de->nd", dmiddle_low, w_proj, preferred_element_type=jnp.float32
    ).astype(jnp.bfloat16)
    dsend = jnp.transpose(
        dattended.reshape(slot_count, piece_len, head_groups, per_dev, HD), (0, 2, 3, 4, 1)
    ).reshape(n_seq, per_dev, HD, piece_len)
    dattn_in = lax.all_to_all(dsend, "seq", split_axis=0, concat_axis=0, tiled=True)
    dout_t = jnp.transpose(dattn_in, (1, 2, 0, 3)).reshape(per_dev, HD, SLOT)
    dpairs = attn_backward(qkv_t, dout_t, attn_t, lse_rows, seg_pairs)
    dback = jnp.transpose(
        dpairs.reshape(per_dev, 3, HD, n_seq, piece_len), (3, 0, 1, 2, 4)
    )
    dreturned = lax.all_to_all(dback, "seq", split_axis=0, concat_axis=0, tiled=True)
    dtokens = jnp.transpose(
        dreturned.reshape(slot_count, head_groups, per_dev, 3, HD, piece_len), (0, 5, 3, 1, 2, 4)
    ).reshape(slot_count, piece_len, 3, HEADS, HD)
    dq_rows = unrotate(dtokens[:, :, 0].astype(jnp.float32), cosine, sine_tab).reshape(row_count, D)
    dk_rows = unrotate(dtokens[:, :, 1].astype(jnp.float32), cosine, sine_tab).reshape(row_count, D)
    dv_rows = dtokens[:, :, 2].astype(jnp.float32).reshape(row_count, D)
    dqkv_low = jnp.concatenate([dq_rows, dk_rows, dv_rows], axis=-1).astype(jnp.bfloat16)
    qkv_local = jnp.einsum(
        "nd,nbf->bdf", norm1_low, dqkv_low.reshape(row_count, n_seq, -1),
        preferred_element_type=jnp.float32,
    )
    dnorm1 = jnp.einsum("nf,df->nd", dqkv_low, w_qkv, preferred_element_type=jnp.float32)
    dinput_norm, gain1_local, bias1_local = norm_back(dnorm1, normed1, inv_std1, norm1_gain)
    input_grad = (dmiddle + dinput_norm).astype(jnp.bfloat16)

    def by_cols(blocks):
        bits = n_seq.bit_length() - 1
        acc = blocks.reshape((2,) * bits + blocks.shape[1:])
        for bit in range(bits):
            mine = (my_index >> bit) & 1
            low = lax.index_in_dim(acc, 0, axis=bits - 1 - bit, keepdims=False)
            high = lax.index_in_dim(acc, 1, axis=bits - 1 - bit, keepdims=False)
            keep = jnp.where(mine == 0, low, high)
            send = jnp.where(mine == 0, high, low)
            partner = [(i, i ^ (1 << bit)) for i in range(n_seq)]
            got = lax.ppermute(send.astype(jnp.bfloat16), "seq", partner)
            acc = keep + got.astype(jnp.float32)
        return acc.astype(jnp.bfloat16)

    def by_rows(col_sum):
        return lax.psum_scatter(col_sum, "batch", scatter_dimension=0, tiled=True).astype(
            jnp.float32
        )

    qkv_grad = by_rows(by_cols(qkv_local))
    proj_grad = by_rows(by_cols(proj_local))
    up_grad = by_rows(by_cols(up_local))
    down_grad = by_rows(by_cols(down_local))
    small_sums = jnp.concatenate([gain1_local, bias1_local, gain2_local, bias2_local, dwa_local])
    for axis in ("seq", "batch"):
        size = lax.axis_size(axis)
        hop = 1
        while hop < size:
            partner = [(i, i ^ hop) for i in range(size)]
            small_sums = small_sums + lax.ppermute(small_sums, axis, partner)
            hop *= 2
    gain1_grad, bias1_grad, gain2_grad, bias2_grad = (
        small_sums[k * D : (k + 1) * D] for k in range(4)
    )
    dwa_grad = small_sums[4 * D :]
    row_lse = jnp.take(lse_all, held_pairs, axis=0).reshape(1, per_dev, SLOT)
    return (
        block_output,
        input_grad,
        history_grad,
        row_lse,
        qkv_grad,
        proj_grad,
        up_grad,
        down_grad,
        gain1_grad,
        bias1_grad,
        gain2_grad,
        bias2_grad,
        dwa_grad,
    )


def solution(mesh):
    placed = (
        P(("batch", "seq"), None),
        P(None, ("batch", "seq"), None),
        P(("batch", "seq"), None),
        P("batch", "seq"),
        P("batch", "seq"),
        P("batch", "seq"),
        P("batch", "seq"),
        P(),
        P(),
        P(),
        P(),
        P(),
        P("batch", None),
        P("batch", None),
    )

    return jax.shard_map(
        local,
        mesh=mesh,
        in_specs=placed,
        out_specs=(
            P(("batch", "seq"), None),
            P(("batch", "seq"), None),
            P(None, ("batch", "seq"), None),
            P("batch", "seq", None),
            P("batch", "seq"),
            P("batch", "seq"),
            P("batch", "seq"),
            P("batch", "seq"),
            P(),
            P(),
            P(),
            P(),
            P(),
        ),
        check_vma=False,
    )
```

```python
import jax
import jax.numpy as jnp
from jax import lax
from jax.sharding import PartitionSpec as P
from jax.experimental import pallas as pl
from jax.experimental.pallas import tpu as pltpu
import functools

D = 768
HEADS = 12
HD = 64
SLOT = 2048
HIST = 8


NORM_EPS = 1e-05
MASKED = -1e30
NT_DIMS = (((1,), (1,)), ((), ()))


def fwd_kernel(seg_ref, q_ref, k_ref, v_ref, o_ref, lse_ref, *, bq, bk, scale):
    pair = pl.program_id(0)
    qi = pl.program_id(1)
    seg_len = seg_ref[pair]
    q_start = qi * bq
    seg_start = (q_start // seg_len) * seg_len
    query = (q_ref[0, 0].astype(jnp.float32).T * scale).astype(jnp.bfloat16)

    def step(j, carry, masked):
        m_old, l_old, acc = carry
        k_off = pl.multiple_of(j * bk, bk)
        key_t = k_ref[0, 0, :, pl.ds(k_off, bk)]
        value_t = v_ref[0, 0, :, pl.ds(k_off, bk)]
        s = jnp.dot(query, key_t, preferred_element_type=jnp.float32)
        if masked:
            rows = q_start + lax.broadcasted_iota(jnp.int32, (bq, bk), 0)
            cols = k_off + lax.broadcasted_iota(jnp.int32, (bq, bk), 1)
            s = jnp.where(cols <= rows, s, MASKED)
        m_new = jnp.maximum(m_old, jnp.max(s, axis=-1, keepdims=True))
        alpha = jnp.exp(m_old - m_new)
        weights = jnp.exp(s - m_new)
        l_new = alpha * l_old + jnp.sum(weights, axis=-1, keepdims=True)
        acc = alpha * acc + lax.dot_general(
            weights.astype(jnp.bfloat16), value_t, NT_DIMS, preferred_element_type=jnp.float32
        )
        return m_new, l_new, acc

    carry = (
        jnp.full((bq, 1), MASKED, jnp.float32),
        jnp.zeros((bq, 1), jnp.float32),
        jnp.zeros((bq, HD), jnp.float32),
    )
    j_diag = q_start // bk
    carry = lax.fori_loop(seg_start // bk, j_diag, lambda j, c: step(j, c, False), carry)
    for r in range(bq // bk):
        carry = step(j_diag + r, carry, True)
    m_fin, l_fin, acc = carry
    o_ref[0] = (acc / l_fin).T.astype(o_ref.dtype)
    lse = m_fin + jnp.log(l_fin)
    lse_ref[0] = jnp.transpose(jnp.broadcast_to(lse, (bq, 128)))[0:1, :]


def attn_forward(qkv_t, seg_pairs, bq=512, bk=512):
    pairs, _, head_size, seq_len = qkv_t.shape
    scale = head_size ** (-0.5)
    n_q = seq_len // bq
    blocks_done = pairs * (seq_len // bk) * (seq_len // bk + 1) // 2
    cost = pl.CostEstimate(
        flops=4 * blocks_done * bk * bk * head_size,
        transcendentals=blocks_done * bk * bk,
        bytes_accessed=pairs * seq_len * head_size * 2 * 4 + pairs * seq_len * 4,
    )
    grid_spec = pltpu.PrefetchScalarGridSpec(
        num_scalar_prefetch=1,
        grid=(pairs, n_q),
        in_specs=[
            pl.BlockSpec((1, 1, head_size, bq), lambda p, i, seg: (p, 0, 0, i)),
            pl.BlockSpec((1, 1, head_size, seq_len), lambda p, i, seg: (p, 1, 0, 0)),
            pl.BlockSpec((1, 1, head_size, seq_len), lambda p, i, seg: (p, 2, 0, 0)),
        ],
        out_specs=[
            pl.BlockSpec((1, head_size, bq), lambda p, i, seg: (p, 0, i)),
            pl.BlockSpec((1, 1, bq), lambda p, i, seg: (p, 0, i)),
        ],
    )
    return pl.pallas_call(
        functools.partial(fwd_kernel, bq=bq, bk=bk, scale=scale),
        grid_spec=grid_spec,
        out_shape=[
            jax.ShapeDtypeStruct((pairs, head_size, seq_len), jnp.bfloat16),
            jax.ShapeDtypeStruct((pairs, 1, seq_len), jnp.float32),
        ],
        cost_estimate=cost,
        name="attn_fwd",
    )(seg_pairs, qkv_t, qkv_t, qkv_t)


def bwd_kernel(seg_ref, q_ref, k_ref, v_ref, do_ref, o_ref, lse_ref, out_ref, dq_acc, *, bk, bq, scale):
    pair = pl.program_id(0)
    kj = pl.program_id(1)

    @pl.when(kj == 0)
    def _():
        dq_acc[...] = jnp.zeros_like(dq_acc)

    seg_len = seg_ref[pair]
    k_start = kj * bk
    seg_end = (k_start // seg_len + 1) * seg_len
    key_t = k_ref[0, 0]
    key = key_t.astype(jnp.float32).T.astype(jnp.bfloat16)
    value_s = (v_ref[0, 0].astype(jnp.float32).T * scale).astype(jnp.bfloat16)

    def step(i, carry, masked):
        dk_t, dv_t = carry
        q_off = pl.multiple_of(i * bq, bq)
        query_t = q_ref[0, 0, :, pl.ds(q_off, bq)]
        query_ts = (query_t.astype(jnp.float32) * scale).astype(jnp.bfloat16)
        dout_t = do_ref[0, :, pl.ds(q_off, bq)]
        out_t = o_ref[0, :, pl.ds(q_off, bq)]
        lse = lse_ref[0, :, pl.ds(q_off, bq)]
        delta = jnp.sum(
            dout_t.astype(jnp.float32) * out_t.astype(jnp.float32), axis=0, keepdims=True
        ) * scale
        s_t = jnp.dot(key, query_ts, preferred_element_type=jnp.float32)
        if masked:
            keys_at = k_start + lax.broadcasted_iota(jnp.int32, (bk, bq), 0)
            queries_at = q_off + lax.broadcasted_iota(jnp.int32, (bk, bq), 1)
            s_t = jnp.where(keys_at <= queries_at, s_t, MASKED)
        p_t = jnp.exp(s_t - lse)
        dv_t = dv_t + lax.dot_general(
            dout_t, p_t.astype(jnp.bfloat16), NT_DIMS, preferred_element_type=jnp.float32
        )
        dp_t = jnp.dot(value_s, dout_t, preferred_element_type=jnp.float32)
        ds_t = (p_t * (dp_t - delta)).astype(jnp.bfloat16)
        dk_t = dk_t + lax.dot_general(query_t, ds_t, NT_DIMS, preferred_element_type=jnp.float32)
        dq_acc[:, pl.ds(q_off, bq)] += jnp.dot(key_t, ds_t, preferred_element_type=jnp.float32)
        return dk_t, dv_t

    carry = (jnp.zeros((HD, bk), jnp.float32), jnp.zeros((HD, bk), jnp.float32))
    for r in range(bk // bq):
        carry = step(k_start // bq + r, carry, True)
    dk_t, dv_t = lax.fori_loop(
        (k_start + bk) // bq, seg_end // bq, lambda i, c: step(i, c, False), carry
    )
    out_ref[0, 0] = dq_acc[:, pl.ds(pl.multiple_of(k_start, bk), bk)].astype(out_ref.dtype)
    out_ref[0, 1] = dk_t.astype(out_ref.dtype)
    out_ref[0, 2] = dv_t.astype(out_ref.dtype)


def attn_backward(qkv_t, dout_t, out_t, lse, seg_pairs, bk=512, bq=512):
    pairs, _, head_size, seq_len = qkv_t.shape
    scale = head_size ** (-0.5)
    n_k = seq_len // bk
    blocks_done = pairs * (seq_len // bq) * (seq_len // bq + 1) // 2
    cost = pl.CostEstimate(
        flops=10 * blocks_done * bq * bq * head_size,
        transcendentals=blocks_done * bq * bq,
        bytes_accessed=pairs * seq_len * head_size * 2 * 8 + pairs * seq_len * 4,
    )
    grid_spec = pltpu.PrefetchScalarGridSpec(
        num_scalar_prefetch=1,
        grid=(pairs, n_k),
        in_specs=[
            pl.BlockSpec((1, 1, head_size, seq_len), lambda p, j, seg: (p, 0, 0, 0)),
            pl.BlockSpec((1, 1, head_size, bk), lambda p, j, seg: (p, 1, 0, j)),
            pl.BlockSpec((1, 1, head_size, bk), lambda p, j, seg: (p, 2, 0, j)),
            pl.BlockSpec((1, head_size, seq_len), lambda p, j, seg: (p, 0, 0)),
            pl.BlockSpec((1, head_size, seq_len), lambda p, j, seg: (p, 0, 0)),
            pl.BlockSpec((1, 1, seq_len), lambda p, j, seg: (p, 0, 0)),
        ],
        out_specs=pl.BlockSpec((1, 3, head_size, bk), lambda p, j, seg: (p, 0, 0, j)),
        scratch_shapes=[pltpu.VMEM((head_size, seq_len), jnp.float32)],
    )
    return pl.pallas_call(
        functools.partial(bwd_kernel, bk=bk, bq=bq, scale=scale),
        grid_spec=grid_spec,
        out_shape=jax.ShapeDtypeStruct((pairs, 3, head_size, seq_len), jnp.bfloat16),
        cost_estimate=cost,
        name="attn_bwd",
    )(seg_pairs, qkv_t, qkv_t, qkv_t, dout_t, out_t, lse)


def norm_rows(values, gain, shift):
    row_mean = jnp.mean(values, axis=-1, keepdims=True)
    centred = values - row_mean
    variance = jnp.mean(centred * centred, axis=-1, keepdims=True)
    inv_std = lax.rsqrt(variance + NORM_EPS)
    normed = centred * inv_std
    return (normed * gain + shift, normed, inv_std)


def norm_back(grad_in, normed, inv_std, gain):
    scaled = grad_in * gain
    centred = (
        scaled
        - jnp.mean(scaled, axis=-1, keepdims=True)
        - normed * jnp.mean(scaled * normed, axis=-1, keepdims=True)
    )
    return (centred * inv_std, jnp.sum(grad_in * normed, axis=0), jnp.sum(grad_in, axis=0))


def rotate(values, cosine, sine_tab):
    half_size = values.shape[-1] // 2
    front = values[..., :half_size]
    behind = values[..., half_size:]
    cos_part = cosine[..., None, :]
    sin_part = sine_tab[..., None, :]
    return jnp.concatenate(
        [front * cos_part - behind * sin_part, behind * cos_part + front * sin_part], axis=-1
    )


def unrotate(values, cosine, sine_tab):
    half_size = values.shape[-1] // 2
    front = values[..., :half_size]
    behind = values[..., half_size:]
    cos_part = cosine[..., None, :]
    sin_part = sine_tab[..., None, :]
    return jnp.concatenate(
        [front * cos_part + behind * sin_part, behind * cos_part - front * sin_part], axis=-1
    )


def local(
    block_input,
    history,
    cotangent,
    qkv_weight,
    proj_weight,
    up_weight,
    down_weight,
    norm1_gain,
    norm1_bias,
    norm2_gain,
    norm2_bias,
    dwa_weights,
    pair_order,
    long_group,
):
    n_seq = lax.axis_size("seq")
    row_count = block_input.shape[0]
    piece_len = SLOT // n_seq
    slot_count = row_count // piece_len
    pair_count = slot_count * HEADS
    per_dev = pair_count // n_seq
    slot_flags = long_group[0]
    seg_len = SLOT // jnp.left_shift(jnp.ones_like(slot_flags), slot_flags)
    position = jnp.arange(SLOT, dtype=jnp.int32)
    doc_place = (position[None, :] % seg_len[:, None]).astype(jnp.float32)
    frequency = jnp.power(10000.0, jnp.arange(HD // 2, dtype=jnp.float32) * (-2.0 / HD))
    angles = doc_place[..., None] * frequency
    my_index = lax.axis_index("seq")
    my_start = my_index * piece_len
    cosine = lax.dynamic_slice_in_dim(jnp.cos(angles), my_start, piece_len, 1)
    sine_tab = lax.dynamic_slice_in_dim(jnp.sin(angles), my_start, piece_len, 1)
    order_row = pair_order[0]
    held_pairs = lax.dynamic_slice_in_dim(order_row, my_index * per_dev, per_dev, 0)
    my_pairs = jnp.arange(per_dev, dtype=jnp.int32) * n_seq + my_index
    seg_pairs = jnp.take(seg_len, my_pairs // HEADS).astype(jnp.int32)
    n_batch = lax.axis_size("batch")
    batch_index = lax.axis_index("batch")

    def gather_rows(local):
        acc = local
        bits = n_batch.bit_length() - 1
        for bit in reversed(range(bits)):
            partner = [(i, i ^ (1 << bit)) for i in range(n_batch)]
            got = lax.ppermute(acc, "batch", partner)
            low = ((batch_index >> bit) & 1) == 0
            acc = jnp.where(low, jnp.stack([acc, got]), jnp.stack([got, acc]))
        return jnp.transpose(acc, list(range(bits))[::-1] + list(range(bits, acc.ndim))).reshape(
            (n_batch,) + local.shape
        )

    qkv_rows = gather_rows(qkv_weight).reshape(-1, qkv_weight.shape[1])
    w_qkv = lax.all_gather(qkv_rows, "seq", axis=1, tiled=True)
    inputs32 = block_input.astype(jnp.float32)
    norm1_out, normed1, inv_std1 = norm_rows(inputs32, norm1_gain, norm1_bias)
    norm1_low = norm1_out.astype(jnp.bfloat16)
    qkv_out = jnp.dot(norm1_low, w_qkv, preferred_element_type=jnp.float32)
    queries = rotate(qkv_out[:, :D].reshape(slot_count, piece_len, HEADS, HD), cosine, sine_tab)
    keys_rot = rotate(
        qkv_out[:, D : 2 * D].reshape(slot_count, piece_len, HEADS, HD), cosine, sine_tab
    )
    values_in = qkv_out[:, 2 * D :].reshape(slot_count, piece_len, HEADS, HD)
    stacked = jnp.stack([queries, keys_rot, values_in], axis=2).astype(jnp.bfloat16)
    send = jnp.transpose(
        jnp.transpose(stacked, (0, 3, 2, 4, 1)).reshape(per_dev, n_seq, 3, HD, piece_len),
        (1, 0, 2, 3, 4),
    )
    incoming = lax.all_to_all(send, "seq", split_axis=0, concat_axis=0, tiled=True)
    grad_out = cotangent.astype(jnp.float32)
    hist_sum = dwa_weights[0] * history[0].astype(jnp.float32)
    for layer_idx in range(1, HIST):
        hist_sum = hist_sum + dwa_weights[layer_idx] * history[layer_idx].astype(jnp.float32)
    history_grad = (dwa_weights[:HIST, None, None] * grad_out[None]).astype(jnp.bfloat16)
    hist_terms = [
        jnp.sum(history[layer_idx].astype(jnp.float32) * grad_out) for layer_idx in range(HIST)
    ]
    hist_sum, history_grad, hist_terms, incoming = lax.optimization_barrier(
        (hist_sum, history_grad, hist_terms, incoming)
    )
    later = (proj_weight, up_weight, down_weight)
    later_flat, _ = lax.optimization_barrier(
        (jnp.concatenate([w.reshape(-1) for w in later]), qkv_rows)
    )
    later_rows = gather_rows(later_flat)
    offset = 0
    later_full = []
    for w in later:
        rows = later_rows[:, offset : offset + w.size].reshape(-1, w.shape[1])
        later_full.append(lax.all_gather(rows, "seq", axis=1, tiled=True))
        offset += w.size
    w_proj, w_up, w_down = later_full
    qkv_t = jnp.transpose(incoming, (1, 2, 3, 0, 4)).reshape(per_dev, 3, HD, SLOT)
    attn_t, lse_rows = attn_forward(qkv_t, seg_pairs)
    back = jnp.transpose(attn_t.reshape(per_dev, HD, n_seq, piece_len), (2, 0, 1, 3))
    returned = lax.all_to_all(back, "seq", split_axis=0, concat_axis=0, tiled=True)
    lse_all = lax.all_gather(lse_rows.reshape(per_dev, SLOT), "seq", axis=0, tiled=True)
    lse_all, returned = lax.optimization_barrier((lse_all, returned))
    attended = jnp.transpose(
        jnp.transpose(returned, (1, 0, 2, 3)).reshape(slot_count, HEADS, HD, piece_len),
        (0, 3, 1, 2),
    ).reshape(row_count, D)
    middle = inputs32 + jnp.dot(attended, w_proj, preferred_element_type=jnp.float32)
    norm2_out, normed2, inv_std2 = norm_rows(middle, norm2_gain, norm2_bias)
    norm2_low = norm2_out.astype(jnp.bfloat16)
    hidden_up = jnp.dot(norm2_low, w_up, preferred_element_type=jnp.float32)
    gelu_out, gelu_pull = jax.vjp(lambda hidden: jax.nn.gelu(hidden, approximate=True), hidden_up)
    gelu_low = gelu_out.astype(jnp.bfloat16)
    block_out = middle + jnp.dot(gelu_low, w_down, preferred_element_type=jnp.float32)
    dwa_out = hist_sum + dwa_weights[HIST] * block_out
    block_output = dwa_out.astype(jnp.bfloat16)
    dwa_terms = hist_terms + [jnp.sum(block_out * grad_out)]
    dwa_local = jnp.stack(dwa_terms)
    dy_full = dwa_weights[HIST] * grad_out
    dmlp_low = dy_full.astype(jnp.bfloat16)
    down_local = jnp.einsum(
        "nf,nbd->bfd", gelu_low, dmlp_low.reshape(row_count, n_seq, -1),
        preferred_element_type=jnp.float32,
    )
    dgelu = jnp.einsum("nd,fd->nf", dmlp_low, w_down, preferred_element_type=jnp.float32)
    dup_low = gelu_pull(dgelu)[0].astype(jnp.bfloat16)
    up_local = jnp.einsum(
        "nd,nbf->bdf", norm2_low, dup_low.reshape(row_count, n_seq, -1),
        preferred_element_type=jnp.float32,
    )
    dnorm2 = jnp.einsum("nf,df->nd", dup_low, w_up, preferred_element_type=jnp.float32)
    dmid_norm, gain2_local, bias2_local = norm_back(dnorm2, normed2, inv_std2, norm2_gain)
    dmiddle = dy_full + dmid_norm
    dmiddle_low = dmiddle.astype(jnp.bfloat16)
    proj_local = jnp.einsum(
        "nd,nbe->bde", attended, dmiddle_low.reshape(row_count, n_seq, -1),
        preferred_element_type=jnp.float32,
    )
    dattended = jnp.einsum(
        "ne,de->nd", dmiddle_low, w_proj, preferred_element_type=jnp.float32
    ).astype(jnp.bfloat16)
    dsend = jnp.transpose(
        jnp.transpose(dattended.reshape(slot_count, piece_len, HEADS, HD), (0, 2, 3, 1)).reshape(
            per_dev, n_seq, HD, piece_len
        ),
        (1, 0, 2, 3),
    )
    dattn_in = lax.all_to_all(dsend, "seq", split_axis=0, concat_axis=0, tiled=True)
    dout_t = jnp.transpose(dattn_in, (1, 2, 0, 3)).reshape(per_dev, HD, SLOT)
    dpairs = attn_backward(qkv_t, dout_t, attn_t, lse_rows, seg_pairs)
    dback = jnp.transpose(
        dpairs.reshape(per_dev, 3, HD, n_seq, piece_len), (3, 0, 1, 2, 4)
    )
    dreturned = lax.all_to_all(dback, "seq", split_axis=0, concat_axis=0, tiled=True)
    dtokens = jnp.transpose(
        jnp.transpose(dreturned, (1, 0, 2, 3, 4)).reshape(slot_count, HEADS, 3, HD, piece_len),
        (0, 4, 2, 1, 3),
    )
    dq_rows = unrotate(dtokens[:, :, 0].astype(jnp.float32), cosine, sine_tab).reshape(row_count, D)
    dk_rows = unrotate(dtokens[:, :, 1].astype(jnp.float32), cosine, sine_tab).reshape(row_count, D)
    dv_rows = dtokens[:, :, 2].astype(jnp.float32).reshape(row_count, D)
    dqkv_low = jnp.concatenate([dq_rows, dk_rows, dv_rows], axis=-1).astype(jnp.bfloat16)
    qkv_local = jnp.einsum(
        "nd,nbf->bdf", norm1_low, dqkv_low.reshape(row_count, n_seq, -1),
        preferred_element_type=jnp.float32,
    )
    dnorm1 = jnp.einsum("nf,df->nd", dqkv_low, w_qkv, preferred_element_type=jnp.float32)
    dinput_norm, gain1_local, bias1_local = norm_back(dnorm1, normed1, inv_std1, norm1_gain)
    input_grad = (dmiddle + dinput_norm).astype(jnp.bfloat16)

    def by_cols(blocks):
        bits = n_seq.bit_length() - 1
        acc = blocks.reshape((2,) * bits + blocks.shape[1:])
        for bit in range(bits):
            mine = (my_index >> bit) & 1
            keep = lax.dynamic_index_in_dim(acc, mine, axis=bits - 1 - bit, keepdims=False)
            send = lax.dynamic_index_in_dim(acc, 1 - mine, axis=bits - 1 - bit, keepdims=False)
            partner = [(i, i ^ (1 << bit)) for i in range(n_seq)]
            got = lax.ppermute(send.astype(jnp.bfloat16), "seq", partner)
            acc = keep + got.astype(jnp.float32)
        return acc.astype(jnp.bfloat16)

    def by_rows(col_sum):
        return lax.psum_scatter(col_sum, "batch", scatter_dimension=0, tiled=True).astype(
            jnp.float32
        )

    qkv_grad = by_rows(by_cols(qkv_local))
    proj_grad = by_rows(by_cols(proj_local))
    up_grad = by_rows(by_cols(up_local))
    down_grad = by_rows(by_cols(down_local))
    small_sums = jnp.concatenate([gain1_local, bias1_local, gain2_local, bias2_local, dwa_local])
    for axis in ("seq", "batch"):
        size = lax.axis_size(axis)
        hop = 1
        while hop < size:
            partner = [(i, i ^ hop) for i in range(size)]
            small_sums = small_sums + lax.ppermute(small_sums, axis, partner)
            hop *= 2
    gain1_grad, bias1_grad, gain2_grad, bias2_grad = (
        small_sums[k * D : (k + 1) * D] for k in range(4)
    )
    dwa_grad = small_sums[4 * D :]
    lse_by_pair = jnp.transpose(lse_all.reshape(n_seq, per_dev, SLOT), (1, 0, 2)).reshape(
        pair_count, SLOT
    )
    row_lse = jnp.take(lse_by_pair, held_pairs, axis=0).reshape(1, per_dev, SLOT)
    return (
        block_output,
        input_grad,
        history_grad,
        row_lse,
        qkv_grad,
        proj_grad,
        up_grad,
        down_grad,
        gain1_grad,
        bias1_grad,
        gain2_grad,
        bias2_grad,
        dwa_grad,
    )


def solution(mesh):
    placed = (
        P(("batch", "seq"), None),
        P(None, ("batch", "seq"), None),
        P(("batch", "seq"), None),
        P("batch", "seq"),
        P("batch", "seq"),
        P("batch", "seq"),
        P("batch", "seq"),
        P(),
        P(),
        P(),
        P(),
        P(),
        P("batch", None),
        P("batch", None),
    )

    return jax.shard_map(
        local,
        mesh=mesh,
        in_specs=placed,
        out_specs=(
            P(("batch", "seq"), None),
            P(("batch", "seq"), None),
            P(None, ("batch", "seq"), None),
            P("batch", "seq", None),
            P("batch", "seq"),
            P("batch", "seq"),
            P("batch", "seq"),
            P("batch", "seq"),
            P(),
            P(),
            P(),
            P(),
            P(),
        ),
        check_vma=False,
    )
```

```python
import jax
import jax.numpy as jnp
from jax import lax
from jax.sharding import PartitionSpec as P
from jax.experimental import pallas as pl
from jax.experimental.pallas import tpu as pltpu
import functools

D = 768
HEADS = 12
HD = 64
SLOT = 2048
HIST = 8


NORM_EPS = 1e-05
MASKED = -1e30
NT_DIMS = (((1,), (1,)), ((), ()))


def fwd_kernel(seg_ref, q_ref, k_ref, v_ref, o_ref, lse_ref, *, bq, bk, scale):
    pair = pl.program_id(0)
    qi = pl.program_id(1)
    seg_len = seg_ref[pair]
    q_start = qi * bq
    seg_start = (q_start // seg_len) * seg_len
    query = (q_ref[0, 0].astype(jnp.float32).T * scale).astype(jnp.bfloat16)

    def step(j, carry, masked):
        m_old, l_old, acc = carry
        k_off = pl.multiple_of(j * bk, bk)
        key_t = k_ref[0, 0, :, pl.ds(k_off, bk)]
        value_t = v_ref[0, 0, :, pl.ds(k_off, bk)]
        s = jnp.dot(query, key_t, preferred_element_type=jnp.float32)
        if masked:
            rows = q_start + lax.broadcasted_iota(jnp.int32, (bq, bk), 0)
            cols = k_off + lax.broadcasted_iota(jnp.int32, (bq, bk), 1)
            s = jnp.where(cols <= rows, s, MASKED)
        m_new = jnp.maximum(m_old, jnp.max(s, axis=-1, keepdims=True))
        alpha = jnp.exp(m_old - m_new)
        weights = jnp.exp(s - m_new)
        l_new = alpha * l_old + jnp.sum(weights, axis=-1, keepdims=True)
        acc = alpha * acc + lax.dot_general(
            weights.astype(jnp.bfloat16), value_t, NT_DIMS, preferred_element_type=jnp.float32
        )
        return m_new, l_new, acc

    carry = (
        jnp.full((bq, 1), MASKED, jnp.float32),
        jnp.zeros((bq, 1), jnp.float32),
        jnp.zeros((bq, HD), jnp.float32),
    )
    j_diag = q_start // bk
    carry = lax.fori_loop(seg_start // bk, j_diag, lambda j, c: step(j, c, False), carry)
    for r in range(bq // bk):
        carry = step(j_diag + r, carry, True)
    m_fin, l_fin, acc = carry
    o_ref[0] = (acc / l_fin).T.astype(o_ref.dtype)
    lse = m_fin + jnp.log(l_fin)
    lse_ref[0] = jnp.transpose(jnp.broadcast_to(lse, (bq, 128)))[0:1, :]


def attn_forward(qkv_t, seg_pairs, bq=512, bk=512):
    pairs, _, head_size, seq_len = qkv_t.shape
    scale = head_size ** (-0.5)
    n_q = seq_len // bq
    blocks_done = pairs * (seq_len // bk) * (seq_len // bk + 1) // 2
    cost = pl.CostEstimate(
        flops=4 * blocks_done * bk * bk * head_size,
        transcendentals=blocks_done * bk * bk,
        bytes_accessed=pairs * seq_len * head_size * 2 * 4 + pairs * seq_len * 4,
    )
    grid_spec = pltpu.PrefetchScalarGridSpec(
        num_scalar_prefetch=1,
        grid=(pairs, n_q),
        in_specs=[
            pl.BlockSpec((1, 1, head_size, bq), lambda p, i, seg: (p, 0, 0, i)),
            pl.BlockSpec((1, 1, head_size, seq_len), lambda p, i, seg: (p, 1, 0, 0)),
            pl.BlockSpec((1, 1, head_size, seq_len), lambda p, i, seg: (p, 2, 0, 0)),
        ],
        out_specs=[
            pl.BlockSpec((1, head_size, bq), lambda p, i, seg: (p, 0, i)),
            pl.BlockSpec((1, 1, bq), lambda p, i, seg: (p, 0, i)),
        ],
    )
    return pl.pallas_call(
        functools.partial(fwd_kernel, bq=bq, bk=bk, scale=scale),
        grid_spec=grid_spec,
        out_shape=[
            jax.ShapeDtypeStruct((pairs, head_size, seq_len), jnp.bfloat16),
            jax.ShapeDtypeStruct((pairs, 1, seq_len), jnp.float32),
        ],
        cost_estimate=cost,
        name="attn_fwd",
    )(seg_pairs, qkv_t, qkv_t, qkv_t)


def bwd_kernel(seg_ref, q_ref, k_ref, v_ref, do_ref, o_ref, lse_ref, out_ref, dq_acc, *, bk, bq, scale):
    pair = pl.program_id(0)
    kj = pl.program_id(1)

    @pl.when(kj == 0)
    def _():
        dq_acc[...] = jnp.zeros_like(dq_acc)

    seg_len = seg_ref[pair]
    k_start = kj * bk
    seg_end = (k_start // seg_len + 1) * seg_len
    key_t = k_ref[0, 0]
    key = key_t.astype(jnp.float32).T.astype(jnp.bfloat16)
    value_s = (v_ref[0, 0].astype(jnp.float32).T * scale).astype(jnp.bfloat16)

    def step(i, carry, masked):
        dk_t, dv_t = carry
        q_off = pl.multiple_of(i * bq, bq)
        query_t = q_ref[0, 0, :, pl.ds(q_off, bq)]
        query_ts = (query_t.astype(jnp.float32) * scale).astype(jnp.bfloat16)
        dout_t = do_ref[0, :, pl.ds(q_off, bq)]
        out_t = o_ref[0, :, pl.ds(q_off, bq)]
        lse = lse_ref[0, :, pl.ds(q_off, bq)]
        delta = jnp.sum(
            dout_t.astype(jnp.float32) * out_t.astype(jnp.float32), axis=0, keepdims=True
        ) * scale
        s_t = jnp.dot(key, query_ts, preferred_element_type=jnp.float32)
        if masked:
            keys_at = k_start + lax.broadcasted_iota(jnp.int32, (bk, bq), 0)
            queries_at = q_off + lax.broadcasted_iota(jnp.int32, (bk, bq), 1)
            s_t = jnp.where(keys_at <= queries_at, s_t, MASKED)
        p_t = jnp.exp(s_t - lse)
        dv_t = dv_t + lax.dot_general(
            dout_t, p_t.astype(jnp.bfloat16), NT_DIMS, preferred_element_type=jnp.float32
        )
        dp_t = jnp.dot(value_s, dout_t, preferred_element_type=jnp.float32)
        ds_t = (p_t * (dp_t - delta)).astype(jnp.bfloat16)
        dk_t = dk_t + lax.dot_general(query_t, ds_t, NT_DIMS, preferred_element_type=jnp.float32)
        dq_acc[:, pl.ds(q_off, bq)] += jnp.dot(key_t, ds_t, preferred_element_type=jnp.float32)
        return dk_t, dv_t

    carry = (jnp.zeros((HD, bk), jnp.float32), jnp.zeros((HD, bk), jnp.float32))
    for r in range(bk // bq):
        carry = step(k_start // bq + r, carry, True)
    dk_t, dv_t = lax.fori_loop(
        (k_start + bk) // bq, seg_end // bq, lambda i, c: step(i, c, False), carry
    )
    out_ref[0, 0] = dq_acc[:, pl.ds(pl.multiple_of(k_start, bk), bk)].astype(out_ref.dtype)
    out_ref[0, 1] = dk_t.astype(out_ref.dtype)
    out_ref[0, 2] = dv_t.astype(out_ref.dtype)


def attn_backward(qkv_t, dout_t, out_t, lse, seg_pairs, bk=512, bq=512):
    pairs, _, head_size, seq_len = qkv_t.shape
    scale = head_size ** (-0.5)
    n_k = seq_len // bk
    blocks_done = pairs * (seq_len // bq) * (seq_len // bq + 1) // 2
    cost = pl.CostEstimate(
        flops=10 * blocks_done * bq * bq * head_size,
        transcendentals=blocks_done * bq * bq,
        bytes_accessed=pairs * seq_len * head_size * 2 * 8 + pairs * seq_len * 4,
    )
    grid_spec = pltpu.PrefetchScalarGridSpec(
        num_scalar_prefetch=1,
        grid=(pairs, n_k),
        in_specs=[
            pl.BlockSpec((1, 1, head_size, seq_len), lambda p, j, seg: (p, 0, 0, 0)),
            pl.BlockSpec((1, 1, head_size, bk), lambda p, j, seg: (p, 1, 0, j)),
            pl.BlockSpec((1, 1, head_size, bk), lambda p, j, seg: (p, 2, 0, j)),
            pl.BlockSpec((1, head_size, seq_len), lambda p, j, seg: (p, 0, 0)),
            pl.BlockSpec((1, head_size, seq_len), lambda p, j, seg: (p, 0, 0)),
            pl.BlockSpec((1, 1, seq_len), lambda p, j, seg: (p, 0, 0)),
        ],
        out_specs=pl.BlockSpec((1, 3, head_size, bk), lambda p, j, seg: (p, 0, 0, j)),
        scratch_shapes=[pltpu.VMEM((head_size, seq_len), jnp.float32)],
    )
    return pl.pallas_call(
        functools.partial(bwd_kernel, bk=bk, bq=bq, scale=scale),
        grid_spec=grid_spec,
        out_shape=jax.ShapeDtypeStruct((pairs, 3, head_size, seq_len), jnp.bfloat16),
        cost_estimate=cost,
        name="attn_bwd",
    )(seg_pairs, qkv_t, qkv_t, qkv_t, dout_t, out_t, lse)


def norm_rows(values, gain, shift):
    row_mean = jnp.mean(values, axis=-1, keepdims=True)
    centred = values - row_mean
    variance = jnp.mean(centred * centred, axis=-1, keepdims=True)
    inv_std = lax.rsqrt(variance + NORM_EPS)
    normed = centred * inv_std
    return (normed * gain + shift, normed, inv_std)


def norm_back(grad_in, normed, inv_std, gain):
    scaled = grad_in * gain
    centred = (
        scaled
        - jnp.mean(scaled, axis=-1, keepdims=True)
        - normed * jnp.mean(scaled * normed, axis=-1, keepdims=True)
    )
    return (centred * inv_std, jnp.sum(grad_in * normed, axis=0), jnp.sum(grad_in, axis=0))


def rotate(values, cosine, sine_tab):
    half_size = values.shape[-1] // 2
    front = values[..., :half_size]
    behind = values[..., half_size:]
    cos_part = cosine[..., None, :]
    sin_part = sine_tab[..., None, :]
    return jnp.concatenate(
        [front * cos_part - behind * sin_part, behind * cos_part + front * sin_part], axis=-1
    )


def unrotate(values, cosine, sine_tab):
    half_size = values.shape[-1] // 2
    front = values[..., :half_size]
    behind = values[..., half_size:]
    cos_part = cosine[..., None, :]
    sin_part = sine_tab[..., None, :]
    return jnp.concatenate(
        [front * cos_part + behind * sin_part, behind * cos_part - front * sin_part], axis=-1
    )


def local(
    block_input,
    history,
    cotangent,
    qkv_weight,
    proj_weight,
    up_weight,
    down_weight,
    norm1_gain,
    norm1_bias,
    norm2_gain,
    norm2_bias,
    dwa_weights,
    pair_order,
    long_group,
):
    n_seq = lax.axis_size("seq")
    row_count = block_input.shape[0]
    piece_len = SLOT // n_seq
    slot_count = row_count // piece_len
    pair_count = slot_count * HEADS
    per_dev = pair_count // n_seq
    slot_flags = long_group[0]
    seg_len = SLOT // jnp.left_shift(jnp.ones_like(slot_flags), slot_flags)
    position = jnp.arange(SLOT, dtype=jnp.int32)
    doc_place = (position[None, :] % seg_len[:, None]).astype(jnp.float32)
    frequency = jnp.power(10000.0, jnp.arange(HD // 2, dtype=jnp.float32) * (-2.0 / HD))
    angles = doc_place[..., None] * frequency
    my_index = lax.axis_index("seq")
    my_start = my_index * piece_len
    cosine = lax.dynamic_slice_in_dim(jnp.cos(angles), my_start, piece_len, 1)
    sine_tab = lax.dynamic_slice_in_dim(jnp.sin(angles), my_start, piece_len, 1)
    head_groups = HEADS // per_dev
    order_row = pair_order[0]
    held_pairs = lax.dynamic_slice_in_dim(order_row, my_index * per_dev, per_dev, 0)
    my_pairs = my_index * per_dev + jnp.arange(per_dev, dtype=jnp.int32)
    seg_pairs = jnp.take(seg_len, my_pairs // HEADS).astype(jnp.int32)
    n_batch = lax.axis_size("batch")
    batch_index = lax.axis_index("batch")

    def gather_rows(local):
        acc = local
        bits = n_batch.bit_length() - 1
        for bit in reversed(range(bits)):
            partner = [(i, i ^ (1 << bit)) for i in range(n_batch)]
            got = lax.ppermute(acc, "batch", partner)
            low = ((batch_index >> bit) & 1) == 0
            acc = jnp.where(low, jnp.stack([acc, got]), jnp.stack([got, acc]))
        return jnp.transpose(acc, list(range(bits))[::-1] + list(range(bits, acc.ndim))).reshape(
            (n_batch,) + local.shape
        )

    qkv_rows = gather_rows(qkv_weight).reshape(-1, qkv_weight.shape[1])
    w_qkv = lax.all_gather(qkv_rows, "seq", axis=1, tiled=True)
    inputs32 = block_input.astype(jnp.float32)
    norm1_out, normed1, inv_std1 = norm_rows(inputs32, norm1_gain, norm1_bias)
    norm1_low = norm1_out.astype(jnp.bfloat16)
    qkv_out = jnp.dot(norm1_low, w_qkv, preferred_element_type=jnp.float32)
    queries = rotate(qkv_out[:, :D].reshape(slot_count, piece_len, HEADS, HD), cosine, sine_tab)
    keys_rot = rotate(
        qkv_out[:, D : 2 * D].reshape(slot_count, piece_len, HEADS, HD), cosine, sine_tab
    )
    values_in = qkv_out[:, 2 * D :].reshape(slot_count, piece_len, HEADS, HD)
    stacked = jnp.stack([queries, keys_rot, values_in], axis=2).astype(jnp.bfloat16)
    send = jnp.transpose(
        stacked.reshape(slot_count, piece_len, 3, head_groups, per_dev, HD), (0, 3, 4, 2, 5, 1)
    ).reshape(n_seq, per_dev, 3, HD, piece_len)
    incoming = lax.all_to_all(send, "seq", split_axis=0, concat_axis=0, tiled=True)
    grad_out = cotangent.astype(jnp.float32)
    hist_sum = dwa_weights[0] * history[0].astype(jnp.float32)
    for layer_idx in range(1, HIST):
        hist_sum = hist_sum + dwa_weights[layer_idx] * history[layer_idx].astype(jnp.float32)
    history_grad = (dwa_weights[:HIST, None, None] * grad_out[None]).astype(jnp.bfloat16)
    hist_terms = [
        jnp.sum(history[layer_idx].astype(jnp.float32) * grad_out) for layer_idx in range(HIST)
    ]
    hist_sum, history_grad, hist_terms, incoming = lax.optimization_barrier(
        (hist_sum, history_grad, hist_terms, incoming)
    )
    later = (proj_weight, up_weight, down_weight)
    later_flat, _ = lax.optimization_barrier(
        (jnp.concatenate([w.reshape(-1) for w in later]), qkv_rows)
    )
    later_rows = gather_rows(later_flat)
    offset = 0
    later_full = []
    for w in later:
        rows = later_rows[:, offset : offset + w.size].reshape(-1, w.shape[1])
        later_full.append(lax.all_gather(rows, "seq", axis=1, tiled=True))
        offset += w.size
    w_proj, w_up, w_down = later_full
    qkv_t = jnp.transpose(incoming, (1, 2, 3, 0, 4)).reshape(per_dev, 3, HD, SLOT)
    attn_t, lse_rows = attn_forward(qkv_t, seg_pairs)
    back = jnp.transpose(attn_t.reshape(per_dev, HD, n_seq, piece_len), (2, 0, 1, 3))
    returned = lax.all_to_all(back, "seq", split_axis=0, concat_axis=0, tiled=True)
    lse_acc = lse_rows.reshape(per_dev, SLOT)
    seq_bits = n_seq.bit_length() - 1
    for bit in reversed(range(seq_bits)):
        partner = [(i, i ^ (1 << bit)) for i in range(n_seq)]
        got = lax.ppermute(lse_acc, "seq", partner)
        low = ((my_index >> bit) & 1) == 0
        lse_acc = jnp.where(low, jnp.stack([lse_acc, got]), jnp.stack([got, lse_acc]))
    lse_all = jnp.transpose(
        lse_acc, list(range(seq_bits))[::-1] + [seq_bits, seq_bits + 1]
    ).reshape(n_seq * per_dev, SLOT)
    attended = jnp.transpose(
        returned.reshape(slot_count, head_groups, per_dev, HD, piece_len), (0, 4, 1, 2, 3)
    ).reshape(row_count, D)
    middle = inputs32 + jnp.dot(attended, w_proj, preferred_element_type=jnp.float32)
    norm2_out, normed2, inv_std2 = norm_rows(middle, norm2_gain, norm2_bias)
    norm2_low = norm2_out.astype(jnp.bfloat16)
    hidden_up = jnp.dot(norm2_low, w_up, preferred_element_type=jnp.float32)
    gelu_out, gelu_pull = jax.vjp(lambda hidden: jax.nn.gelu(hidden, approximate=True), hidden_up)
    gelu_low = gelu_out.astype(jnp.bfloat16)
    block_out = middle + jnp.dot(gelu_low, w_down, preferred_element_type=jnp.float32)
    dwa_out = hist_sum + dwa_weights[HIST] * block_out
    block_output = dwa_out.astype(jnp.bfloat16)
    dwa_terms = hist_terms + [jnp.sum(block_out * grad_out)]
    dwa_local = jnp.stack(dwa_terms)
    dy_full = dwa_weights[HIST] * grad_out
    dmlp_low = dy_full.astype(jnp.bfloat16)
    down_local = jnp.einsum(
        "nf,nbd->bfd", gelu_low, dmlp_low.reshape(row_count, n_seq, -1),
        preferred_element_type=jnp.float32,
    )
    dgelu = jnp.einsum("nd,fd->nf", dmlp_low, w_down, preferred_element_type=jnp.float32)
    dup_low = gelu_pull(dgelu)[0].astype(jnp.bfloat16)
    up_local = jnp.einsum(
        "nd,nbf->bdf", norm2_low, dup_low.reshape(row_count, n_seq, -1),
        preferred_element_type=jnp.float32,
    )
    dnorm2 = jnp.einsum("nf,df->nd", dup_low, w_up, preferred_element_type=jnp.float32)
    dmid_norm, gain2_local, bias2_local = norm_back(dnorm2, normed2, inv_std2, norm2_gain)
    dmiddle = dy_full + dmid_norm
    dmiddle_low = dmiddle.astype(jnp.bfloat16)
    proj_local = jnp.einsum(
        "nd,nbe->bde", attended, dmiddle_low.reshape(row_count, n_seq, -1),
        preferred_element_type=jnp.float32,
    )
    dattended = jnp.einsum(
        "ne,de->nd", dmiddle_low, w_proj, preferred_element_type=jnp.float32
    ).astype(jnp.bfloat16)
    dsend = jnp.transpose(
        dattended.reshape(slot_count, piece_len, head_groups, per_dev, HD), (0, 2, 3, 4, 1)
    ).reshape(n_seq, per_dev, HD, piece_len)
    dattn_in = lax.all_to_all(dsend, "seq", split_axis=0, concat_axis=0, tiled=True)
    dout_t = jnp.transpose(dattn_in, (1, 2, 0, 3)).reshape(per_dev, HD, SLOT)
    dpairs = attn_backward(qkv_t, dout_t, attn_t, lse_rows, seg_pairs)
    dback = jnp.transpose(
        dpairs.reshape(per_dev, 3, HD, n_seq, piece_len), (3, 0, 1, 2, 4)
    )
    dreturned = lax.all_to_all(dback, "seq", split_axis=0, concat_axis=0, tiled=True)
    dtokens = jnp.transpose(
        dreturned.reshape(slot_count, head_groups, per_dev, 3, HD, piece_len), (0, 5, 3, 1, 2, 4)
    ).reshape(slot_count, piece_len, 3, HEADS, HD)
    dq_rows = unrotate(dtokens[:, :, 0].astype(jnp.float32), cosine, sine_tab).reshape(row_count, D)
    dk_rows = unrotate(dtokens[:, :, 1].astype(jnp.float32), cosine, sine_tab).reshape(row_count, D)
    dv_rows = dtokens[:, :, 2].astype(jnp.float32).reshape(row_count, D)
    dqkv_low = jnp.concatenate([dq_rows, dk_rows, dv_rows], axis=-1).astype(jnp.bfloat16)
    qkv_local = jnp.einsum(
        "nd,nbf->bdf", norm1_low, dqkv_low.reshape(row_count, n_seq, -1),
        preferred_element_type=jnp.float32,
    )
    dnorm1 = jnp.einsum("nf,df->nd", dqkv_low, w_qkv, preferred_element_type=jnp.float32)
    dinput_norm, gain1_local, bias1_local = norm_back(dnorm1, normed1, inv_std1, norm1_gain)
    input_grad = (dmiddle + dinput_norm).astype(jnp.bfloat16)

    def by_cols(blocks):
        bits = n_seq.bit_length() - 1
        acc = blocks.reshape((2,) * bits + blocks.shape[1:])
        for bit in range(bits):
            mine = (my_index >> bit) & 1
            keep = lax.dynamic_index_in_dim(acc, mine, axis=bits - 1 - bit, keepdims=False)
            send = lax.dynamic_index_in_dim(acc, 1 - mine, axis=bits - 1 - bit, keepdims=False)
            partner = [(i, i ^ (1 << bit)) for i in range(n_seq)]
            got = lax.ppermute(send.astype(jnp.bfloat16), "seq", partner)
            acc = keep + got.astype(jnp.float32)
        return acc.astype(jnp.bfloat16)

    def by_rows(col_sum):
        return lax.psum_scatter(col_sum, "batch", scatter_dimension=0, tiled=True).astype(
            jnp.float32
        )

    qkv_grad = by_rows(by_cols(qkv_local))
    proj_grad = by_rows(by_cols(proj_local))
    up_grad = by_rows(by_cols(up_local))
    down_grad = by_rows(by_cols(down_local))
    small_sums = jnp.concatenate([gain1_local, bias1_local, gain2_local, bias2_local, dwa_local])
    for axis in ("seq", "batch"):
        size = lax.axis_size(axis)
        hop = 1
        while hop < size:
            partner = [(i, i ^ hop) for i in range(size)]
            small_sums = small_sums + lax.ppermute(small_sums, axis, partner)
            hop *= 2
    gain1_grad, bias1_grad, gain2_grad, bias2_grad = (
        small_sums[k * D : (k + 1) * D] for k in range(4)
    )
    dwa_grad = small_sums[4 * D :]
    row_lse = jnp.take(lse_all, held_pairs, axis=0).reshape(1, per_dev, SLOT)
    return (
        block_output,
        input_grad,
        history_grad,
        row_lse,
        qkv_grad,
        proj_grad,
        up_grad,
        down_grad,
        gain1_grad,
        bias1_grad,
        gain2_grad,
        bias2_grad,
        dwa_grad,
    )


def solution(mesh):
    placed = (
        P(("batch", "seq"), None),
        P(None, ("batch", "seq"), None),
        P(("batch", "seq"), None),
        P("batch", "seq"),
        P("batch", "seq"),
        P("batch", "seq"),
        P("batch", "seq"),
        P(),
        P(),
        P(),
        P(),
        P(),
        P("batch", None),
        P("batch", None),
    )

    return jax.shard_map(
        local,
        mesh=mesh,
        in_specs=placed,
        out_specs=(
            P(("batch", "seq"), None),
            P(("batch", "seq"), None),
            P(None, ("batch", "seq"), None),
            P("batch", "seq", None),
            P("batch", "seq"),
            P("batch", "seq"),
            P("batch", "seq"),
            P("batch", "seq"),
            P(),
            P(),
            P(),
            P(),
            P(),
        ),
        check_vma=False,
    )
```

```python
import jax
import jax.numpy as jnp
from jax import lax
from jax.sharding import PartitionSpec as P
from jax.experimental import pallas as pl
from jax.experimental.pallas import tpu as pltpu
import functools

D = 768
HEADS = 12
HD = 64
SLOT = 2048
HIST = 8


NORM_EPS = 1e-05
MASKED = -1e30
NT_DIMS = (((1,), (1,)), ((), ()))


def fwd_kernel(seg_ref, q_ref, k_ref, v_ref, o_ref, lse_ref, *, bq, bk, scale):
    pair = pl.program_id(0)
    qi = pl.program_id(1)
    seg_len = seg_ref[pair]
    q_start = qi * bq
    seg_start = (q_start // seg_len) * seg_len
    query = (q_ref[0, 0].astype(jnp.float32).T * scale).astype(jnp.bfloat16)

    def step(j, carry, masked):
        m_old, l_old, acc = carry
        k_off = pl.multiple_of(j * bk, bk)
        key_t = k_ref[0, 0, :, pl.ds(k_off, bk)]
        value_t = v_ref[0, 0, :, pl.ds(k_off, bk)]
        s = jnp.dot(query, key_t, preferred_element_type=jnp.float32)
        if masked:
            rows = q_start + lax.broadcasted_iota(jnp.int32, (bq, bk), 0)
            cols = k_off + lax.broadcasted_iota(jnp.int32, (bq, bk), 1)
            s = jnp.where(cols <= rows, s, MASKED)
        m_new = jnp.maximum(m_old, jnp.max(s, axis=-1, keepdims=True))
        alpha = jnp.exp(m_old - m_new)
        weights = jnp.exp(s - m_new)
        l_new = alpha * l_old + jnp.sum(weights, axis=-1, keepdims=True)
        acc = alpha * acc + lax.dot_general(
            weights.astype(jnp.bfloat16), value_t, NT_DIMS, preferred_element_type=jnp.float32
        )
        return m_new, l_new, acc

    carry = (
        jnp.full((bq, 1), MASKED, jnp.float32),
        jnp.zeros((bq, 1), jnp.float32),
        jnp.zeros((bq, HD), jnp.float32),
    )
    j_diag = q_start // bk
    carry = lax.fori_loop(seg_start // bk, j_diag, lambda j, c: step(j, c, False), carry)
    for r in range(bq // bk):
        carry = step(j_diag + r, carry, True)
    m_fin, l_fin, acc = carry
    o_ref[0] = (acc / l_fin).T.astype(o_ref.dtype)
    lse = m_fin + jnp.log(l_fin)
    lse_ref[0] = jnp.transpose(jnp.broadcast_to(lse, (bq, 128)))[0:1, :]


def attn_forward(qkv_t, seg_pairs, bq=512, bk=512):
    pairs, _, head_size, seq_len = qkv_t.shape
    scale = head_size ** (-0.5)
    n_q = seq_len // bq
    blocks_done = pairs * (seq_len // bk) * (seq_len // bk + 1) // 2
    cost = pl.CostEstimate(
        flops=4 * blocks_done * bk * bk * head_size,
        transcendentals=blocks_done * bk * bk,
        bytes_accessed=pairs * seq_len * head_size * 2 * 4 + pairs * seq_len * 4,
    )
    grid_spec = pltpu.PrefetchScalarGridSpec(
        num_scalar_prefetch=1,
        grid=(pairs, n_q),
        in_specs=[
            pl.BlockSpec((1, 1, head_size, bq), lambda p, i, seg: (p, 0, 0, i)),
            pl.BlockSpec((1, 1, head_size, seq_len), lambda p, i, seg: (p, 1, 0, 0)),
            pl.BlockSpec((1, 1, head_size, seq_len), lambda p, i, seg: (p, 2, 0, 0)),
        ],
        out_specs=[
            pl.BlockSpec((1, head_size, bq), lambda p, i, seg: (p, 0, i)),
            pl.BlockSpec((1, 1, bq), lambda p, i, seg: (p, 0, i)),
        ],
    )
    return pl.pallas_call(
        functools.partial(fwd_kernel, bq=bq, bk=bk, scale=scale),
        grid_spec=grid_spec,
        out_shape=[
            jax.ShapeDtypeStruct((pairs, head_size, seq_len), jnp.bfloat16),
            jax.ShapeDtypeStruct((pairs, 1, seq_len), jnp.float32),
        ],
        cost_estimate=cost,
        name="attn_fwd",
    )(seg_pairs, qkv_t, qkv_t, qkv_t)


def bwd_kernel(seg_ref, q_ref, k_ref, v_ref, do_ref, o_ref, lse_ref, out_ref, dq_acc, *, bk, bq, scale):
    pair = pl.program_id(0)
    kj = pl.program_id(1)

    @pl.when(kj == 0)
    def _():
        dq_acc[...] = jnp.zeros_like(dq_acc)

    seg_len = seg_ref[pair]
    k_start = kj * bk
    seg_end = (k_start // seg_len + 1) * seg_len
    key_t = k_ref[0, 0]
    key = key_t.astype(jnp.float32).T.astype(jnp.bfloat16)
    value_s = (v_ref[0, 0].astype(jnp.float32).T * scale).astype(jnp.bfloat16)

    def step(i, carry, masked):
        dk_t, dv_t = carry
        q_off = pl.multiple_of(i * bq, bq)
        query_t = q_ref[0, 0, :, pl.ds(q_off, bq)]
        query_ts = (query_t.astype(jnp.float32) * scale).astype(jnp.bfloat16)
        dout_t = do_ref[0, :, pl.ds(q_off, bq)]
        out_t = o_ref[0, :, pl.ds(q_off, bq)]
        lse = lse_ref[0, :, pl.ds(q_off, bq)]
        delta = jnp.sum(
            dout_t.astype(jnp.float32) * out_t.astype(jnp.float32), axis=0, keepdims=True
        ) * scale
        s_t = jnp.dot(key, query_ts, preferred_element_type=jnp.float32)
        if masked:
            keys_at = k_start + lax.broadcasted_iota(jnp.int32, (bk, bq), 0)
            queries_at = q_off + lax.broadcasted_iota(jnp.int32, (bk, bq), 1)
            s_t = jnp.where(keys_at <= queries_at, s_t, MASKED)
        p_t = jnp.exp(s_t - lse)
        dv_t = dv_t + lax.dot_general(
            dout_t, p_t.astype(jnp.bfloat16), NT_DIMS, preferred_element_type=jnp.float32
        )
        dp_t = jnp.dot(value_s, dout_t, preferred_element_type=jnp.float32)
        ds_t = (p_t * (dp_t - delta)).astype(jnp.bfloat16)
        dk_t = dk_t + lax.dot_general(query_t, ds_t, NT_DIMS, preferred_element_type=jnp.float32)
        dq_acc[:, pl.ds(q_off, bq)] += jnp.dot(key_t, ds_t, preferred_element_type=jnp.float32)
        return dk_t, dv_t

    carry = (jnp.zeros((HD, bk), jnp.float32), jnp.zeros((HD, bk), jnp.float32))
    for r in range(bk // bq):
        carry = step(k_start // bq + r, carry, True)
    dk_t, dv_t = lax.fori_loop(
        (k_start + bk) // bq, seg_end // bq, lambda i, c: step(i, c, False), carry
    )
    out_ref[0, 0] = dq_acc[:, pl.ds(pl.multiple_of(k_start, bk), bk)].astype(out_ref.dtype)
    out_ref[0, 1] = dk_t.astype(out_ref.dtype)
    out_ref[0, 2] = dv_t.astype(out_ref.dtype)


def attn_backward(qkv_t, dout_t, out_t, lse, seg_pairs, bk=512, bq=512):
    pairs, _, head_size, seq_len = qkv_t.shape
    scale = head_size ** (-0.5)
    n_k = seq_len // bk
    blocks_done = pairs * (seq_len // bq) * (seq_len // bq + 1) // 2
    cost = pl.CostEstimate(
        flops=10 * blocks_done * bq * bq * head_size,
        transcendentals=blocks_done * bq * bq,
        bytes_accessed=pairs * seq_len * head_size * 2 * 8 + pairs * seq_len * 4,
    )
    grid_spec = pltpu.PrefetchScalarGridSpec(
        num_scalar_prefetch=1,
        grid=(pairs, n_k),
        in_specs=[
            pl.BlockSpec((1, 1, head_size, seq_len), lambda p, j, seg: (p, 0, 0, 0)),
            pl.BlockSpec((1, 1, head_size, bk), lambda p, j, seg: (p, 1, 0, j)),
            pl.BlockSpec((1, 1, head_size, bk), lambda p, j, seg: (p, 2, 0, j)),
            pl.BlockSpec((1, head_size, seq_len), lambda p, j, seg: (p, 0, 0)),
            pl.BlockSpec((1, head_size, seq_len), lambda p, j, seg: (p, 0, 0)),
            pl.BlockSpec((1, 1, seq_len), lambda p, j, seg: (p, 0, 0)),
        ],
        out_specs=pl.BlockSpec((1, 3, head_size, bk), lambda p, j, seg: (p, 0, 0, j)),
        scratch_shapes=[pltpu.VMEM((head_size, seq_len), jnp.float32)],
    )
    return pl.pallas_call(
        functools.partial(bwd_kernel, bk=bk, bq=bq, scale=scale),
        grid_spec=grid_spec,
        out_shape=jax.ShapeDtypeStruct((pairs, 3, head_size, seq_len), jnp.bfloat16),
        cost_estimate=cost,
        name="attn_bwd",
    )(seg_pairs, qkv_t, qkv_t, qkv_t, dout_t, out_t, lse)


def norm_rows(values, gain, shift):
    row_mean = jnp.mean(values, axis=-1, keepdims=True)
    centred = values - row_mean
    variance = jnp.mean(centred * centred, axis=-1, keepdims=True)
    inv_std = lax.rsqrt(variance + NORM_EPS)
    normed = centred * inv_std
    return (normed * gain + shift, normed, inv_std)


def norm_back(grad_in, normed, inv_std, gain):
    scaled = grad_in * gain
    centred = (
        scaled
        - jnp.mean(scaled, axis=-1, keepdims=True)
        - normed * jnp.mean(scaled * normed, axis=-1, keepdims=True)
    )
    return (centred * inv_std, jnp.sum(grad_in * normed, axis=0), jnp.sum(grad_in, axis=0))


def rotate(values, cosine, sine_tab):
    half_size = values.shape[-1] // 2
    front = values[..., :half_size]
    behind = values[..., half_size:]
    cos_part = cosine[..., None, :]
    sin_part = sine_tab[..., None, :]
    return jnp.concatenate(
        [front * cos_part - behind * sin_part, behind * cos_part + front * sin_part], axis=-1
    )


def unrotate(values, cosine, sine_tab):
    half_size = values.shape[-1] // 2
    front = values[..., :half_size]
    behind = values[..., half_size:]
    cos_part = cosine[..., None, :]
    sin_part = sine_tab[..., None, :]
    return jnp.concatenate(
        [front * cos_part + behind * sin_part, behind * cos_part - front * sin_part], axis=-1
    )


def local(
    block_input,
    history,
    cotangent,
    qkv_weight,
    proj_weight,
    up_weight,
    down_weight,
    norm1_gain,
    norm1_bias,
    norm2_gain,
    norm2_bias,
    dwa_weights,
    pair_order,
    long_group,
):
    n_seq = lax.axis_size("seq")
    row_count = block_input.shape[0]
    piece_len = SLOT // n_seq
    slot_count = row_count // piece_len
    pair_count = slot_count * HEADS
    per_dev = pair_count // n_seq
    slot_flags = long_group[0]
    seg_len = SLOT // jnp.left_shift(jnp.ones_like(slot_flags), slot_flags)
    position = jnp.arange(SLOT, dtype=jnp.int32)
    doc_place = (position[None, :] % seg_len[:, None]).astype(jnp.float32)
    frequency = jnp.power(10000.0, jnp.arange(HD // 2, dtype=jnp.float32) * (-2.0 / HD))
    angles = doc_place[..., None] * frequency
    my_index = lax.axis_index("seq")
    my_start = my_index * piece_len
    cosine = lax.dynamic_slice_in_dim(jnp.cos(angles), my_start, piece_len, 1)
    sine_tab = lax.dynamic_slice_in_dim(jnp.sin(angles), my_start, piece_len, 1)
    head_groups = HEADS // per_dev
    order_row = pair_order[0]
    held_pairs = lax.dynamic_slice_in_dim(order_row, my_index * per_dev, per_dev, 0)
    my_pairs = my_index * per_dev + jnp.arange(per_dev, dtype=jnp.int32)
    seg_pairs = jnp.take(seg_len, my_pairs // HEADS).astype(jnp.int32)
    n_batch = lax.axis_size("batch")
    batch_index = lax.axis_index("batch")

    def gather_rows(local):
        acc = local
        bits = n_batch.bit_length() - 1
        for bit in reversed(range(bits)):
            partner = [(i, i ^ (1 << bit)) for i in range(n_batch)]
            got = lax.ppermute(acc, "batch", partner)
            low = ((batch_index >> bit) & 1) == 0
            acc = jnp.where(low, jnp.stack([acc, got]), jnp.stack([got, acc]))
        return jnp.transpose(acc, list(range(bits))[::-1] + list(range(bits, acc.ndim))).reshape(
            (n_batch,) + local.shape
        )

    qkv_rows = gather_rows(qkv_weight).reshape(-1, qkv_weight.shape[1])
    w_qkv = lax.all_gather(qkv_rows, "seq", axis=1, tiled=True)
    inputs32 = block_input.astype(jnp.float32)
    norm1_out, normed1, inv_std1 = norm_rows(inputs32, norm1_gain, norm1_bias)
    norm1_low = norm1_out.astype(jnp.bfloat16)
    qkv_out = jnp.dot(norm1_low, w_qkv, preferred_element_type=jnp.float32)
    queries = rotate(qkv_out[:, :D].reshape(slot_count, piece_len, HEADS, HD), cosine, sine_tab)
    keys_rot = rotate(
        qkv_out[:, D : 2 * D].reshape(slot_count, piece_len, HEADS, HD), cosine, sine_tab
    )
    values_in = qkv_out[:, 2 * D :].reshape(slot_count, piece_len, HEADS, HD)
    stacked = jnp.stack([queries, keys_rot, values_in], axis=2).astype(jnp.bfloat16)
    send = jnp.transpose(
        stacked.reshape(slot_count, piece_len, 3, head_groups, per_dev, HD), (0, 3, 4, 2, 5, 1)
    ).reshape(n_seq, per_dev, 3, HD, piece_len)
    incoming = lax.all_to_all(send, "seq", split_axis=0, concat_axis=0, tiled=True)
    grad_out = cotangent.astype(jnp.float32)
    hist_sum = dwa_weights[0] * history[0].astype(jnp.float32)
    for layer_idx in range(1, HIST):
        hist_sum = hist_sum + dwa_weights[layer_idx] * history[layer_idx].astype(jnp.float32)
    history_grad = (dwa_weights[:HIST, None, None] * grad_out[None]).astype(jnp.bfloat16)
    hist_terms = [
        jnp.sum(history[layer_idx].astype(jnp.float32) * grad_out) for layer_idx in range(HIST)
    ]
    hist_sum, history_grad, hist_terms, incoming = lax.optimization_barrier(
        (hist_sum, history_grad, hist_terms, incoming)
    )
    later = (proj_weight, up_weight, down_weight)
    later_flat, _ = lax.optimization_barrier(
        (jnp.concatenate([w.reshape(-1) for w in later]), qkv_rows)
    )
    later_rows = gather_rows(later_flat)
    offset = 0
    later_full = []
    for w in later:
        rows = later_rows[:, offset : offset + w.size].reshape(-1, w.shape[1])
        later_full.append(lax.all_gather(rows, "seq", axis=1, tiled=True))
        offset += w.size
    w_proj, w_up, w_down = later_full
    qkv_t = jnp.transpose(incoming, (1, 2, 3, 0, 4)).reshape(per_dev, 3, HD, SLOT)
    attn_t, lse_rows = attn_forward(qkv_t, seg_pairs)
    back = jnp.transpose(attn_t.reshape(per_dev, HD, n_seq, piece_len), (2, 0, 1, 3))
    returned = lax.all_to_all(back, "seq", split_axis=0, concat_axis=0, tiled=True)
    lse_all = lax.all_gather(lse_rows.reshape(per_dev, SLOT), "seq", axis=0, tiled=True)
    lse_all, returned = lax.optimization_barrier((lse_all, returned))
    attended = jnp.transpose(
        returned.reshape(slot_count, head_groups, per_dev, HD, piece_len), (0, 4, 1, 2, 3)
    ).reshape(row_count, D)
    middle = inputs32 + jnp.dot(attended, w_proj, preferred_element_type=jnp.float32)
    norm2_out, normed2, inv_std2 = norm_rows(middle, norm2_gain, norm2_bias)
    norm2_low = norm2_out.astype(jnp.bfloat16)
    hidden_up = jnp.dot(norm2_low, w_up, preferred_element_type=jnp.float32)
    gelu_out, gelu_pull = jax.vjp(lambda hidden: jax.nn.gelu(hidden, approximate=True), hidden_up)
    gelu_low = gelu_out.astype(jnp.bfloat16)
    block_out = middle + jnp.dot(gelu_low, w_down, preferred_element_type=jnp.float32)
    dwa_out = hist_sum + dwa_weights[HIST] * block_out
    block_output = dwa_out.astype(jnp.bfloat16)
    dwa_terms = hist_terms + [jnp.sum(block_out * grad_out)]
    dwa_local = jnp.stack(dwa_terms)
    dy_full = dwa_weights[HIST] * grad_out
    dmlp_low = dy_full.astype(jnp.bfloat16)
    down_local = jnp.einsum(
        "nf,nbd->bfd", gelu_low, dmlp_low.reshape(row_count, n_seq, -1),
        preferred_element_type=jnp.float32,
    )
    dgelu = jnp.einsum("nd,fd->nf", dmlp_low, w_down, preferred_element_type=jnp.float32)
    dup_low = gelu_pull(dgelu)[0].astype(jnp.bfloat16)
    up_local = jnp.einsum(
        "nd,nbf->bdf", norm2_low, dup_low.reshape(row_count, n_seq, -1),
        preferred_element_type=jnp.float32,
    )
    dnorm2 = jnp.einsum("nf,df->nd", dup_low, w_up, preferred_element_type=jnp.float32)
    dmid_norm, gain2_local, bias2_local = norm_back(dnorm2, normed2, inv_std2, norm2_gain)
    dmiddle = dy_full + dmid_norm
    dmiddle_low = dmiddle.astype(jnp.bfloat16)
    proj_local = jnp.einsum(
        "nd,nbe->bde", attended, dmiddle_low.reshape(row_count, n_seq, -1),
        preferred_element_type=jnp.float32,
    )
    dattended = jnp.einsum(
        "ne,de->nd", dmiddle_low, w_proj, preferred_element_type=jnp.float32
    ).astype(jnp.bfloat16)
    dsend = jnp.transpose(
        dattended.reshape(slot_count, piece_len, head_groups, per_dev, HD), (0, 2, 3, 4, 1)
    ).reshape(n_seq, per_dev, HD, piece_len)

    def by_cols(blocks):
        bits = n_seq.bit_length() - 1
        acc = blocks.reshape((2,) * bits + blocks.shape[1:])
        for bit in range(bits):
            mine = (my_index >> bit) & 1
            keep = lax.dynamic_index_in_dim(acc, mine, axis=bits - 1 - bit, keepdims=False)
            send = lax.dynamic_index_in_dim(acc, 1 - mine, axis=bits - 1 - bit, keepdims=False)
            partner = [(i, i ^ (1 << bit)) for i in range(n_seq)]
            got = lax.ppermute(send.astype(jnp.bfloat16), "seq", partner)
            acc = keep + got.astype(jnp.float32)
        return acc.astype(jnp.bfloat16)

    def by_rows(col_sum):
        return lax.psum_scatter(col_sum, "batch", scatter_dimension=0, tiled=True).astype(
            jnp.float32
        )

    down_cols = by_cols(down_local)
    up_cols = by_cols(up_local)
    dattn_in = lax.all_to_all(dsend, "seq", split_axis=0, concat_axis=0, tiled=True)
    down_cols, up_cols, dattn_in = lax.optimization_barrier((down_cols, up_cols, dattn_in))
    dout_t = jnp.transpose(dattn_in, (1, 2, 0, 3)).reshape(per_dev, HD, SLOT)
    dpairs = attn_backward(qkv_t, dout_t, attn_t, lse_rows, seg_pairs)
    dback = jnp.transpose(
        dpairs.reshape(per_dev, 3, HD, n_seq, piece_len), (3, 0, 1, 2, 4)
    )
    dreturned = lax.all_to_all(dback, "seq", split_axis=0, concat_axis=0, tiled=True)
    dtokens = jnp.transpose(
        dreturned.reshape(slot_count, head_groups, per_dev, 3, HD, piece_len), (0, 5, 3, 1, 2, 4)
    ).reshape(slot_count, piece_len, 3, HEADS, HD)
    dq_rows = unrotate(dtokens[:, :, 0].astype(jnp.float32), cosine, sine_tab).reshape(row_count, D)
    dk_rows = unrotate(dtokens[:, :, 1].astype(jnp.float32), cosine, sine_tab).reshape(row_count, D)
    dv_rows = dtokens[:, :, 2].astype(jnp.float32).reshape(row_count, D)
    dqkv_low = jnp.concatenate([dq_rows, dk_rows, dv_rows], axis=-1).astype(jnp.bfloat16)
    qkv_local = jnp.einsum(
        "nd,nbf->bdf", norm1_low, dqkv_low.reshape(row_count, n_seq, -1),
        preferred_element_type=jnp.float32,
    )
    dnorm1 = jnp.einsum("nf,df->nd", dqkv_low, w_qkv, preferred_element_type=jnp.float32)
    dinput_norm, gain1_local, bias1_local = norm_back(dnorm1, normed1, inv_std1, norm1_gain)
    input_grad = (dmiddle + dinput_norm).astype(jnp.bfloat16)
    qkv_grad = by_rows(by_cols(qkv_local))
    proj_grad = by_rows(by_cols(proj_local))
    up_grad = by_rows(up_cols)
    down_grad = by_rows(down_cols)
    small_sums = jnp.concatenate([gain1_local, bias1_local, gain2_local, bias2_local, dwa_local])
    for axis in ("seq", "batch"):
        size = lax.axis_size(axis)
        hop = 1
        while hop < size:
            partner = [(i, i ^ hop) for i in range(size)]
            small_sums = small_sums + lax.ppermute(small_sums, axis, partner)
            hop *= 2
    gain1_grad, bias1_grad, gain2_grad, bias2_grad = (
        small_sums[k * D : (k + 1) * D] for k in range(4)
    )
    dwa_grad = small_sums[4 * D :]
    row_lse = jnp.take(lse_all, held_pairs, axis=0).reshape(1, per_dev, SLOT)
    return (
        block_output,
        input_grad,
        history_grad,
        row_lse,
        qkv_grad,
        proj_grad,
        up_grad,
        down_grad,
        gain1_grad,
        bias1_grad,
        gain2_grad,
        bias2_grad,
        dwa_grad,
    )


def solution(mesh):
    placed = (
        P(("batch", "seq"), None),
        P(None, ("batch", "seq"), None),
        P(("batch", "seq"), None),
        P("batch", "seq"),
        P("batch", "seq"),
        P("batch", "seq"),
        P("batch", "seq"),
        P(),
        P(),
        P(),
        P(),
        P(),
        P("batch", None),
        P("batch", None),
    )

    return jax.shard_map(
        local,
        mesh=mesh,
        in_specs=placed,
        out_specs=(
            P(("batch", "seq"), None),
            P(("batch", "seq"), None),
            P(None, ("batch", "seq"), None),
            P("batch", "seq", None),
            P("batch", "seq"),
            P("batch", "seq"),
            P("batch", "seq"),
            P("batch", "seq"),
            P(),
            P(),
            P(),
            P(),
            P(),
        ),
        check_vma=False,
    )
```

```python
import jax
import jax.numpy as jnp
from jax import lax
from jax.sharding import PartitionSpec as P
from jax.experimental import pallas as pl
from jax.experimental.pallas import tpu as pltpu
import functools

D = 768
HEADS = 12
HD = 64
SLOT = 2048
HIST = 8


NORM_EPS = 1e-05
MASKED = -1e30


def fwd_kernel(seg_ref, q_ref, k_ref, v_ref, o_ref, lse_ref, *, bq, bk, scale):
    pair = pl.program_id(0)
    qi = pl.program_id(1)
    seg_len = seg_ref[pair]
    q_start = qi * bq
    seg_start = (q_start // seg_len) * seg_len
    query_t = (q_ref[0, 0].astype(jnp.float32) * scale).astype(jnp.bfloat16)

    def step(j, carry, masked):
        m_old, l_old, acc = carry
        k_off = pl.multiple_of(j * bk, bk)
        key = k_ref[0, 0, :, pl.ds(k_off, bk)].astype(jnp.float32).T.astype(jnp.bfloat16)
        value_t = v_ref[0, 0, :, pl.ds(k_off, bk)]
        s_t = jnp.dot(key, query_t, preferred_element_type=jnp.float32)
        if masked:
            keys_at = k_off + lax.broadcasted_iota(jnp.int32, (bk, bq), 0)
            queries_at = q_start + lax.broadcasted_iota(jnp.int32, (bk, bq), 1)
            s_t = jnp.where(keys_at <= queries_at, s_t, MASKED)
        m_new = jnp.maximum(m_old, jnp.max(s_t, axis=0, keepdims=True))
        alpha = jnp.exp(m_old - m_new)
        weights = jnp.exp(s_t - m_new)
        l_new = alpha * l_old + jnp.sum(weights, axis=0, keepdims=True)
        acc = alpha * acc + jnp.dot(
            value_t, weights.astype(jnp.bfloat16), preferred_element_type=jnp.float32
        )
        return m_new, l_new, acc

    carry = (
        jnp.full((1, bq), MASKED, jnp.float32),
        jnp.zeros((1, bq), jnp.float32),
        jnp.zeros((HD, bq), jnp.float32),
    )
    j_diag = q_start // bk
    carry = lax.fori_loop(seg_start // bk, j_diag, lambda j, c: step(j, c, False), carry)
    for r in range(bq // bk):
        carry = step(j_diag + r, carry, True)
    m_fin, l_fin, acc = carry
    o_ref[0] = (acc / l_fin).astype(o_ref.dtype)
    lse_ref[0] = m_fin + jnp.log(l_fin)


def attn_forward(qkv_t, seg_pairs, bq=512, bk=512):
    pairs, _, head_size, seq_len = qkv_t.shape
    scale = head_size ** (-0.5)
    n_q = seq_len // bq
    blocks_done = pairs * (seq_len // bk) * (seq_len // bk + 1) // 2
    cost = pl.CostEstimate(
        flops=4 * blocks_done * bk * bk * head_size,
        transcendentals=blocks_done * bk * bk,
        bytes_accessed=pairs * seq_len * head_size * 2 * 4 + pairs * seq_len * 4,
    )
    grid_spec = pltpu.PrefetchScalarGridSpec(
        num_scalar_prefetch=1,
        grid=(pairs, n_q),
        in_specs=[
            pl.BlockSpec((1, 1, head_size, bq), lambda p, i, seg: (p, 0, 0, i)),
            pl.BlockSpec((1, 1, head_size, seq_len), lambda p, i, seg: (p, 1, 0, 0)),
            pl.BlockSpec((1, 1, head_size, seq_len), lambda p, i, seg: (p, 2, 0, 0)),
        ],
        out_specs=[
            pl.BlockSpec((1, head_size, bq), lambda p, i, seg: (p, 0, i)),
            pl.BlockSpec((1, 1, bq), lambda p, i, seg: (p, 0, i)),
        ],
    )
    return pl.pallas_call(
        functools.partial(fwd_kernel, bq=bq, bk=bk, scale=scale),
        grid_spec=grid_spec,
        out_shape=[
            jax.ShapeDtypeStruct((pairs, head_size, seq_len), jnp.bfloat16),
            jax.ShapeDtypeStruct((pairs, 1, seq_len), jnp.float32),
        ],
        cost_estimate=cost,
        name="attn_fwd",
    )(seg_pairs, qkv_t, qkv_t, qkv_t)


def bwd_kernel(seg_ref, q_ref, k_ref, v_ref, do_ref, o_ref, lse_ref, out_ref, dq_acc, *, bk, bq, scale):
    pair = pl.program_id(0)
    kj = pl.program_id(1)

    @pl.when(kj == 0)
    def _():
        dq_acc[...] = jnp.zeros_like(dq_acc)

    seg_len = seg_ref[pair]
    k_start = kj * bk
    seg_end = (k_start // seg_len + 1) * seg_len
    key_t = k_ref[0, 0]
    key = key_t.astype(jnp.float32).T.astype(jnp.bfloat16)
    value_s = (v_ref[0, 0].astype(jnp.float32).T * scale).astype(jnp.bfloat16)

    def step(i, carry, masked):
        dk_t, dv_t = carry
        q_off = pl.multiple_of(i * bq, bq)
        query_t = q_ref[0, 0, :, pl.ds(q_off, bq)]
        query_ts = (query_t.astype(jnp.float32) * scale).astype(jnp.bfloat16)
        dout_t = do_ref[0, :, pl.ds(q_off, bq)]
        out_t = o_ref[0, :, pl.ds(q_off, bq)]
        lse = lse_ref[0, :, pl.ds(q_off, bq)]
        delta = jnp.sum(
            dout_t.astype(jnp.float32) * out_t.astype(jnp.float32), axis=0, keepdims=True
        ) * scale
        s_t = jnp.dot(key, query_ts, preferred_element_type=jnp.float32)
        if masked:
            keys_at = k_start + lax.broadcasted_iota(jnp.int32, (bk, bq), 0)
            queries_at = q_off + lax.broadcasted_iota(jnp.int32, (bk, bq), 1)
            s_t = jnp.where(keys_at <= queries_at, s_t, MASKED)
        p_t = jnp.exp(s_t - lse)
        dout = dout_t.astype(jnp.float32).T.astype(jnp.bfloat16)
        query = query_t.astype(jnp.float32).T.astype(jnp.bfloat16)
        dv_t = dv_t + jnp.dot(p_t.astype(jnp.bfloat16), dout, preferred_element_type=jnp.float32)
        dp_t = jnp.dot(value_s, dout_t, preferred_element_type=jnp.float32)
        ds_t = (p_t * (dp_t - delta)).astype(jnp.bfloat16)
        dk_t = dk_t + jnp.dot(ds_t, query, preferred_element_type=jnp.float32)
        dq_acc[:, pl.ds(q_off, bq)] += jnp.dot(key_t, ds_t, preferred_element_type=jnp.float32)
        return dk_t, dv_t

    carry = (jnp.zeros((bk, HD), jnp.float32), jnp.zeros((bk, HD), jnp.float32))
    for r in range(bk // bq):
        carry = step(k_start // bq + r, carry, True)
    dk_t, dv_t = lax.fori_loop(
        (k_start + bk) // bq, seg_end // bq, lambda i, c: step(i, c, False), carry
    )
    out_ref[0, 0] = dq_acc[:, pl.ds(pl.multiple_of(k_start, bk), bk)].astype(out_ref.dtype)
    out_ref[0, 1] = dk_t.T.astype(out_ref.dtype)
    out_ref[0, 2] = dv_t.T.astype(out_ref.dtype)


def attn_backward(qkv_t, dout_t, out_t, lse, seg_pairs, bk=512, bq=512):
    pairs, _, head_size, seq_len = qkv_t.shape
    scale = head_size ** (-0.5)
    n_k = seq_len // bk
    blocks_done = pairs * (seq_len // bq) * (seq_len // bq + 1) // 2
    cost = pl.CostEstimate(
        flops=10 * blocks_done * bq * bq * head_size,
        transcendentals=blocks_done * bq * bq,
        bytes_accessed=pairs * seq_len * head_size * 2 * 8 + pairs * seq_len * 4,
    )
    grid_spec = pltpu.PrefetchScalarGridSpec(
        num_scalar_prefetch=1,
        grid=(pairs, n_k),
        in_specs=[
            pl.BlockSpec((1, 1, head_size, seq_len), lambda p, j, seg: (p, 0, 0, 0)),
            pl.BlockSpec((1, 1, head_size, bk), lambda p, j, seg: (p, 1, 0, j)),
            pl.BlockSpec((1, 1, head_size, bk), lambda p, j, seg: (p, 2, 0, j)),
            pl.BlockSpec((1, head_size, seq_len), lambda p, j, seg: (p, 0, 0)),
            pl.BlockSpec((1, head_size, seq_len), lambda p, j, seg: (p, 0, 0)),
            pl.BlockSpec((1, 1, seq_len), lambda p, j, seg: (p, 0, 0)),
        ],
        out_specs=pl.BlockSpec((1, 3, head_size, bk), lambda p, j, seg: (p, 0, 0, j)),
        scratch_shapes=[pltpu.VMEM((head_size, seq_len), jnp.float32)],
    )
    return pl.pallas_call(
        functools.partial(bwd_kernel, bk=bk, bq=bq, scale=scale),
        grid_spec=grid_spec,
        out_shape=jax.ShapeDtypeStruct((pairs, 3, head_size, seq_len), jnp.bfloat16),
        cost_estimate=cost,
        name="attn_bwd",
    )(seg_pairs, qkv_t, qkv_t, qkv_t, dout_t, out_t, lse)


def norm_rows(values, gain, shift):
    row_mean = jnp.mean(values, axis=-1, keepdims=True)
    centred = values - row_mean
    variance = jnp.mean(centred * centred, axis=-1, keepdims=True)
    inv_std = lax.rsqrt(variance + NORM_EPS)
    normed = centred * inv_std
    return (normed * gain + shift, normed, inv_std)


def norm_back(grad_in, normed, inv_std, gain):
    scaled = grad_in * gain
    centred = (
        scaled
        - jnp.mean(scaled, axis=-1, keepdims=True)
        - normed * jnp.mean(scaled * normed, axis=-1, keepdims=True)
    )
    return (centred * inv_std, jnp.sum(grad_in * normed, axis=0), jnp.sum(grad_in, axis=0))


def rotate(values, cosine, sine_tab):
    half_size = values.shape[-1] // 2
    front = values[..., :half_size]
    behind = values[..., half_size:]
    cos_part = cosine[..., None, :]
    sin_part = sine_tab[..., None, :]
    return jnp.concatenate(
        [front * cos_part - behind * sin_part, behind * cos_part + front * sin_part], axis=-1
    )


def unrotate(values, cosine, sine_tab):
    half_size = values.shape[-1] // 2
    front = values[..., :half_size]
    behind = values[..., half_size:]
    cos_part = cosine[..., None, :]
    sin_part = sine_tab[..., None, :]
    return jnp.concatenate(
        [front * cos_part + behind * sin_part, behind * cos_part - front * sin_part], axis=-1
    )


def local(
    block_input,
    history,
    cotangent,
    qkv_weight,
    proj_weight,
    up_weight,
    down_weight,
    norm1_gain,
    norm1_bias,
    norm2_gain,
    norm2_bias,
    dwa_weights,
    pair_order,
    long_group,
):
    n_seq = lax.axis_size("seq")
    row_count = block_input.shape[0]
    piece_len = SLOT // n_seq
    slot_count = row_count // piece_len
    pair_count = slot_count * HEADS
    per_dev = pair_count // n_seq
    slot_flags = long_group[0]
    seg_len = SLOT // jnp.left_shift(jnp.ones_like(slot_flags), slot_flags)
    position = jnp.arange(SLOT, dtype=jnp.int32)
    doc_place = (position[None, :] % seg_len[:, None]).astype(jnp.float32)
    frequency = jnp.power(10000.0, jnp.arange(HD // 2, dtype=jnp.float32) * (-2.0 / HD))
    angles = doc_place[..., None] * frequency
    my_index = lax.axis_index("seq")
    my_start = my_index * piece_len
    cosine = lax.dynamic_slice_in_dim(jnp.cos(angles), my_start, piece_len, 1)
    sine_tab = lax.dynamic_slice_in_dim(jnp.sin(angles), my_start, piece_len, 1)
    head_groups = HEADS // per_dev
    order_row = pair_order[0]
    held_pairs = lax.dynamic_slice_in_dim(order_row, my_index * per_dev, per_dev, 0)
    my_pairs = my_index * per_dev + jnp.arange(per_dev, dtype=jnp.int32)
    seg_pairs = jnp.take(seg_len, my_pairs // HEADS).astype(jnp.int32)
    n_batch = lax.axis_size("batch")
    batch_index = lax.axis_index("batch")

    def gather_rows(local):
        acc = local
        bits = n_batch.bit_length() - 1
        for bit in reversed(range(bits)):
            partner = [(i, i ^ (1 << bit)) for i in range(n_batch)]
            got = lax.ppermute(acc, "batch", partner)
            low = ((batch_index >> bit) & 1) == 0
            acc = jnp.where(low, jnp.stack([acc, got]), jnp.stack([got, acc]))
        return jnp.transpose(acc, list(range(bits))[::-1] + list(range(bits, acc.ndim))).reshape(
            (n_batch,) + local.shape
        )

    qkv_rows = gather_rows(qkv_weight).reshape(-1, qkv_weight.shape[1])
    w_qkv = lax.all_gather(qkv_rows, "seq", axis=1, tiled=True)
    inputs32 = block_input.astype(jnp.float32)
    norm1_out, normed1, inv_std1 = norm_rows(inputs32, norm1_gain, norm1_bias)
    norm1_low = norm1_out.astype(jnp.bfloat16)
    qkv_out = jnp.dot(norm1_low, w_qkv, preferred_element_type=jnp.float32)
    queries = rotate(qkv_out[:, :D].reshape(slot_count, piece_len, HEADS, HD), cosine, sine_tab)
    keys_rot = rotate(
        qkv_out[:, D : 2 * D].reshape(slot_count, piece_len, HEADS, HD), cosine, sine_tab
    )
    values_in = qkv_out[:, 2 * D :].reshape(slot_count, piece_len, HEADS, HD)
    stacked = jnp.stack([queries, keys_rot, values_in], axis=2).astype(jnp.bfloat16)
    send = jnp.transpose(
        stacked.reshape(slot_count, piece_len, 3, head_groups, per_dev, HD), (0, 3, 4, 2, 5, 1)
    ).reshape(n_seq, per_dev, 3, HD, piece_len)
    incoming = lax.all_to_all(send, "seq", split_axis=0, concat_axis=0, tiled=True)
    grad_out = cotangent.astype(jnp.float32)
    hist_sum = dwa_weights[0] * history[0].astype(jnp.float32)
    for layer_idx in range(1, HIST):
        hist_sum = hist_sum + dwa_weights[layer_idx] * history[layer_idx].astype(jnp.float32)
    history_grad = (dwa_weights[:HIST, None, None] * grad_out[None]).astype(jnp.bfloat16)
    hist_terms = [
        jnp.sum(history[layer_idx].astype(jnp.float32) * grad_out) for layer_idx in range(HIST)
    ]
    hist_sum, history_grad, hist_terms, incoming = lax.optimization_barrier(
        (hist_sum, history_grad, hist_terms, incoming)
    )
    later = (proj_weight, up_weight, down_weight)
    later_flat, _ = lax.optimization_barrier(
        (jnp.concatenate([w.reshape(-1) for w in later]), qkv_rows)
    )
    later_rows = gather_rows(later_flat)
    offset = 0
    later_full = []
    for w in later:
        rows = later_rows[:, offset : offset + w.size].reshape(-1, w.shape[1])
        later_full.append(lax.all_gather(rows, "seq", axis=1, tiled=True))
        offset += w.size
    w_proj, w_up, w_down = later_full
    qkv_t = jnp.transpose(incoming, (1, 2, 3, 0, 4)).reshape(per_dev, 3, HD, SLOT)
    attn_t, lse_rows = attn_forward(qkv_t, seg_pairs)
    back = jnp.transpose(attn_t.reshape(per_dev, HD, n_seq, piece_len), (2, 0, 1, 3))
    returned = lax.all_to_all(back, "seq", split_axis=0, concat_axis=0, tiled=True)
    lse_all = lax.all_gather(lse_rows.reshape(per_dev, SLOT), "seq", axis=0, tiled=True)
    lse_all, returned = lax.optimization_barrier((lse_all, returned))
    attended = jnp.transpose(
        returned.reshape(slot_count, head_groups, per_dev, HD, piece_len), (0, 4, 1, 2, 3)
    ).reshape(row_count, D)
    middle = inputs32 + jnp.dot(attended, w_proj, preferred_element_type=jnp.float32)
    norm2_out, normed2, inv_std2 = norm_rows(middle, norm2_gain, norm2_bias)
    norm2_low = norm2_out.astype(jnp.bfloat16)
    hidden_up = jnp.dot(norm2_low, w_up, preferred_element_type=jnp.float32)
    gelu_out, gelu_pull = jax.vjp(lambda hidden: jax.nn.gelu(hidden, approximate=True), hidden_up)
    gelu_low = gelu_out.astype(jnp.bfloat16)
    block_out = middle + jnp.dot(gelu_low, w_down, preferred_element_type=jnp.float32)
    dwa_out = hist_sum + dwa_weights[HIST] * block_out
    block_output = dwa_out.astype(jnp.bfloat16)
    dwa_terms = hist_terms + [jnp.sum(block_out * grad_out)]
    dwa_local = jnp.stack(dwa_terms)
    dy_full = dwa_weights[HIST] * grad_out
    dmlp_low = dy_full.astype(jnp.bfloat16)
    down_local = jnp.einsum(
        "nf,nbd->bfd", gelu_low, dmlp_low.reshape(row_count, n_seq, -1),
        preferred_element_type=jnp.float32,
    )
    dgelu = jnp.einsum("nd,fd->nf", dmlp_low, w_down, preferred_element_type=jnp.float32)
    dup_low = gelu_pull(dgelu)[0].astype(jnp.bfloat16)
    up_local = jnp.einsum(
        "nd,nbf->bdf", norm2_low, dup_low.reshape(row_count, n_seq, -1),
        preferred_element_type=jnp.float32,
    )
    dnorm2 = jnp.einsum("nf,df->nd", dup_low, w_up, preferred_element_type=jnp.float32)
    dmid_norm, gain2_local, bias2_local = norm_back(dnorm2, normed2, inv_std2, norm2_gain)
    dmiddle = dy_full + dmid_norm
    dmiddle_low = dmiddle.astype(jnp.bfloat16)
    proj_local = jnp.einsum(
        "nd,nbe->bde", attended, dmiddle_low.reshape(row_count, n_seq, -1),
        preferred_element_type=jnp.float32,
    )
    dattended = jnp.einsum(
        "ne,de->nd", dmiddle_low, w_proj, preferred_element_type=jnp.float32
    ).astype(jnp.bfloat16)
    dsend = jnp.transpose(
        dattended.reshape(slot_count, piece_len, head_groups, per_dev, HD), (0, 2, 3, 4, 1)
    ).reshape(n_seq, per_dev, HD, piece_len)
    dattn_in = lax.all_to_all(dsend, "seq", split_axis=0, concat_axis=0, tiled=True)
    dout_t = jnp.transpose(dattn_in, (1, 2, 0, 3)).reshape(per_dev, HD, SLOT)
    dpairs = attn_backward(qkv_t, dout_t, attn_t, lse_rows, seg_pairs)
    dback = jnp.transpose(
        dpairs.reshape(per_dev, 3, HD, n_seq, piece_len), (3, 0, 1, 2, 4)
    )
    dreturned = lax.all_to_all(dback, "seq", split_axis=0, concat_axis=0, tiled=True)
    dtokens = jnp.transpose(
        dreturned.reshape(slot_count, head_groups, per_dev, 3, HD, piece_len), (0, 5, 3, 1, 2, 4)
    ).reshape(slot_count, piece_len, 3, HEADS, HD)
    dq_rows = unrotate(dtokens[:, :, 0].astype(jnp.float32), cosine, sine_tab).reshape(row_count, D)
    dk_rows = unrotate(dtokens[:, :, 1].astype(jnp.float32), cosine, sine_tab).reshape(row_count, D)
    dv_rows = dtokens[:, :, 2].astype(jnp.float32).reshape(row_count, D)
    dqkv_low = jnp.concatenate([dq_rows, dk_rows, dv_rows], axis=-1).astype(jnp.bfloat16)
    qkv_local = jnp.einsum(
        "nd,nbf->bdf", norm1_low, dqkv_low.reshape(row_count, n_seq, -1),
        preferred_element_type=jnp.float32,
    )
    dnorm1 = jnp.einsum("nf,df->nd", dqkv_low, w_qkv, preferred_element_type=jnp.float32)
    dinput_norm, gain1_local, bias1_local = norm_back(dnorm1, normed1, inv_std1, norm1_gain)
    input_grad = (dmiddle + dinput_norm).astype(jnp.bfloat16)

    def by_cols(blocks):
        bits = n_seq.bit_length() - 1
        acc = blocks.reshape((2,) * bits + blocks.shape[1:])
        for bit in range(bits):
            mine = (my_index >> bit) & 1
            keep = lax.dynamic_index_in_dim(acc, mine, axis=bits - 1 - bit, keepdims=False)
            send = lax.dynamic_index_in_dim(acc, 1 - mine, axis=bits - 1 - bit, keepdims=False)
            partner = [(i, i ^ (1 << bit)) for i in range(n_seq)]
            got = lax.ppermute(send.astype(jnp.bfloat16), "seq", partner)
            acc = keep + got.astype(jnp.float32)
        return acc.astype(jnp.bfloat16)

    def by_rows(col_sum):
        return lax.psum_scatter(col_sum, "batch", scatter_dimension=0, tiled=True).astype(
            jnp.float32
        )

    qkv_grad = by_rows(by_cols(qkv_local))
    proj_grad = by_rows(by_cols(proj_local))
    up_grad = by_rows(by_cols(up_local))
    down_grad = by_rows(by_cols(down_local))
    small_sums = jnp.concatenate([gain1_local, bias1_local, gain2_local, bias2_local, dwa_local])
    for axis in ("seq", "batch"):
        size = lax.axis_size(axis)
        hop = 1
        while hop < size:
            partner = [(i, i ^ hop) for i in range(size)]
            small_sums = small_sums + lax.ppermute(small_sums, axis, partner)
            hop *= 2
    gain1_grad, bias1_grad, gain2_grad, bias2_grad = (
        small_sums[k * D : (k + 1) * D] for k in range(4)
    )
    dwa_grad = small_sums[4 * D :]
    row_lse = jnp.take(lse_all, held_pairs, axis=0).reshape(1, per_dev, SLOT)
    return (
        block_output,
        input_grad,
        history_grad,
        row_lse,
        qkv_grad,
        proj_grad,
        up_grad,
        down_grad,
        gain1_grad,
        bias1_grad,
        gain2_grad,
        bias2_grad,
        dwa_grad,
    )


def solution(mesh):
    placed = (
        P(("batch", "seq"), None),
        P(None, ("batch", "seq"), None),
        P(("batch", "seq"), None),
        P("batch", "seq"),
        P("batch", "seq"),
        P("batch", "seq"),
        P("batch", "seq"),
        P(),
        P(),
        P(),
        P(),
        P(),
        P("batch", None),
        P("batch", None),
    )

    return jax.shard_map(
        local,
        mesh=mesh,
        in_specs=placed,
        out_specs=(
            P(("batch", "seq"), None),
            P(("batch", "seq"), None),
            P(None, ("batch", "seq"), None),
            P("batch", "seq", None),
            P("batch", "seq"),
            P("batch", "seq"),
            P("batch", "seq"),
            P("batch", "seq"),
            P(),
            P(),
            P(),
            P(),
            P(),
        ),
        check_vma=False,
    )
```

```python
import jax
import jax.numpy as jnp
from jax import lax
from jax.sharding import PartitionSpec as P
from jax.experimental import pallas as pl
from jax.experimental.pallas import tpu as pltpu
import functools

D = 768
HEADS = 12
HD = 64
SLOT = 2048
HIST = 8


NORM_EPS = 1e-05
MASKED = -1e30
NT_DIMS = (((1,), (1,)), ((), ()))


def fwd_kernel(seg_ref, q_ref, k_ref, v_ref, o_ref, lse_ref, *, bq, bk, scale):
    pair = pl.program_id(0)
    qi = pl.program_id(1)
    seg_len = seg_ref[pair]
    q_start = qi * bq
    seg_start = (q_start // seg_len) * seg_len
    query = (q_ref[0, 0].astype(jnp.float32).T * scale).astype(jnp.bfloat16)

    def step(j, carry, masked):
        m_old, l_old, acc = carry
        k_off = pl.multiple_of(j * bk, bk)
        key_t = k_ref[0, 0, :, pl.ds(k_off, bk)]
        value_t = v_ref[0, 0, :, pl.ds(k_off, bk)]
        s = jnp.dot(query, key_t, preferred_element_type=jnp.float32)
        if masked:
            rows = q_start + lax.broadcasted_iota(jnp.int32, (bq, bk), 0)
            cols = k_off + lax.broadcasted_iota(jnp.int32, (bq, bk), 1)
            s = jnp.where(cols <= rows, s, MASKED)
        m_new = jnp.maximum(m_old, jnp.max(s, axis=-1, keepdims=True))
        alpha = jnp.exp(m_old - m_new)
        weights = jnp.exp(s - m_new)
        l_new = alpha * l_old + jnp.sum(weights, axis=-1, keepdims=True)
        acc = alpha * acc + lax.dot_general(
            weights.astype(jnp.bfloat16), value_t, NT_DIMS, preferred_element_type=jnp.float32
        )
        return m_new, l_new, acc

    carry = (
        jnp.full((bq, 1), MASKED, jnp.float32),
        jnp.zeros((bq, 1), jnp.float32),
        jnp.zeros((bq, HD), jnp.float32),
    )
    j_diag = q_start // bk
    carry = lax.fori_loop(seg_start // bk, j_diag, lambda j, c: step(j, c, False), carry)
    for r in range(bq // bk):
        carry = step(j_diag + r, carry, True)
    m_fin, l_fin, acc = carry
    o_ref[0] = (acc / l_fin).T.astype(o_ref.dtype)
    lse = m_fin + jnp.log(l_fin)
    lse_ref[0] = jnp.transpose(jnp.broadcast_to(lse, (bq, 128)))[0:1, :]


def attn_forward(qkv_t, seg_pairs, bq=512, bk=512):
    pairs, _, head_size, seq_len = qkv_t.shape
    scale = head_size ** (-0.5)
    n_q = seq_len // bq
    blocks_done = pairs * (seq_len // bk) * (seq_len // bk + 1) // 2
    cost = pl.CostEstimate(
        flops=4 * blocks_done * bk * bk * head_size,
        transcendentals=blocks_done * bk * bk,
        bytes_accessed=pairs * seq_len * head_size * 2 * 4 + pairs * seq_len * 4,
    )
    grid_spec = pltpu.PrefetchScalarGridSpec(
        num_scalar_prefetch=1,
        grid=(pairs, n_q),
        in_specs=[
            pl.BlockSpec((1, 1, head_size, bq), lambda p, i, seg: (p, 0, 0, i)),
            pl.BlockSpec((1, 1, head_size, seq_len), lambda p, i, seg: (p, 1, 0, 0)),
            pl.BlockSpec((1, 1, head_size, seq_len), lambda p, i, seg: (p, 2, 0, 0)),
        ],
        out_specs=[
            pl.BlockSpec((1, head_size, bq), lambda p, i, seg: (p, 0, i)),
            pl.BlockSpec((1, 1, bq), lambda p, i, seg: (p, 0, i)),
        ],
    )
    return pl.pallas_call(
        functools.partial(fwd_kernel, bq=bq, bk=bk, scale=scale),
        grid_spec=grid_spec,
        out_shape=[
            jax.ShapeDtypeStruct((pairs, head_size, seq_len), jnp.bfloat16),
            jax.ShapeDtypeStruct((pairs, 1, seq_len), jnp.float32),
        ],
        cost_estimate=cost,
        name="attn_fwd",
    )(seg_pairs, qkv_t, qkv_t, qkv_t)


def bwd_kernel(seg_ref, q_ref, k_ref, v_ref, do_ref, o_ref, lse_ref, out_ref, dq_acc, *, bk, bq, scale):
    pair = pl.program_id(0)
    kj = pl.program_id(1)

    @pl.when(kj == 0)
    def _():
        dq_acc[...] = jnp.zeros_like(dq_acc)

    seg_len = seg_ref[pair]
    k_start = kj * bk
    seg_end = (k_start // seg_len + 1) * seg_len
    key_t = k_ref[0, 0]
    key = key_t.astype(jnp.float32).T.astype(jnp.bfloat16)
    value_s = (v_ref[0, 0].astype(jnp.float32).T * scale).astype(jnp.bfloat16)

    def step(i, carry, masked):
        dk_t, dv_t = carry
        q_off = pl.multiple_of(i * bq, bq)
        query_t = q_ref[0, 0, :, pl.ds(q_off, bq)]
        query_ts = (query_t.astype(jnp.float32) * scale).astype(jnp.bfloat16)
        dout_t = do_ref[0, :, pl.ds(q_off, bq)]
        out_t = o_ref[0, :, pl.ds(q_off, bq)]
        lse = lse_ref[0, :, pl.ds(q_off, bq)]
        delta = jnp.sum(
            dout_t.astype(jnp.float32) * out_t.astype(jnp.float32), axis=0, keepdims=True
        ) * scale
        s_t = jnp.dot(key, query_ts, preferred_element_type=jnp.float32)
        if masked:
            keys_at = k_start + lax.broadcasted_iota(jnp.int32, (bk, bq), 0)
            queries_at = q_off + lax.broadcasted_iota(jnp.int32, (bk, bq), 1)
            s_t = jnp.where(keys_at <= queries_at, s_t, MASKED)
        p_t = jnp.exp(s_t - lse)
        dv_t = dv_t + lax.dot_general(
            dout_t, p_t.astype(jnp.bfloat16), NT_DIMS, preferred_element_type=jnp.float32
        )
        dp_t = jnp.dot(value_s, dout_t, preferred_element_type=jnp.float32)
        ds_t = (p_t * (dp_t - delta)).astype(jnp.bfloat16)
        dk_t = dk_t + lax.dot_general(query_t, ds_t, NT_DIMS, preferred_element_type=jnp.float32)
        dq_acc[:, pl.ds(q_off, bq)] += jnp.dot(key_t, ds_t, preferred_element_type=jnp.float32)
        return dk_t, dv_t

    carry = (jnp.zeros((HD, bk), jnp.float32), jnp.zeros((HD, bk), jnp.float32))
    for r in range(bk // bq):
        carry = step(k_start // bq + r, carry, True)
    dk_t, dv_t = lax.fori_loop(
        (k_start + bk) // bq, seg_end // bq, lambda i, c: step(i, c, False), carry
    )
    out_ref[0, 0] = dq_acc[:, pl.ds(pl.multiple_of(k_start, bk), bk)].astype(out_ref.dtype)
    out_ref[0, 1] = dk_t.astype(out_ref.dtype)
    out_ref[0, 2] = dv_t.astype(out_ref.dtype)


def attn_backward(qkv_t, dout_t, out_t, lse, seg_pairs, bk=512, bq=512):
    pairs, _, head_size, seq_len = qkv_t.shape
    scale = head_size ** (-0.5)
    n_k = seq_len // bk
    blocks_done = pairs * (seq_len // bq) * (seq_len // bq + 1) // 2
    cost = pl.CostEstimate(
        flops=10 * blocks_done * bq * bq * head_size,
        transcendentals=blocks_done * bq * bq,
        bytes_accessed=pairs * seq_len * head_size * 2 * 8 + pairs * seq_len * 4,
    )
    grid_spec = pltpu.PrefetchScalarGridSpec(
        num_scalar_prefetch=1,
        grid=(pairs, n_k),
        in_specs=[
            pl.BlockSpec((1, 1, head_size, seq_len), lambda p, j, seg: (p, 0, 0, 0)),
            pl.BlockSpec((1, 1, head_size, bk), lambda p, j, seg: (p, 1, 0, j)),
            pl.BlockSpec((1, 1, head_size, bk), lambda p, j, seg: (p, 2, 0, j)),
            pl.BlockSpec((1, head_size, seq_len), lambda p, j, seg: (p, 0, 0)),
            pl.BlockSpec((1, head_size, seq_len), lambda p, j, seg: (p, 0, 0)),
            pl.BlockSpec((1, 1, seq_len), lambda p, j, seg: (p, 0, 0)),
        ],
        out_specs=pl.BlockSpec((1, 3, head_size, bk), lambda p, j, seg: (p, 0, 0, j)),
        scratch_shapes=[pltpu.VMEM((head_size, seq_len), jnp.float32)],
    )
    return pl.pallas_call(
        functools.partial(bwd_kernel, bk=bk, bq=bq, scale=scale),
        grid_spec=grid_spec,
        out_shape=jax.ShapeDtypeStruct((pairs, 3, head_size, seq_len), jnp.bfloat16),
        cost_estimate=cost,
        name="attn_bwd",
    )(seg_pairs, qkv_t, qkv_t, qkv_t, dout_t, out_t, lse)


def norm_rows(values, gain, shift):
    row_mean = jnp.mean(values, axis=-1, keepdims=True)
    centred = values - row_mean
    variance = jnp.mean(centred * centred, axis=-1, keepdims=True)
    inv_std = lax.rsqrt(variance + NORM_EPS)
    normed = centred * inv_std
    return (normed * gain + shift, normed, inv_std)


def norm_back(grad_in, normed, inv_std, gain):
    scaled = grad_in * gain
    centred = (
        scaled
        - jnp.mean(scaled, axis=-1, keepdims=True)
        - normed * jnp.mean(scaled * normed, axis=-1, keepdims=True)
    )
    return (centred * inv_std, jnp.sum(grad_in * normed, axis=0), jnp.sum(grad_in, axis=0))


def rotate(values, cosine, sine_tab):
    half_size = values.shape[-1] // 2
    front = values[..., :half_size]
    behind = values[..., half_size:]
    cos_part = cosine[..., None, :]
    sin_part = sine_tab[..., None, :]
    return jnp.concatenate(
        [front * cos_part - behind * sin_part, behind * cos_part + front * sin_part], axis=-1
    )


def unrotate(values, cosine, sine_tab):
    half_size = values.shape[-1] // 2
    front = values[..., :half_size]
    behind = values[..., half_size:]
    cos_part = cosine[..., None, :]
    sin_part = sine_tab[..., None, :]
    return jnp.concatenate(
        [front * cos_part + behind * sin_part, behind * cos_part - front * sin_part], axis=-1
    )


def local(
    block_input,
    history,
    cotangent,
    qkv_weight,
    proj_weight,
    up_weight,
    down_weight,
    norm1_gain,
    norm1_bias,
    norm2_gain,
    norm2_bias,
    dwa_weights,
    pair_order,
    long_group,
):
    n_seq = lax.axis_size("seq")
    row_count = block_input.shape[0]
    piece_len = SLOT // n_seq
    slot_count = row_count // piece_len
    pair_count = slot_count * HEADS
    per_dev = pair_count // n_seq
    slot_flags = long_group[0]
    seg_len = SLOT // jnp.left_shift(jnp.ones_like(slot_flags), slot_flags)
    position = jnp.arange(SLOT, dtype=jnp.int32)
    doc_place = (position[None, :] % seg_len[:, None]).astype(jnp.float32)
    frequency = jnp.power(10000.0, jnp.arange(HD // 2, dtype=jnp.float32) * (-2.0 / HD))
    angles = doc_place[..., None] * frequency
    my_index = lax.axis_index("seq")
    my_start = my_index * piece_len
    cosine = lax.dynamic_slice_in_dim(jnp.cos(angles), my_start, piece_len, 1)
    sine_tab = lax.dynamic_slice_in_dim(jnp.sin(angles), my_start, piece_len, 1)
    head_groups = HEADS // per_dev
    order_row = pair_order[0]
    held_pairs = lax.dynamic_slice_in_dim(order_row, my_index * per_dev, per_dev, 0)
    my_pairs = my_index * per_dev + jnp.arange(per_dev, dtype=jnp.int32)
    seg_pairs = jnp.take(seg_len, my_pairs // HEADS).astype(jnp.int32)
    n_batch = lax.axis_size("batch")
    batch_index = lax.axis_index("batch")

    def gather_rows(local):
        acc = local
        bits = n_batch.bit_length() - 1
        for bit in reversed(range(bits)):
            partner = [(i, i ^ (1 << bit)) for i in range(n_batch)]
            got = lax.ppermute(acc, "batch", partner)
            low = ((batch_index >> bit) & 1) == 0
            acc = jnp.where(low, jnp.stack([acc, got]), jnp.stack([got, acc]))
        return jnp.transpose(acc, list(range(bits))[::-1] + list(range(bits, acc.ndim))).reshape(
            (n_batch,) + local.shape
        )

    qkv_rows = lax.all_gather(qkv_weight, "seq", axis=1, tiled=True)
    w_qkv = gather_rows(qkv_rows).reshape(-1, qkv_rows.shape[1])
    inputs32 = block_input.astype(jnp.float32)
    norm1_out, normed1, inv_std1 = norm_rows(inputs32, norm1_gain, norm1_bias)
    norm1_low = norm1_out.astype(jnp.bfloat16)
    qkv_out = jnp.dot(norm1_low, w_qkv, preferred_element_type=jnp.float32)
    queries = rotate(qkv_out[:, :D].reshape(slot_count, piece_len, HEADS, HD), cosine, sine_tab)
    keys_rot = rotate(
        qkv_out[:, D : 2 * D].reshape(slot_count, piece_len, HEADS, HD), cosine, sine_tab
    )
    values_in = qkv_out[:, 2 * D :].reshape(slot_count, piece_len, HEADS, HD)
    stacked = jnp.stack([queries, keys_rot, values_in], axis=2).astype(jnp.bfloat16)
    send = jnp.transpose(
        stacked.reshape(slot_count, piece_len, 3, head_groups, per_dev, HD), (0, 3, 4, 2, 5, 1)
    ).reshape(n_seq, per_dev, 3, HD, piece_len)
    incoming = lax.all_to_all(send, "seq", split_axis=0, concat_axis=0, tiled=True)
    grad_out = cotangent.astype(jnp.float32)
    hist_sum = dwa_weights[0] * history[0].astype(jnp.float32)
    for layer_idx in range(1, HIST):
        hist_sum = hist_sum + dwa_weights[layer_idx] * history[layer_idx].astype(jnp.float32)
    history_grad = (dwa_weights[:HIST, None, None] * grad_out[None]).astype(jnp.bfloat16)
    hist_terms = [
        jnp.sum(history[layer_idx].astype(jnp.float32) * grad_out) for layer_idx in range(HIST)
    ]
    hist_sum, history_grad, hist_terms, incoming = lax.optimization_barrier(
        (hist_sum, history_grad, hist_terms, incoming)
    )
    later = (proj_weight, up_weight, down_weight)
    later_flat, _ = lax.optimization_barrier(
        (jnp.concatenate([w.reshape(-1) for w in later]), qkv_rows)
    )
    later_rows = gather_rows(later_flat)
    offset = 0
    later_full = []
    for w in later:
        rows = later_rows[:, offset : offset + w.size].reshape(-1, w.shape[1])
        later_full.append(lax.all_gather(rows, "seq", axis=1, tiled=True))
        offset += w.size
    w_proj, w_up, w_down = later_full
    qkv_t = jnp.transpose(incoming, (1, 2, 3, 0, 4)).reshape(per_dev, 3, HD, SLOT)
    attn_t, lse_rows = attn_forward(qkv_t, seg_pairs)
    back = jnp.transpose(attn_t.reshape(per_dev, HD, n_seq, piece_len), (2, 0, 1, 3))
    returned = lax.all_to_all(back, "seq", split_axis=0, concat_axis=0, tiled=True)
    lse_all = lax.all_gather(lse_rows.reshape(per_dev, SLOT), "seq", axis=0, tiled=True)
    lse_all, returned = lax.optimization_barrier((lse_all, returned))
    attended = jnp.transpose(
        returned.reshape(slot_count, head_groups, per_dev, HD, piece_len), (0, 4, 1, 2, 3)
    ).reshape(row_count, D)
    middle = inputs32 + jnp.dot(attended, w_proj, preferred_element_type=jnp.float32)
    norm2_out, normed2, inv_std2 = norm_rows(middle, norm2_gain, norm2_bias)
    norm2_low = norm2_out.astype(jnp.bfloat16)
    hidden_up = jnp.dot(norm2_low, w_up, preferred_element_type=jnp.float32)
    gelu_out, gelu_pull = jax.vjp(lambda hidden: jax.nn.gelu(hidden, approximate=True), hidden_up)
    gelu_low = gelu_out.astype(jnp.bfloat16)
    block_out = middle + jnp.dot(gelu_low, w_down, preferred_element_type=jnp.float32)
    dwa_out = hist_sum + dwa_weights[HIST] * block_out
    block_output = dwa_out.astype(jnp.bfloat16)
    dwa_terms = hist_terms + [jnp.sum(block_out * grad_out)]
    dwa_local = jnp.stack(dwa_terms)
    dy_full = dwa_weights[HIST] * grad_out
    dmlp_low = dy_full.astype(jnp.bfloat16)
    down_local = jnp.einsum(
        "nf,nbd->bfd", gelu_low, dmlp_low.reshape(row_count, n_seq, -1),
        preferred_element_type=jnp.float32,
    )
    dgelu = jnp.einsum("nd,fd->nf", dmlp_low, w_down, preferred_element_type=jnp.float32)
    dup_low = gelu_pull(dgelu)[0].astype(jnp.bfloat16)
    up_local = jnp.einsum(
        "nd,nbf->bdf", norm2_low, dup_low.reshape(row_count, n_seq, -1),
        preferred_element_type=jnp.float32,
    )
    dnorm2 = jnp.einsum("nf,df->nd", dup_low, w_up, preferred_element_type=jnp.float32)
    dmid_norm, gain2_local, bias2_local = norm_back(dnorm2, normed2, inv_std2, norm2_gain)
    dmiddle = dy_full + dmid_norm
    dmiddle_low = dmiddle.astype(jnp.bfloat16)
    proj_local = jnp.einsum(
        "nd,nbe->bde", attended, dmiddle_low.reshape(row_count, n_seq, -1),
        preferred_element_type=jnp.float32,
    )
    dattended = jnp.einsum(
        "ne,de->nd", dmiddle_low, w_proj, preferred_element_type=jnp.float32
    ).astype(jnp.bfloat16)
    dsend = jnp.transpose(
        dattended.reshape(slot_count, piece_len, head_groups, per_dev, HD), (0, 2, 3, 4, 1)
    ).reshape(n_seq, per_dev, HD, piece_len)
    dattn_in = lax.all_to_all(dsend, "seq", split_axis=0, concat_axis=0, tiled=True)
    dout_t = jnp.transpose(dattn_in, (1, 2, 0, 3)).reshape(per_dev, HD, SLOT)
    dpairs = attn_backward(qkv_t, dout_t, attn_t, lse_rows, seg_pairs)
    dback = jnp.transpose(
        dpairs.reshape(per_dev, 3, HD, n_seq, piece_len), (3, 0, 1, 2, 4)
    )
    dreturned = lax.all_to_all(dback, "seq", split_axis=0, concat_axis=0, tiled=True)
    dtokens = jnp.transpose(
        dreturned.reshape(slot_count, head_groups, per_dev, 3, HD, piece_len), (0, 5, 3, 1, 2, 4)
    ).reshape(slot_count, piece_len, 3, HEADS, HD)
    dq_rows = unrotate(dtokens[:, :, 0].astype(jnp.float32), cosine, sine_tab).reshape(row_count, D)
    dk_rows = unrotate(dtokens[:, :, 1].astype(jnp.float32), cosine, sine_tab).reshape(row_count, D)
    dv_rows = dtokens[:, :, 2].astype(jnp.float32).reshape(row_count, D)
    dqkv_low = jnp.concatenate([dq_rows, dk_rows, dv_rows], axis=-1).astype(jnp.bfloat16)
    qkv_local = jnp.einsum(
        "nd,nbf->bdf", norm1_low, dqkv_low.reshape(row_count, n_seq, -1),
        preferred_element_type=jnp.float32,
    )
    dnorm1 = jnp.einsum("nf,df->nd", dqkv_low, w_qkv, preferred_element_type=jnp.float32)
    dinput_norm, gain1_local, bias1_local = norm_back(dnorm1, normed1, inv_std1, norm1_gain)
    input_grad = (dmiddle + dinput_norm).astype(jnp.bfloat16)

    def by_cols(blocks):
        bits = n_seq.bit_length() - 1
        acc = blocks.reshape((2,) * bits + blocks.shape[1:])
        for bit in range(bits):
            mine = (my_index >> bit) & 1
            keep = lax.dynamic_index_in_dim(acc, mine, axis=bits - 1 - bit, keepdims=False)
            send = lax.dynamic_index_in_dim(acc, 1 - mine, axis=bits - 1 - bit, keepdims=False)
            partner = [(i, i ^ (1 << bit)) for i in range(n_seq)]
            got = lax.ppermute(send.astype(jnp.bfloat16), "seq", partner)
            acc = keep + got.astype(jnp.float32)
        return acc.astype(jnp.bfloat16)

    def by_rows(col_sum):
        return lax.psum_scatter(col_sum, "batch", scatter_dimension=0, tiled=True).astype(
            jnp.float32
        )

    qkv_grad = by_rows(by_cols(qkv_local))
    proj_grad = by_rows(by_cols(proj_local))
    up_grad = by_rows(by_cols(up_local))
    down_grad = by_rows(by_cols(down_local))
    small_sums = jnp.concatenate([gain1_local, bias1_local, gain2_local, bias2_local, dwa_local])
    for axis in ("seq", "batch"):
        size = lax.axis_size(axis)
        hop = 1
        while hop < size:
            partner = [(i, i ^ hop) for i in range(size)]
            small_sums = small_sums + lax.ppermute(small_sums, axis, partner)
            hop *= 2
    gain1_grad, bias1_grad, gain2_grad, bias2_grad = (
        small_sums[k * D : (k + 1) * D] for k in range(4)
    )
    dwa_grad = small_sums[4 * D :]
    row_lse = jnp.take(lse_all, held_pairs, axis=0).reshape(1, per_dev, SLOT)
    return (
        block_output,
        input_grad,
        history_grad,
        row_lse,
        qkv_grad,
        proj_grad,
        up_grad,
        down_grad,
        gain1_grad,
        bias1_grad,
        gain2_grad,
        bias2_grad,
        dwa_grad,
    )


def solution(mesh):
    placed = (
        P(("batch", "seq"), None),
        P(None, ("batch", "seq"), None),
        P(("batch", "seq"), None),
        P("batch", "seq"),
        P("batch", "seq"),
        P("batch", "seq"),
        P("batch", "seq"),
        P(),
        P(),
        P(),
        P(),
        P(),
        P("batch", None),
        P("batch", None),
    )

    return jax.shard_map(
        local,
        mesh=mesh,
        in_specs=placed,
        out_specs=(
            P(("batch", "seq"), None),
            P(("batch", "seq"), None),
            P(None, ("batch", "seq"), None),
            P("batch", "seq", None),
            P("batch", "seq"),
            P("batch", "seq"),
            P("batch", "seq"),
            P("batch", "seq"),
            P(),
            P(),
            P(),
            P(),
            P(),
        ),
        check_vma=False,
    )
```
